32 devices in a mesh: slab: 8 (over z, x), orient: 4 (over y, core).
Axes of the slice: x: 2, y: 2, z: 4, core: 2. Of those that a mesh axis runs over, the one named last changes fastest.
Arguments:
- tiles: bfloat16 [192, 1, 128, 128], P('slab'), may hold values from -8 to 8
- assigned_worker: int32 [192], P('slab'), may hold values from -1 to 7, as said below
- wedge_mask: int32 [128, 128], replicated, may hold values 0 or 1
- template_volume: float32 [64, 64, 64], replicated, may hold values from -6 to 6
- rotation_samples: int32 [64, 4096], P('orient', 'slab'), may hold values from 0 to 262143
Outputs:
- scores: bfloat16 [192, 128, 128], P('slab', 'orient')
The draws below stay inside these ranges and needn't reach their ends.
Inputs may be any that keep to these rules, and one draw needn't show every extreme that they name: `assigned_worker`: the occupied slots of each slab index come first. Slab indices 2m and 2m+1 hold 24 occupied slots together, and some slab index has all 24 occupied. The occupied slots, taken in slot order over all slab indices, are dealt to the workers in turn, so every worker receives exactly 12 tiles and at most 3 from one slab index.
All inputs are finite; a program needn't handle non-finite values.
Results may differ from the reference program's by a relative error of at most 0.0085.
Values may be sent and summed in bfloat16 or wider, within the bound.
No kernel may reach another device: no remote copies, remote signals or barrier semaphores. Data moves between devices by JAX's collectives and lax.ppermute only.
A program may use at most 128 MiB of HBM per device.

```python
import math
import jax
import jax.numpy as jnp
from jax import lax

TILE = 128
BOX = 64
PLANES = 1
HOME = 24
ORIENT = 64
TILES_ALL = 192


def draw_tiles(key, part):
    array_shape = (TILES_ALL, PLANES, TILE, TILE)
    base_key = jax.random.fold_in(key, 0)
    values = jax.random.normal(base_key, array_shape, jnp.float32)
    return jnp.clip(values, -8.0, 8.0).astype(jnp.bfloat16)


def draw_assigned_worker(key, part):
    slab_count = TILES_ALL // HOME
    half_home = HOME // 2
    pair_count = slab_count // 2
    spread_draw = jax.random.randint(jax.random.fold_in(key, 11), (pair_count,), 0, half_home + 1)
    spread_draw = spread_draw.at[0].set(half_home)
    counts = jnp.stack([half_home - spread_draw, half_home + spread_draw], axis=1).reshape(-1)
    starts = jnp.cumsum(counts) - counts
    slot_index = jnp.arange(HOME, dtype=jnp.int32)
    global_rank = starts[:, None] + slot_index[None, :]
    worker = jnp.where(slot_index[None, :] < counts[:, None], global_rank % slab_count, -1)
    return worker.reshape(-1).astype(jnp.int32)


def place_ends(entries, key, least, top_value):
    shape = entries.shape
    spot = [jax.random.randint(jax.random.fold_in(key, axis), (), 0, shape[axis]) for axis in range(len(shape))]
    entries = entries.at[tuple(spot)].set(least)
    longest = shape.index(max(shape))
    spot[longest] = (spot[longest] + 1) % shape[longest]
    return entries.at[tuple(spot)].set(top_value)


def scatter_about(own_key, shape, deviation, bound, held_as=jnp.bfloat16):
    entries = deviation * jax.random.normal(own_key, shape, jnp.float32)
    return jnp.clip(entries, min=-bound, max=bound).astype(held_as)


def setup_inputs(seed: int = 0) -> dict:
    arg_keys = jax.random.split(jax.random.key(seed), 6)
    return {
        "tiles": draw_tiles(jax.random.fold_in(arg_keys[5], 71), 0),
        "assigned_worker": draw_assigned_worker(jax.random.fold_in(arg_keys[5], 71), 0),
        "wedge_mask": place_ends((jax.random.randint(arg_keys[2], (TILE, TILE), 0, 4) < 3).astype(jnp.int32), jax.random.fold_in(arg_keys[2], 1), 0, 1),
        "template_volume": scatter_about(arg_keys[3], (BOX, BOX, BOX), 1.0, 6.0, jnp.float32),
        "rotation_samples": place_ends(jax.random.randint(arg_keys[4], (ORIENT, PLANES * BOX * BOX), 0, BOX * BOX * BOX), jax.random.fold_in(arg_keys[4], 1), 0, (BOX * BOX * BOX) - 1).astype(jnp.int32),
    }


def tables(length):
    counter = jnp.arange(length, dtype=jnp.int32)
    angles = (counter[:, None] * counter[None, :] % length).astype(jnp.float32) * (2.0 * math.pi / length)
    return (jnp.cos(angles).astype(jnp.bfloat16), jnp.sin(angles).astype(jnp.bfloat16))

def band_table(length, box_edge):
    counter = jnp.arange(length, dtype=jnp.int32)
    offsets = (counter[None, :] - counter[:, None]) % length
    return (offsets < box_edge).astype(jnp.float32)

def right_mul(values, table):
    return jnp.einsum('...ab,bc->...ac', values.astype(jnp.float32), table.astype(jnp.float32))

def left_mul(table, values):
    return jnp.einsum('ka,...ab->...kb', table.astype(jnp.float32), values.astype(jnp.float32))

def forward_two(values, cosine_table, sine_table):
    first_real = right_mul(values, cosine_table).astype(jnp.bfloat16)
    first_imag = (-right_mul(values, sine_table)).astype(jnp.bfloat16)
    second_real = (left_mul(cosine_table, first_real) + left_mul(sine_table, first_imag)).astype(jnp.bfloat16)
    second_imag = (left_mul(cosine_table, first_imag) - left_mul(sine_table, first_real)).astype(jnp.bfloat16)
    return (second_real, second_imag)

def inverse_real(real_part, imag_part, cosine_table, sine_table):
    length = real_part.shape[-1]
    first_real = (right_mul(real_part, cosine_table) - right_mul(imag_part, sine_table)).astype(jnp.bfloat16)
    first_imag = (right_mul(imag_part, cosine_table) + right_mul(real_part, sine_table)).astype(jnp.bfloat16)
    return (left_mul(cosine_table, first_real) - left_mul(sine_table, first_imag)) * (1.0 / (length * length))

def filtered(values, wedge_weight, cosine_table, sine_table):
    spec_real, spec_imag = forward_two(values, cosine_table, sine_table)
    return inverse_real(spec_real * wedge_weight, spec_imag * wedge_weight, cosine_table, sine_table).astype(jnp.bfloat16)

def make_templates(template_volume, rotation_samples, box_edge, planes, tile_len, cosine_table, sine_table):
    count = rotation_samples.shape[0]
    sampled = jnp.take(template_volume.reshape(-1), rotation_samples, axis=0)
    sampled = sampled.reshape(count, planes, box_edge, box_edge).astype(jnp.bfloat16)
    padded = jnp.zeros((count, planes, tile_len, tile_len), jnp.bfloat16).at[:, :, :box_edge, :box_edge].set(sampled)
    template_norm = jnp.sqrt(lax.optimization_barrier(jnp.sum(jnp.square(sampled.astype(jnp.float32)), axis=(1, 2, 3))) + 1e-05)
    spec_real, spec_imag = forward_two(padded, cosine_table, sine_table)
    return (spec_real, spec_imag, template_norm)

def score_tiles(slab_field, templ_real, templ_imag, template_norm, cosine_table, sine_table, band_sum, box_edge):
    planes = slab_field.shape[1]
    field_real, field_imag = forward_two(slab_field, cosine_table, sine_table)
    left_real = field_real.astype(jnp.float32)[:, None]
    left_imag = field_imag.astype(jnp.float32)[:, None]
    right_real = templ_real.astype(jnp.float32)[None]
    right_imag = templ_imag.astype(jnp.float32)[None]
    prod_real = lax.optimization_barrier(jnp.sum(left_real * right_real + left_imag * right_imag, axis=2)).astype(jnp.bfloat16)
    prod_imag = lax.optimization_barrier(jnp.sum(left_imag * right_real - left_real * right_imag, axis=2)).astype(jnp.bfloat16)
    correlation = inverse_real(prod_real, prod_imag, cosine_table, sine_table)
    energy = lax.optimization_barrier(jnp.sum(jnp.square(slab_field.astype(jnp.float32)), axis=1))
    summed = jnp.einsum('ka,nab,lb->nkl', band_sum, energy, band_sum, precision=lax.Precision.HIGHEST)
    local_rms = jnp.sqrt(summed / (box_edge * box_edge * planes) + 1e-05)
    ratio = correlation / (local_rms[:, None] * template_norm[None, :, None, None])
    return lax.optimization_barrier(jnp.max(ratio, axis=1))

def reference(tiles, assigned_worker, wedge_mask, template_volume, rotation_samples):
    tile_len = tiles.shape[-1]
    planes = tiles.shape[1]
    box_edge = template_volume.shape[0]
    cosine_table, sine_table = tables(tile_len)
    band_sum = band_table(tile_len, box_edge)
    wedge_weight = wedge_mask.astype(jnp.bfloat16)
    templ_real, templ_imag, template_norm = make_templates(template_volume, rotation_samples, box_edge, planes, tile_len, cosine_table, sine_table)

    def score_one(values):
        slab_field = filtered(values, wedge_weight, cosine_table, sine_table)[None]
        best = score_tiles(slab_field, templ_real, templ_imag, template_norm, cosine_table, sine_table, band_sum, box_edge)
        return best[0].astype(jnp.bfloat16)
    results = lax.map(score_one, tiles)
    occupied = (assigned_worker >= 0)[:, None, None]
    return jnp.where(occupied, results, jnp.zeros_like(results))
```

```python
import math

import jax
import jax.numpy as jnp
from jax import lax
from jax.experimental import pallas as pl
from jax.experimental.pallas import tpu as pltpu
from jax.sharding import PartitionSpec as P


def partner(block, axis, bit):
    count = lax.axis_size(axis)
    route = []
    for low in range(count):
        high = low | 1 << bit
        if high != low and high < count:
            route += [(low, high), (high, low)]
    return lax.ppermute(block, axis, route)


def tables(length):
    counter = jnp.arange(length, dtype=jnp.int32)
    angles = (counter[:, None] * counter[None, :] % length).astype(jnp.float32) * (
        2.0 * math.pi / length
    )
    return (jnp.cos(angles).astype(jnp.bfloat16), jnp.sin(angles).astype(jnp.bfloat16))


def band_table(length, box_edge):
    counter = jnp.arange(length, dtype=jnp.int32)
    offsets = (counter[None, :] - counter[:, None]) % length
    return (offsets < box_edge).astype(jnp.float32)


def right_mul(values, table):
    return jnp.einsum("...ab,bc->...ac", values, table, preferred_element_type=jnp.float32)


def left_mul(table, values):
    return jnp.einsum("ka,...ab->...kb", table, values, preferred_element_type=jnp.float32)


def forward_two(values, cosine_table, sine_table):
    first_real = right_mul(values, cosine_table).astype(jnp.bfloat16)
    first_imag = (-right_mul(values, sine_table)).astype(jnp.bfloat16)
    second_real = (left_mul(cosine_table, first_real) + left_mul(sine_table, first_imag)).astype(
        jnp.bfloat16
    )
    second_imag = (left_mul(cosine_table, first_imag) - left_mul(sine_table, first_real)).astype(
        jnp.bfloat16
    )
    return (second_real, second_imag)


def inverse_real(real_part, imag_part, cosine_table, sine_table):
    length = real_part.shape[-1]
    first_real = (right_mul(real_part, cosine_table) - right_mul(imag_part, sine_table)).astype(
        jnp.bfloat16
    )
    first_imag = (right_mul(imag_part, cosine_table) + right_mul(real_part, sine_table)).astype(
        jnp.bfloat16
    )
    return (left_mul(cosine_table, first_real) - left_mul(sine_table, first_imag)) * (
        1.0 / (length * length)
    )


def filtered(values, wedge_weight, cosine_table, sine_table):
    spec_real, spec_imag = forward_two(values, cosine_table, sine_table)
    return inverse_real(
        spec_real * wedge_weight, spec_imag * wedge_weight, cosine_table, sine_table
    ).astype(jnp.bfloat16)


def pick_rows(chosen, source):
    counter = jnp.arange(source.shape[0], dtype=jnp.int32)
    selector = (chosen[:, None] == counter[None, :]).astype(source.dtype)
    flat = source.reshape(source.shape[0], -1)
    picked = jnp.dot(selector, flat, preferred_element_type=jnp.float32).astype(source.dtype)
    return picked.reshape((chosen.shape[0],) + source.shape[1:])


def pick_kernel(index_ref, table_ref, out_ref):
    columns = table_ref.shape[0]
    rows_in_table = table_ref.shape[1]
    lanes = index_ref.shape[1]
    shift = columns.bit_length() - 1

    def body(step, carry):
        index = index_ref[pl.ds(step, 1), :]
        high = jnp.right_shift(index, shift)
        low = jnp.bitwise_and(index, columns - 1)
        row_hot = (lax.broadcasted_iota(jnp.int32, (rows_in_table, lanes), 0) == high).astype(
            jnp.bfloat16
        )
        picked_rows = jnp.dot(table_ref[...], row_hot, preferred_element_type=jnp.float32)
        column_hot = lax.broadcasted_iota(jnp.int32, (columns, lanes), 0) == low
        chosen = jnp.where(column_hot, picked_rows, 0.0)
        out_ref[pl.ds(step, 1), :] = jnp.sum(chosen, axis=0, keepdims=True)
        return carry

    lax.fori_loop(0, index_ref.shape[0], body, 0)


def sample_template(template_volume, rotation_samples):
    total = template_volume.size
    columns = 512
    table_t = template_volume.reshape(total // columns, columns).T.astype(jnp.bfloat16)
    count = rotation_samples.size
    lanes = 256 if count % 256 == 0 else 128
    index = rotation_samples.reshape(count // lanes, lanes)
    picked = pl.pallas_call(
        pick_kernel,
        out_shape=jax.ShapeDtypeStruct(index.shape, jnp.float32),
        in_specs=[pl.BlockSpec(memory_space=pltpu.VMEM)] * 2,
        out_specs=pl.BlockSpec(memory_space=pltpu.VMEM),
    )(index, table_t)
    return picked.reshape(rotation_samples.shape).astype(jnp.bfloat16)


def make_templates(
    template_volume, rotation_samples, box_edge, planes, tile_len, cosine_table, sine_table
):
    count = rotation_samples.shape[0]
    sampled_part = sample_template(template_volume, rotation_samples)
    sampled = lax.all_gather(sampled_part[None], "slab", axis=0, tiled=True)
    sampled = jnp.transpose(sampled, (1, 0, 2))
    sampled = sampled.reshape(count, planes, box_edge, box_edge)
    padded = jnp.pad(sampled, ((0, 0), (0, 0), (0, tile_len - box_edge), (0, tile_len - box_edge)))
    template_norm = jnp.sqrt(
        jnp.sum(jnp.square(sampled.astype(jnp.float32)), axis=(1, 2, 3)) + 1e-05
    )
    spec_real, spec_imag = forward_two(padded, cosine_table, sine_table)
    return (spec_real, spec_imag, template_norm)


def score_tiles(
    slab_field, templ_real, templ_imag, template_norm, cosine_table, sine_table, band_sum, box_edge
):
    planes = slab_field.shape[1]
    field_real, field_imag = forward_two(slab_field, cosine_table, sine_table)
    left_real = field_real.astype(jnp.float32)[:, None]
    left_imag = field_imag.astype(jnp.float32)[:, None]
    right_real = templ_real.astype(jnp.float32)[None]
    right_imag = templ_imag.astype(jnp.float32)[None]
    prod_real = jnp.sum(left_real * right_real + left_imag * right_imag, axis=2).astype(
        jnp.bfloat16
    )
    prod_imag = jnp.sum(left_imag * right_real - left_real * right_imag, axis=2).astype(
        jnp.bfloat16
    )
    correlation = inverse_real(prod_real, prod_imag, cosine_table, sine_table)
    energy = jnp.sum(jnp.square(slab_field.astype(jnp.float32)), axis=1)
    summed = jnp.einsum(
        "ka,nab,lb->nkl", band_sum, energy, band_sum, precision=lax.Precision.HIGHEST
    )
    local_rms = jnp.sqrt(summed / (box_edge * box_edge * planes) + 1e-05)
    ratio = correlation / (local_rms[:, None] * template_norm[None, :, None, None])
    return jnp.max(ratio, axis=1)


def orient_max(best):
    groups = lax.axis_size("orient")
    parts = lax.all_to_all(best, "orient", split_axis=1, concat_axis=0, tiled=True)
    stacked = parts.reshape(groups, best.shape[0], parts.shape[1], parts.shape[2])
    return jnp.max(stacked, axis=0)


def per_device(tiles, assigned_worker, wedge_mask, template_volume, rotation_samples):
    tile_len = tiles.shape[-1]
    planes = tiles.shape[1]
    home_slots = tiles.shape[0]
    work_slots = home_slots // 2
    box_edge = template_volume.shape[0]
    cosine_table, sine_table = tables(tile_len)
    band_sum = band_table(tile_len, box_edge)
    wedge_weight = wedge_mask.astype(jnp.bfloat16)
    templ_real, templ_imag, template_norm = make_templates(
        template_volume, rotation_samples, box_edge, planes, tile_len, cosine_table, sine_table
    )
    occupied = assigned_worker >= 0
    own_count = jnp.sum(occupied.astype(jnp.int32))
    partner_tiles = partner(tiles[work_slots:], "slab", 0)
    counter = jnp.arange(work_slots, dtype=jnp.int32)
    keep_own = (counter < own_count)[:, None, None, None]
    moved_in = pick_rows(counter - own_count, partner_tiles)
    gathered = jnp.where(keep_own, tiles[:work_slots], moved_in)
    slab_field = filtered(gathered, wedge_weight, cosine_table, sine_table)
    best = score_tiles(
        slab_field,
        templ_real,
        templ_imag,
        template_norm,
        cosine_table,
        sine_table,
        band_sum,
        box_edge,
    )
    best_rows = orient_max(best.astype(jnp.bfloat16))
    outgoing = pick_rows(counter + own_count, best_rows)
    returned = partner(outgoing, "slab", 0)
    result = jnp.concatenate([best_rows, returned], axis=0)
    return jnp.where(occupied[:, None, None], result, jnp.zeros_like(result))


def solution(mesh):
    return jax.shard_map(
        per_device,
        mesh=mesh,
        in_specs=(P("slab", None, None, None), P("slab"), P(), P(), P("orient", "slab")),
        out_specs=P("slab", "orient", None),
        check_vma=False,
    )
```

```python
import math

import jax
import jax.numpy as jnp
from jax import lax
from jax.experimental import pallas as pl
from jax.experimental.pallas import tpu as pltpu
from jax.sharding import PartitionSpec as P


def partner(block, axis, bit):
    count = lax.axis_size(axis)
    route = []
    for low in range(count):
        high = low | 1 << bit
        if high != low and high < count:
            route += [(low, high), (high, low)]
    return lax.ppermute(block, axis, route)


def tables(length):
    counter = jnp.arange(length, dtype=jnp.int32)
    angles = (counter[:, None] * counter[None, :] % length).astype(jnp.float32) * (
        2.0 * math.pi / length
    )
    return (jnp.cos(angles).astype(jnp.bfloat16), jnp.sin(angles).astype(jnp.bfloat16))


def band_table(length, box_edge):
    counter = jnp.arange(length, dtype=jnp.int32)
    offsets = (counter[None, :] - counter[:, None]) % length
    return (offsets < box_edge).astype(jnp.float32)


def right_mul(values, table):
    return jnp.einsum("...ab,bc->...ac", values, table, preferred_element_type=jnp.float32)


def left_mul(table, values):
    return jnp.einsum("ka,...ab->...kb", table, values, preferred_element_type=jnp.float32)


def forward_two(values, cosine_table, sine_table):
    first_real = right_mul(values, cosine_table).astype(jnp.bfloat16)
    first_imag = (-right_mul(values, sine_table)).astype(jnp.bfloat16)
    second_real = (left_mul(cosine_table, first_real) + left_mul(sine_table, first_imag)).astype(
        jnp.bfloat16
    )
    second_imag = (left_mul(cosine_table, first_imag) - left_mul(sine_table, first_real)).astype(
        jnp.bfloat16
    )
    return (second_real, second_imag)


def inverse_real(real_part, imag_part, cosine_table, sine_table):
    length = real_part.shape[-1]
    first_real = (right_mul(real_part, cosine_table) - right_mul(imag_part, sine_table)).astype(
        jnp.bfloat16
    )
    first_imag = (right_mul(imag_part, cosine_table) + right_mul(real_part, sine_table)).astype(
        jnp.bfloat16
    )
    return (left_mul(cosine_table, first_real) - left_mul(sine_table, first_imag)) * (
        1.0 / (length * length)
    )


def filtered(values, wedge_weight, cosine_table, sine_table):
    spec_real, spec_imag = forward_two(values, cosine_table, sine_table)
    return inverse_real(
        spec_real * wedge_weight, spec_imag * wedge_weight, cosine_table, sine_table
    ).astype(jnp.bfloat16)


def pick_rows(chosen, source):
    counter = jnp.arange(source.shape[0], dtype=jnp.int32)
    selector = (chosen[:, None] == counter[None, :]).astype(source.dtype)
    flat = source.reshape(source.shape[0], -1)
    picked = jnp.dot(selector, flat, preferred_element_type=jnp.float32).astype(source.dtype)
    return picked.reshape((chosen.shape[0],) + source.shape[1:])


def pick_kernel(index_ref, table_ref, out_ref):
    columns = table_ref.shape[0]
    rows_in_table = table_ref.shape[1]
    lanes = index_ref.shape[1]
    shift = columns.bit_length() - 1

    def body(step, carry):
        index = index_ref[pl.ds(step, 1), :]
        high = jnp.right_shift(index, shift)
        low = jnp.bitwise_and(index, columns - 1)
        row_hot = (lax.broadcasted_iota(jnp.int32, (rows_in_table, lanes), 0) == high).astype(
            jnp.bfloat16
        )
        picked_rows = jnp.dot(table_ref[...], row_hot, preferred_element_type=jnp.float32)
        column_hot = lax.broadcasted_iota(jnp.int32, (columns, lanes), 0) == low
        chosen = jnp.where(column_hot, picked_rows, 0.0)
        out_ref[pl.ds(step, 1), :] = jnp.sum(chosen, axis=0, keepdims=True)
        return carry

    lax.fori_loop(0, index_ref.shape[0], body, 0)


def sample_template(template_volume, rotation_samples):
    total = template_volume.size
    columns = 512
    table_t = template_volume.reshape(total // columns, columns).T.astype(jnp.bfloat16)
    count = rotation_samples.size
    lanes = 256 if count % 256 == 0 else 128
    index = rotation_samples.reshape(count // lanes, lanes)
    picked = pl.pallas_call(
        pick_kernel,
        out_shape=jax.ShapeDtypeStruct(index.shape, jnp.float32),
        in_specs=[pl.BlockSpec(memory_space=pltpu.VMEM)] * 2,
        out_specs=pl.BlockSpec(memory_space=pltpu.VMEM),
    )(index, table_t)
    return picked.reshape(rotation_samples.shape).astype(jnp.bfloat16)


def share_samples(template_volume, rotation_samples):
    sampled_part = sample_template(template_volume, rotation_samples)
    slab_count = lax.axis_size("slab")
    slot = lax.axis_index("slab")
    holder = (jnp.arange(slab_count, dtype=jnp.int32) == slot)[:, None, None]
    spread = jnp.where(holder, sampled_part[None], jnp.zeros_like(sampled_part)[None])
    return lax.psum(spread, "slab")


def make_templates(sampled, box_edge, planes, tile_len, cosine_table, sine_table):
    count = sampled.shape[1]
    sampled = jnp.transpose(sampled, (1, 0, 2))
    sampled = sampled.reshape(count, planes, box_edge, box_edge)
    padded = jnp.pad(sampled, ((0, 0), (0, 0), (0, tile_len - box_edge), (0, tile_len - box_edge)))
    template_norm = jnp.sqrt(
        jnp.sum(jnp.square(sampled.astype(jnp.float32)), axis=(1, 2, 3)) + 1e-05
    )
    spec_real, spec_imag = forward_two(padded, cosine_table, sine_table)
    return (spec_real, spec_imag, template_norm)


def score_tiles(
    slab_field, templ_real, templ_imag, template_norm, cosine_table, sine_table, band_sum, box_edge
):
    planes = slab_field.shape[1]
    field_real, field_imag = forward_two(slab_field, cosine_table, sine_table)
    left_real = field_real.astype(jnp.float32)[:, None]
    left_imag = field_imag.astype(jnp.float32)[:, None]
    right_real = templ_real.astype(jnp.float32)[None]
    right_imag = templ_imag.astype(jnp.float32)[None]
    prod_real = jnp.sum(left_real * right_real + left_imag * right_imag, axis=2).astype(
        jnp.bfloat16
    )
    prod_imag = jnp.sum(left_imag * right_real - left_real * right_imag, axis=2).astype(
        jnp.bfloat16
    )
    correlation = inverse_real(prod_real, prod_imag, cosine_table, sine_table)
    energy = jnp.sum(jnp.square(slab_field.astype(jnp.float32)), axis=1)
    summed = jnp.einsum(
        "ka,nab,lb->nkl", band_sum, energy, band_sum, precision=lax.Precision.HIGHEST
    )
    local_rms = jnp.sqrt(summed / (box_edge * box_edge * planes) + 1e-05)
    ratio = correlation / (local_rms[:, None] * template_norm[None, :, None, None])
    return jnp.max(ratio, axis=1)


def orient_max(best):
    groups = lax.axis_size("orient")
    parts = lax.all_to_all(best, "orient", split_axis=1, concat_axis=0, tiled=True)
    stacked = parts.reshape(groups, best.shape[0], parts.shape[1], parts.shape[2])
    return jnp.max(stacked, axis=0)


def per_device(tiles, assigned_worker, wedge_mask, template_volume, rotation_samples):
    tile_len = tiles.shape[-1]
    planes = tiles.shape[1]
    home_slots = tiles.shape[0]
    work_slots = home_slots // 2
    box_edge = template_volume.shape[0]
    cosine_table, sine_table = tables(tile_len)
    band_sum = band_table(tile_len, box_edge)
    wedge_weight = wedge_mask.astype(jnp.bfloat16)
    sampled = share_samples(template_volume, rotation_samples)
    occupied = assigned_worker >= 0
    own_count = jnp.sum(occupied.astype(jnp.int32))
    partner_tiles = partner(tiles[work_slots:], "slab", 0)
    counter = jnp.arange(work_slots, dtype=jnp.int32)
    keep_own = (counter < own_count)[:, None, None, None]
    moved_in = pick_rows(counter - own_count, partner_tiles)
    gathered = jnp.where(keep_own, tiles[:work_slots], moved_in)
    slab_field = filtered(gathered, wedge_weight, cosine_table, sine_table)
    sampled, slab_field = lax.optimization_barrier((sampled, slab_field))
    templ_real, templ_imag, template_norm = make_templates(
        sampled, box_edge, planes, tile_len, cosine_table, sine_table
    )
    best = score_tiles(
        slab_field,
        templ_real,
        templ_imag,
        template_norm,
        cosine_table,
        sine_table,
        band_sum,
        box_edge,
    )
    best_rows = orient_max(best.astype(jnp.bfloat16))
    outgoing = pick_rows(counter + own_count, best_rows)
    returned = partner(outgoing, "slab", 0)
    result = jnp.concatenate([best_rows, returned], axis=0)
    return jnp.where(occupied[:, None, None], result, jnp.zeros_like(result))


def solution(mesh):
    return jax.shard_map(
        per_device,
        mesh=mesh,
        in_specs=(P("slab", None, None, None), P("slab"), P(), P(), P("orient", "slab")),
        out_specs=P("slab", "orient", None),
        check_vma=False,
    )
```

```python
import math

import jax
import jax.numpy as jnp
from jax import lax
from jax.experimental import pallas as pl
from jax.experimental.pallas import tpu as pltpu
from jax.sharding import PartitionSpec as P


def partner(block, axis, bit):
    count = lax.axis_size(axis)
    route = []
    for low in range(count):
        high = low | 1 << bit
        if high != low and high < count:
            route += [(low, high), (high, low)]
    return lax.ppermute(block, axis, route)


def tables(length):
    counter = jnp.arange(length, dtype=jnp.int32)
    angles = (counter[:, None] * counter[None, :] % length).astype(jnp.float32) * (
        2.0 * math.pi / length
    )
    return (jnp.cos(angles).astype(jnp.bfloat16), jnp.sin(angles).astype(jnp.bfloat16))


def band_table(length, box_edge):
    counter = jnp.arange(length, dtype=jnp.int32)
    offsets = (counter[None, :] - counter[:, None]) % length
    return (offsets < box_edge).astype(jnp.float32)


def right_mul(values, table):
    return jnp.einsum("...ab,bc->...ac", values, table, preferred_element_type=jnp.float32)


def left_mul(table, values):
    return jnp.einsum("ka,...ab->...kb", table, values, preferred_element_type=jnp.float32)


def forward_two(values, cosine_table, sine_table):
    first_real = right_mul(values, cosine_table).astype(jnp.bfloat16)
    first_imag = (-right_mul(values, sine_table)).astype(jnp.bfloat16)
    second_real = (left_mul(cosine_table, first_real) + left_mul(sine_table, first_imag)).astype(
        jnp.bfloat16
    )
    second_imag = (left_mul(cosine_table, first_imag) - left_mul(sine_table, first_real)).astype(
        jnp.bfloat16
    )
    return (second_real, second_imag)


def inverse_real(real_part, imag_part, cosine_table, sine_table):
    length = real_part.shape[-1]
    first_real = (right_mul(real_part, cosine_table) - right_mul(imag_part, sine_table)).astype(
        jnp.bfloat16
    )
    first_imag = (right_mul(imag_part, cosine_table) + right_mul(real_part, sine_table)).astype(
        jnp.bfloat16
    )
    return (left_mul(cosine_table, first_real) - left_mul(sine_table, first_imag)) * (
        1.0 / (length * length)
    )


def filtered(values, wedge_weight, cosine_table, sine_table):
    spec_real, spec_imag = forward_two(values, cosine_table, sine_table)
    return inverse_real(
        spec_real * wedge_weight, spec_imag * wedge_weight, cosine_table, sine_table
    ).astype(jnp.bfloat16)


def pick_rows(chosen, source):
    counter = jnp.arange(source.shape[0], dtype=jnp.int32)
    selector = (chosen[:, None] == counter[None, :]).astype(source.dtype)
    flat = source.reshape(source.shape[0], -1)
    picked = jnp.dot(selector, flat, preferred_element_type=jnp.float32).astype(source.dtype)
    return picked.reshape((chosen.shape[0],) + source.shape[1:])


def pick_kernel(index_ref, table_ref, out_ref):
    columns = table_ref.shape[0]
    rows_in_table = table_ref.shape[1]
    lanes = index_ref.shape[1]
    shift = columns.bit_length() - 1

    def body(step, carry):
        index = index_ref[pl.ds(step, 1), :]
        high = jnp.right_shift(index, shift)
        low = jnp.bitwise_and(index, columns - 1)
        row_hot = (lax.broadcasted_iota(jnp.int32, (rows_in_table, lanes), 0) == high).astype(
            jnp.bfloat16
        )
        picked_rows = jnp.dot(table_ref[...], row_hot, preferred_element_type=jnp.float32)
        column_hot = lax.broadcasted_iota(jnp.int32, (columns, lanes), 0) == low
        chosen = jnp.where(column_hot, picked_rows, 0.0)
        out_ref[pl.ds(step, 1), :] = jnp.sum(chosen, axis=0, keepdims=True)
        return carry

    lax.fori_loop(0, index_ref.shape[0], body, 0)


def sample_template(template_volume, rotation_samples):
    total = template_volume.size
    columns = 512
    table_t = template_volume.reshape(total // columns, columns).T.astype(jnp.bfloat16)
    count = rotation_samples.size
    lanes = 256 if count % 256 == 0 else 128
    index = rotation_samples.reshape(count // lanes, lanes)
    picked = pl.pallas_call(
        pick_kernel,
        out_shape=jax.ShapeDtypeStruct(index.shape, jnp.float32),
        in_specs=[pl.BlockSpec(memory_space=pltpu.VMEM)] * 2,
        out_specs=pl.BlockSpec(memory_space=pltpu.VMEM),
    )(index, table_t)
    return picked.reshape(rotation_samples.shape).astype(jnp.bfloat16)


def share_samples(template_volume, rotation_samples):
    sampled_part = sample_template(template_volume, rotation_samples)
    slab_count = lax.axis_size("slab")
    slot = lax.axis_index("slab")
    held = sampled_part[None]
    bit = 0
    while (1 << bit) < slab_count:
        held = jnp.concatenate([held, partner(held, "slab", bit)], axis=0)
        bit += 1
    order = jnp.bitwise_xor(jnp.arange(slab_count, dtype=jnp.int32), slot)
    return pick_rows(order, held)


def make_templates(sampled, box_edge, planes, tile_len, cosine_table, sine_table):
    count = sampled.shape[1]
    sampled = jnp.transpose(sampled, (1, 0, 2))
    sampled = sampled.reshape(count, planes, box_edge, box_edge)
    padded = jnp.pad(sampled, ((0, 0), (0, 0), (0, tile_len - box_edge), (0, tile_len - box_edge)))
    template_norm = jnp.sqrt(
        jnp.sum(jnp.square(sampled.astype(jnp.float32)), axis=(1, 2, 3)) + 1e-05
    )
    spec_real, spec_imag = forward_two(padded, cosine_table, sine_table)
    return (spec_real, spec_imag, template_norm)


def score_tiles(
    slab_field, templ_real, templ_imag, template_norm, cosine_table, sine_table, band_sum, box_edge
):
    planes = slab_field.shape[1]
    field_real, field_imag = forward_two(slab_field, cosine_table, sine_table)
    left_real = field_real.astype(jnp.float32)[:, None]
    left_imag = field_imag.astype(jnp.float32)[:, None]
    right_real = templ_real.astype(jnp.float32)[None]
    right_imag = templ_imag.astype(jnp.float32)[None]
    prod_real = jnp.sum(left_real * right_real + left_imag * right_imag, axis=2).astype(
        jnp.bfloat16
    )
    prod_imag = jnp.sum(left_imag * right_real - left_real * right_imag, axis=2).astype(
        jnp.bfloat16
    )
    correlation = inverse_real(prod_real, prod_imag, cosine_table, sine_table)
    energy = jnp.sum(jnp.square(slab_field.astype(jnp.float32)), axis=1)
    summed = jnp.einsum(
        "ka,nab,lb->nkl", band_sum, energy, band_sum, precision=lax.Precision.HIGHEST
    )
    local_rms = jnp.sqrt(summed / (box_edge * box_edge * planes) + 1e-05)
    ratio = correlation / (local_rms[:, None] * template_norm[None, :, None, None])
    return jnp.max(ratio, axis=1)


def orient_max(best):
    groups = lax.axis_size("orient")
    parts = lax.all_to_all(best, "orient", split_axis=1, concat_axis=0, tiled=True)
    stacked = parts.reshape(groups, best.shape[0], parts.shape[1], parts.shape[2])
    return jnp.max(stacked, axis=0)


def per_device(tiles, assigned_worker, wedge_mask, template_volume, rotation_samples):
    tile_len = tiles.shape[-1]
    planes = tiles.shape[1]
    home_slots = tiles.shape[0]
    work_slots = home_slots // 2
    box_edge = template_volume.shape[0]
    cosine_table, sine_table = tables(tile_len)
    band_sum = band_table(tile_len, box_edge)
    wedge_weight = wedge_mask.astype(jnp.bfloat16)
    sampled = share_samples(template_volume, rotation_samples)
    occupied = assigned_worker >= 0
    own_count = jnp.sum(occupied.astype(jnp.int32))
    partner_tiles = partner(tiles[work_slots:], "slab", 0)
    counter = jnp.arange(work_slots, dtype=jnp.int32)
    keep_own = (counter < own_count)[:, None, None, None]
    moved_in = pick_rows(counter - own_count, partner_tiles)
    gathered = jnp.where(keep_own, tiles[:work_slots], moved_in)
    slab_field = filtered(gathered, wedge_weight, cosine_table, sine_table)
    sampled, slab_field = lax.optimization_barrier((sampled, slab_field))
    templ_real, templ_imag, template_norm = make_templates(
        sampled, box_edge, planes, tile_len, cosine_table, sine_table
    )
    best = score_tiles(
        slab_field,
        templ_real,
        templ_imag,
        template_norm,
        cosine_table,
        sine_table,
        band_sum,
        box_edge,
    )
    best_rows = orient_max(best.astype(jnp.bfloat16))
    outgoing = pick_rows(counter + own_count, best_rows)
    returned = partner(outgoing, "slab", 0)
    result = jnp.concatenate([best_rows, returned], axis=0)
    return jnp.where(occupied[:, None, None], result, jnp.zeros_like(result))


def solution(mesh):
    return jax.shard_map(
        per_device,
        mesh=mesh,
        in_specs=(P("slab", None, None, None), P("slab"), P(), P(), P("orient", "slab")),
        out_specs=P("slab", "orient", None),
        check_vma=False,
    )
```

```python
import math

import jax
import jax.numpy as jnp
from jax import lax
from jax.experimental import pallas as pl
from jax.experimental.pallas import tpu as pltpu
from jax.sharding import PartitionSpec as P


def partner(block, axis, bit):
    count = lax.axis_size(axis)
    route = []
    for low in range(count):
        high = low | 1 << bit
        if high != low and high < count:
            route += [(low, high), (high, low)]
    return lax.ppermute(block, axis, route)


def tables(length):
    counter = jnp.arange(length, dtype=jnp.int32)
    angles = (counter[:, None] * counter[None, :] % length).astype(jnp.float32) * (
        2.0 * math.pi / length
    )
    return (jnp.cos(angles).astype(jnp.bfloat16), jnp.sin(angles).astype(jnp.bfloat16))


def band_table(length, box_edge):
    counter = jnp.arange(length, dtype=jnp.int32)
    offsets = (counter[None, :] - counter[:, None]) % length
    return (offsets < box_edge).astype(jnp.float32)


def right_mul(values, table):
    return jnp.einsum("...ab,bc->...ac", values, table, preferred_element_type=jnp.float32)


def left_mul(table, values):
    return jnp.einsum("ka,...ab->...kb", table, values, preferred_element_type=jnp.float32)


def forward_two(values, cosine_table, sine_table):
    first_real = right_mul(values, cosine_table).astype(jnp.bfloat16)
    first_imag = (-right_mul(values, sine_table)).astype(jnp.bfloat16)
    second_real = (left_mul(cosine_table, first_real) + left_mul(sine_table, first_imag)).astype(
        jnp.bfloat16
    )
    second_imag = (left_mul(cosine_table, first_imag) - left_mul(sine_table, first_real)).astype(
        jnp.bfloat16
    )
    return (second_real, second_imag)


def inverse_real(real_part, imag_part, cosine_table, sine_table):
    length = real_part.shape[-1]
    first_real = (right_mul(real_part, cosine_table) - right_mul(imag_part, sine_table)).astype(
        jnp.bfloat16
    )
    first_imag = (right_mul(imag_part, cosine_table) + right_mul(real_part, sine_table)).astype(
        jnp.bfloat16
    )
    return (left_mul(cosine_table, first_real) - left_mul(sine_table, first_imag)) * (
        1.0 / (length * length)
    )


def filtered(values, wedge_weight, cosine_table, sine_table):
    spec_real, spec_imag = forward_two(values, cosine_table, sine_table)
    return inverse_real(
        spec_real * wedge_weight, spec_imag * wedge_weight, cosine_table, sine_table
    ).astype(jnp.bfloat16)


def pick_rows(chosen, source):
    counter = jnp.arange(source.shape[0], dtype=jnp.int32)
    selector = (chosen[:, None] == counter[None, :]).astype(source.dtype)
    flat = source.reshape(source.shape[0], -1)
    picked = jnp.dot(selector, flat, preferred_element_type=jnp.float32).astype(source.dtype)
    return picked.reshape((chosen.shape[0],) + source.shape[1:])


def pick_kernel(index_ref, table_ref, out_ref):
    columns = table_ref.shape[0]
    rows_in_table = table_ref.shape[1]
    lanes = index_ref.shape[1]
    shift = columns.bit_length() - 1

    def body(step, carry):
        index = index_ref[pl.ds(step, 1), :]
        high = jnp.right_shift(index, shift)
        low = jnp.bitwise_and(index, columns - 1)
        row_hot = (lax.broadcasted_iota(jnp.int32, (rows_in_table, lanes), 0) == high).astype(
            jnp.bfloat16
        )
        picked_rows = jnp.dot(table_ref[...], row_hot, preferred_element_type=jnp.float32)
        column_hot = lax.broadcasted_iota(jnp.int32, (columns, lanes), 0) == low
        chosen = jnp.where(column_hot, picked_rows, 0.0)
        out_ref[pl.ds(step, 1), :] = jnp.sum(chosen, axis=0, keepdims=True)
        return carry

    lax.fori_loop(0, index_ref.shape[0], body, 0)


def sample_template(template_volume, rotation_samples):
    total = template_volume.size
    columns = 512
    table_t = template_volume.reshape(total // columns, columns).T.astype(jnp.bfloat16)
    count = rotation_samples.size
    lanes = 256 if count % 256 == 0 else 128
    index = rotation_samples.reshape(count // lanes, lanes)
    picked = pl.pallas_call(
        pick_kernel,
        out_shape=jax.ShapeDtypeStruct(index.shape, jnp.float32),
        in_specs=[pl.BlockSpec(memory_space=pltpu.VMEM)] * 2,
        out_specs=pl.BlockSpec(memory_space=pltpu.VMEM),
    )(index, table_t)
    return picked.reshape(rotation_samples.shape).astype(jnp.bfloat16)


def share_samples(template_volume, rotation_samples):
    sampled_part = sample_template(template_volume, rotation_samples)
    slab_count = lax.axis_size("slab")
    slot = lax.axis_index("slab")
    held = sampled_part[None]
    bit = 0
    while (1 << bit) < slab_count:
        held = jnp.concatenate([held, partner(held, "slab", bit)], axis=0)
        bit += 1
    order = jnp.bitwise_xor(jnp.arange(slab_count, dtype=jnp.int32), slot)
    return pick_rows(order, held)


def make_templates(sampled, box_edge, planes, tile_len, cosine_table, sine_table):
    count = sampled.shape[1]
    sampled = jnp.transpose(sampled, (1, 0, 2))
    sampled = sampled.reshape(count, planes, box_edge, box_edge)
    padded = jnp.pad(sampled, ((0, 0), (0, 0), (0, tile_len - box_edge), (0, tile_len - box_edge)))
    template_norm = jnp.sqrt(
        jnp.sum(jnp.square(sampled.astype(jnp.float32)), axis=(1, 2, 3)) + 1e-05
    )
    spec_real, spec_imag = forward_two(padded, cosine_table, sine_table)
    return (spec_real, spec_imag, template_norm)


def score_kernel(
    scale_ref, field_re_ref, field_im_ref, templ_re_ref, templ_im_ref, mix_ref, cos_ref, sin_ref,
    rms_ref, out_ref, best_ref
):
    planes = field_re_ref.shape[0]
    length = field_re_ref.shape[-1]
    best_ref[...] = jnp.full(best_ref.shape, -jnp.inf, jnp.float32)

    def body(orient, carry):
        prod_re = None
        prod_im = None
        for plane in range(planes):
            fr = field_re_ref[plane].astype(jnp.float32)
            fi = field_im_ref[plane].astype(jnp.float32)
            tr = templ_re_ref[orient, plane].astype(jnp.float32)
            ti = templ_im_ref[orient, plane].astype(jnp.float32)
            part_re = fr * tr + fi * ti
            part_im = fi * tr - fr * ti
            prod_re = part_re if prod_re is None else prod_re + part_re
            prod_im = part_im if prod_im is None else prod_im + part_im
        joined = jnp.concatenate(
            [prod_re.astype(jnp.bfloat16), prod_im.astype(jnp.bfloat16)], axis=1
        )
        first = jnp.dot(joined, mix_ref[...], preferred_element_type=jnp.float32).astype(
            jnp.bfloat16
        )
        corr = jnp.dot(cos_ref[...], first[:, :length], preferred_element_type=jnp.float32) - jnp.dot(
            sin_ref[...], first[:, length:], preferred_element_type=jnp.float32
        )
        best_ref[...] = jnp.maximum(best_ref[...], corr * scale_ref[orient])
        return carry

    lax.fori_loop(0, templ_re_ref.shape[0], body, 0, unroll=2)
    out_ref[...] = (best_ref[...] / rms_ref[...]).astype(out_ref.dtype)


def score_tiles(
    slab_field, templ_real, templ_imag, template_norm, cosine_table, sine_table, band_sum, box_edge
):
    planes = slab_field.shape[1]
    length = slab_field.shape[-1]
    field_real, field_imag = forward_two(slab_field, cosine_table, sine_table)
    energy = jnp.sum(jnp.square(slab_field.astype(jnp.float32)), axis=1)
    summed = jnp.einsum(
        "ka,nab,lb->nkl", band_sum, energy, band_sum, precision=lax.Precision.HIGHEST
    )
    local_rms = jnp.sqrt(summed / (box_edge * box_edge * planes) + 1e-05)
    scale = (1.0 / template_norm) * (1.0 / (length * length))
    mix = jnp.concatenate(
        [
            jnp.concatenate([cosine_table, sine_table], axis=1),
            jnp.concatenate([-sine_table, cosine_table], axis=1),
        ],
        axis=0,
    )
    tiles = slab_field.shape[0]
    count = templ_real.shape[0]
    tile_block = pl.BlockSpec((None, planes, length, length), lambda t: (t, 0, 0, 0))
    templ_block = pl.BlockSpec((count, planes, length, length), lambda t: (0, 0, 0, 0))
    return pl.pallas_call(
        score_kernel,
        grid=(tiles,),
        out_shape=jax.ShapeDtypeStruct((tiles, length, length), jnp.bfloat16),
        in_specs=[
            pl.BlockSpec(memory_space=pltpu.SMEM),
            tile_block,
            tile_block,
            templ_block,
            templ_block,
            pl.BlockSpec((2 * length, 2 * length), lambda t: (0, 0)),
            pl.BlockSpec((length, length), lambda t: (0, 0)),
            pl.BlockSpec((length, length), lambda t: (0, 0)),
            pl.BlockSpec((None, length, length), lambda t: (t, 0, 0)),
        ],
        out_specs=pl.BlockSpec((None, length, length), lambda t: (t, 0, 0)),
        scratch_shapes=[pltpu.VMEM((length, length), jnp.float32)],
    )(
        scale,
        field_real,
        field_imag,
        templ_real,
        templ_imag,
        mix,
        cosine_table,
        sine_table,
        local_rms,
    )


def orient_max(best):
    groups = lax.axis_size("orient")
    parts = lax.all_to_all(best, "orient", split_axis=1, concat_axis=0, tiled=True)
    stacked = parts.reshape(groups, best.shape[0], parts.shape[1], parts.shape[2])
    return jnp.max(stacked, axis=0)


def per_device(tiles, assigned_worker, wedge_mask, template_volume, rotation_samples):
    tile_len = tiles.shape[-1]
    planes = tiles.shape[1]
    home_slots = tiles.shape[0]
    work_slots = home_slots // 2
    box_edge = template_volume.shape[0]
    cosine_table, sine_table = tables(tile_len)
    band_sum = band_table(tile_len, box_edge)
    wedge_weight = wedge_mask.astype(jnp.bfloat16)
    sampled = share_samples(template_volume, rotation_samples)
    occupied = assigned_worker >= 0
    own_count = jnp.sum(occupied.astype(jnp.int32))
    partner_tiles = partner(tiles[work_slots:], "slab", 0)
    counter = jnp.arange(work_slots, dtype=jnp.int32)
    keep_own = (counter < own_count)[:, None, None, None]
    moved_in = pick_rows(counter - own_count, partner_tiles)
    gathered = jnp.where(keep_own, tiles[:work_slots], moved_in)
    slab_field = filtered(gathered, wedge_weight, cosine_table, sine_table)
    sampled, slab_field = lax.optimization_barrier((sampled, slab_field))
    templ_real, templ_imag, template_norm = make_templates(
        sampled, box_edge, planes, tile_len, cosine_table, sine_table
    )
    best = score_tiles(
        slab_field,
        templ_real,
        templ_imag,
        template_norm,
        cosine_table,
        sine_table,
        band_sum,
        box_edge,
    )
    best_rows = orient_max(best)
    outgoing = pick_rows(counter + own_count, best_rows)
    returned = partner(outgoing, "slab", 0)
    result = jnp.concatenate([best_rows, returned], axis=0)
    return jnp.where(occupied[:, None, None], result, jnp.zeros_like(result))


def solution(mesh):
    return jax.shard_map(
        per_device,
        mesh=mesh,
        in_specs=(P("slab", None, None, None), P("slab"), P(), P(), P("orient", "slab")),
        out_specs=P("slab", "orient", None),
        check_vma=False,
    )
```

```python
import math

import jax
import jax.numpy as jnp
from jax import lax
from jax.experimental import pallas as pl
from jax.experimental.pallas import tpu as pltpu
from jax.sharding import PartitionSpec as P


def partner(block, axis, bit):
    count = lax.axis_size(axis)
    route = []
    for low in range(count):
        high = low | 1 << bit
        if high != low and high < count:
            route += [(low, high), (high, low)]
    return lax.ppermute(block, axis, route)


def tables(length):
    counter = jnp.arange(length, dtype=jnp.int32)
    angles = (counter[:, None] * counter[None, :] % length).astype(jnp.float32) * (
        2.0 * math.pi / length
    )
    return (jnp.cos(angles).astype(jnp.bfloat16), jnp.sin(angles).astype(jnp.bfloat16))


def band_table(length, box_edge):
    counter = jnp.arange(length, dtype=jnp.int32)
    offsets = (counter[None, :] - counter[:, None]) % length
    return (offsets < box_edge).astype(jnp.float32)


def right_mul(values, table):
    return jnp.einsum("...ab,bc->...ac", values, table, preferred_element_type=jnp.float32)


def left_mul(table, values):
    return jnp.einsum("ka,...ab->...kb", table, values, preferred_element_type=jnp.float32)


def forward_two(values, cosine_table, sine_table):
    first_real = right_mul(values, cosine_table).astype(jnp.bfloat16)
    first_imag = (-right_mul(values, sine_table)).astype(jnp.bfloat16)
    second_real = (left_mul(cosine_table, first_real) + left_mul(sine_table, first_imag)).astype(
        jnp.bfloat16
    )
    second_imag = (left_mul(cosine_table, first_imag) - left_mul(sine_table, first_real)).astype(
        jnp.bfloat16
    )
    return (second_real, second_imag)


def inverse_real(real_part, imag_part, cosine_table, sine_table):
    length = real_part.shape[-1]
    first_real = (right_mul(real_part, cosine_table) - right_mul(imag_part, sine_table)).astype(
        jnp.bfloat16
    )
    first_imag = (right_mul(imag_part, cosine_table) + right_mul(real_part, sine_table)).astype(
        jnp.bfloat16
    )
    return (left_mul(cosine_table, first_real) - left_mul(sine_table, first_imag)) * (
        1.0 / (length * length)
    )


def filtered(values, wedge_weight, cosine_table, sine_table):
    spec_real, spec_imag = forward_two(values, cosine_table, sine_table)
    return inverse_real(
        spec_real * wedge_weight, spec_imag * wedge_weight, cosine_table, sine_table
    ).astype(jnp.bfloat16)


def pick_rows(chosen, source):
    counter = jnp.arange(source.shape[0], dtype=jnp.int32)
    selector = (chosen[:, None] == counter[None, :]).astype(source.dtype)
    flat = source.reshape(source.shape[0], -1)
    picked = jnp.dot(selector, flat, preferred_element_type=jnp.float32).astype(source.dtype)
    return picked.reshape((chosen.shape[0],) + source.shape[1:])


def pick_kernel(index_ref, table_ref, out_ref):
    columns = table_ref.shape[0]
    rows_in_table = table_ref.shape[1]
    lanes = index_ref.shape[1]
    shift = columns.bit_length() - 1

    def body(step, carry):
        index = index_ref[pl.ds(step, 1), :]
        high = jnp.right_shift(index, shift)
        low = jnp.bitwise_and(index, columns - 1)
        row_hot = (lax.broadcasted_iota(jnp.int32, (rows_in_table, lanes), 0) == high).astype(
            jnp.bfloat16
        )
        picked_rows = jnp.dot(table_ref[...], row_hot, preferred_element_type=jnp.float32)
        column_hot = lax.broadcasted_iota(jnp.int32, (columns, lanes), 0) == low
        chosen = jnp.where(column_hot, picked_rows, 0.0)
        out_ref[pl.ds(step, 1), :] = jnp.sum(chosen, axis=0, keepdims=True)
        return carry

    lax.fori_loop(0, index_ref.shape[0], body, 0)


def sample_template(template_volume, rotation_samples):
    total = template_volume.size
    columns = 512
    table_t = template_volume.reshape(total // columns, columns).T.astype(jnp.bfloat16)
    count = rotation_samples.size
    lanes = 256 if count % 256 == 0 else 128
    index = rotation_samples.reshape(count // lanes, lanes)
    picked = pl.pallas_call(
        pick_kernel,
        out_shape=jax.ShapeDtypeStruct(index.shape, jnp.float32),
        in_specs=[pl.BlockSpec(memory_space=pltpu.VMEM)] * 2,
        out_specs=pl.BlockSpec(memory_space=pltpu.VMEM),
    )(index, table_t)
    return picked.reshape(rotation_samples.shape).astype(jnp.bfloat16)


def share_samples(template_volume, rotation_samples):
    sampled_part = sample_template(template_volume, rotation_samples)
    slab_count = lax.axis_size("slab")
    slot = lax.axis_index("slab")
    held = sampled_part[None]
    bit = 0
    while (1 << bit) < slab_count:
        held = jnp.concatenate([held, partner(held, "slab", bit)], axis=0)
        bit += 1
    order = jnp.bitwise_xor(jnp.arange(slab_count, dtype=jnp.int32), slot)
    return pick_rows(order, held)


def make_templates(sampled, box_edge, planes, tile_len, cosine_table, sine_table):
    count = sampled.shape[1]
    sampled = jnp.transpose(sampled, (1, 0, 2))
    sampled = sampled.reshape(count, planes, box_edge, box_edge)
    padded = jnp.pad(sampled, ((0, 0), (0, 0), (0, tile_len - box_edge), (0, tile_len - box_edge)))
    template_norm = jnp.sqrt(
        jnp.sum(jnp.square(sampled.astype(jnp.float32)), axis=(1, 2, 3)) + 1e-05
    )
    spec_real, spec_imag = forward_two(padded, cosine_table, sine_table)
    return (spec_real, spec_imag, template_norm)


def score_kernel(
    scale_ref, field_re_ref, field_im_ref, templ_re_ref, templ_im_ref, mix_ref, back_ref,
    rms_ref, out_ref, best_ref
):
    planes = field_re_ref.shape[0]
    length = field_re_ref.shape[-1]
    group = 4 if templ_re_ref.shape[0] % 4 == 0 else 1
    best_ref[...] = jnp.full(best_ref.shape, -jnp.inf, jnp.float32)

    def body(step, carry):
        joined = []
        for member in range(group):
            orient = step * group + member
            prod_re = None
            prod_im = None
            for plane in range(planes):
                fr = field_re_ref[plane]
                fi = field_im_ref[plane]
                tr = templ_re_ref[orient, plane]
                ti = templ_im_ref[orient, plane]
                part_re = fr * tr + fi * ti
                part_im = fi * tr - fr * ti
                prod_re = part_re if prod_re is None else prod_re + part_re
                prod_im = part_im if prod_im is None else prod_im + part_im
            joined.append(
                jnp.concatenate(
                    [prod_re.astype(jnp.bfloat16), prod_im.astype(jnp.bfloat16)], axis=1
                )
            )
        joined = jnp.concatenate(joined, axis=0)
        first = jnp.dot(joined, mix_ref[...], preferred_element_type=jnp.float32).astype(
            jnp.bfloat16
        )
        stacked = []
        for member in range(group):
            rows = first[member * length : (member + 1) * length]
            stacked.append(jnp.concatenate([rows[:, :length], rows[:, length:]], axis=0))
        stacked = jnp.concatenate(stacked, axis=1)
        corr = jnp.dot(back_ref[...], stacked, preferred_element_type=jnp.float32)
        best = best_ref[...]
        for member in range(group):
            orient = step * group + member
            best = jnp.maximum(
                best, corr[:, member * length : (member + 1) * length] * scale_ref[orient]
            )
        best_ref[...] = best
        return carry

    lax.fori_loop(0, templ_re_ref.shape[0] // group, body, 0)
    out_ref[...] = (best_ref[...] / rms_ref[...]).astype(out_ref.dtype)


def score_tiles(
    slab_field, templ_real, templ_imag, template_norm, cosine_table, sine_table, band_sum, box_edge
):
    planes = slab_field.shape[1]
    length = slab_field.shape[-1]
    field_real, field_imag = forward_two(slab_field, cosine_table, sine_table)
    energy = jnp.sum(jnp.square(slab_field.astype(jnp.float32)), axis=1)
    summed = jnp.einsum(
        "ka,nab,lb->nkl", band_sum, energy, band_sum, precision=lax.Precision.HIGHEST
    )
    local_rms = jnp.sqrt(summed / (box_edge * box_edge * planes) + 1e-05)
    scale = (1.0 / template_norm) * (1.0 / (length * length))
    mix = jnp.concatenate(
        [
            jnp.concatenate([cosine_table, sine_table], axis=1),
            jnp.concatenate([-sine_table, cosine_table], axis=1),
        ],
        axis=0,
    )
    back = jnp.concatenate([cosine_table, -sine_table], axis=1)
    tiles = slab_field.shape[0]
    count = templ_real.shape[0]
    tile_block = pl.BlockSpec((None, planes, length, length), lambda t: (t, 0, 0, 0))
    templ_block = pl.BlockSpec((count, planes, length, length), lambda t: (0, 0, 0, 0))
    return pl.pallas_call(
        score_kernel,
        grid=(tiles,),
        out_shape=jax.ShapeDtypeStruct((tiles, length, length), jnp.bfloat16),
        in_specs=[
            pl.BlockSpec(memory_space=pltpu.SMEM),
            tile_block,
            tile_block,
            templ_block,
            templ_block,
            pl.BlockSpec((2 * length, 2 * length), lambda t: (0, 0)),
            pl.BlockSpec((length, 2 * length), lambda t: (0, 0)),
            pl.BlockSpec((None, length, length), lambda t: (t, 0, 0)),
        ],
        out_specs=pl.BlockSpec((None, length, length), lambda t: (t, 0, 0)),
        scratch_shapes=[pltpu.VMEM((length, length), jnp.float32)],
    )(
        scale,
        field_real.astype(jnp.float32),
        field_imag.astype(jnp.float32),
        templ_real.astype(jnp.float32),
        templ_imag.astype(jnp.float32),
        mix,
        back,
        local_rms,
    )


def orient_max(best):
    groups = lax.axis_size("orient")
    parts = lax.all_to_all(best, "orient", split_axis=1, concat_axis=0, tiled=True)
    stacked = parts.reshape(groups, best.shape[0], parts.shape[1], parts.shape[2])
    return jnp.max(stacked, axis=0)


def per_device(tiles, assigned_worker, wedge_mask, template_volume, rotation_samples):
    tile_len = tiles.shape[-1]
    planes = tiles.shape[1]
    home_slots = tiles.shape[0]
    work_slots = home_slots // 2
    box_edge = template_volume.shape[0]
    cosine_table, sine_table = tables(tile_len)
    band_sum = band_table(tile_len, box_edge)
    wedge_weight = wedge_mask.astype(jnp.bfloat16)
    sampled = share_samples(template_volume, rotation_samples)
    occupied = assigned_worker >= 0
    own_count = jnp.sum(occupied.astype(jnp.int32))
    partner_tiles = partner(tiles[work_slots:], "slab", 0)
    counter = jnp.arange(work_slots, dtype=jnp.int32)
    keep_own = (counter < own_count)[:, None, None, None]
    moved_in = pick_rows(counter - own_count, partner_tiles)
    gathered = jnp.where(keep_own, tiles[:work_slots], moved_in)
    slab_field = filtered(gathered, wedge_weight, cosine_table, sine_table)
    sampled, slab_field = lax.optimization_barrier((sampled, slab_field))
    templ_real, templ_imag, template_norm = make_templates(
        sampled, box_edge, planes, tile_len, cosine_table, sine_table
    )
    best = score_tiles(
        slab_field,
        templ_real,
        templ_imag,
        template_norm,
        cosine_table,
        sine_table,
        band_sum,
        box_edge,
    )
    best_rows = orient_max(best)
    outgoing = pick_rows(counter + own_count, best_rows)
    returned = partner(outgoing, "slab", 0)
    result = jnp.concatenate([best_rows, returned], axis=0)
    return jnp.where(occupied[:, None, None], result, jnp.zeros_like(result))


def solution(mesh):
    return jax.shard_map(
        per_device,
        mesh=mesh,
        in_specs=(P("slab", None, None, None), P("slab"), P(), P(), P("orient", "slab")),
        out_specs=P("slab", "orient", None),
        check_vma=False,
    )
```

```python
import math

import jax
import jax.numpy as jnp
from jax import lax
from jax.experimental import pallas as pl
from jax.experimental.pallas import tpu as pltpu
from jax.sharding import PartitionSpec as P


def partner(block, axis, bit):
    count = lax.axis_size(axis)
    route = []
    for low in range(count):
        high = low | 1 << bit
        if high != low and high < count:
            route += [(low, high), (high, low)]
    return lax.ppermute(block, axis, route)


def tables(length):
    counter = jnp.arange(length, dtype=jnp.int32)
    angles = (counter[:, None] * counter[None, :] % length).astype(jnp.float32) * (
        2.0 * math.pi / length
    )
    return (jnp.cos(angles).astype(jnp.bfloat16), jnp.sin(angles).astype(jnp.bfloat16))


def band_table(length, box_edge):
    counter = jnp.arange(length, dtype=jnp.int32)
    offsets = (counter[None, :] - counter[:, None]) % length
    return (offsets < box_edge).astype(jnp.float32)


def right_mul(values, table):
    return jnp.einsum("...ab,bc->...ac", values, table, preferred_element_type=jnp.float32)


def left_mul(table, values):
    return jnp.einsum("ka,...ab->...kb", table, values, preferred_element_type=jnp.float32)


def forward_two(values, cosine_table, sine_table):
    first_real = right_mul(values, cosine_table).astype(jnp.bfloat16)
    first_imag = (-right_mul(values, sine_table)).astype(jnp.bfloat16)
    second_real = (left_mul(cosine_table, first_real) + left_mul(sine_table, first_imag)).astype(
        jnp.bfloat16
    )
    second_imag = (left_mul(cosine_table, first_imag) - left_mul(sine_table, first_real)).astype(
        jnp.bfloat16
    )
    return (second_real, second_imag)


def inverse_real(real_part, imag_part, cosine_table, sine_table):
    length = real_part.shape[-1]
    first_real = (right_mul(real_part, cosine_table) - right_mul(imag_part, sine_table)).astype(
        jnp.bfloat16
    )
    first_imag = (right_mul(imag_part, cosine_table) + right_mul(real_part, sine_table)).astype(
        jnp.bfloat16
    )
    return (left_mul(cosine_table, first_real) - left_mul(sine_table, first_imag)) * (
        1.0 / (length * length)
    )


def filtered(values, wedge_weight, cosine_table, sine_table):
    spec_real, spec_imag = forward_two(values, cosine_table, sine_table)
    return inverse_real(
        spec_real * wedge_weight, spec_imag * wedge_weight, cosine_table, sine_table
    ).astype(jnp.bfloat16)


def pick_rows(chosen, source):
    counter = jnp.arange(source.shape[0], dtype=jnp.int32)
    selector = (chosen[:, None] == counter[None, :]).astype(source.dtype)
    flat = source.reshape(source.shape[0], -1)
    picked = jnp.dot(selector, flat, preferred_element_type=jnp.float32).astype(source.dtype)
    return picked.reshape((chosen.shape[0],) + source.shape[1:])


def pick_kernel(index_ref, table_ref, out_ref):
    columns = table_ref.shape[0]
    rows_in_table = table_ref.shape[1]
    lanes = index_ref.shape[1]
    shift = columns.bit_length() - 1

    def body(step, carry):
        index = index_ref[pl.ds(step, 1), :]
        high = jnp.right_shift(index, shift)
        low = jnp.bitwise_and(index, columns - 1)
        row_hot = (lax.broadcasted_iota(jnp.int32, (rows_in_table, lanes), 0) == high).astype(
            jnp.bfloat16
        )
        picked_rows = jnp.dot(table_ref[...], row_hot, preferred_element_type=jnp.float32)
        column_hot = lax.broadcasted_iota(jnp.int32, (columns, lanes), 0) == low
        chosen = jnp.where(column_hot, picked_rows, 0.0)
        out_ref[pl.ds(step, 1), :] = jnp.sum(chosen, axis=0, keepdims=True)
        return carry

    lax.fori_loop(0, index_ref.shape[0], body, 0)


def sample_template(template_volume, rotation_samples):
    total = template_volume.size
    columns = 512
    table_t = template_volume.reshape(total // columns, columns).T.astype(jnp.bfloat16)
    count = rotation_samples.size
    lanes = 256 if count % 256 == 0 else 128
    index = rotation_samples.reshape(count // lanes, lanes)
    picked = pl.pallas_call(
        pick_kernel,
        out_shape=jax.ShapeDtypeStruct(index.shape, jnp.float32),
        in_specs=[pl.BlockSpec(memory_space=pltpu.VMEM)] * 2,
        out_specs=pl.BlockSpec(memory_space=pltpu.VMEM),
    )(index, table_t)
    return picked.reshape(rotation_samples.shape).astype(jnp.bfloat16)


def share_samples(template_volume, rotation_samples):
    sampled_part = sample_template(template_volume, rotation_samples)
    slab_count = lax.axis_size("slab")
    slot = lax.axis_index("slab")
    held = sampled_part[None]
    bit = 0
    while (1 << bit) < slab_count:
        held = jnp.concatenate([held, partner(held, "slab", bit)], axis=0)
        bit += 1
    order = jnp.bitwise_xor(jnp.arange(slab_count, dtype=jnp.int32), slot)
    return pick_rows(order, held)


def spectrum_planes(values_ref, across_ref, down_ref):
    width = across_ref.shape[1] // 2
    real_parts = []
    imag_parts = []
    for plane in range(values_ref.shape[0]):
        first = jnp.dot(values_ref[plane], across_ref[...], preferred_element_type=jnp.float32)
        first = first.astype(jnp.bfloat16)
        stacked = jnp.concatenate([first[:, :width], first[:, width:]], axis=0)
        second = jnp.dot(down_ref[...], stacked, preferred_element_type=jnp.float32)
        second = second.astype(jnp.bfloat16)
        half = second.shape[0] // 2
        real_parts.append(second[:half])
        imag_parts.append(second[half:])
    return real_parts, imag_parts


def template_kernel(values_ref, across_ref, down_ref, real_ref, imag_ref):
    real_parts, imag_parts = spectrum_planes(values_ref, across_ref, down_ref)
    for plane in range(len(real_parts)):
        real_ref[plane] = real_parts[plane].astype(jnp.float32)
        imag_ref[plane] = imag_parts[plane].astype(jnp.float32)


def field_kernel(
    values_ref, wedge_ref, across_ref, mix_ref, back_ref, real_ref, imag_ref, energy_ref, field_ref
):
    length = values_ref.shape[-1]
    real_parts, imag_parts = spectrum_planes(values_ref, across_ref, mix_ref)
    energy = None
    for plane in range(len(real_parts)):
        masked = jnp.concatenate(
            [real_parts[plane] * wedge_ref[...], imag_parts[plane] * wedge_ref[...]], axis=1
        )
        first = jnp.dot(masked, mix_ref[...], preferred_element_type=jnp.float32)
        first = first.astype(jnp.bfloat16)
        stacked = jnp.concatenate([first[:, :length], first[:, length:]], axis=0)
        field = jnp.dot(back_ref[...], stacked, preferred_element_type=jnp.float32)
        field = (field * (1.0 / (length * length))).astype(jnp.bfloat16)
        field_ref[plane] = field
        square = jnp.square(field.astype(jnp.float32))
        energy = square if energy is None else energy + square
    energy_ref[...] = energy
    real_parts, imag_parts = spectrum_planes(field_ref, across_ref, mix_ref)
    for plane in range(len(real_parts)):
        real_ref[plane] = real_parts[plane].astype(jnp.float32)
        imag_ref[plane] = imag_parts[plane].astype(jnp.float32)


def make_templates(sampled, box_edge, planes, cosine_table, sine_table):
    count = sampled.shape[1]
    length = cosine_table.shape[0]
    sampled = jnp.transpose(sampled, (1, 0, 2))
    sampled = sampled.reshape(count, planes, box_edge, box_edge)
    template_norm = jnp.sqrt(
        jnp.sum(jnp.square(sampled.astype(jnp.float32)), axis=(1, 2, 3)) + 1e-05
    )
    across = jnp.concatenate([cosine_table[:box_edge], -sine_table[:box_edge]], axis=1)
    down = jnp.concatenate(
        [
            jnp.concatenate([cosine_table[:, :box_edge], sine_table[:, :box_edge]], axis=1),
            jnp.concatenate([-sine_table[:, :box_edge], cosine_table[:, :box_edge]], axis=1),
        ],
        axis=0,
    )
    spec_block = pl.BlockSpec((None, planes, length, length), lambda o: (o, 0, 0, 0))
    spec_shape = jax.ShapeDtypeStruct((count, planes, length, length), jnp.float32)
    spec_real, spec_imag = pl.pallas_call(
        template_kernel,
        grid=(count,),
        out_shape=(spec_shape, spec_shape),
        in_specs=[
            pl.BlockSpec((None, planes, box_edge, box_edge), lambda o: (o, 0, 0, 0)),
            pl.BlockSpec(across.shape, lambda o: (0, 0)),
            pl.BlockSpec(down.shape, lambda o: (0, 0)),
        ],
        out_specs=(spec_block, spec_block),
    )(sampled, across, down)
    return (spec_real, spec_imag, template_norm)


def field_spectra(gathered, wedge_weight, cosine_table, sine_table):
    tiles, planes, length, _ = gathered.shape
    across = jnp.concatenate([cosine_table, -sine_table], axis=1)
    mix = jnp.concatenate(
        [
            jnp.concatenate([cosine_table, sine_table], axis=1),
            jnp.concatenate([-sine_table, cosine_table], axis=1),
        ],
        axis=0,
    )
    back = jnp.concatenate([cosine_table, -sine_table], axis=1)
    tile_block = pl.BlockSpec((None, planes, length, length), lambda t: (t, 0, 0, 0))
    spec_shape = jax.ShapeDtypeStruct((tiles, planes, length, length), jnp.float32)
    return pl.pallas_call(
        field_kernel,
        grid=(tiles,),
        out_shape=(
            spec_shape,
            spec_shape,
            jax.ShapeDtypeStruct((tiles, length, length), jnp.float32),
        ),
        in_specs=[
            tile_block,
            pl.BlockSpec((length, length), lambda t: (0, 0)),
            pl.BlockSpec(across.shape, lambda t: (0, 0)),
            pl.BlockSpec(mix.shape, lambda t: (0, 0)),
            pl.BlockSpec(back.shape, lambda t: (0, 0)),
        ],
        out_specs=(
            tile_block,
            tile_block,
            pl.BlockSpec((None, length, length), lambda t: (t, 0, 0)),
        ),
        scratch_shapes=[pltpu.VMEM((planes, length, length), jnp.bfloat16)],
    )(gathered, wedge_weight, across, mix, back)


def score_kernel(
    scale_ref, field_re_ref, field_im_ref, templ_re_ref, templ_im_ref, mix_ref, back_ref,
    rms_ref, out_ref, best_ref
):
    planes = field_re_ref.shape[0]
    length = field_re_ref.shape[-1]
    group = 4 if templ_re_ref.shape[0] % 4 == 0 else 1
    best_ref[...] = jnp.full(best_ref.shape, -jnp.inf, jnp.float32)

    def body(step, carry):
        joined = []
        for member in range(group):
            orient = step * group + member
            prod_re = None
            prod_im = None
            for plane in range(planes):
                fr = field_re_ref[plane]
                fi = field_im_ref[plane]
                tr = templ_re_ref[orient, plane]
                ti = templ_im_ref[orient, plane]
                part_re = fr * tr + fi * ti
                part_im = fi * tr - fr * ti
                prod_re = part_re if prod_re is None else prod_re + part_re
                prod_im = part_im if prod_im is None else prod_im + part_im
            joined.append(
                jnp.concatenate(
                    [prod_re.astype(jnp.bfloat16), prod_im.astype(jnp.bfloat16)], axis=1
                )
            )
        joined = jnp.concatenate(joined, axis=0)
        first = jnp.dot(joined, mix_ref[...], preferred_element_type=jnp.float32).astype(
            jnp.bfloat16
        )
        stacked = []
        for member in range(group):
            rows = first[member * length : (member + 1) * length]
            stacked.append(jnp.concatenate([rows[:, :length], rows[:, length:]], axis=0))
        stacked = jnp.concatenate(stacked, axis=1)
        corr = jnp.dot(back_ref[...], stacked, preferred_element_type=jnp.float32)
        best = best_ref[...]
        for member in range(group):
            orient = step * group + member
            best = jnp.maximum(
                best, corr[:, member * length : (member + 1) * length] * scale_ref[orient]
            )
        best_ref[...] = best
        return carry

    lax.fori_loop(0, templ_re_ref.shape[0] // group, body, 0)
    out_ref[...] = (best_ref[...] / rms_ref[...]).astype(out_ref.dtype)


def score_tiles(
    field_real, field_imag, energy, templ_real, templ_imag, template_norm, cosine_table,
    sine_table, band_sum, box_edge
):
    planes = field_real.shape[1]
    length = field_real.shape[-1]
    summed = jnp.einsum(
        "ka,nab,lb->nkl", band_sum, energy, band_sum, precision=lax.Precision.HIGHEST
    )
    local_rms = jnp.sqrt(summed / (box_edge * box_edge * planes) + 1e-05)
    scale = (1.0 / template_norm) * (1.0 / (length * length))
    mix = jnp.concatenate(
        [
            jnp.concatenate([cosine_table, sine_table], axis=1),
            jnp.concatenate([-sine_table, cosine_table], axis=1),
        ],
        axis=0,
    )
    back = jnp.concatenate([cosine_table, -sine_table], axis=1)
    tiles = field_real.shape[0]
    count = templ_real.shape[0]
    tile_block = pl.BlockSpec((None, planes, length, length), lambda t: (t, 0, 0, 0))
    templ_block = pl.BlockSpec((count, planes, length, length), lambda t: (0, 0, 0, 0))
    return pl.pallas_call(
        score_kernel,
        grid=(tiles,),
        out_shape=jax.ShapeDtypeStruct((tiles, length, length), jnp.bfloat16),
        in_specs=[
            pl.BlockSpec(memory_space=pltpu.SMEM),
            tile_block,
            tile_block,
            templ_block,
            templ_block,
            pl.BlockSpec((2 * length, 2 * length), lambda t: (0, 0)),
            pl.BlockSpec((length, 2 * length), lambda t: (0, 0)),
            pl.BlockSpec((None, length, length), lambda t: (t, 0, 0)),
        ],
        out_specs=pl.BlockSpec((None, length, length), lambda t: (t, 0, 0)),
        scratch_shapes=[pltpu.VMEM((length, length), jnp.float32)],
    )(
        scale,
        field_real,
        field_imag,
        templ_real,
        templ_imag,
        mix,
        back,
        local_rms,
    )


def orient_max(best):
    groups = lax.axis_size("orient")
    parts = lax.all_to_all(best, "orient", split_axis=1, concat_axis=0, tiled=True)
    stacked = parts.reshape(groups, best.shape[0], parts.shape[1], parts.shape[2])
    return jnp.max(stacked, axis=0)


def per_device(tiles, assigned_worker, wedge_mask, template_volume, rotation_samples):
    tile_len = tiles.shape[-1]
    planes = tiles.shape[1]
    home_slots = tiles.shape[0]
    work_slots = home_slots // 2
    box_edge = template_volume.shape[0]
    cosine_table, sine_table = tables(tile_len)
    band_sum = band_table(tile_len, box_edge)
    wedge_weight = wedge_mask.astype(jnp.bfloat16)
    sampled = share_samples(template_volume, rotation_samples)
    occupied = assigned_worker >= 0
    own_count = jnp.sum(occupied.astype(jnp.int32))
    partner_tiles = partner(tiles[work_slots:], "slab", 0)
    counter = jnp.arange(work_slots, dtype=jnp.int32)
    keep_own = (counter < own_count)[:, None, None, None]
    moved_in = pick_rows(counter - own_count, partner_tiles)
    gathered = jnp.where(keep_own, tiles[:work_slots], moved_in)
    field_real, field_imag, energy = field_spectra(
        gathered, wedge_weight, cosine_table, sine_table
    )
    templ_real, templ_imag, template_norm = make_templates(
        sampled, box_edge, planes, cosine_table, sine_table
    )
    best = score_tiles(
        field_real,
        field_imag,
        energy,
        templ_real,
        templ_imag,
        template_norm,
        cosine_table,
        sine_table,
        band_sum,
        box_edge,
    )
    best_rows = orient_max(best)
    outgoing = pick_rows(counter + own_count, best_rows)
    returned = partner(outgoing, "slab", 0)
    result = jnp.concatenate([best_rows, returned], axis=0)
    return jnp.where(occupied[:, None, None], result, jnp.zeros_like(result))


def solution(mesh):
    return jax.shard_map(
        per_device,
        mesh=mesh,
        in_specs=(P("slab", None, None, None), P("slab"), P(), P(), P("orient", "slab")),
        out_specs=P("slab", "orient", None),
        check_vma=False,
    )
```

```python
import math

import jax
import jax.numpy as jnp
from jax import lax
from jax.experimental import pallas as pl
from jax.experimental.pallas import tpu as pltpu
from jax.sharding import PartitionSpec as P


def partner(block, axis, bit):
    count = lax.axis_size(axis)
    route = []
    for low in range(count):
        high = low | 1 << bit
        if high != low and high < count:
            route += [(low, high), (high, low)]
    return lax.ppermute(block, axis, route)


def tables(length):
    counter = jnp.arange(length, dtype=jnp.int32)
    angles = (counter[:, None] * counter[None, :] % length).astype(jnp.float32) * (
        2.0 * math.pi / length
    )
    return (jnp.cos(angles).astype(jnp.bfloat16), jnp.sin(angles).astype(jnp.bfloat16))


def band_table(length, box_edge):
    counter = jnp.arange(length, dtype=jnp.int32)
    offsets = (counter[None, :] - counter[:, None]) % length
    return (offsets < box_edge).astype(jnp.float32)


def right_mul(values, table):
    return jnp.einsum("...ab,bc->...ac", values, table, preferred_element_type=jnp.float32)


def left_mul(table, values):
    return jnp.einsum("ka,...ab->...kb", table, values, preferred_element_type=jnp.float32)


def forward_two(values, cosine_table, sine_table):
    first_real = right_mul(values, cosine_table).astype(jnp.bfloat16)
    first_imag = (-right_mul(values, sine_table)).astype(jnp.bfloat16)
    second_real = (left_mul(cosine_table, first_real) + left_mul(sine_table, first_imag)).astype(
        jnp.bfloat16
    )
    second_imag = (left_mul(cosine_table, first_imag) - left_mul(sine_table, first_real)).astype(
        jnp.bfloat16
    )
    return (second_real, second_imag)


def inverse_real(real_part, imag_part, cosine_table, sine_table):
    length = real_part.shape[-1]
    first_real = (right_mul(real_part, cosine_table) - right_mul(imag_part, sine_table)).astype(
        jnp.bfloat16
    )
    first_imag = (right_mul(imag_part, cosine_table) + right_mul(real_part, sine_table)).astype(
        jnp.bfloat16
    )
    return (left_mul(cosine_table, first_real) - left_mul(sine_table, first_imag)) * (
        1.0 / (length * length)
    )


def filtered(values, wedge_weight, cosine_table, sine_table):
    spec_real, spec_imag = forward_two(values, cosine_table, sine_table)
    return inverse_real(
        spec_real * wedge_weight, spec_imag * wedge_weight, cosine_table, sine_table
    ).astype(jnp.bfloat16)


def pick_rows(chosen, source):
    counter = jnp.arange(source.shape[0], dtype=jnp.int32)
    selector = (chosen[:, None] == counter[None, :]).astype(source.dtype)
    flat = source.reshape(source.shape[0], -1)
    picked = jnp.dot(selector, flat, preferred_element_type=jnp.float32).astype(source.dtype)
    return picked.reshape((chosen.shape[0],) + source.shape[1:])


def pick_kernel(index_ref, table_ref, out_ref):
    columns = table_ref.shape[0]
    rows_in_table = table_ref.shape[1]
    lanes = index_ref.shape[1]
    shift = columns.bit_length() - 1

    def body(step, carry):
        index = index_ref[pl.ds(step, 1), :]
        high = jnp.right_shift(index, shift)
        low = jnp.bitwise_and(index, columns - 1)
        row_hot = (lax.broadcasted_iota(jnp.int32, (rows_in_table, lanes), 0) == high).astype(
            jnp.bfloat16
        )
        picked_rows = jnp.dot(table_ref[...], row_hot, preferred_element_type=jnp.float32)
        column_hot = lax.broadcasted_iota(jnp.int32, (columns, lanes), 0) == low
        chosen = jnp.where(column_hot, picked_rows, 0.0)
        out_ref[pl.ds(step, 1), :] = jnp.sum(chosen, axis=0, keepdims=True)
        return carry

    lax.fori_loop(0, index_ref.shape[0], body, 0)


def sample_template(template_volume, rotation_samples):
    total = template_volume.size
    columns = 512
    table_t = template_volume.reshape(total // columns, columns).T.astype(jnp.bfloat16)
    count = rotation_samples.size
    lanes = 256 if count % 256 == 0 else 128
    index = rotation_samples.reshape(count // lanes, lanes)
    picked = pl.pallas_call(
        pick_kernel,
        out_shape=jax.ShapeDtypeStruct(index.shape, jnp.float32),
        in_specs=[pl.BlockSpec(memory_space=pltpu.VMEM)] * 2,
        out_specs=pl.BlockSpec(memory_space=pltpu.VMEM),
    )(index, table_t)
    return picked.reshape(rotation_samples.shape).astype(jnp.bfloat16)


def share_samples(template_volume, rotation_samples):
    sampled_part = sample_template(template_volume, rotation_samples)
    slab_count = lax.axis_size("slab")
    slot = lax.axis_index("slab")
    held = sampled_part[None]
    bit = 0
    while (1 << bit) < slab_count:
        held = jnp.concatenate([held, partner(held, "slab", bit)], axis=0)
        bit += 1
    order = jnp.bitwise_xor(jnp.arange(slab_count, dtype=jnp.int32), slot)
    return pick_rows(order, held)


def rows_to_blocks(values, rows):
    count = values.shape[0] // rows
    return jnp.concatenate([values[i * rows : (i + 1) * rows] for i in range(count)], axis=1)


def blocks_to_rows(values, width):
    count = values.shape[1] // width
    return jnp.concatenate(
        [values[:, i * width : (i + 1) * width] for i in range(count)], axis=0
    )


def forward_rows(values, across, down):
    width = across.shape[1] // 2
    height = down.shape[1] // 2
    first = jnp.dot(values, across, preferred_element_type=jnp.float32).astype(jnp.bfloat16)
    stacked = jnp.concatenate(
        [rows_to_blocks(first[:, :width], height), rows_to_blocks(first[:, width:], height)],
        axis=0,
    )
    second = jnp.dot(down, stacked, preferred_element_type=jnp.float32).astype(jnp.bfloat16)
    return second[:width], second[width:]


def inverse_blocks(real_part, imag_part, mix, back):
    length = real_part.shape[0]
    joined = jnp.concatenate(
        [blocks_to_rows(real_part, length), blocks_to_rows(imag_part, length)], axis=1
    )
    first = jnp.dot(joined, mix, preferred_element_type=jnp.float32).astype(jnp.bfloat16)
    stacked = jnp.concatenate(
        [rows_to_blocks(first[:, :length], length), rows_to_blocks(first[:, length:], length)],
        axis=0,
    )
    return jnp.dot(back, stacked, preferred_element_type=jnp.float32)


def template_kernel(values_ref, across_ref, down_ref, real_ref, imag_ref):
    real_part, imag_part = forward_rows(values_ref[...], across_ref[...], down_ref[...])
    real_ref[...] = real_part.astype(jnp.float32)
    imag_ref[...] = imag_part.astype(jnp.float32)


def field_kernel(
    values_ref, wedge_ref, across_ref, mix_ref, back_ref, real_ref, imag_ref, energy_ref
):
    length = values_ref.shape[-1]
    maps = values_ref.shape[0] // length
    planes = maps // energy_ref.shape[0]
    mix = mix_ref[...]
    real_part, imag_part = forward_rows(values_ref[...], across_ref[...], mix)
    wedge = jnp.concatenate([wedge_ref[...]] * maps, axis=1)
    field = inverse_blocks(real_part * wedge, imag_part * wedge, mix, back_ref[...])
    field = (field * (1.0 / (length * length))).astype(jnp.bfloat16)
    square = jnp.square(field.astype(jnp.float32))
    for tile in range(energy_ref.shape[0]):
        energy = None
        for plane in range(planes):
            index = tile * planes + plane
            part = square[:, index * length : (index + 1) * length]
            energy = part if energy is None else energy + part
        energy_ref[tile] = energy
    real_part, imag_part = forward_rows(blocks_to_rows(field, length), across_ref[...], mix)
    real_ref[...] = real_part.astype(jnp.float32)
    imag_ref[...] = imag_part.astype(jnp.float32)


def whole_call(kernel, out_shape, *args):
    return pl.pallas_call(
        kernel,
        out_shape=out_shape,
        in_specs=[pl.BlockSpec(memory_space=pltpu.VMEM)] * len(args),
        out_specs=tuple(pl.BlockSpec(memory_space=pltpu.VMEM) for _ in out_shape),
    )(*args)


def make_templates(sampled, box_edge, planes, cosine_table, sine_table):
    count = sampled.shape[1]
    length = cosine_table.shape[0]
    sampled = jnp.transpose(sampled, (1, 0, 2))
    sampled = sampled.reshape(count, planes, box_edge, box_edge)
    template_norm = jnp.sqrt(
        jnp.sum(jnp.square(sampled.astype(jnp.float32)), axis=(1, 2, 3)) + 1e-05
    )
    across = jnp.concatenate([cosine_table[:box_edge], -sine_table[:box_edge]], axis=1)
    down = jnp.concatenate(
        [
            jnp.concatenate([cosine_table[:, :box_edge], sine_table[:, :box_edge]], axis=1),
            jnp.concatenate([-sine_table[:, :box_edge], cosine_table[:, :box_edge]], axis=1),
        ],
        axis=0,
    )
    spec_shape = jax.ShapeDtypeStruct((length, count * planes * length), jnp.float32)
    spec_real, spec_imag = whole_call(
        template_kernel,
        (spec_shape, spec_shape),
        sampled.reshape(count * planes * box_edge, box_edge),
        across,
        down,
    )
    return (spec_real, spec_imag, template_norm)


def field_spectra(gathered, wedge_weight, cosine_table, sine_table):
    tiles, planes, length, _ = gathered.shape
    across = jnp.concatenate([cosine_table, -sine_table], axis=1)
    mix = jnp.concatenate(
        [
            jnp.concatenate([cosine_table, sine_table], axis=1),
            jnp.concatenate([-sine_table, cosine_table], axis=1),
        ],
        axis=0,
    )
    back = jnp.concatenate([cosine_table, -sine_table], axis=1)
    spec_shape = jax.ShapeDtypeStruct((length, tiles * planes * length), jnp.float32)
    return whole_call(
        field_kernel,
        (spec_shape, spec_shape, jax.ShapeDtypeStruct((tiles, length, length), jnp.float32)),
        gathered.reshape(tiles * planes * length, length),
        wedge_weight,
        across,
        mix,
        back,
    )


def score_kernel(
    scale_ref, field_re_ref, field_im_ref, templ_re_ref, templ_im_ref, mix_ref, back_ref,
    rms_ref, out_ref
):
    length = field_re_ref.shape[0]
    planes = field_re_ref.shape[1] // length
    count = templ_re_ref.shape[1] // (planes * length)
    group = 4 if count % 4 == 0 else 1

    def lanes(index):
        return slice(index * length, (index + 1) * length)

    best = None
    for step in range(count // group):
        joined = []
        for member in range(group):
            orient = step * group + member
            prod_re = None
            prod_im = None
            for plane in range(planes):
                fr = field_re_ref[:, lanes(plane)]
                fi = field_im_ref[:, lanes(plane)]
                tr = templ_re_ref[:, lanes(orient * planes + plane)]
                ti = templ_im_ref[:, lanes(orient * planes + plane)]
                part_re = fr * tr + fi * ti
                part_im = fi * tr - fr * ti
                prod_re = part_re if prod_re is None else prod_re + part_re
                prod_im = part_im if prod_im is None else prod_im + part_im
            joined.append(
                jnp.concatenate(
                    [prod_re.astype(jnp.bfloat16), prod_im.astype(jnp.bfloat16)], axis=1
                )
            )
        joined = jnp.concatenate(joined, axis=0)
        first = jnp.dot(joined, mix_ref[...], preferred_element_type=jnp.float32).astype(
            jnp.bfloat16
        )
        stacked = jnp.concatenate(
            [rows_to_blocks(first[:, :length], length), rows_to_blocks(first[:, length:], length)],
            axis=0,
        )
        corr = jnp.dot(back_ref[...], stacked, preferred_element_type=jnp.float32)
        for member in range(group):
            orient = step * group + member
            value = corr[:, lanes(member)] * scale_ref[orient]
            best = value if best is None else jnp.maximum(best, value)
    out_ref[...] = (best / rms_ref[...]).astype(out_ref.dtype)


def score_tiles(
    field_real, field_imag, energy, templ_real, templ_imag, template_norm, cosine_table,
    sine_table, band_sum, box_edge
):
    length = field_real.shape[0]
    planes = field_real.shape[1] // (energy.shape[0] * length)
    summed = jnp.einsum(
        "ka,nab,lb->nkl", band_sum, energy, band_sum, precision=lax.Precision.HIGHEST
    )
    local_rms = jnp.sqrt(summed / (box_edge * box_edge * planes) + 1e-05)
    scale = (1.0 / template_norm) * (1.0 / (length * length))
    mix = jnp.concatenate(
        [
            jnp.concatenate([cosine_table, sine_table], axis=1),
            jnp.concatenate([-sine_table, cosine_table], axis=1),
        ],
        axis=0,
    )
    back = jnp.concatenate([cosine_table, -sine_table], axis=1)
    tiles = energy.shape[0]
    tile_block = pl.BlockSpec((length, planes * length), lambda t: (0, t))
    templ_block = pl.BlockSpec(templ_real.shape, lambda t: (0, 0))
    return pl.pallas_call(
        score_kernel,
        grid=(tiles,),
        out_shape=jax.ShapeDtypeStruct((tiles, length, length), jnp.bfloat16),
        in_specs=[
            pl.BlockSpec(memory_space=pltpu.SMEM),
            tile_block,
            tile_block,
            templ_block,
            templ_block,
            pl.BlockSpec((2 * length, 2 * length), lambda t: (0, 0)),
            pl.BlockSpec((length, 2 * length), lambda t: (0, 0)),
            pl.BlockSpec((None, length, length), lambda t: (t, 0, 0)),
        ],
        out_specs=pl.BlockSpec((None, length, length), lambda t: (t, 0, 0)),
    )(
        scale,
        field_real,
        field_imag,
        templ_real,
        templ_imag,
        mix,
        back,
        local_rms,
    )


def orient_max(best):
    groups = lax.axis_size("orient")
    parts = lax.all_to_all(best, "orient", split_axis=1, concat_axis=0, tiled=True)
    stacked = parts.reshape(groups, best.shape[0], parts.shape[1], parts.shape[2])
    return jnp.max(stacked, axis=0)


def per_device(tiles, assigned_worker, wedge_mask, template_volume, rotation_samples):
    tile_len = tiles.shape[-1]
    planes = tiles.shape[1]
    home_slots = tiles.shape[0]
    work_slots = home_slots // 2
    box_edge = template_volume.shape[0]
    cosine_table, sine_table = tables(tile_len)
    band_sum = band_table(tile_len, box_edge)
    wedge_weight = wedge_mask.astype(jnp.bfloat16)
    sampled = share_samples(template_volume, rotation_samples)
    occupied = assigned_worker >= 0
    own_count = jnp.sum(occupied.astype(jnp.int32))
    partner_tiles = partner(tiles[work_slots:], "slab", 0)
    counter = jnp.arange(work_slots, dtype=jnp.int32)
    keep_own = (counter < own_count)[:, None, None, None]
    moved_in = pick_rows(counter - own_count, partner_tiles)
    gathered = jnp.where(keep_own, tiles[:work_slots], moved_in)
    field_real, field_imag, energy = field_spectra(
        gathered, wedge_weight, cosine_table, sine_table
    )
    templ_real, templ_imag, template_norm = make_templates(
        sampled, box_edge, planes, cosine_table, sine_table
    )
    best = score_tiles(
        field_real,
        field_imag,
        energy,
        templ_real,
        templ_imag,
        template_norm,
        cosine_table,
        sine_table,
        band_sum,
        box_edge,
    )
    best_rows = orient_max(best)
    outgoing = pick_rows(counter + own_count, best_rows)
    returned = partner(outgoing, "slab", 0)
    result = jnp.concatenate([best_rows, returned], axis=0)
    return jnp.where(occupied[:, None, None], result, jnp.zeros_like(result))


def solution(mesh):
    return jax.shard_map(
        per_device,
        mesh=mesh,
        in_specs=(P("slab", None, None, None), P("slab"), P(), P(), P("orient", "slab")),
        out_specs=P("slab", "orient", None),
        check_vma=False,
    )
```

```python
import math

import jax
import ml_dtypes
import numpy as np
import jax.numpy as jnp
from jax import lax
from jax.experimental import pallas as pl
from jax.experimental.pallas import tpu as pltpu
from jax.sharding import PartitionSpec as P


def partner(block, axis, bit):
    count = lax.axis_size(axis)
    route = []
    for low in range(count):
        high = low | 1 << bit
        if high != low and high < count:
            route += [(low, high), (high, low)]
    return lax.ppermute(block, axis, route)


def tables(length):
    counter = np.arange(length, dtype=np.int32)
    angles = (counter[:, None] * counter[None, :] % length).astype(np.float32) * np.float32(
        2.0 * math.pi / length
    )
    wide = angles.astype(np.float64)
    cosine = np.cos(wide).astype(np.float32).astype(ml_dtypes.bfloat16)
    sine = np.sin(wide).astype(np.float32).astype(ml_dtypes.bfloat16)
    return cosine, sine


def band_table(length, box_edge):
    counter = np.arange(length, dtype=np.int32)
    offsets = (counter[None, :] - counter[:, None]) % length
    return jnp.asarray((offsets < box_edge).astype(np.float32))


def transform_tables(length, box_edge):
    cosine, sine = tables(length)
    across = np.concatenate([cosine, -sine], axis=1)
    mix = np.concatenate(
        [np.concatenate([cosine, sine], axis=1), np.concatenate([-sine, cosine], axis=1)], axis=0
    )
    box_across = np.concatenate([cosine[:box_edge], -sine[:box_edge]], axis=1)
    box_down = np.concatenate(
        [
            np.concatenate([cosine[:, :box_edge], sine[:, :box_edge]], axis=1),
            np.concatenate([-sine[:, :box_edge], cosine[:, :box_edge]], axis=1),
        ],
        axis=0,
    )
    return {
        name: jnp.asarray(value)
        for name, value in (
            ("across", across),
            ("mix", mix),
            ("box_across", box_across),
            ("box_down", box_down),
        )
    }


def pick_rows(chosen, source):
    counter = jnp.arange(source.shape[0], dtype=jnp.int32)
    selector = (chosen[:, None] == counter[None, :]).astype(source.dtype)
    flat = source.reshape(source.shape[0], -1)
    picked = jnp.dot(selector, flat, preferred_element_type=jnp.float32).astype(source.dtype)
    return picked.reshape((chosen.shape[0],) + source.shape[1:])


def pick_kernel(index_ref, table_ref, out_ref, picked_ref):
    columns = table_ref.shape[0]
    rows_in_table = table_ref.shape[1]
    lanes = index_ref.shape[1]
    shift = columns.bit_length() - 1

    def body(step, carry):
        index = index_ref[pl.ds(step, 1), :]
        high = jnp.right_shift(index, shift)
        low = jnp.bitwise_and(index, columns - 1)
        row_hot = (lax.broadcasted_iota(jnp.int32, (rows_in_table, lanes), 0) == high).astype(
            jnp.bfloat16
        )
        picked_rows = jnp.dot(table_ref[...], row_hot, preferred_element_type=jnp.float32)
        column_hot = lax.broadcasted_iota(jnp.int32, (columns, lanes), 0) == low
        chosen = jnp.where(column_hot, picked_rows, 0.0)
        picked_ref[pl.ds(step, 1), :] = jnp.sum(chosen, axis=0, keepdims=True)
        return carry

    lax.fori_loop(0, index_ref.shape[0], body, 0)
    out_ref[...] = picked_ref[...].astype(out_ref.dtype)


def sample_template(template_volume, rotation_samples):
    total = template_volume.size
    columns = 512
    table_t = template_volume.reshape(total // columns, columns).T.astype(jnp.bfloat16)
    return pl.pallas_call(
        pick_kernel,
        out_shape=jax.ShapeDtypeStruct(rotation_samples.shape, jnp.bfloat16),
        in_specs=[pl.BlockSpec(memory_space=pltpu.VMEM)] * 2,
        out_specs=pl.BlockSpec(memory_space=pltpu.VMEM),
        scratch_shapes=[pltpu.VMEM(rotation_samples.shape, jnp.float32)],
    )(rotation_samples, table_t)


def share_samples(template_volume, rotation_samples):
    sampled_part = sample_template(template_volume, rotation_samples)
    slab_count = lax.axis_size("slab")
    slot = lax.axis_index("slab")
    held = sampled_part[None]
    bit = 0
    while (1 << bit) < slab_count:
        held = jnp.concatenate([held, partner(held, "slab", bit)], axis=0)
        bit += 1
    order = jnp.bitwise_xor(jnp.arange(slab_count, dtype=jnp.int32), slot)
    return pick_rows(order, held)


def rows_to_blocks(values, rows):
    count = values.shape[0] // rows
    return jnp.concatenate([values[i * rows : (i + 1) * rows] for i in range(count)], axis=1)


def blocks_to_rows(values, width):
    count = values.shape[1] // width
    return jnp.concatenate(
        [values[:, i * width : (i + 1) * width] for i in range(count)], axis=0
    )


def forward_rows(values, across, down):
    width = across.shape[1] // 2
    height = down.shape[1] // 2
    first = jnp.dot(values, across, preferred_element_type=jnp.float32).astype(jnp.bfloat16)
    stacked = jnp.concatenate(
        [rows_to_blocks(first[:, :width], height), rows_to_blocks(first[:, width:], height)],
        axis=0,
    )
    second = jnp.dot(down, stacked, preferred_element_type=jnp.float32).astype(jnp.bfloat16)
    return second[:width], second[width:]


def inverse_blocks(real_part, imag_part, mix, back):
    length = real_part.shape[0]
    joined = jnp.concatenate(
        [blocks_to_rows(real_part, length), blocks_to_rows(imag_part, length)], axis=1
    )
    first = jnp.dot(joined, mix, preferred_element_type=jnp.float32).astype(jnp.bfloat16)
    stacked = jnp.concatenate(
        [rows_to_blocks(first[:, :length], length), rows_to_blocks(first[:, length:], length)],
        axis=0,
    )
    return jnp.dot(back, stacked, preferred_element_type=jnp.float32)


def template_kernel(values_ref, across_ref, down_ref, real_ref, imag_ref):
    real_part, imag_part = forward_rows(values_ref[...], across_ref[...], down_ref[...])
    real_ref[...] = real_part.astype(jnp.float32)
    imag_ref[...] = imag_part.astype(jnp.float32)


def field_kernel(
    values_ref, wedge_ref, across_ref, mix_ref, back_ref, real_ref, imag_ref, energy_ref
):
    length = values_ref.shape[-1]
    maps = values_ref.shape[0] // length
    planes = maps // energy_ref.shape[0]
    mix = mix_ref[...]
    real_part, imag_part = forward_rows(values_ref[...], across_ref[...], mix)
    wedge = jnp.concatenate([wedge_ref[...]] * maps, axis=1)
    field = inverse_blocks(real_part * wedge, imag_part * wedge, mix, back_ref[...])
    field = (field * (1.0 / (length * length))).astype(jnp.bfloat16)
    square = jnp.square(field.astype(jnp.float32))
    for tile in range(energy_ref.shape[0]):
        energy = None
        for plane in range(planes):
            index = tile * planes + plane
            part = square[:, index * length : (index + 1) * length]
            energy = part if energy is None else energy + part
        energy_ref[tile] = energy
    real_part, imag_part = forward_rows(blocks_to_rows(field, length), across_ref[...], mix)
    real_ref[...] = real_part.astype(jnp.float32)
    imag_ref[...] = imag_part.astype(jnp.float32)


def whole_call(kernel, out_shape, *args):
    return pl.pallas_call(
        kernel,
        out_shape=out_shape,
        in_specs=[pl.BlockSpec(memory_space=pltpu.VMEM)] * len(args),
        out_specs=tuple(pl.BlockSpec(memory_space=pltpu.VMEM) for _ in out_shape),
    )(*args)


def make_templates(sampled, box_edge, planes, table):
    count = sampled.shape[1]
    length = table["across"].shape[0]
    sampled = jnp.transpose(sampled, (1, 0, 2))
    sampled = sampled.reshape(count, planes, box_edge, box_edge)
    template_norm = jnp.sqrt(
        jnp.sum(jnp.square(sampled.astype(jnp.float32)), axis=(1, 2, 3)) + 1e-05
    )
    spec_shape = jax.ShapeDtypeStruct((length, count * planes * length), jnp.float32)
    spec_real, spec_imag = whole_call(
        template_kernel,
        (spec_shape, spec_shape),
        sampled.reshape(count * planes * box_edge, box_edge),
        table["box_across"],
        table["box_down"],
    )
    return (spec_real, spec_imag, template_norm)


def field_spectra(gathered, wedge_weight, table):
    tiles, planes, length, _ = gathered.shape
    spec_shape = jax.ShapeDtypeStruct((length, tiles * planes * length), jnp.float32)
    return whole_call(
        field_kernel,
        (spec_shape, spec_shape, jax.ShapeDtypeStruct((tiles, length, length), jnp.float32)),
        gathered.reshape(tiles * planes * length, length),
        wedge_weight,
        table["across"],
        table["mix"],
        table["across"],
    )


def score_kernel(
    scale_ref, field_re_ref, field_im_ref, templ_re_ref, templ_im_ref, mix_ref, back_ref,
    rms_ref, out_ref
):
    length = field_re_ref.shape[0]
    per_step = rms_ref.shape[0]
    planes = field_re_ref.shape[1] // (per_step * length)
    count = templ_re_ref.shape[1] // (planes * length)
    group = 8 if count % 8 == 0 else 1

    def lanes(index):
        return slice(index * length, (index + 1) * length)

    for tile in range(per_step):
        best = None
        for step in range(count // group):
            joined = []
            for member in range(group):
                orient = step * group + member
                prod_re = None
                prod_im = None
                for plane in range(planes):
                    fr = field_re_ref[:, lanes(tile * planes + plane)]
                    fi = field_im_ref[:, lanes(tile * planes + plane)]
                    tr = templ_re_ref[:, lanes(orient * planes + plane)]
                    ti = templ_im_ref[:, lanes(orient * planes + plane)]
                    part_re = fr * tr + fi * ti
                    part_im = fi * tr - fr * ti
                    prod_re = part_re if prod_re is None else prod_re + part_re
                    prod_im = part_im if prod_im is None else prod_im + part_im
                joined.append(
                    jnp.concatenate(
                        [prod_re.astype(jnp.bfloat16), prod_im.astype(jnp.bfloat16)], axis=1
                    )
                )
            joined = jnp.concatenate(joined, axis=0)
            first = jnp.dot(joined, mix_ref[...], preferred_element_type=jnp.float32).astype(
                jnp.bfloat16
            )
            stacked = jnp.concatenate(
                [
                    rows_to_blocks(first[:, :length], length),
                    rows_to_blocks(first[:, length:], length),
                ],
                axis=0,
            )
            corr = jnp.dot(back_ref[...], stacked, preferred_element_type=jnp.float32)
            for member in range(group):
                orient = step * group + member
                value = corr[:, lanes(member)] * scale_ref[orient]
                best = value if best is None else jnp.maximum(best, value)
        out_ref[tile] = (best / rms_ref[tile]).astype(out_ref.dtype)


def score_tiles(
    field_real, field_imag, energy, templ_real, templ_imag, template_norm, table, band_sum,
    box_edge
):
    length = field_real.shape[0]
    planes = field_real.shape[1] // (energy.shape[0] * length)
    summed = jnp.einsum(
        "ka,nab,lb->nkl", band_sum, energy, band_sum, precision=lax.Precision.HIGHEST
    )
    local_rms = jnp.sqrt(summed / (box_edge * box_edge * planes) + 1e-05)
    scale = (1.0 / template_norm) * (1.0 / (length * length))
    mix = table["mix"]
    back = table["across"]
    tiles = energy.shape[0]
    per_step = 2 if tiles % 2 == 0 else 1
    tile_block = pl.BlockSpec((length, per_step * planes * length), lambda t: (0, t))
    templ_block = pl.BlockSpec(templ_real.shape, lambda t: (0, 0))
    return pl.pallas_call(
        score_kernel,
        grid=(tiles // per_step,),
        out_shape=jax.ShapeDtypeStruct((tiles, length, length), jnp.bfloat16),
        in_specs=[
            pl.BlockSpec(memory_space=pltpu.SMEM),
            tile_block,
            tile_block,
            templ_block,
            templ_block,
            pl.BlockSpec((2 * length, 2 * length), lambda t: (0, 0)),
            pl.BlockSpec((length, 2 * length), lambda t: (0, 0)),
            pl.BlockSpec((per_step, length, length), lambda t: (t, 0, 0)),
        ],
        out_specs=pl.BlockSpec((per_step, length, length), lambda t: (t, 0, 0)),
    )(
        scale,
        field_real,
        field_imag,
        templ_real,
        templ_imag,
        mix,
        back,
        local_rms,
    )


def orient_max(best):
    groups = lax.axis_size("orient")
    parts = lax.all_to_all(best, "orient", split_axis=1, concat_axis=0, tiled=True)
    stacked = parts.reshape(groups, best.shape[0], parts.shape[1], parts.shape[2])
    return jnp.max(stacked, axis=0)


def per_device(tiles, assigned_worker, wedge_mask, template_volume, rotation_samples):
    tile_len = tiles.shape[-1]
    planes = tiles.shape[1]
    home_slots = tiles.shape[0]
    work_slots = home_slots // 2
    box_edge = template_volume.shape[0]
    table = transform_tables(tile_len, box_edge)
    band_sum = band_table(tile_len, box_edge)
    wedge_weight = wedge_mask.astype(jnp.bfloat16)
    sampled = share_samples(template_volume, rotation_samples)
    occupied = assigned_worker >= 0
    own_count = jnp.sum(occupied.astype(jnp.int32))
    partner_tiles = partner(tiles[work_slots:], "slab", 0)
    counter = jnp.arange(work_slots, dtype=jnp.int32)
    keep_own = (counter < own_count)[:, None, None, None]
    moved_in = pick_rows(counter - own_count, partner_tiles)
    gathered = jnp.where(keep_own, tiles[:work_slots], moved_in)
    field_real, field_imag, energy = field_spectra(gathered, wedge_weight, table)
    templ_real, templ_imag, template_norm = make_templates(sampled, box_edge, planes, table)
    best = score_tiles(
        field_real,
        field_imag,
        energy,
        templ_real,
        templ_imag,
        template_norm,
        table,
        band_sum,
        box_edge,
    )
    best_rows = orient_max(best)
    outgoing = pick_rows(counter + own_count, best_rows)
    returned = partner(outgoing, "slab", 0)
    result = jnp.concatenate([best_rows, returned], axis=0)
    return jnp.where(occupied[:, None, None], result, jnp.zeros_like(result))


def solution(mesh):
    return jax.shard_map(
        per_device,
        mesh=mesh,
        in_specs=(P("slab", None, None, None), P("slab"), P(), P(), P("orient", "slab")),
        out_specs=P("slab", "orient", None),
        check_vma=False,
    )
```

```python
import functools
import math

import jax
import ml_dtypes
import numpy as np
import jax.numpy as jnp
from jax import lax
from jax.experimental import pallas as pl
from jax.experimental.pallas import tpu as pltpu
from jax.sharding import PartitionSpec as P


def partner(block, axis, bit):
    count = lax.axis_size(axis)
    route = []
    for low in range(count):
        high = low | 1 << bit
        if high != low and high < count:
            route += [(low, high), (high, low)]
    return lax.ppermute(block, axis, route)


def tables(length):
    counter = np.arange(length, dtype=np.int32)
    angles = (counter[:, None] * counter[None, :] % length).astype(np.float32) * np.float32(
        2.0 * math.pi / length
    )
    wide = angles.astype(np.float64)
    cosine = np.cos(wide).astype(np.float32).astype(ml_dtypes.bfloat16)
    sine = np.sin(wide).astype(np.float32).astype(ml_dtypes.bfloat16)
    return cosine, sine


def band_table(length, box_edge):
    counter = np.arange(length, dtype=np.int32)
    offsets = (counter[None, :] - counter[:, None]) % length
    return jnp.asarray((offsets < box_edge).astype(np.float32))


def transform_tables(length, box_edge):
    cosine, sine = tables(length)
    across = np.concatenate([cosine, -sine], axis=1)
    mix = np.concatenate(
        [np.concatenate([cosine, sine], axis=1), np.concatenate([-sine, cosine], axis=1)], axis=0
    )
    box_across = np.concatenate([cosine[:box_edge], -sine[:box_edge]], axis=1)
    box_down = np.concatenate(
        [
            np.concatenate([cosine[:, :box_edge], sine[:, :box_edge]], axis=1),
            np.concatenate([-sine[:, :box_edge], cosine[:, :box_edge]], axis=1),
        ],
        axis=0,
    )
    return {
        name: jnp.asarray(value)
        for name, value in (
            ("across", across),
            ("mix", mix),
            ("box_across", box_across),
            ("box_down", box_down),
        )
    }


def pick_rows(chosen, source):
    counter = jnp.arange(source.shape[0], dtype=jnp.int32)
    selector = (chosen[:, None] == counter[None, :]).astype(source.dtype)
    flat = source.reshape(source.shape[0], -1)
    picked = jnp.dot(selector, flat, preferred_element_type=jnp.float32).astype(source.dtype)
    return picked.reshape((chosen.shape[0],) + source.shape[1:])


def pick_kernel(index_ref, table_ref, out_ref, picked_ref):
    columns = table_ref.shape[0]
    rows_in_table = table_ref.shape[1]
    lanes = index_ref.shape[1]
    shift = columns.bit_length() - 1

    def body(step, carry):
        index = index_ref[pl.ds(step, 1), :]
        high = jnp.right_shift(index, shift)
        low = jnp.bitwise_and(index, columns - 1)
        row_hot = (lax.broadcasted_iota(jnp.int32, (rows_in_table, lanes), 0) == high).astype(
            jnp.bfloat16
        )
        picked_rows = jnp.dot(table_ref[...], row_hot, preferred_element_type=jnp.float32)
        column_hot = lax.broadcasted_iota(jnp.int32, (columns, lanes), 0) == low
        chosen = jnp.where(column_hot, picked_rows, 0.0)
        picked_ref[pl.ds(step, 1), :] = jnp.sum(chosen, axis=0, keepdims=True)
        return carry

    lax.fori_loop(0, index_ref.shape[0], body, 0)
    out_ref[...] = picked_ref[...].astype(out_ref.dtype)


def sample_template(template_volume, rotation_samples):
    total = template_volume.size
    columns = 512
    table_t = template_volume.reshape(total // columns, columns).T.astype(jnp.bfloat16)
    return pl.pallas_call(
        pick_kernel,
        out_shape=jax.ShapeDtypeStruct(rotation_samples.shape, jnp.bfloat16),
        in_specs=[pl.BlockSpec(memory_space=pltpu.VMEM)] * 2,
        out_specs=pl.BlockSpec(memory_space=pltpu.VMEM),
        scratch_shapes=[pltpu.VMEM(rotation_samples.shape, jnp.float32)],
    )(rotation_samples, table_t)


def share_samples(template_volume, rotation_samples, tiles_half):
    sampled_part = sample_template(template_volume, rotation_samples)
    slab_count = lax.axis_size("slab")
    slot = lax.axis_index("slab")
    held = sampled_part[None]
    length = tiles_half.shape[-1]
    count = sampled_part.size
    bit = 0
    partner_tiles = None
    if slab_count > 1 and count % length == 0 and count // length <= length:
        rows = count // length
        packed = jnp.pad(
            sampled_part.reshape(1, 1, rows, length),
            ((0, 0), (0, tiles_half.shape[1] - 1), (0, length - rows), (0, 0)),
        )
        received = partner(jnp.concatenate([tiles_half, packed], axis=0), "slab", 0)
        partner_tiles = received[:-1]
        moved = received[-1, 0, :rows].reshape(held.shape)
        held = jnp.concatenate([held, moved], axis=0)
        bit = 1
    while (1 << bit) < slab_count:
        held = jnp.concatenate([held, partner(held, "slab", bit)], axis=0)
        bit += 1
    if partner_tiles is None:
        partner_tiles = partner(tiles_half, "slab", 0)
    order = jnp.bitwise_xor(jnp.arange(slab_count, dtype=jnp.int32), slot)
    return pick_rows(order, held), partner_tiles


def rows_to_blocks(values, rows):
    count = values.shape[0] // rows
    return jnp.concatenate([values[i * rows : (i + 1) * rows] for i in range(count)], axis=1)


def blocks_to_rows(values, width):
    count = values.shape[1] // width
    return jnp.concatenate(
        [values[:, i * width : (i + 1) * width] for i in range(count)], axis=0
    )


def forward_rows(values, across, down):
    width = across.shape[1] // 2
    height = down.shape[1] // 2
    first = jnp.dot(values, across, preferred_element_type=jnp.float32).astype(jnp.bfloat16)
    stacked = jnp.concatenate(
        [rows_to_blocks(first[:, :width], height), rows_to_blocks(first[:, width:], height)],
        axis=0,
    )
    second = jnp.dot(down, stacked, preferred_element_type=jnp.float32).astype(jnp.bfloat16)
    return second[:width], second[width:]


def inverse_blocks(real_part, imag_part, mix, back):
    length = real_part.shape[0]
    joined = jnp.concatenate(
        [blocks_to_rows(real_part, length), blocks_to_rows(imag_part, length)], axis=1
    )
    first = jnp.dot(joined, mix, preferred_element_type=jnp.float32).astype(jnp.bfloat16)
    stacked = jnp.concatenate(
        [rows_to_blocks(first[:, :length], length), rows_to_blocks(first[:, length:], length)],
        axis=0,
    )
    return jnp.dot(back, stacked, preferred_element_type=jnp.float32)


def template_kernel(values_ref, across_ref, down_ref, real_ref, imag_ref):
    real_part, imag_part = forward_rows(values_ref[...], across_ref[...], down_ref[...])
    real_ref[...] = real_part.astype(jnp.float32)
    imag_ref[...] = imag_part.astype(jnp.float32)


def split_three(values):
    high = values.astype(jnp.bfloat16)
    rest = values - high.astype(jnp.float32)
    middle = rest.astype(jnp.bfloat16)
    low = (rest - middle.astype(jnp.float32)).astype(jnp.bfloat16)
    return (high, middle, low)


def exact_dot(left, right, left_exact):
    total = None
    if left_exact:
        for part in split_three(right):
            term = jnp.dot(left, part, preferred_element_type=jnp.float32)
            total = term if total is None else total + term
    else:
        for part in split_three(left):
            term = jnp.dot(part, right, preferred_element_type=jnp.float32)
            total = term if total is None else total + term
    return total


def field_kernel(
    values_ref, wedge_ref, across_ref, mix_ref, back_ref, band_ref, band_t_ref, real_ref,
    imag_ref, rms_ref, *, box_edge
):
    length = values_ref.shape[-1]
    maps = values_ref.shape[0] // length
    tiles = rms_ref.shape[0]
    planes = maps // tiles
    mix = mix_ref[...]
    real_part, imag_part = forward_rows(values_ref[...], across_ref[...], mix)
    wedge = jnp.concatenate([wedge_ref[...]] * maps, axis=1)
    field = inverse_blocks(real_part * wedge, imag_part * wedge, mix, back_ref[...])
    field = (field * (1.0 / (length * length))).astype(jnp.bfloat16)
    square = jnp.square(field.astype(jnp.float32))
    energies = []
    for tile in range(tiles):
        energy = None
        for plane in range(planes):
            index = tile * planes + plane
            part = square[:, index * length : (index + 1) * length]
            energy = part if energy is None else energy + part
        energies.append(energy)
    energy = jnp.concatenate(energies, axis=1)
    summed = exact_dot(band_ref[...], energy, True)
    summed = exact_dot(blocks_to_rows(summed, length), band_t_ref[...], False)
    for tile in range(tiles):
        part = summed[tile * length : (tile + 1) * length]
        rms_ref[tile] = jnp.sqrt(part / (box_edge * box_edge * planes) + 1e-05)
    real_part, imag_part = forward_rows(blocks_to_rows(field, length), across_ref[...], mix)
    real_ref[...] = real_part.astype(jnp.float32)
    imag_ref[...] = imag_part.astype(jnp.float32)


def whole_call(kernel, out_shape, *args):
    return pl.pallas_call(
        kernel,
        out_shape=out_shape,
        in_specs=[pl.BlockSpec(memory_space=pltpu.VMEM)] * len(args),
        out_specs=tuple(pl.BlockSpec(memory_space=pltpu.VMEM) for _ in out_shape),
    )(*args)


def make_templates(sampled, box_edge, planes, table):
    count = sampled.shape[1]
    length = table["across"].shape[0]
    sampled = jnp.transpose(sampled, (1, 0, 2))
    sampled = sampled.reshape(count, planes, box_edge, box_edge)
    template_norm = jnp.sqrt(
        jnp.sum(jnp.square(sampled.astype(jnp.float32)), axis=(1, 2, 3)) + 1e-05
    )
    spec_shape = jax.ShapeDtypeStruct((length, count * planes * length), jnp.float32)
    spec_real, spec_imag = whole_call(
        template_kernel,
        (spec_shape, spec_shape),
        sampled.reshape(count * planes * box_edge, box_edge),
        table["box_across"],
        table["box_down"],
    )
    return (spec_real, spec_imag, template_norm)


def field_spectra(gathered, wedge_weight, table, band_sum, box_edge):
    tiles, planes, length, _ = gathered.shape
    spec_shape = jax.ShapeDtypeStruct((length, tiles * planes * length), jnp.float32)
    return whole_call(
        functools.partial(field_kernel, box_edge=box_edge),
        (spec_shape, spec_shape, jax.ShapeDtypeStruct((tiles, length, length), jnp.float32)),
        gathered.reshape(tiles * planes * length, length),
        wedge_weight,
        table["across"],
        table["mix"],
        table["across"],
        band_sum.astype(jnp.bfloat16),
        band_sum.T.astype(jnp.bfloat16),
    )


def score_kernel(
    scale_ref, field_re_ref, field_im_ref, templ_re_ref, templ_im_ref, mix_ref, back_ref,
    rms_ref, out_ref
):
    length = field_re_ref.shape[0]
    per_step = rms_ref.shape[0]
    planes = field_re_ref.shape[1] // (per_step * length)
    count = templ_re_ref.shape[1] // (planes * length)
    group = 8 if count % 8 == 0 else 1

    def lanes(index):
        return slice(index * length, (index + 1) * length)

    for tile in range(per_step):
        best = None
        for step in range(count // group):
            joined = []
            for member in range(group):
                orient = step * group + member
                prod_re = None
                prod_im = None
                for plane in range(planes):
                    fr = field_re_ref[:, lanes(tile * planes + plane)]
                    fi = field_im_ref[:, lanes(tile * planes + plane)]
                    tr = templ_re_ref[:, lanes(orient * planes + plane)]
                    ti = templ_im_ref[:, lanes(orient * planes + plane)]
                    part_re = fr * tr + fi * ti
                    part_im = fi * tr - fr * ti
                    prod_re = part_re if prod_re is None else prod_re + part_re
                    prod_im = part_im if prod_im is None else prod_im + part_im
                joined.append(
                    jnp.concatenate(
                        [prod_re.astype(jnp.bfloat16), prod_im.astype(jnp.bfloat16)], axis=1
                    )
                )
            joined = jnp.concatenate(joined, axis=0)
            first = jnp.dot(joined, mix_ref[...], preferred_element_type=jnp.float32).astype(
                jnp.bfloat16
            )
            stacked = jnp.concatenate(
                [
                    rows_to_blocks(first[:, :length], length),
                    rows_to_blocks(first[:, length:], length),
                ],
                axis=0,
            )
            corr = jnp.dot(back_ref[...], stacked, preferred_element_type=jnp.float32)
            for member in range(group):
                orient = step * group + member
                value = corr[:, lanes(member)] * scale_ref[orient]
                best = value if best is None else jnp.maximum(best, value)
        out_ref[tile] = (best / rms_ref[tile]).astype(out_ref.dtype)


def score_tiles(
    field_real, field_imag, local_rms, templ_real, templ_imag, template_norm, table
):
    length = field_real.shape[0]
    planes = field_real.shape[1] // (local_rms.shape[0] * length)
    scale = (1.0 / template_norm) * (1.0 / (length * length))
    mix = table["mix"]
    back = table["across"]
    tiles = local_rms.shape[0]
    per_step = 2 if tiles % 2 == 0 else 1
    tile_block = pl.BlockSpec((length, per_step * planes * length), lambda t: (0, t))
    templ_block = pl.BlockSpec(templ_real.shape, lambda t: (0, 0))
    return pl.pallas_call(
        score_kernel,
        grid=(tiles // per_step,),
        out_shape=jax.ShapeDtypeStruct((tiles, length, length), jnp.bfloat16),
        in_specs=[
            pl.BlockSpec(memory_space=pltpu.SMEM),
            tile_block,
            tile_block,
            templ_block,
            templ_block,
            pl.BlockSpec((2 * length, 2 * length), lambda t: (0, 0)),
            pl.BlockSpec((length, 2 * length), lambda t: (0, 0)),
            pl.BlockSpec((per_step, length, length), lambda t: (t, 0, 0)),
        ],
        out_specs=pl.BlockSpec((per_step, length, length), lambda t: (t, 0, 0)),
    )(
        scale,
        field_real,
        field_imag,
        templ_real,
        templ_imag,
        mix,
        back,
        local_rms,
    )


def orient_max(best):
    groups = lax.axis_size("orient")
    parts = lax.all_to_all(best, "orient", split_axis=1, concat_axis=0, tiled=True)
    stacked = parts.reshape(groups, best.shape[0], parts.shape[1], parts.shape[2])
    return jnp.max(stacked, axis=0)


def per_device(tiles, assigned_worker, wedge_mask, template_volume, rotation_samples):
    tile_len = tiles.shape[-1]
    planes = tiles.shape[1]
    home_slots = tiles.shape[0]
    work_slots = home_slots // 2
    box_edge = template_volume.shape[0]
    table = transform_tables(tile_len, box_edge)
    band_sum = band_table(tile_len, box_edge)
    wedge_weight = wedge_mask.astype(jnp.bfloat16)
    sampled, partner_tiles = share_samples(template_volume, rotation_samples, tiles[work_slots:])
    occupied = assigned_worker >= 0
    own_count = jnp.sum(occupied.astype(jnp.int32))
    counter = jnp.arange(work_slots, dtype=jnp.int32)
    keep_own = (counter < own_count)[:, None, None, None]
    moved_in = pick_rows(counter - own_count, partner_tiles)
    gathered = jnp.where(keep_own, tiles[:work_slots], moved_in)
    field_real, field_imag, local_rms = field_spectra(
        gathered, wedge_weight, table, band_sum, box_edge
    )
    templ_real, templ_imag, template_norm = make_templates(sampled, box_edge, planes, table)
    best = score_tiles(
        field_real,
        field_imag,
        local_rms,
        templ_real,
        templ_imag,
        template_norm,
        table,
    )
    best_rows = orient_max(best)
    outgoing = pick_rows(counter + own_count, best_rows)
    returned = partner(outgoing, "slab", 0)
    result = jnp.concatenate([best_rows, returned], axis=0)
    return jnp.where(occupied[:, None, None], result, jnp.zeros_like(result))


def solution(mesh):
    return jax.shard_map(
        per_device,
        mesh=mesh,
        in_specs=(P("slab", None, None, None), P("slab"), P(), P(), P("orient", "slab")),
        out_specs=P("slab", "orient", None),
        check_vma=False,
    )
```

```python
import functools
import math

import jax
import ml_dtypes
import numpy as np
import jax.numpy as jnp
from jax import lax
from jax.experimental import pallas as pl
from jax.experimental.pallas import tpu as pltpu
from jax.sharding import PartitionSpec as P


def partner(block, axis, bit):
    count = lax.axis_size(axis)
    route = []
    for low in range(count):
        high = low | 1 << bit
        if high != low and high < count:
            route += [(low, high), (high, low)]
    return lax.ppermute(block, axis, route)


def tables(length):
    counter = np.arange(length, dtype=np.int32)
    angles = (counter[:, None] * counter[None, :] % length).astype(np.float32) * np.float32(
        2.0 * math.pi / length
    )
    wide = angles.astype(np.float64)
    cosine = np.cos(wide).astype(np.float32).astype(ml_dtypes.bfloat16)
    sine = np.sin(wide).astype(np.float32).astype(ml_dtypes.bfloat16)
    return cosine, sine


def band_table(length, box_edge):
    counter = np.arange(length, dtype=np.int32)
    offsets = (counter[None, :] - counter[:, None]) % length
    return jnp.asarray((offsets < box_edge).astype(np.float32))


def transform_tables(length, box_edge):
    cosine, sine = tables(length)
    across = np.concatenate([cosine, -sine], axis=1)
    mix = np.concatenate(
        [np.concatenate([cosine, sine], axis=1), np.concatenate([-sine, cosine], axis=1)], axis=0
    )
    box_across = np.concatenate([cosine[:box_edge], -sine[:box_edge]], axis=1)
    box_down = np.concatenate(
        [
            np.concatenate([cosine[:, :box_edge], sine[:, :box_edge]], axis=1),
            np.concatenate([-sine[:, :box_edge], cosine[:, :box_edge]], axis=1),
        ],
        axis=0,
    )
    return {
        name: jnp.asarray(value)
        for name, value in (
            ("across", across),
            ("mix", mix),
            ("box_across", box_across),
            ("box_down", box_down),
        )
    }


def pick_rows(chosen, source):
    counter = jnp.arange(source.shape[0], dtype=jnp.int32)
    selector = (chosen[:, None] == counter[None, :]).astype(source.dtype)
    flat = source.reshape(source.shape[0], -1)
    picked = jnp.dot(selector, flat, preferred_element_type=jnp.float32).astype(source.dtype)
    return picked.reshape((chosen.shape[0],) + source.shape[1:])


def pick_kernel(index_ref, table_ref, out_ref, picked_ref):
    columns = table_ref.shape[0]
    rows_in_table = table_ref.shape[1]
    lanes = index_ref.shape[1]
    shift = columns.bit_length() - 1

    def body(step, carry):
        index = index_ref[pl.ds(step, 1), :]
        high = jnp.right_shift(index, shift)
        low = jnp.bitwise_and(index, columns - 1)
        row_hot = (lax.broadcasted_iota(jnp.int32, (rows_in_table, lanes), 0) == high).astype(
            jnp.bfloat16
        )
        picked_rows = jnp.dot(table_ref[...], row_hot, preferred_element_type=jnp.float32)
        column_hot = lax.broadcasted_iota(jnp.int32, (columns, lanes), 0) == low
        chosen = jnp.where(column_hot, picked_rows, 0.0)
        picked_ref[pl.ds(step, 1), :] = jnp.sum(chosen, axis=0, keepdims=True)
        return carry

    lax.fori_loop(0, index_ref.shape[0], body, 0)
    out_ref[...] = picked_ref[...].astype(out_ref.dtype)


def sample_template(template_volume, rotation_samples):
    total = template_volume.size
    columns = 512
    table_t = template_volume.reshape(total // columns, columns).T.astype(jnp.bfloat16)
    return pl.pallas_call(
        pick_kernel,
        out_shape=jax.ShapeDtypeStruct(rotation_samples.shape, jnp.bfloat16),
        in_specs=[pl.BlockSpec(memory_space=pltpu.VMEM)] * 2,
        out_specs=pl.BlockSpec(memory_space=pltpu.VMEM),
        scratch_shapes=[pltpu.VMEM(rotation_samples.shape, jnp.float32)],
    )(rotation_samples, table_t)


def share_samples(template_volume, rotation_samples):
    sampled_part = sample_template(template_volume, rotation_samples)
    slab_count = lax.axis_size("slab")
    slot = lax.axis_index("slab")
    held = sampled_part[None]
    bit = 0
    while (1 << bit) < slab_count:
        held = jnp.concatenate([held, partner(held, "slab", bit)], axis=0)
        bit += 1
    order = jnp.bitwise_xor(jnp.arange(slab_count, dtype=jnp.int32), slot)
    return pick_rows(order, held)


def rows_to_blocks(values, rows):
    count = values.shape[0] // rows
    return jnp.concatenate([values[i * rows : (i + 1) * rows] for i in range(count)], axis=1)


def blocks_to_rows(values, width):
    count = values.shape[1] // width
    return jnp.concatenate(
        [values[:, i * width : (i + 1) * width] for i in range(count)], axis=0
    )


def forward_rows(values, across, down):
    width = across.shape[1] // 2
    height = down.shape[1] // 2
    first = jnp.dot(values, across, preferred_element_type=jnp.float32).astype(jnp.bfloat16)
    stacked = jnp.concatenate(
        [rows_to_blocks(first[:, :width], height), rows_to_blocks(first[:, width:], height)],
        axis=0,
    )
    second = jnp.dot(down, stacked, preferred_element_type=jnp.float32).astype(jnp.bfloat16)
    return second[:width], second[width:]


def inverse_blocks(real_part, imag_part, mix, back):
    length = real_part.shape[0]
    joined = jnp.concatenate(
        [blocks_to_rows(real_part, length), blocks_to_rows(imag_part, length)], axis=1
    )
    first = jnp.dot(joined, mix, preferred_element_type=jnp.float32).astype(jnp.bfloat16)
    stacked = jnp.concatenate(
        [rows_to_blocks(first[:, :length], length), rows_to_blocks(first[:, length:], length)],
        axis=0,
    )
    return jnp.dot(back, stacked, preferred_element_type=jnp.float32)


def template_kernel(values_ref, across_ref, down_ref, real_ref, imag_ref):
    real_part, imag_part = forward_rows(values_ref[...], across_ref[...], down_ref[...])
    real_ref[...] = real_part.astype(jnp.float32)
    imag_ref[...] = imag_part.astype(jnp.float32)


def split_three(values):
    high = values.astype(jnp.bfloat16)
    rest = values - high.astype(jnp.float32)
    middle = rest.astype(jnp.bfloat16)
    low = (rest - middle.astype(jnp.float32)).astype(jnp.bfloat16)
    return (high, middle, low)


def exact_dot(left, right, left_exact):
    total = None
    if left_exact:
        for part in split_three(right):
            term = jnp.dot(left, part, preferred_element_type=jnp.float32)
            total = term if total is None else total + term
    else:
        for part in split_three(left):
            term = jnp.dot(part, right, preferred_element_type=jnp.float32)
            total = term if total is None else total + term
    return total


def field_kernel(
    values_ref, wedge_ref, across_ref, mix_ref, back_ref, band_ref, band_t_ref, real_ref,
    imag_ref, rms_ref, *, box_edge
):
    length = values_ref.shape[-1]
    maps = values_ref.shape[0] // length
    tiles = rms_ref.shape[0]
    planes = maps // tiles
    mix = mix_ref[...]
    real_part, imag_part = forward_rows(values_ref[...], across_ref[...], mix)
    wedge = jnp.concatenate([wedge_ref[...]] * maps, axis=1)
    field = inverse_blocks(real_part * wedge, imag_part * wedge, mix, back_ref[...])
    field = (field * (1.0 / (length * length))).astype(jnp.bfloat16)
    square = jnp.square(field.astype(jnp.float32))
    energies = []
    for tile in range(tiles):
        energy = None
        for plane in range(planes):
            index = tile * planes + plane
            part = square[:, index * length : (index + 1) * length]
            energy = part if energy is None else energy + part
        energies.append(energy)
    energy = jnp.concatenate(energies, axis=1)
    summed = exact_dot(band_ref[...], energy, True)
    summed = exact_dot(blocks_to_rows(summed, length), band_t_ref[...], False)
    for tile in range(tiles):
        part = summed[tile * length : (tile + 1) * length]
        rms_ref[tile] = jnp.sqrt(part / (box_edge * box_edge * planes) + 1e-05)
    real_part, imag_part = forward_rows(blocks_to_rows(field, length), across_ref[...], mix)
    real_ref[...] = real_part.astype(jnp.float32)
    imag_ref[...] = imag_part.astype(jnp.float32)


def whole_call(kernel, out_shape, *args):
    return pl.pallas_call(
        kernel,
        out_shape=out_shape,
        in_specs=[pl.BlockSpec(memory_space=pltpu.VMEM)] * len(args),
        out_specs=tuple(pl.BlockSpec(memory_space=pltpu.VMEM) for _ in out_shape),
    )(*args)


def make_templates(sampled, box_edge, planes, table):
    count = sampled.shape[1]
    length = table["across"].shape[0]
    sampled = jnp.transpose(sampled, (1, 0, 2))
    sampled = sampled.reshape(count, planes, box_edge, box_edge)
    template_norm = jnp.sqrt(
        jnp.sum(jnp.square(sampled.astype(jnp.float32)), axis=(1, 2, 3)) + 1e-05
    )
    spec_shape = jax.ShapeDtypeStruct((length, count * planes * length), jnp.float32)
    spec_real, spec_imag = whole_call(
        template_kernel,
        (spec_shape, spec_shape),
        sampled.reshape(count * planes * box_edge, box_edge),
        table["box_across"],
        table["box_down"],
    )
    return (spec_real, spec_imag, template_norm)


def field_spectra(gathered, wedge_weight, table, band_sum, box_edge):
    tiles, planes, length, _ = gathered.shape
    spec_shape = jax.ShapeDtypeStruct((length, tiles * planes * length), jnp.float32)
    return whole_call(
        functools.partial(field_kernel, box_edge=box_edge),
        (spec_shape, spec_shape, jax.ShapeDtypeStruct((tiles, length, length), jnp.float32)),
        gathered.reshape(tiles * planes * length, length),
        wedge_weight,
        table["across"],
        table["mix"],
        table["across"],
        band_sum.astype(jnp.bfloat16),
        band_sum.T.astype(jnp.bfloat16),
    )


def score_kernel(
    scale_ref, field_re_ref, field_im_ref, templ_re_ref, templ_im_ref, mix_ref, back_ref,
    rms_ref, out_ref
):
    length = field_re_ref.shape[0]
    per_step = rms_ref.shape[0]
    planes = field_re_ref.shape[1] // (per_step * length)
    count = templ_re_ref.shape[1] // (planes * length)
    group = 8 if count % 8 == 0 else 1

    def lanes(index):
        return slice(index * length, (index + 1) * length)

    for tile in range(per_step):
        best = None
        for step in range(count // group):
            joined = []
            for member in range(group):
                orient = step * group + member
                prod_re = None
                prod_im = None
                for plane in range(planes):
                    fr = field_re_ref[:, lanes(tile * planes + plane)]
                    fi = field_im_ref[:, lanes(tile * planes + plane)]
                    tr = templ_re_ref[:, lanes(orient * planes + plane)]
                    ti = templ_im_ref[:, lanes(orient * planes + plane)]
                    part_re = fr * tr + fi * ti
                    part_im = fi * tr - fr * ti
                    prod_re = part_re if prod_re is None else prod_re + part_re
                    prod_im = part_im if prod_im is None else prod_im + part_im
                joined.append(
                    jnp.concatenate(
                        [prod_re.astype(jnp.bfloat16), prod_im.astype(jnp.bfloat16)], axis=1
                    )
                )
            joined = jnp.concatenate(joined, axis=0)
            first = jnp.dot(joined, mix_ref[...], preferred_element_type=jnp.float32).astype(
                jnp.bfloat16
            )
            stacked = jnp.concatenate(
                [
                    rows_to_blocks(first[:, :length], length),
                    rows_to_blocks(first[:, length:], length),
                ],
                axis=0,
            )
            corr = jnp.dot(back_ref[...], stacked, preferred_element_type=jnp.float32)
            for member in range(group):
                orient = step * group + member
                value = corr[:, lanes(member)] * scale_ref[orient]
                best = value if best is None else jnp.maximum(best, value)
        result = (best / rms_ref[tile]).astype(out_ref.dtype)
        chunk = out_ref.shape[2]
        for part in range(out_ref.shape[0]):
            out_ref[part, tile] = result[part * chunk : (part + 1) * chunk]


def score_tiles(
    field_real, field_imag, local_rms, templ_real, templ_imag, template_norm, table
):
    length = field_real.shape[0]
    planes = field_real.shape[1] // (local_rms.shape[0] * length)
    scale = (1.0 / template_norm) * (1.0 / (length * length))
    mix = table["mix"]
    back = table["across"]
    tiles = local_rms.shape[0]
    groups = lax.axis_size("orient")
    per_step = 2 if tiles % 2 == 0 else 1
    tile_block = pl.BlockSpec((length, per_step * planes * length), lambda t: (0, t))
    templ_block = pl.BlockSpec(templ_real.shape, lambda t: (0, 0))
    return pl.pallas_call(
        score_kernel,
        grid=(tiles // per_step,),
        out_shape=jax.ShapeDtypeStruct((groups, tiles, length // groups, length), jnp.bfloat16),
        in_specs=[
            pl.BlockSpec(memory_space=pltpu.SMEM),
            tile_block,
            tile_block,
            templ_block,
            templ_block,
            pl.BlockSpec((2 * length, 2 * length), lambda t: (0, 0)),
            pl.BlockSpec((length, 2 * length), lambda t: (0, 0)),
            pl.BlockSpec((per_step, length, length), lambda t: (t, 0, 0)),
        ],
        out_specs=pl.BlockSpec(
            (groups, per_step, length // groups, length), lambda t: (0, t, 0, 0)
        ),
    )(
        scale,
        field_real,
        field_imag,
        templ_real,
        templ_imag,
        mix,
        back,
        local_rms,
    )


def orient_max(best):
    parts = lax.all_to_all(best, "orient", split_axis=0, concat_axis=0, tiled=True)
    return jnp.max(parts, axis=0)


def per_device(tiles, assigned_worker, wedge_mask, template_volume, rotation_samples):
    tile_len = tiles.shape[-1]
    planes = tiles.shape[1]
    home_slots = tiles.shape[0]
    work_slots = home_slots // 2
    box_edge = template_volume.shape[0]
    table = transform_tables(tile_len, box_edge)
    band_sum = band_table(tile_len, box_edge)
    wedge_weight = wedge_mask.astype(jnp.bfloat16)
    sampled = share_samples(template_volume, rotation_samples)
    partner_tiles = partner(tiles[work_slots:], "slab", 0)
    occupied = assigned_worker >= 0
    own_count = jnp.sum(occupied.astype(jnp.int32))
    counter = jnp.arange(work_slots, dtype=jnp.int32)
    keep_own = (counter < own_count)[:, None, None, None]
    moved_in = pick_rows(counter - own_count, partner_tiles)
    gathered = jnp.where(keep_own, tiles[:work_slots], moved_in)
    field_real, field_imag, local_rms = field_spectra(
        gathered, wedge_weight, table, band_sum, box_edge
    )
    templ_real, templ_imag, template_norm = make_templates(sampled, box_edge, planes, table)
    best = score_tiles(
        field_real,
        field_imag,
        local_rms,
        templ_real,
        templ_imag,
        template_norm,
        table,
    )
    best_rows = orient_max(best)
    outgoing = pick_rows(counter + own_count, best_rows)
    returned = partner(outgoing, "slab", 0)
    result = jnp.concatenate([best_rows, returned], axis=0)
    return jnp.where(occupied[:, None, None], result, jnp.zeros_like(result))


def solution(mesh):
    return jax.shard_map(
        per_device,
        mesh=mesh,
        in_specs=(P("slab", None, None, None), P("slab"), P(), P(), P("orient", "slab")),
        out_specs=P("slab", "orient", None),
        check_vma=False,
    )
```

```python
import functools
import math

import jax
import ml_dtypes
import numpy as np
import jax.numpy as jnp
from jax import lax
from jax.experimental import pallas as pl
from jax.experimental.pallas import tpu as pltpu
from jax.sharding import PartitionSpec as P


def partner(block, axis, bit):
    count = lax.axis_size(axis)
    route = []
    for low in range(count):
        high = low | 1 << bit
        if high != low and high < count:
            route += [(low, high), (high, low)]
    return lax.ppermute(block, axis, route)


def tables(length):
    counter = np.arange(length, dtype=np.int32)
    angles = (counter[:, None] * counter[None, :] % length).astype(np.float32) * np.float32(
        2.0 * math.pi / length
    )
    wide = angles.astype(np.float64)
    cosine = np.cos(wide).astype(np.float32).astype(ml_dtypes.bfloat16)
    sine = np.sin(wide).astype(np.float32).astype(ml_dtypes.bfloat16)
    return cosine, sine


def band_table(length, box_edge):
    counter = np.arange(length, dtype=np.int32)
    offsets = (counter[None, :] - counter[:, None]) % length
    return jnp.asarray((offsets < box_edge).astype(np.float32))


def transform_tables(length, box_edge):
    cosine, sine = tables(length)
    across = np.concatenate([cosine, -sine], axis=1)
    mix = np.concatenate(
        [np.concatenate([cosine, sine], axis=1), np.concatenate([-sine, cosine], axis=1)], axis=0
    )
    box_across = np.concatenate([cosine[:box_edge], -sine[:box_edge]], axis=1)
    box_down = np.concatenate(
        [
            np.concatenate([cosine[:, :box_edge], sine[:, :box_edge]], axis=1),
            np.concatenate([-sine[:, :box_edge], cosine[:, :box_edge]], axis=1),
        ],
        axis=0,
    )
    return {
        name: jnp.asarray(value)
        for name, value in (
            ("across", across),
            ("mix", mix),
            ("box_across", box_across),
            ("box_down", box_down),
        )
    }


def pick_rows(chosen, source):
    counter = jnp.arange(source.shape[0], dtype=jnp.int32)
    selector = (chosen[:, None] == counter[None, :]).astype(source.dtype)
    flat = source.reshape(source.shape[0], -1)
    picked = jnp.dot(selector, flat, preferred_element_type=jnp.float32).astype(source.dtype)
    return picked.reshape((chosen.shape[0],) + source.shape[1:])


def pick_kernel(index_ref, table_ref, out_ref, picked_ref):
    columns = table_ref.shape[0]
    rows_in_table = table_ref.shape[1]
    lanes = index_ref.shape[1]
    shift = columns.bit_length() - 1

    def body(step, carry):
        index = index_ref[pl.ds(step, 1), :]
        high = jnp.right_shift(index, shift)
        low = jnp.bitwise_and(index, columns - 1)
        row_hot = (lax.broadcasted_iota(jnp.int32, (rows_in_table, lanes), 0) == high).astype(
            jnp.bfloat16
        )
        picked_rows = jnp.dot(table_ref[...], row_hot, preferred_element_type=jnp.float32)
        column_hot = lax.broadcasted_iota(jnp.int32, (columns, lanes), 0) == low
        chosen = jnp.where(column_hot, picked_rows, 0.0)
        picked_ref[pl.ds(step, 1), :] = jnp.sum(chosen, axis=0, keepdims=True)
        return carry

    lax.fori_loop(0, index_ref.shape[0], body, 0)
    out_ref[...] = picked_ref[...].astype(out_ref.dtype)


def sample_template(template_volume, rotation_samples):
    total = template_volume.size
    columns = 512
    table_t = template_volume.reshape(total // columns, columns).T.astype(jnp.bfloat16)
    return pl.pallas_call(
        pick_kernel,
        out_shape=jax.ShapeDtypeStruct(rotation_samples.shape, jnp.bfloat16),
        in_specs=[pl.BlockSpec(memory_space=pltpu.VMEM)] * 2,
        out_specs=pl.BlockSpec(memory_space=pltpu.VMEM),
        scratch_shapes=[pltpu.VMEM(rotation_samples.shape, jnp.float32)],
    )(rotation_samples, table_t)


def share_samples(template_volume, rotation_samples):
    sampled_part = sample_template(template_volume, rotation_samples)
    slab_count = lax.axis_size("slab")
    spread = jnp.broadcast_to(sampled_part[None], (slab_count,) + sampled_part.shape)
    return lax.all_to_all(spread, "slab", 0, 0, tiled=True)


def rows_to_blocks(values, rows):
    count = values.shape[0] // rows
    return jnp.concatenate([values[i * rows : (i + 1) * rows] for i in range(count)], axis=1)


def blocks_to_rows(values, width):
    count = values.shape[1] // width
    return jnp.concatenate(
        [values[:, i * width : (i + 1) * width] for i in range(count)], axis=0
    )


def forward_rows(values, across, down):
    width = across.shape[1] // 2
    height = down.shape[1] // 2
    first = jnp.dot(values, across, preferred_element_type=jnp.float32).astype(jnp.bfloat16)
    stacked = jnp.concatenate(
        [rows_to_blocks(first[:, :width], height), rows_to_blocks(first[:, width:], height)],
        axis=0,
    )
    second = jnp.dot(down, stacked, preferred_element_type=jnp.float32).astype(jnp.bfloat16)
    return second[:width], second[width:]


def inverse_blocks(real_part, imag_part, mix, back):
    length = real_part.shape[0]
    joined = jnp.concatenate(
        [blocks_to_rows(real_part, length), blocks_to_rows(imag_part, length)], axis=1
    )
    first = jnp.dot(joined, mix, preferred_element_type=jnp.float32).astype(jnp.bfloat16)
    stacked = jnp.concatenate(
        [rows_to_blocks(first[:, :length], length), rows_to_blocks(first[:, length:], length)],
        axis=0,
    )
    return jnp.dot(back, stacked, preferred_element_type=jnp.float32)


def template_kernel(values_ref, across_ref, down_ref, real_ref, imag_ref):
    real_part, imag_part = forward_rows(values_ref[...], across_ref[...], down_ref[...])
    real_ref[...] = real_part.astype(jnp.float32)
    imag_ref[...] = imag_part.astype(jnp.float32)


def split_three(values):
    high = values.astype(jnp.bfloat16)
    rest = values - high.astype(jnp.float32)
    middle = rest.astype(jnp.bfloat16)
    low = (rest - middle.astype(jnp.float32)).astype(jnp.bfloat16)
    return (high, middle, low)


def exact_dot(left, right, left_exact):
    total = None
    if left_exact:
        for part in split_three(right):
            term = jnp.dot(left, part, preferred_element_type=jnp.float32)
            total = term if total is None else total + term
    else:
        for part in split_three(left):
            term = jnp.dot(part, right, preferred_element_type=jnp.float32)
            total = term if total is None else total + term
    return total


def field_kernel(
    values_ref, wedge_ref, across_ref, mix_ref, back_ref, band_ref, band_t_ref, real_ref,
    imag_ref, rms_ref, *, box_edge
):
    length = values_ref.shape[-1]
    maps = values_ref.shape[0] // length
    tiles = rms_ref.shape[0]
    planes = maps // tiles
    mix = mix_ref[...]
    real_part, imag_part = forward_rows(values_ref[...], across_ref[...], mix)
    wedge = jnp.concatenate([wedge_ref[...]] * maps, axis=1)
    field = inverse_blocks(real_part * wedge, imag_part * wedge, mix, back_ref[...])
    field = (field * (1.0 / (length * length))).astype(jnp.bfloat16)
    square = jnp.square(field.astype(jnp.float32))
    energies = []
    for tile in range(tiles):
        energy = None
        for plane in range(planes):
            index = tile * planes + plane
            part = square[:, index * length : (index + 1) * length]
            energy = part if energy is None else energy + part
        energies.append(energy)
    energy = jnp.concatenate(energies, axis=1)
    summed = exact_dot(band_ref[...], energy, True)
    summed = exact_dot(blocks_to_rows(summed, length), band_t_ref[...], False)
    for tile in range(tiles):
        part = summed[tile * length : (tile + 1) * length]
        rms_ref[tile] = jnp.sqrt(part / (box_edge * box_edge * planes) + 1e-05)
    real_part, imag_part = forward_rows(blocks_to_rows(field, length), across_ref[...], mix)
    real_ref[...] = real_part.astype(jnp.float32)
    imag_ref[...] = imag_part.astype(jnp.float32)


def whole_call(kernel, out_shape, *args):
    return pl.pallas_call(
        kernel,
        out_shape=out_shape,
        in_specs=[pl.BlockSpec(memory_space=pltpu.VMEM)] * len(args),
        out_specs=tuple(pl.BlockSpec(memory_space=pltpu.VMEM) for _ in out_shape),
    )(*args)


def make_templates(sampled, box_edge, planes, table):
    count = sampled.shape[1]
    length = table["across"].shape[0]
    sampled = jnp.transpose(sampled, (1, 0, 2))
    sampled = sampled.reshape(count, planes, box_edge, box_edge)
    template_norm = jnp.sqrt(
        jnp.sum(jnp.square(sampled.astype(jnp.float32)), axis=(1, 2, 3)) + 1e-05
    )
    spec_shape = jax.ShapeDtypeStruct((length, count * planes * length), jnp.float32)
    spec_real, spec_imag = whole_call(
        template_kernel,
        (spec_shape, spec_shape),
        sampled.reshape(count * planes * box_edge, box_edge),
        table["box_across"],
        table["box_down"],
    )
    return (spec_real, spec_imag, template_norm)


def field_spectra(gathered, wedge_weight, table, band_sum, box_edge):
    tiles, planes, length, _ = gathered.shape
    spec_shape = jax.ShapeDtypeStruct((length, tiles * planes * length), jnp.float32)
    return whole_call(
        functools.partial(field_kernel, box_edge=box_edge),
        (spec_shape, spec_shape, jax.ShapeDtypeStruct((tiles, length, length), jnp.float32)),
        gathered.reshape(tiles * planes * length, length),
        wedge_weight,
        table["across"],
        table["mix"],
        table["across"],
        band_sum.astype(jnp.bfloat16),
        band_sum.T.astype(jnp.bfloat16),
    )


def score_kernel(
    scale_ref, field_re_ref, field_im_ref, templ_re_ref, templ_im_ref, mix_ref, back_ref,
    rms_ref, out_ref
):
    length = field_re_ref.shape[0]
    per_step = rms_ref.shape[0]
    planes = field_re_ref.shape[1] // (per_step * length)
    count = templ_re_ref.shape[1] // (planes * length)
    group = 8 if count % 8 == 0 else 1

    def lanes(index):
        return slice(index * length, (index + 1) * length)

    for tile in range(per_step):
        best = None
        for step in range(count // group):
            joined = []
            for member in range(group):
                orient = step * group + member
                prod_re = None
                prod_im = None
                for plane in range(planes):
                    fr = field_re_ref[:, lanes(tile * planes + plane)]
                    fi = field_im_ref[:, lanes(tile * planes + plane)]
                    tr = templ_re_ref[:, lanes(orient * planes + plane)]
                    ti = templ_im_ref[:, lanes(orient * planes + plane)]
                    part_re = fr * tr + fi * ti
                    part_im = fi * tr - fr * ti
                    prod_re = part_re if prod_re is None else prod_re + part_re
                    prod_im = part_im if prod_im is None else prod_im + part_im
                joined.append(
                    jnp.concatenate(
                        [prod_re.astype(jnp.bfloat16), prod_im.astype(jnp.bfloat16)], axis=1
                    )
                )
            joined = jnp.concatenate(joined, axis=0)
            first = jnp.dot(joined, mix_ref[...], preferred_element_type=jnp.float32).astype(
                jnp.bfloat16
            )
            stacked = jnp.concatenate(
                [
                    rows_to_blocks(first[:, :length], length),
                    rows_to_blocks(first[:, length:], length),
                ],
                axis=0,
            )
            corr = jnp.dot(back_ref[...], stacked, preferred_element_type=jnp.float32)
            for member in range(group):
                orient = step * group + member
                value = corr[:, lanes(member)] * scale_ref[orient]
                best = value if best is None else jnp.maximum(best, value)
        result = (best / rms_ref[tile]).astype(out_ref.dtype)
        chunk = out_ref.shape[2]
        for part in range(out_ref.shape[0]):
            out_ref[part, tile] = result[part * chunk : (part + 1) * chunk]


def score_tiles(
    field_real, field_imag, local_rms, templ_real, templ_imag, template_norm, table
):
    length = field_real.shape[0]
    planes = field_real.shape[1] // (local_rms.shape[0] * length)
    scale = (1.0 / template_norm) * (1.0 / (length * length))
    mix = table["mix"]
    back = table["across"]
    tiles = local_rms.shape[0]
    groups = lax.axis_size("orient")
    per_step = 2 if tiles % 2 == 0 else 1
    tile_block = pl.BlockSpec((length, per_step * planes * length), lambda t: (0, t))
    templ_block = pl.BlockSpec(templ_real.shape, lambda t: (0, 0))
    return pl.pallas_call(
        score_kernel,
        grid=(tiles // per_step,),
        out_shape=jax.ShapeDtypeStruct((groups, tiles, length // groups, length), jnp.bfloat16),
        in_specs=[
            pl.BlockSpec(memory_space=pltpu.SMEM),
            tile_block,
            tile_block,
            templ_block,
            templ_block,
            pl.BlockSpec((2 * length, 2 * length), lambda t: (0, 0)),
            pl.BlockSpec((length, 2 * length), lambda t: (0, 0)),
            pl.BlockSpec((per_step, length, length), lambda t: (t, 0, 0)),
        ],
        out_specs=pl.BlockSpec(
            (groups, per_step, length // groups, length), lambda t: (0, t, 0, 0)
        ),
    )(
        scale,
        field_real,
        field_imag,
        templ_real,
        templ_imag,
        mix,
        back,
        local_rms,
    )


def orient_max(best):
    parts = lax.all_to_all(best, "orient", split_axis=0, concat_axis=0, tiled=True)
    return jnp.max(parts, axis=0)


def per_device(tiles, assigned_worker, wedge_mask, template_volume, rotation_samples):
    tile_len = tiles.shape[-1]
    planes = tiles.shape[1]
    home_slots = tiles.shape[0]
    work_slots = home_slots // 2
    box_edge = template_volume.shape[0]
    table = transform_tables(tile_len, box_edge)
    band_sum = band_table(tile_len, box_edge)
    wedge_weight = wedge_mask.astype(jnp.bfloat16)
    sampled = share_samples(template_volume, rotation_samples)
    partner_tiles = partner(tiles[work_slots:], "slab", 0)
    occupied = assigned_worker >= 0
    own_count = jnp.sum(occupied.astype(jnp.int32))
    counter = jnp.arange(work_slots, dtype=jnp.int32)
    keep_own = (counter < own_count)[:, None, None, None]
    moved_in = pick_rows(counter - own_count, partner_tiles)
    gathered = jnp.where(keep_own, tiles[:work_slots], moved_in)
    field_real, field_imag, local_rms = field_spectra(
        gathered, wedge_weight, table, band_sum, box_edge
    )
    templ_real, templ_imag, template_norm = make_templates(sampled, box_edge, planes, table)
    best = score_tiles(
        field_real,
        field_imag,
        local_rms,
        templ_real,
        templ_imag,
        template_norm,
        table,
    )
    best_rows = orient_max(best)
    outgoing = pick_rows(counter + own_count, best_rows)
    returned = partner(outgoing, "slab", 0)
    result = jnp.concatenate([best_rows, returned], axis=0)
    return jnp.where(occupied[:, None, None], result, jnp.zeros_like(result))


def solution(mesh):
    return jax.shard_map(
        per_device,
        mesh=mesh,
        in_specs=(P("slab", None, None, None), P("slab"), P(), P(), P("orient", "slab")),
        out_specs=P("slab", "orient", None),
        check_vma=False,
    )
```

```python
import functools
import math

import jax
import ml_dtypes
import numpy as np
import jax.numpy as jnp
from jax import lax
from jax.experimental import pallas as pl
from jax.experimental.pallas import tpu as pltpu
from jax.sharding import PartitionSpec as P


def partner(block, axis, bit):
    count = lax.axis_size(axis)
    route = []
    for low in range(count):
        high = low | 1 << bit
        if high != low and high < count:
            route += [(low, high), (high, low)]
    return lax.ppermute(block, axis, route)


def tables(length):
    counter = np.arange(length, dtype=np.int32)
    angles = (counter[:, None] * counter[None, :] % length).astype(np.float32) * np.float32(
        2.0 * math.pi / length
    )
    wide = angles.astype(np.float64)
    cosine = np.cos(wide).astype(np.float32).astype(ml_dtypes.bfloat16)
    sine = np.sin(wide).astype(np.float32).astype(ml_dtypes.bfloat16)
    return cosine, sine


def band_table(length, box_edge):
    counter = np.arange(length, dtype=np.int32)
    offsets = (counter[None, :] - counter[:, None]) % length
    return jnp.asarray((offsets < box_edge).astype(np.float32))


def transform_tables(length, box_edge):
    cosine, sine = tables(length)
    across = np.concatenate([cosine, -sine], axis=1)
    mix = np.concatenate(
        [np.concatenate([cosine, sine], axis=1), np.concatenate([-sine, cosine], axis=1)], axis=0
    )
    box_across = np.concatenate([cosine[:box_edge], -sine[:box_edge]], axis=1)
    box_down = np.concatenate(
        [
            np.concatenate([cosine[:, :box_edge], sine[:, :box_edge]], axis=1),
            np.concatenate([-sine[:, :box_edge], cosine[:, :box_edge]], axis=1),
        ],
        axis=0,
    )
    return {
        name: jnp.asarray(value)
        for name, value in (
            ("across", across),
            ("mix", mix),
            ("box_across", box_across),
            ("box_down", box_down),
        )
    }


def pick_rows(chosen, source):
    counter = jnp.arange(source.shape[0], dtype=jnp.int32)
    selector = (chosen[:, None] == counter[None, :]).astype(source.dtype)
    flat = source.reshape(source.shape[0], -1)
    picked = jnp.dot(selector, flat, preferred_element_type=jnp.float32).astype(source.dtype)
    return picked.reshape((chosen.shape[0],) + source.shape[1:])


def pick_kernel(index_ref, table_ref, out_ref, picked_ref):
    columns = table_ref.shape[0]
    rows_in_table = table_ref.shape[1]
    lanes = index_ref.shape[1]
    shift = columns.bit_length() - 1

    def body(step, carry):
        index = index_ref[pl.ds(step, 1), :]
        high = jnp.right_shift(index, shift)
        low = jnp.bitwise_and(index, columns - 1)
        row_hot = (lax.broadcasted_iota(jnp.int32, (rows_in_table, lanes), 0) == high).astype(
            jnp.bfloat16
        )
        picked_rows = jnp.dot(table_ref[...], row_hot, preferred_element_type=jnp.float32)
        column_hot = lax.broadcasted_iota(jnp.int32, (columns, lanes), 0) == low
        chosen = jnp.where(column_hot, picked_rows, 0.0)
        picked_ref[pl.ds(step, 1), :] = jnp.sum(chosen, axis=0, keepdims=True)
        return carry

    lax.fori_loop(0, index_ref.shape[0], body, 0)
    out_ref[...] = picked_ref[...].astype(out_ref.dtype)


def sample_template(template_volume, rotation_samples):
    total = template_volume.size
    columns = 512
    table_t = template_volume.reshape(total // columns, columns).T.astype(jnp.bfloat16)
    return pl.pallas_call(
        pick_kernel,
        out_shape=jax.ShapeDtypeStruct(rotation_samples.shape, jnp.bfloat16),
        in_specs=[pl.BlockSpec(memory_space=pltpu.VMEM)] * 2,
        out_specs=pl.BlockSpec(memory_space=pltpu.VMEM),
        scratch_shapes=[pltpu.VMEM(rotation_samples.shape, jnp.float32)],
    )(rotation_samples, table_t)


def share_samples(template_volume, rotation_samples):
    sampled_part = sample_template(template_volume, rotation_samples)
    slab_count = lax.axis_size("slab")
    spread = jnp.broadcast_to(sampled_part[None], (slab_count,) + sampled_part.shape)
    return lax.all_to_all(spread, "slab", 0, 0, tiled=True)


def rows_to_blocks(values, rows):
    count = values.shape[0] // rows
    return jnp.concatenate([values[i * rows : (i + 1) * rows] for i in range(count)], axis=1)


def blocks_to_rows(values, width):
    count = values.shape[1] // width
    return jnp.concatenate(
        [values[:, i * width : (i + 1) * width] for i in range(count)], axis=0
    )


def forward_rows(values, across, down):
    width = across.shape[1] // 2
    height = down.shape[1] // 2
    first = jnp.dot(values, across, preferred_element_type=jnp.float32).astype(jnp.bfloat16)
    stacked = jnp.concatenate(
        [rows_to_blocks(first[:, :width], height), rows_to_blocks(first[:, width:], height)],
        axis=0,
    )
    second = jnp.dot(down, stacked, preferred_element_type=jnp.float32).astype(jnp.bfloat16)
    return second[:width], second[width:]


def inverse_blocks(real_part, imag_part, mix, back):
    length = real_part.shape[0]
    joined = jnp.concatenate(
        [blocks_to_rows(real_part, length), blocks_to_rows(imag_part, length)], axis=1
    )
    first = jnp.dot(joined, mix, preferred_element_type=jnp.float32).astype(jnp.bfloat16)
    stacked = jnp.concatenate(
        [rows_to_blocks(first[:, :length], length), rows_to_blocks(first[:, length:], length)],
        axis=0,
    )
    return jnp.dot(back, stacked, preferred_element_type=jnp.float32)


def template_kernel(values_ref, across_ref, down_ref, real_ref, imag_ref):
    real_part, imag_part = forward_rows(values_ref[...], across_ref[...], down_ref[...])
    real_ref[...] = real_part.astype(jnp.float32)
    imag_ref[...] = imag_part.astype(jnp.float32)


def split_three(values):
    high = values.astype(jnp.bfloat16)
    rest = values - high.astype(jnp.float32)
    middle = rest.astype(jnp.bfloat16)
    low = (rest - middle.astype(jnp.float32)).astype(jnp.bfloat16)
    return (high, middle, low)


def exact_dot(left, right, left_exact):
    total = None
    if left_exact:
        for part in split_three(right):
            term = jnp.dot(left, part, preferred_element_type=jnp.float32)
            total = term if total is None else total + term
    else:
        for part in split_three(left):
            term = jnp.dot(part, right, preferred_element_type=jnp.float32)
            total = term if total is None else total + term
    return total


def field_kernel(
    values_ref, wedge_ref, across_ref, mix_ref, back_ref, band_ref, band_t_ref, real_ref,
    imag_ref, rms_ref, *, box_edge
):
    length = values_ref.shape[-1]
    maps = values_ref.shape[0] // length
    tiles = rms_ref.shape[0]
    planes = maps // tiles
    mix = mix_ref[...]
    real_part, imag_part = forward_rows(values_ref[...], across_ref[...], mix)
    wedge = jnp.concatenate([wedge_ref[...]] * maps, axis=1)
    field = inverse_blocks(real_part * wedge, imag_part * wedge, mix, back_ref[...])
    field = (field * (1.0 / (length * length))).astype(jnp.bfloat16)
    square = jnp.square(field.astype(jnp.float32))
    energies = []
    for tile in range(tiles):
        energy = None
        for plane in range(planes):
            index = tile * planes + plane
            part = square[:, index * length : (index + 1) * length]
            energy = part if energy is None else energy + part
        energies.append(energy)
    energy = jnp.concatenate(energies, axis=1)
    summed = exact_dot(band_ref[...], energy, True)
    summed = exact_dot(blocks_to_rows(summed, length), band_t_ref[...], False)
    for tile in range(tiles):
        part = summed[tile * length : (tile + 1) * length]
        rms_ref[tile] = jnp.sqrt(part / (box_edge * box_edge * planes) + 1e-05)
    real_part, imag_part = forward_rows(blocks_to_rows(field, length), across_ref[...], mix)
    real_ref[...] = real_part.astype(jnp.float32)
    imag_ref[...] = imag_part.astype(jnp.float32)


def whole_call(kernel, out_shape, *args):
    return pl.pallas_call(
        kernel,
        out_shape=out_shape,
        in_specs=[pl.BlockSpec(memory_space=pltpu.VMEM)] * len(args),
        out_specs=tuple(pl.BlockSpec(memory_space=pltpu.VMEM) for _ in out_shape),
    )(*args)


def make_templates(sampled, box_edge, planes, table):
    count = sampled.shape[1]
    length = table["across"].shape[0]
    sampled = jnp.transpose(sampled, (1, 0, 2))
    sampled = sampled.reshape(count, planes, box_edge, box_edge)
    template_norm = jnp.sqrt(
        jnp.sum(jnp.square(sampled.astype(jnp.float32)), axis=(1, 2, 3)) + 1e-05
    )
    spec_shape = jax.ShapeDtypeStruct((length, count * planes * length), jnp.float32)
    spec_real, spec_imag = whole_call(
        template_kernel,
        (spec_shape, spec_shape),
        sampled.reshape(count * planes * box_edge, box_edge),
        table["box_across"],
        table["box_down"],
    )
    return (spec_real, spec_imag, template_norm)


def field_spectra(gathered, wedge_weight, table, band_sum, box_edge):
    tiles, planes, length, _ = gathered.shape
    spec_shape = jax.ShapeDtypeStruct((length, tiles * planes * length), jnp.float32)
    return whole_call(
        functools.partial(field_kernel, box_edge=box_edge),
        (spec_shape, spec_shape, jax.ShapeDtypeStruct((tiles, length, length), jnp.float32)),
        gathered.reshape(tiles * planes * length, length),
        wedge_weight,
        table["across"],
        table["mix"],
        table["across"],
        band_sum.astype(jnp.bfloat16),
        band_sum.T.astype(jnp.bfloat16),
    )


def score_kernel(
    scale_ref, field_re_ref, field_im_ref, templ_re_ref, templ_im_ref, mix_ref, back_ref,
    rms_ref, out_ref
):
    length = field_re_ref.shape[0]
    per_step = rms_ref.shape[0]
    planes = field_re_ref.shape[1] // (per_step * length)
    count = templ_re_ref.shape[1] // (planes * length)
    group = 8 if count % 8 == 0 else 1

    def lanes(index):
        return slice(index * length, (index + 1) * length)

    for tile in range(per_step):
        best = None
        for step in range(count // group):
            joined = []
            for member in range(group):
                orient = step * group + member
                prod_re = None
                prod_im = None
                for plane in range(planes):
                    fr = field_re_ref[:, lanes(tile * planes + plane)]
                    fi = field_im_ref[:, lanes(tile * planes + plane)]
                    tr = templ_re_ref[:, lanes(orient * planes + plane)]
                    ti = templ_im_ref[:, lanes(orient * planes + plane)]
                    part_re = fr * tr + fi * ti
                    part_im = fi * tr - fr * ti
                    prod_re = part_re if prod_re is None else prod_re + part_re
                    prod_im = part_im if prod_im is None else prod_im + part_im
                joined.append(
                    jnp.concatenate(
                        [prod_re.astype(jnp.bfloat16), prod_im.astype(jnp.bfloat16)], axis=1
                    )
                )
            joined = jnp.concatenate(joined, axis=0)
            first = jnp.dot(joined, mix_ref[...], preferred_element_type=jnp.float32).astype(
                jnp.bfloat16
            )
            stacked = jnp.concatenate(
                [
                    rows_to_blocks(first[:, :length], length),
                    rows_to_blocks(first[:, length:], length),
                ],
                axis=0,
            )
            corr = jnp.dot(back_ref[...], stacked, preferred_element_type=jnp.float32)
            for member in range(group):
                orient = step * group + member
                value = corr[:, lanes(member)] * scale_ref[orient]
                best = value if best is None else jnp.maximum(best, value)
        result = (best / rms_ref[tile]).astype(out_ref.dtype)
        chunk = out_ref.shape[2]
        for part in range(out_ref.shape[0]):
            out_ref[part, tile] = result[part * chunk : (part + 1) * chunk]


def score_tiles(
    field_real, field_imag, local_rms, templ_real, templ_imag, template_norm, table
):
    length = field_real.shape[0]
    planes = field_real.shape[1] // (local_rms.shape[0] * length)
    scale = (1.0 / template_norm) * (1.0 / (length * length))
    mix = table["mix"]
    back = table["across"]
    tiles = local_rms.shape[0]
    groups = lax.axis_size("orient")
    per_step = 2 if tiles % 2 == 0 else 1
    tile_block = pl.BlockSpec((length, per_step * planes * length), lambda t: (0, t))
    templ_block = pl.BlockSpec(templ_real.shape, lambda t: (0, 0))
    return pl.pallas_call(
        score_kernel,
        grid=(tiles // per_step,),
        out_shape=jax.ShapeDtypeStruct((groups, tiles, length // groups, length), jnp.bfloat16),
        in_specs=[
            pl.BlockSpec(memory_space=pltpu.SMEM),
            tile_block,
            tile_block,
            templ_block,
            templ_block,
            pl.BlockSpec((2 * length, 2 * length), lambda t: (0, 0)),
            pl.BlockSpec((length, 2 * length), lambda t: (0, 0)),
            pl.BlockSpec((per_step, length, length), lambda t: (t, 0, 0)),
        ],
        out_specs=pl.BlockSpec(
            (groups, per_step, length // groups, length), lambda t: (0, t, 0, 0)
        ),
    )(
        scale,
        field_real,
        field_imag,
        templ_real,
        templ_imag,
        mix,
        back,
        local_rms,
    )


def orient_max(best):
    parts = lax.all_to_all(best, "orient", split_axis=0, concat_axis=0, tiled=True)
    return jnp.max(parts, axis=0)


def per_device(tiles, assigned_worker, wedge_mask, template_volume, rotation_samples):
    tile_len = tiles.shape[-1]
    planes = tiles.shape[1]
    home_slots = tiles.shape[0]
    work_slots = home_slots // 2
    box_edge = template_volume.shape[0]
    table = transform_tables(tile_len, box_edge)
    band_sum = band_table(tile_len, box_edge)
    wedge_weight = wedge_mask.astype(jnp.bfloat16)
    sampled = share_samples(template_volume, rotation_samples)
    partner_tiles = partner(tiles[work_slots:], "slab", 0)
    occupied = assigned_worker >= 0
    own_count = jnp.sum(occupied.astype(jnp.int32))
    counter = jnp.arange(work_slots, dtype=jnp.int32)
    keep_own = (counter < own_count)[:, None, None, None]
    moved_in = pick_rows(counter - own_count, partner_tiles)
    gathered = jnp.where(keep_own, tiles[:work_slots], moved_in)
    field_real, field_imag, local_rms = field_spectra(
        gathered, wedge_weight, table, band_sum, box_edge
    )
    sampled, field_real = lax.optimization_barrier((sampled, field_real))
    templ_real, templ_imag, template_norm = make_templates(sampled, box_edge, planes, table)
    best = score_tiles(
        field_real,
        field_imag,
        local_rms,
        templ_real,
        templ_imag,
        template_norm,
        table,
    )
    best_rows = orient_max(best)
    outgoing = pick_rows(counter + own_count, best_rows)
    returned = partner(outgoing, "slab", 0)
    result = jnp.concatenate([best_rows, returned], axis=0)
    return jnp.where(occupied[:, None, None], result, jnp.zeros_like(result))


def solution(mesh):
    return jax.shard_map(
        per_device,
        mesh=mesh,
        in_specs=(P("slab", None, None, None), P("slab"), P(), P(), P("orient", "slab")),
        out_specs=P("slab", "orient", None),
        check_vma=False,
    )
```

```python
import functools
import math

import jax
import ml_dtypes
import numpy as np
import jax.numpy as jnp
from jax import lax
from jax.experimental import pallas as pl
from jax.experimental.pallas import tpu as pltpu
from jax.sharding import PartitionSpec as P


def partner(block, axis, bit):
    count = lax.axis_size(axis)
    route = []
    for low in range(count):
        high = low | 1 << bit
        if high != low and high < count:
            route += [(low, high), (high, low)]
    return lax.ppermute(block, axis, route)


def tables(length):
    counter = np.arange(length, dtype=np.int32)
    angles = (counter[:, None] * counter[None, :] % length).astype(np.float32) * np.float32(
        2.0 * math.pi / length
    )
    wide = angles.astype(np.float64)
    cosine = np.cos(wide).astype(np.float32).astype(ml_dtypes.bfloat16)
    sine = np.sin(wide).astype(np.float32).astype(ml_dtypes.bfloat16)
    return cosine, sine


def band_table(length, box_edge):
    counter = np.arange(length, dtype=np.int32)
    offsets = (counter[None, :] - counter[:, None]) % length
    return jnp.asarray((offsets < box_edge).astype(np.float32))


def transform_tables(length, box_edge):
    cosine, sine = tables(length)
    across = np.concatenate([cosine, -sine], axis=1)
    mix = np.concatenate(
        [np.concatenate([cosine, sine], axis=1), np.concatenate([-sine, cosine], axis=1)], axis=0
    )
    box_across = np.concatenate([cosine[:box_edge], -sine[:box_edge]], axis=1)
    box_down = np.concatenate(
        [
            np.concatenate([cosine[:, :box_edge], sine[:, :box_edge]], axis=1),
            np.concatenate([-sine[:, :box_edge], cosine[:, :box_edge]], axis=1),
        ],
        axis=0,
    )
    return {
        name: jnp.asarray(value)
        for name, value in (
            ("across", across),
            ("mix", mix),
            ("box_across", box_across),
            ("box_down", box_down),
        )
    }


def pick_rows(chosen, source):
    counter = jnp.arange(source.shape[0], dtype=jnp.int32)
    selector = (chosen[:, None] == counter[None, :]).astype(source.dtype)
    flat = source.reshape(source.shape[0], -1)
    picked = jnp.dot(selector, flat, preferred_element_type=jnp.float32).astype(source.dtype)
    return picked.reshape((chosen.shape[0],) + source.shape[1:])


def pick_kernel(index_ref, table_ref, out_ref, picked_ref):
    columns = table_ref.shape[0]
    rows_in_table = table_ref.shape[1]
    lanes = index_ref.shape[1]
    shift = columns.bit_length() - 1

    def body(step, carry):
        index = index_ref[pl.ds(step, 1), :]
        high = jnp.right_shift(index, shift)
        low = jnp.bitwise_and(index, columns - 1)
        row_hot = (lax.broadcasted_iota(jnp.int32, (rows_in_table, lanes), 0) == high).astype(
            jnp.bfloat16
        )
        picked_rows = jnp.dot(table_ref[...], row_hot, preferred_element_type=jnp.float32)
        column_hot = lax.broadcasted_iota(jnp.int32, (columns, lanes), 0) == low
        chosen = jnp.where(column_hot, picked_rows, 0.0)
        picked_ref[pl.ds(step, 1), :] = jnp.sum(chosen, axis=0, keepdims=True)
        return carry

    lax.fori_loop(0, index_ref.shape[0], body, 0)
    picked = picked_ref[...].astype(out_ref.dtype)
    for copy in range(out_ref.shape[0]):
        out_ref[copy] = picked


def sample_template(template_volume, rotation_samples, copies):
    total = template_volume.size
    columns = 512
    table_t = template_volume.reshape(total // columns, columns).T.astype(jnp.bfloat16)
    return pl.pallas_call(
        pick_kernel,
        out_shape=jax.ShapeDtypeStruct((copies,) + rotation_samples.shape, jnp.bfloat16),
        in_specs=[pl.BlockSpec(memory_space=pltpu.VMEM)] * 2,
        out_specs=pl.BlockSpec(memory_space=pltpu.VMEM),
        scratch_shapes=[pltpu.VMEM(rotation_samples.shape, jnp.float32)],
    )(rotation_samples, table_t)


def share_samples(template_volume, rotation_samples):
    slab_count = lax.axis_size("slab")
    spread = sample_template(template_volume, rotation_samples, slab_count)
    return lax.all_to_all(spread, "slab", 0, 0, tiled=True)


def rows_to_blocks(values, rows):
    count = values.shape[0] // rows
    return jnp.concatenate([values[i * rows : (i + 1) * rows] for i in range(count)], axis=1)


def blocks_to_rows(values, width):
    count = values.shape[1] // width
    return jnp.concatenate(
        [values[:, i * width : (i + 1) * width] for i in range(count)], axis=0
    )


def forward_rows(values, across, down):
    width = across.shape[1] // 2
    height = down.shape[1] // 2
    first = jnp.dot(values, across, preferred_element_type=jnp.float32).astype(jnp.bfloat16)
    stacked = jnp.concatenate(
        [rows_to_blocks(first[:, :width], height), rows_to_blocks(first[:, width:], height)],
        axis=0,
    )
    second = jnp.dot(down, stacked, preferred_element_type=jnp.float32).astype(jnp.bfloat16)
    return second[:width], second[width:]


def inverse_blocks(real_part, imag_part, mix, back):
    length = real_part.shape[0]
    joined = jnp.concatenate(
        [blocks_to_rows(real_part, length), blocks_to_rows(imag_part, length)], axis=1
    )
    first = jnp.dot(joined, mix, preferred_element_type=jnp.float32).astype(jnp.bfloat16)
    stacked = jnp.concatenate(
        [rows_to_blocks(first[:, :length], length), rows_to_blocks(first[:, length:], length)],
        axis=0,
    )
    return jnp.dot(back, stacked, preferred_element_type=jnp.float32)


def template_kernel(values_ref, across_ref, down_ref, real_ref, imag_ref):
    real_part, imag_part = forward_rows(values_ref[...], across_ref[...], down_ref[...])
    real_ref[...] = real_part.astype(jnp.float32)
    imag_ref[...] = imag_part.astype(jnp.float32)


def split_three(values):
    high = values.astype(jnp.bfloat16)
    rest = values - high.astype(jnp.float32)
    middle = rest.astype(jnp.bfloat16)
    low = (rest - middle.astype(jnp.float32)).astype(jnp.bfloat16)
    return (high, middle, low)


def exact_dot(left, right, left_exact):
    total = None
    if left_exact:
        for part in split_three(right):
            term = jnp.dot(left, part, preferred_element_type=jnp.float32)
            total = term if total is None else total + term
    else:
        for part in split_three(left):
            term = jnp.dot(part, right, preferred_element_type=jnp.float32)
            total = term if total is None else total + term
    return total


def field_kernel(
    values_ref, wedge_ref, across_ref, mix_ref, back_ref, band_ref, band_t_ref, real_ref,
    imag_ref, rms_ref, *, box_edge
):
    length = values_ref.shape[-1]
    maps = values_ref.shape[0] // length
    tiles = rms_ref.shape[0]
    planes = maps // tiles
    mix = mix_ref[...]
    real_part, imag_part = forward_rows(values_ref[...], across_ref[...], mix)
    wedge = jnp.concatenate([wedge_ref[...]] * maps, axis=1)
    field = inverse_blocks(real_part * wedge, imag_part * wedge, mix, back_ref[...])
    field = (field * (1.0 / (length * length))).astype(jnp.bfloat16)
    square = jnp.square(field.astype(jnp.float32))
    energies = []
    for tile in range(tiles):
        energy = None
        for plane in range(planes):
            index = tile * planes + plane
            part = square[:, index * length : (index + 1) * length]
            energy = part if energy is None else energy + part
        energies.append(energy)
    energy = jnp.concatenate(energies, axis=1)
    summed = exact_dot(band_ref[...], energy, True)
    summed = exact_dot(blocks_to_rows(summed, length), band_t_ref[...], False)
    for tile in range(tiles):
        part = summed[tile * length : (tile + 1) * length]
        rms_ref[tile] = jnp.sqrt(part / (box_edge * box_edge * planes) + 1e-05)
    real_part, imag_part = forward_rows(blocks_to_rows(field, length), across_ref[...], mix)
    real_ref[...] = real_part.astype(jnp.float32)
    imag_ref[...] = imag_part.astype(jnp.float32)


def whole_call(kernel, out_shape, *args):
    return pl.pallas_call(
        kernel,
        out_shape=out_shape,
        in_specs=[pl.BlockSpec(memory_space=pltpu.VMEM)] * len(args),
        out_specs=tuple(pl.BlockSpec(memory_space=pltpu.VMEM) for _ in out_shape),
    )(*args)


def make_templates(sampled, box_edge, planes, table):
    count = sampled.shape[1]
    length = table["across"].shape[0]
    sampled = jnp.transpose(sampled, (1, 0, 2))
    sampled = sampled.reshape(count, planes, box_edge, box_edge)
    template_norm = jnp.sqrt(
        jnp.sum(jnp.square(sampled.astype(jnp.float32)), axis=(1, 2, 3)) + 1e-05
    )
    spec_shape = jax.ShapeDtypeStruct((length, count * planes * length), jnp.float32)
    spec_real, spec_imag = whole_call(
        template_kernel,
        (spec_shape, spec_shape),
        sampled.reshape(count * planes * box_edge, box_edge),
        table["box_across"],
        table["box_down"],
    )
    return (spec_real, spec_imag, template_norm)


def field_spectra(gathered, wedge_weight, table, band_sum, box_edge):
    tiles, planes, length, _ = gathered.shape
    spec_shape = jax.ShapeDtypeStruct((length, tiles * planes * length), jnp.float32)
    return whole_call(
        functools.partial(field_kernel, box_edge=box_edge),
        (spec_shape, spec_shape, jax.ShapeDtypeStruct((tiles, length, length), jnp.float32)),
        gathered.reshape(tiles * planes * length, length),
        wedge_weight,
        table["across"],
        table["mix"],
        table["across"],
        band_sum.astype(jnp.bfloat16),
        band_sum.T.astype(jnp.bfloat16),
    )


def score_kernel(
    scale_ref, field_re_ref, field_im_ref, templ_re_ref, templ_im_ref, mix_ref, back_ref,
    rms_ref, out_ref
):
    length = field_re_ref.shape[0]
    per_step = rms_ref.shape[0]
    planes = field_re_ref.shape[1] // (per_step * length)
    count = templ_re_ref.shape[1] // (planes * length)
    group = 8 if count % 8 == 0 else 1

    def lanes(index):
        return slice(index * length, (index + 1) * length)

    for tile in range(per_step):
        best = None
        for step in range(count // group):
            joined = []
            for member in range(group):
                orient = step * group + member
                prod_re = None
                prod_im = None
                for plane in range(planes):
                    fr = field_re_ref[:, lanes(tile * planes + plane)]
                    fi = field_im_ref[:, lanes(tile * planes + plane)]
                    tr = templ_re_ref[:, lanes(orient * planes + plane)]
                    ti = templ_im_ref[:, lanes(orient * planes + plane)]
                    part_re = fr * tr + fi * ti
                    part_im = fi * tr - fr * ti
                    prod_re = part_re if prod_re is None else prod_re + part_re
                    prod_im = part_im if prod_im is None else prod_im + part_im
                joined.append(
                    jnp.concatenate(
                        [prod_re.astype(jnp.bfloat16), prod_im.astype(jnp.bfloat16)], axis=1
                    )
                )
            joined = jnp.concatenate(joined, axis=0)
            first = jnp.dot(joined, mix_ref[...], preferred_element_type=jnp.float32).astype(
                jnp.bfloat16
            )
            stacked = jnp.concatenate(
                [
                    rows_to_blocks(first[:, :length], length),
                    rows_to_blocks(first[:, length:], length),
                ],
                axis=0,
            )
            corr = jnp.dot(back_ref[...], stacked, preferred_element_type=jnp.float32)
            for member in range(group):
                orient = step * group + member
                value = corr[:, lanes(member)] * scale_ref[orient]
                best = value if best is None else jnp.maximum(best, value)
        result = (best / rms_ref[tile]).astype(out_ref.dtype)
        chunk = out_ref.shape[2]
        for part in range(out_ref.shape[0]):
            out_ref[part, tile] = result[part * chunk : (part + 1) * chunk]


def score_tiles(
    field_real, field_imag, local_rms, templ_real, templ_imag, template_norm, table
):
    length = field_real.shape[0]
    planes = field_real.shape[1] // (local_rms.shape[0] * length)
    scale = (1.0 / template_norm) * (1.0 / (length * length))
    mix = table["mix"]
    back = table["across"]
    tiles = local_rms.shape[0]
    groups = lax.axis_size("orient")
    per_step = 2 if tiles % 2 == 0 else 1
    tile_block = pl.BlockSpec((length, per_step * planes * length), lambda t: (0, t))
    templ_block = pl.BlockSpec(templ_real.shape, lambda t: (0, 0))
    return pl.pallas_call(
        score_kernel,
        grid=(tiles // per_step,),
        out_shape=jax.ShapeDtypeStruct((groups, tiles, length // groups, length), jnp.bfloat16),
        in_specs=[
            pl.BlockSpec(memory_space=pltpu.SMEM),
            tile_block,
            tile_block,
            templ_block,
            templ_block,
            pl.BlockSpec((2 * length, 2 * length), lambda t: (0, 0)),
            pl.BlockSpec((length, 2 * length), lambda t: (0, 0)),
            pl.BlockSpec((per_step, length, length), lambda t: (t, 0, 0)),
        ],
        out_specs=pl.BlockSpec(
            (groups, per_step, length // groups, length), lambda t: (0, t, 0, 0)
        ),
    )(
        scale,
        field_real,
        field_imag,
        templ_real,
        templ_imag,
        mix,
        back,
        local_rms,
    )


def orient_max(best):
    parts = lax.all_to_all(best, "orient", split_axis=0, concat_axis=0, tiled=True)
    return jnp.max(parts, axis=0)


def per_device(tiles, assigned_worker, wedge_mask, template_volume, rotation_samples):
    tile_len = tiles.shape[-1]
    planes = tiles.shape[1]
    home_slots = tiles.shape[0]
    work_slots = home_slots // 2
    box_edge = template_volume.shape[0]
    table = transform_tables(tile_len, box_edge)
    band_sum = band_table(tile_len, box_edge)
    wedge_weight = wedge_mask.astype(jnp.bfloat16)
    sampled = share_samples(template_volume, rotation_samples)
    partner_tiles = partner(tiles, "slab", 0)[work_slots:]
    occupied = assigned_worker >= 0
    own_count = jnp.sum(occupied.astype(jnp.int32))
    counter = jnp.arange(work_slots, dtype=jnp.int32)
    keep_own = (counter < own_count)[:, None, None, None]
    moved_in = pick_rows(counter - own_count, partner_tiles)
    gathered = jnp.where(keep_own, tiles[:work_slots], moved_in)
    field_real, field_imag, local_rms = field_spectra(
        gathered, wedge_weight, table, band_sum, box_edge
    )
    sampled, field_real = lax.optimization_barrier((sampled, field_real))
    templ_real, templ_imag, template_norm = make_templates(sampled, box_edge, planes, table)
    best = score_tiles(
        field_real,
        field_imag,
        local_rms,
        templ_real,
        templ_imag,
        template_norm,
        table,
    )
    best_rows = orient_max(best)
    outgoing = pick_rows(counter + own_count, best_rows)
    returned = partner(outgoing, "slab", 0)
    result = jnp.concatenate([best_rows, returned], axis=0)
    return jnp.where(occupied[:, None, None], result, jnp.zeros_like(result))


def solution(mesh):
    return jax.shard_map(
        per_device,
        mesh=mesh,
        in_specs=(P("slab", None, None, None), P("slab"), P(), P(), P("orient", "slab")),
        out_specs=P("slab", "orient", None),
        check_vma=False,
    )
```

```python
import functools
import math

import jax
import ml_dtypes
import numpy as np
import jax.numpy as jnp
from jax import lax
from jax.experimental import pallas as pl
from jax.experimental.pallas import tpu as pltpu
from jax.sharding import PartitionSpec as P


def partner(block, axis, bit):
    count = lax.axis_size(axis)
    route = []
    for low in range(count):
        high = low | 1 << bit
        if high != low and high < count:
            route += [(low, high), (high, low)]
    return lax.ppermute(block, axis, route)


def tables(length):
    counter = np.arange(length, dtype=np.int32)
    angles = (counter[:, None] * counter[None, :] % length).astype(np.float32) * np.float32(
        2.0 * math.pi / length
    )
    wide = angles.astype(np.float64)
    cosine = np.cos(wide).astype(np.float32).astype(ml_dtypes.bfloat16)
    sine = np.sin(wide).astype(np.float32).astype(ml_dtypes.bfloat16)
    return cosine, sine


def band_table(length, box_edge):
    counter = np.arange(length, dtype=np.int32)
    offsets = (counter[None, :] - counter[:, None]) % length
    return jnp.asarray((offsets < box_edge).astype(np.float32))


def transform_tables(length, box_edge):
    cosine, sine = tables(length)
    across = np.concatenate([cosine, -sine], axis=1)
    mix = np.concatenate(
        [np.concatenate([cosine, sine], axis=1), np.concatenate([-sine, cosine], axis=1)], axis=0
    )
    box_across = np.concatenate([cosine[:box_edge], -sine[:box_edge]], axis=1)
    box_down = np.concatenate(
        [
            np.concatenate([cosine[:, :box_edge], sine[:, :box_edge]], axis=1),
            np.concatenate([-sine[:, :box_edge], cosine[:, :box_edge]], axis=1),
        ],
        axis=0,
    )
    return {
        name: jnp.asarray(value)
        for name, value in (
            ("across", across),
            ("mix", mix),
            ("box_across", box_across),
            ("box_down", box_down),
        )
    }


def pick_rows(chosen, source):
    counter = jnp.arange(source.shape[0], dtype=jnp.int32)
    selector = (chosen[:, None] == counter[None, :]).astype(source.dtype)
    flat = source.reshape(source.shape[0], -1)
    picked = jnp.dot(selector, flat, preferred_element_type=jnp.float32).astype(source.dtype)
    return picked.reshape((chosen.shape[0],) + source.shape[1:])


def pick_kernel(index_ref, table_ref, out_ref, picked_ref):
    columns = table_ref.shape[0]
    rows_in_table = table_ref.shape[1]
    lanes = index_ref.shape[1]
    shift = columns.bit_length() - 1

    def body(step, carry):
        index = index_ref[pl.ds(step, 1), :]
        high = jnp.right_shift(index, shift)
        low = jnp.bitwise_and(index, columns - 1)
        row_hot = (lax.broadcasted_iota(jnp.int32, (rows_in_table, lanes), 0) == high).astype(
            jnp.bfloat16
        )
        picked_rows = jnp.dot(table_ref[...], row_hot, preferred_element_type=jnp.float32)
        column_hot = lax.broadcasted_iota(jnp.int32, (columns, lanes), 0) == low
        chosen = jnp.where(column_hot, picked_rows, 0.0)
        picked_ref[pl.ds(step, 1), :] = jnp.sum(chosen, axis=0, keepdims=True)
        return carry

    lax.fori_loop(0, index_ref.shape[0], body, 0)
    picked = picked_ref[...].astype(out_ref.dtype)
    for copy in range(out_ref.shape[0]):
        out_ref[copy] = picked


def sample_template(template_volume, rotation_samples, copies):
    total = template_volume.size
    columns = 512
    table_t = template_volume.reshape(total // columns, columns).T.astype(jnp.bfloat16)
    return pl.pallas_call(
        pick_kernel,
        out_shape=jax.ShapeDtypeStruct((copies,) + rotation_samples.shape, jnp.bfloat16),
        in_specs=[pl.BlockSpec(memory_space=pltpu.VMEM)] * 2,
        out_specs=pl.BlockSpec(memory_space=pltpu.VMEM),
        scratch_shapes=[pltpu.VMEM(rotation_samples.shape, jnp.float32)],
    )(rotation_samples, table_t)


def share_samples(template_volume, rotation_samples):
    slab_count = lax.axis_size("slab")
    spread = sample_template(template_volume, rotation_samples, slab_count)
    return lax.all_to_all(spread, "slab", 0, 0, tiled=True)


def rows_to_blocks(values, rows):
    count = values.shape[0] // rows
    return jnp.concatenate([values[i * rows : (i + 1) * rows] for i in range(count)], axis=1)


def blocks_to_rows(values, width):
    count = values.shape[1] // width
    return jnp.concatenate(
        [values[:, i * width : (i + 1) * width] for i in range(count)], axis=0
    )


def forward_rows(values, across, down):
    width = across.shape[1] // 2
    height = down.shape[1] // 2
    first = jnp.dot(values, across, preferred_element_type=jnp.float32).astype(jnp.bfloat16)
    stacked = jnp.concatenate(
        [rows_to_blocks(first[:, :width], height), rows_to_blocks(first[:, width:], height)],
        axis=0,
    )
    second = jnp.dot(down, stacked, preferred_element_type=jnp.float32).astype(jnp.bfloat16)
    return second[:width], second[width:]


def inverse_blocks(real_part, imag_part, mix, back):
    length = real_part.shape[0]
    joined = jnp.concatenate(
        [blocks_to_rows(real_part, length), blocks_to_rows(imag_part, length)], axis=1
    )
    first = jnp.dot(joined, mix, preferred_element_type=jnp.float32).astype(jnp.bfloat16)
    stacked = jnp.concatenate(
        [rows_to_blocks(first[:, :length], length), rows_to_blocks(first[:, length:], length)],
        axis=0,
    )
    return jnp.dot(back, stacked, preferred_element_type=jnp.float32)


def template_kernel(values_ref, across_ref, down_ref, real_ref, imag_ref):
    real_part, imag_part = forward_rows(values_ref[...], across_ref[...], down_ref[...])
    real_ref[...] = real_part.astype(jnp.float32)
    imag_ref[...] = imag_part.astype(jnp.float32)


def split_three(values):
    high = values.astype(jnp.bfloat16)
    rest = values - high.astype(jnp.float32)
    middle = rest.astype(jnp.bfloat16)
    low = (rest - middle.astype(jnp.float32)).astype(jnp.bfloat16)
    return (high, middle, low)


def exact_dot(left, right, left_exact):
    total = None
    if left_exact:
        for part in split_three(right):
            term = jnp.dot(left, part, preferred_element_type=jnp.float32)
            total = term if total is None else total + term
    else:
        for part in split_three(left):
            term = jnp.dot(part, right, preferred_element_type=jnp.float32)
            total = term if total is None else total + term
    return total


def field_kernel(
    values_ref, wedge_ref, across_ref, mix_ref, back_ref, band_ref, band_t_ref, real_ref,
    imag_ref, rms_ref, *, box_edge
):
    length = values_ref.shape[-1]
    maps = values_ref.shape[0] // length
    tiles = rms_ref.shape[0]
    planes = maps // tiles
    mix = mix_ref[...]
    real_part, imag_part = forward_rows(values_ref[...], across_ref[...], mix)
    wedge = jnp.concatenate([wedge_ref[...]] * maps, axis=1)
    field = inverse_blocks(real_part * wedge, imag_part * wedge, mix, back_ref[...])
    field = (field * (1.0 / (length * length))).astype(jnp.bfloat16)
    square = jnp.square(field.astype(jnp.float32))
    energies = []
    for tile in range(tiles):
        energy = None
        for plane in range(planes):
            index = tile * planes + plane
            part = square[:, index * length : (index + 1) * length]
            energy = part if energy is None else energy + part
        energies.append(energy)
    energy = jnp.concatenate(energies, axis=1)
    summed = exact_dot(band_ref[...], energy, True)
    summed = exact_dot(blocks_to_rows(summed, length), band_t_ref[...], False)
    for tile in range(tiles):
        part = summed[tile * length : (tile + 1) * length]
        rms_ref[tile] = jnp.sqrt(part / (box_edge * box_edge * planes) + 1e-05)
    real_part, imag_part = forward_rows(blocks_to_rows(field, length), across_ref[...], mix)
    real_ref[...] = real_part.astype(jnp.float32)
    imag_ref[...] = imag_part.astype(jnp.float32)


def whole_call(kernel, out_shape, *args):
    return pl.pallas_call(
        kernel,
        out_shape=out_shape,
        in_specs=[pl.BlockSpec(memory_space=pltpu.VMEM)] * len(args),
        out_specs=tuple(pl.BlockSpec(memory_space=pltpu.VMEM) for _ in out_shape),
    )(*args)


def make_templates(sampled, box_edge, planes, table):
    count = sampled.shape[1]
    length = table["across"].shape[0]
    sampled = jnp.transpose(sampled, (1, 0, 2))
    sampled = sampled.reshape(count, planes, box_edge, box_edge)
    template_norm = jnp.sqrt(
        jnp.sum(jnp.square(sampled.astype(jnp.float32)), axis=(1, 2, 3)) + 1e-05
    )
    spec_shape = jax.ShapeDtypeStruct((length, count * planes * length), jnp.float32)
    spec_real, spec_imag = whole_call(
        template_kernel,
        (spec_shape, spec_shape),
        sampled.reshape(count * planes * box_edge, box_edge),
        table["box_across"],
        table["box_down"],
    )
    return (spec_real, spec_imag, template_norm)


def field_spectra(gathered, wedge_weight, table, band_sum, box_edge):
    tiles, planes, length, _ = gathered.shape
    spec_shape = jax.ShapeDtypeStruct((length, tiles * planes * length), jnp.float32)
    return whole_call(
        functools.partial(field_kernel, box_edge=box_edge),
        (spec_shape, spec_shape, jax.ShapeDtypeStruct((tiles, length, length), jnp.float32)),
        gathered.reshape(tiles * planes * length, length),
        wedge_weight,
        table["across"],
        table["mix"],
        table["across"],
        band_sum.astype(jnp.bfloat16),
        band_sum.T.astype(jnp.bfloat16),
    )


def score_kernel(
    scale_ref, field_re_ref, field_im_ref, templ_re_ref, templ_im_ref, mix_ref, back_ref,
    rms_ref, out_ref
):
    length = field_re_ref.shape[0]
    per_step = rms_ref.shape[0]
    planes = field_re_ref.shape[1] // (per_step * length)
    count = templ_re_ref.shape[1] // (planes * length)
    group = 8 if count % 8 == 0 else 1

    def lanes(index):
        return slice(index * length, (index + 1) * length)

    for tile in range(per_step):
        best = None
        for step in range(count // group):
            joined = []
            for member in range(group):
                orient = step * group + member
                prod_re = None
                prod_im = None
                for plane in range(planes):
                    fr = field_re_ref[:, lanes(tile * planes + plane)]
                    fi = field_im_ref[:, lanes(tile * planes + plane)]
                    tr = templ_re_ref[:, lanes(orient * planes + plane)]
                    ti = templ_im_ref[:, lanes(orient * planes + plane)]
                    part_re = fr * tr + fi * ti
                    part_im = fi * tr - fr * ti
                    prod_re = part_re if prod_re is None else prod_re + part_re
                    prod_im = part_im if prod_im is None else prod_im + part_im
                joined.append(
                    jnp.concatenate(
                        [prod_re.astype(jnp.bfloat16), prod_im.astype(jnp.bfloat16)], axis=1
                    )
                )
            joined = jnp.concatenate(joined, axis=0)
            first = jnp.dot(joined, mix_ref[...], preferred_element_type=jnp.float32).astype(
                jnp.bfloat16
            )
            stacked = jnp.concatenate(
                [
                    rows_to_blocks(first[:, :length], length),
                    rows_to_blocks(first[:, length:], length),
                ],
                axis=0,
            )
            corr = jnp.dot(back_ref[...], stacked, preferred_element_type=jnp.float32)
            for member in range(group):
                orient = step * group + member
                value = corr[:, lanes(member)] * scale_ref[orient]
                best = value if best is None else jnp.maximum(best, value)
        result = (best / rms_ref[tile]).astype(out_ref.dtype)
        chunk = out_ref.shape[2]
        for part in range(out_ref.shape[0]):
            out_ref[part, tile] = result[part * chunk : (part + 1) * chunk]


def score_tiles(
    field_real, field_imag, local_rms, templ_real, templ_imag, template_norm, table
):
    length = field_real.shape[0]
    planes = field_real.shape[1] // (local_rms.shape[0] * length)
    scale = (1.0 / template_norm) * (1.0 / (length * length))
    mix = table["mix"]
    back = table["across"]
    tiles = local_rms.shape[0]
    groups = lax.axis_size("orient")
    per_step = 2 if tiles % 2 == 0 else 1
    tile_block = pl.BlockSpec((length, per_step * planes * length), lambda t: (0, t))
    templ_block = pl.BlockSpec(templ_real.shape, lambda t: (0, 0))
    return pl.pallas_call(
        score_kernel,
        grid=(tiles // per_step,),
        out_shape=jax.ShapeDtypeStruct((groups, tiles, length // groups, length), jnp.bfloat16),
        in_specs=[
            pl.BlockSpec(memory_space=pltpu.SMEM),
            tile_block,
            tile_block,
            templ_block,
            templ_block,
            pl.BlockSpec((2 * length, 2 * length), lambda t: (0, 0)),
            pl.BlockSpec((length, 2 * length), lambda t: (0, 0)),
            pl.BlockSpec((per_step, length, length), lambda t: (t, 0, 0)),
        ],
        out_specs=pl.BlockSpec(
            (groups, per_step, length // groups, length), lambda t: (0, t, 0, 0)
        ),
    )(
        scale,
        field_real,
        field_imag,
        templ_real,
        templ_imag,
        mix,
        back,
        local_rms,
    )


def orient_max(best):
    groups = lax.axis_size("orient")
    slot = lax.axis_index("orient")
    result = lax.dynamic_index_in_dim(best, slot, axis=0, keepdims=False)
    for shift in range(1, groups):
        target = lax.rem(slot + shift, groups)
        outgoing = lax.dynamic_index_in_dim(best, target, axis=0, keepdims=False)
        route = [(source, (source + shift) % groups) for source in range(groups)]
        result = jnp.maximum(result, lax.ppermute(outgoing, "orient", route))
    return result


def per_device(tiles, assigned_worker, wedge_mask, template_volume, rotation_samples):
    tile_len = tiles.shape[-1]
    planes = tiles.shape[1]
    home_slots = tiles.shape[0]
    work_slots = home_slots // 2
    box_edge = template_volume.shape[0]
    table = transform_tables(tile_len, box_edge)
    band_sum = band_table(tile_len, box_edge)
    wedge_weight = wedge_mask.astype(jnp.bfloat16)
    sampled = share_samples(template_volume, rotation_samples)
    partner_tiles = partner(tiles, "slab", 0)[work_slots:]
    occupied = assigned_worker >= 0
    own_count = jnp.sum(occupied.astype(jnp.int32))
    counter = jnp.arange(work_slots, dtype=jnp.int32)
    keep_own = (counter < own_count)[:, None, None, None]
    moved_in = pick_rows(counter - own_count, partner_tiles)
    gathered = jnp.where(keep_own, tiles[:work_slots], moved_in)
    field_real, field_imag, local_rms = field_spectra(
        gathered, wedge_weight, table, band_sum, box_edge
    )
    sampled, field_real = lax.optimization_barrier((sampled, field_real))
    templ_real, templ_imag, template_norm = make_templates(sampled, box_edge, planes, table)
    best = score_tiles(
        field_real,
        field_imag,
        local_rms,
        templ_real,
        templ_imag,
        template_norm,
        table,
    )
    best_rows = orient_max(best)
    outgoing = pick_rows(counter + own_count, best_rows)
    returned = partner(outgoing, "slab", 0)
    result = jnp.concatenate([best_rows, returned], axis=0)
    return jnp.where(occupied[:, None, None], result, jnp.zeros_like(result))


def solution(mesh):
    return jax.shard_map(
        per_device,
        mesh=mesh,
        in_specs=(P("slab", None, None, None), P("slab"), P(), P(), P("orient", "slab")),
        out_specs=P("slab", "orient", None),
        check_vma=False,
    )
```

```python
import functools
import math

import jax
import ml_dtypes
import numpy as np
import jax.numpy as jnp
from jax import lax
from jax.experimental import pallas as pl
from jax.experimental.pallas import tpu as pltpu
from jax.sharding import PartitionSpec as P


def partner(block, axis, bit):
    count = lax.axis_size(axis)
    route = []
    for low in range(count):
        high = low | 1 << bit
        if high != low and high < count:
            route += [(low, high), (high, low)]
    return lax.ppermute(block, axis, route)


def tables(length):
    counter = np.arange(length, dtype=np.int32)
    angles = (counter[:, None] * counter[None, :] % length).astype(np.float32) * np.float32(
        2.0 * math.pi / length
    )
    wide = angles.astype(np.float64)
    cosine = np.cos(wide).astype(np.float32).astype(ml_dtypes.bfloat16)
    sine = np.sin(wide).astype(np.float32).astype(ml_dtypes.bfloat16)
    return cosine, sine


def band_table(length, box_edge):
    counter = np.arange(length, dtype=np.int32)
    offsets = (counter[None, :] - counter[:, None]) % length
    return jnp.asarray((offsets < box_edge).astype(np.float32))


def transform_tables(length, box_edge):
    cosine, sine = tables(length)
    across = np.concatenate([cosine, -sine], axis=1)
    mix = np.concatenate(
        [np.concatenate([cosine, sine], axis=1), np.concatenate([-sine, cosine], axis=1)], axis=0
    )
    box_across = np.concatenate([cosine[:box_edge], -sine[:box_edge]], axis=1)
    box_down = np.concatenate(
        [
            np.concatenate([cosine[:, :box_edge], sine[:, :box_edge]], axis=1),
            np.concatenate([-sine[:, :box_edge], cosine[:, :box_edge]], axis=1),
        ],
        axis=0,
    )
    return {
        name: jnp.asarray(value)
        for name, value in (
            ("across", across),
            ("mix", mix),
            ("box_across", box_across),
            ("box_down", box_down),
        )
    }


def pick_rows(chosen, source):
    counter = jnp.arange(source.shape[0], dtype=jnp.int32)
    selector = (chosen[:, None] == counter[None, :]).astype(source.dtype)
    flat = source.reshape(source.shape[0], -1)
    picked = jnp.dot(selector, flat, preferred_element_type=jnp.float32).astype(source.dtype)
    return picked.reshape((chosen.shape[0],) + source.shape[1:])


def pick_kernel(index_ref, table_ref, out_ref, picked_ref):
    columns = table_ref.shape[0]
    rows_in_table = table_ref.shape[1]
    lanes = index_ref.shape[1]
    shift = columns.bit_length() - 1

    def body(step, carry):
        index = index_ref[pl.ds(step, 1), :]
        high = jnp.right_shift(index, shift)
        low = jnp.bitwise_and(index, columns - 1)
        row_hot = (lax.broadcasted_iota(jnp.int32, (rows_in_table, lanes), 0) == high).astype(
            jnp.bfloat16
        )
        picked_rows = jnp.dot(table_ref[...], row_hot, preferred_element_type=jnp.float32)
        column_hot = lax.broadcasted_iota(jnp.int32, (columns, lanes), 0) == low
        chosen = jnp.where(column_hot, picked_rows, 0.0)
        picked_ref[pl.ds(step, 1), :] = jnp.sum(chosen, axis=0, keepdims=True)
        return carry

    lax.fori_loop(0, index_ref.shape[0], body, 0)
    picked = picked_ref[...].astype(out_ref.dtype)
    for copy in range(out_ref.shape[0]):
        out_ref[copy] = picked


def sample_template(template_volume, rotation_samples, copies):
    total = template_volume.size
    columns = 512
    table_t = template_volume.reshape(total // columns, columns).T.astype(jnp.bfloat16)
    return pl.pallas_call(
        pick_kernel,
        out_shape=jax.ShapeDtypeStruct((copies,) + rotation_samples.shape, jnp.bfloat16),
        in_specs=[pl.BlockSpec(memory_space=pltpu.VMEM)] * 2,
        out_specs=pl.BlockSpec(memory_space=pltpu.VMEM),
        scratch_shapes=[pltpu.VMEM(rotation_samples.shape, jnp.float32)],
    )(rotation_samples, table_t)


def share_samples(template_volume, rotation_samples):
    slab_count = lax.axis_size("slab")
    spread = sample_template(template_volume, rotation_samples, slab_count)
    return lax.all_to_all(spread, "slab", 0, 0, tiled=True)


def rows_to_blocks(values, rows):
    count = values.shape[0] // rows
    return jnp.concatenate([values[i * rows : (i + 1) * rows] for i in range(count)], axis=1)


def blocks_to_rows(values, width):
    count = values.shape[1] // width
    return jnp.concatenate(
        [values[:, i * width : (i + 1) * width] for i in range(count)], axis=0
    )


def forward_rows(values, across, down):
    width = across.shape[1] // 2
    height = down.shape[1] // 2
    first = jnp.dot(values, across, preferred_element_type=jnp.float32).astype(jnp.bfloat16)
    stacked = jnp.concatenate(
        [rows_to_blocks(first[:, :width], height), rows_to_blocks(first[:, width:], height)],
        axis=0,
    )
    second = jnp.dot(down, stacked, preferred_element_type=jnp.float32).astype(jnp.bfloat16)
    return second[:width], second[width:]


def inverse_blocks(real_part, imag_part, mix, back):
    length = real_part.shape[0]
    joined = jnp.concatenate(
        [blocks_to_rows(real_part, length), blocks_to_rows(imag_part, length)], axis=1
    )
    first = jnp.dot(joined, mix, preferred_element_type=jnp.float32).astype(jnp.bfloat16)
    stacked = jnp.concatenate(
        [rows_to_blocks(first[:, :length], length), rows_to_blocks(first[:, length:], length)],
        axis=0,
    )
    return jnp.dot(back, stacked, preferred_element_type=jnp.float32)


def template_kernel(values_ref, across_ref, down_ref, real_ref, imag_ref):
    real_part, imag_part = forward_rows(values_ref[...], across_ref[...], down_ref[...])
    real_ref[...] = real_part.astype(jnp.float32)
    imag_ref[...] = imag_part.astype(jnp.float32)


def split_three(values):
    high = values.astype(jnp.bfloat16)
    rest = values - high.astype(jnp.float32)
    middle = rest.astype(jnp.bfloat16)
    low = (rest - middle.astype(jnp.float32)).astype(jnp.bfloat16)
    return (high, middle, low)


def exact_dot(left, right, left_exact):
    total = None
    if left_exact:
        for part in split_three(right):
            term = jnp.dot(left, part, preferred_element_type=jnp.float32)
            total = term if total is None else total + term
    else:
        for part in split_three(left):
            term = jnp.dot(part, right, preferred_element_type=jnp.float32)
            total = term if total is None else total + term
    return total


def field_kernel(
    values_ref, wedge_ref, across_ref, mix_ref, back_ref, band_ref, band_t_ref, real_ref,
    imag_ref, rms_ref, *, box_edge
):
    length = values_ref.shape[-1]
    maps = values_ref.shape[0] // length
    tiles = rms_ref.shape[0]
    planes = maps // tiles
    mix = mix_ref[...]
    real_part, imag_part = forward_rows(values_ref[...], across_ref[...], mix)
    wedge = jnp.concatenate([wedge_ref[...]] * maps, axis=1)
    field = inverse_blocks(real_part * wedge, imag_part * wedge, mix, back_ref[...])
    field = (field * (1.0 / (length * length))).astype(jnp.bfloat16)
    square = jnp.square(field.astype(jnp.float32))
    energies = []
    for tile in range(tiles):
        energy = None
        for plane in range(planes):
            index = tile * planes + plane
            part = square[:, index * length : (index + 1) * length]
            energy = part if energy is None else energy + part
        energies.append(energy)
    energy = jnp.concatenate(energies, axis=1)
    summed = exact_dot(band_ref[...], energy, True)
    summed = exact_dot(blocks_to_rows(summed, length), band_t_ref[...], False)
    for tile in range(tiles):
        part = summed[tile * length : (tile + 1) * length]
        rms_ref[tile] = jnp.sqrt(part / (box_edge * box_edge * planes) + 1e-05)
    real_part, imag_part = forward_rows(blocks_to_rows(field, length), across_ref[...], mix)
    real_ref[...] = real_part.astype(jnp.float32)
    imag_ref[...] = imag_part.astype(jnp.float32)


def whole_call(kernel, out_shape, *args):
    return pl.pallas_call(
        kernel,
        out_shape=out_shape,
        in_specs=[pl.BlockSpec(memory_space=pltpu.VMEM)] * len(args),
        out_specs=tuple(pl.BlockSpec(memory_space=pltpu.VMEM) for _ in out_shape),
    )(*args)


def make_templates(sampled, box_edge, planes, table):
    count = sampled.shape[1]
    length = table["across"].shape[0]
    sampled = jnp.transpose(sampled, (1, 0, 2))
    sampled = sampled.reshape(count, planes, box_edge, box_edge)
    template_norm = jnp.sqrt(
        jnp.sum(jnp.square(sampled.astype(jnp.float32)), axis=(1, 2, 3)) + 1e-05
    )
    spec_shape = jax.ShapeDtypeStruct((length, count * planes * length), jnp.float32)
    spec_real, spec_imag = whole_call(
        template_kernel,
        (spec_shape, spec_shape),
        sampled.reshape(count * planes * box_edge, box_edge),
        table["box_across"],
        table["box_down"],
    )
    return (spec_real, spec_imag, template_norm)


def field_spectra(gathered, wedge_weight, table, band_sum, box_edge):
    tiles, planes, length, _ = gathered.shape
    spec_shape = jax.ShapeDtypeStruct((length, tiles * planes * length), jnp.float32)
    return whole_call(
        functools.partial(field_kernel, box_edge=box_edge),
        (spec_shape, spec_shape, jax.ShapeDtypeStruct((tiles, length, length), jnp.float32)),
        gathered.reshape(tiles * planes * length, length),
        wedge_weight,
        table["across"],
        table["mix"],
        table["across"],
        band_sum.astype(jnp.bfloat16),
        band_sum.T.astype(jnp.bfloat16),
    )


def score_kernel(
    scale_ref, field_re_ref, field_im_ref, templ_re_ref, templ_im_ref, mix_ref, back_ref,
    rms_ref, out_ref
):
    length = field_re_ref.shape[0]
    per_step = rms_ref.shape[0]
    planes = field_re_ref.shape[1] // (per_step * length)
    count = templ_re_ref.shape[1] // (planes * length)
    group = 8 if count % 8 == 0 else 1

    def lanes(index):
        return slice(index * length, (index + 1) * length)

    for tile in range(per_step):
        best = None
        for step in range(count // group):
            joined = []
            for member in range(group):
                orient = step * group + member
                prod_re = None
                prod_im = None
                for plane in range(planes):
                    fr = field_re_ref[:, lanes(tile * planes + plane)]
                    fi = field_im_ref[:, lanes(tile * planes + plane)]
                    tr = templ_re_ref[:, lanes(orient * planes + plane)]
                    ti = templ_im_ref[:, lanes(orient * planes + plane)]
                    part_re = fr * tr + fi * ti
                    part_im = fi * tr - fr * ti
                    prod_re = part_re if prod_re is None else prod_re + part_re
                    prod_im = part_im if prod_im is None else prod_im + part_im
                joined.append(
                    jnp.concatenate(
                        [prod_re.astype(jnp.bfloat16), prod_im.astype(jnp.bfloat16)], axis=1
                    )
                )
            joined = jnp.concatenate(joined, axis=0)
            first = jnp.dot(joined, mix_ref[...], preferred_element_type=jnp.float32).astype(
                jnp.bfloat16
            )
            stacked = jnp.concatenate(
                [
                    rows_to_blocks(first[:, :length], length),
                    rows_to_blocks(first[:, length:], length),
                ],
                axis=0,
            )
            corr = jnp.dot(back_ref[...], stacked, preferred_element_type=jnp.float32)
            for member in range(group):
                orient = step * group + member
                value = corr[:, lanes(member)] * scale_ref[orient]
                best = value if best is None else jnp.maximum(best, value)
        result = (best / rms_ref[tile]).astype(out_ref.dtype)
        chunk = out_ref.shape[2]
        for part in range(out_ref.shape[0]):
            out_ref[part, tile] = result[part * chunk : (part + 1) * chunk]


def score_tiles(
    field_real, field_imag, local_rms, templ_real, templ_imag, template_norm, table
):
    length = field_real.shape[0]
    planes = field_real.shape[1] // (local_rms.shape[0] * length)
    scale = (1.0 / template_norm) * (1.0 / (length * length))
    mix = table["mix"]
    back = table["across"]
    tiles = local_rms.shape[0]
    groups = lax.axis_size("orient")
    per_step = 2 if tiles % 2 == 0 else 1
    tile_block = pl.BlockSpec((length, per_step * planes * length), lambda t: (0, t))
    templ_block = pl.BlockSpec(templ_real.shape, lambda t: (0, 0))
    return pl.pallas_call(
        score_kernel,
        grid=(tiles // per_step,),
        out_shape=jax.ShapeDtypeStruct((groups, tiles, length // groups, length), jnp.bfloat16),
        in_specs=[
            pl.BlockSpec(memory_space=pltpu.SMEM),
            tile_block,
            tile_block,
            templ_block,
            templ_block,
            pl.BlockSpec((2 * length, 2 * length), lambda t: (0, 0)),
            pl.BlockSpec((length, 2 * length), lambda t: (0, 0)),
            pl.BlockSpec((per_step, length, length), lambda t: (t, 0, 0)),
        ],
        out_specs=pl.BlockSpec(
            (groups, per_step, length // groups, length), lambda t: (0, t, 0, 0)
        ),
    )(
        scale,
        field_real,
        field_imag,
        templ_real,
        templ_imag,
        mix,
        back,
        local_rms,
    )


def orient_max(best):
    groups = lax.axis_size("orient")
    slabs = lax.axis_size("slab")
    slot = lax.axis_index("orient")
    mine = lax.dynamic_index_in_dim(best, slot, axis=0, keepdims=False)
    theirs = None
    for shift in range(groups):
        target = lax.rem(slot + shift, groups)
        outgoing = lax.dynamic_index_in_dim(best, target, axis=0, keepdims=False)
        if shift:
            route = [(source, (source + shift) % groups) for source in range(groups)]
            mine = jnp.maximum(mine, lax.ppermute(outgoing, "orient", route))
        route = []
        for low in range(slabs):
            high = low ^ 1
            if high < slabs:
                for source in range(groups):
                    route.append((low * groups + source, high * groups + (source + shift) % groups))
        moved = lax.ppermute(outgoing, ("slab", "orient"), route)
        theirs = moved if theirs is None else jnp.maximum(theirs, moved)
    return mine, theirs


def per_device(tiles, assigned_worker, wedge_mask, template_volume, rotation_samples):
    tile_len = tiles.shape[-1]
    planes = tiles.shape[1]
    home_slots = tiles.shape[0]
    work_slots = home_slots // 2
    box_edge = template_volume.shape[0]
    table = transform_tables(tile_len, box_edge)
    band_sum = band_table(tile_len, box_edge)
    wedge_weight = wedge_mask.astype(jnp.bfloat16)
    sampled = share_samples(template_volume, rotation_samples)
    partner_tiles = partner(tiles, "slab", 0)[work_slots:]
    occupied = assigned_worker >= 0
    own_count = jnp.sum(occupied.astype(jnp.int32))
    counter = jnp.arange(work_slots, dtype=jnp.int32)
    keep_own = (counter < own_count)[:, None, None, None]
    moved_in = pick_rows(counter - own_count, partner_tiles)
    gathered = jnp.where(keep_own, tiles[:work_slots], moved_in)
    field_real, field_imag, local_rms = field_spectra(
        gathered, wedge_weight, table, band_sum, box_edge
    )
    sampled, field_real = lax.optimization_barrier((sampled, field_real))
    templ_real, templ_imag, template_norm = make_templates(sampled, box_edge, planes, table)
    best = score_tiles(
        field_real,
        field_imag,
        local_rms,
        templ_real,
        templ_imag,
        template_norm,
        table,
    )
    best_rows, partner_rows = orient_max(best)
    returned = pick_rows(counter + (home_slots - own_count), partner_rows)
    result = jnp.concatenate([best_rows, returned], axis=0)
    return jnp.where(occupied[:, None, None], result, jnp.zeros_like(result))


def solution(mesh):
    return jax.shard_map(
        per_device,
        mesh=mesh,
        in_specs=(P("slab", None, None, None), P("slab"), P(), P(), P("orient", "slab")),
        out_specs=P("slab", "orient", None),
        check_vma=False,
    )
```

```python
import functools
import math

import jax
import ml_dtypes
import numpy as np
import jax.numpy as jnp
from jax import lax
from jax.experimental import pallas as pl
from jax.experimental.pallas import tpu as pltpu
from jax.sharding import PartitionSpec as P


def partner(block, axis, bit):
    count = lax.axis_size(axis)
    route = []
    for low in range(count):
        high = low | 1 << bit
        if high != low and high < count:
            route += [(low, high), (high, low)]
    return lax.ppermute(block, axis, route)


def tables(length):
    counter = np.arange(length, dtype=np.int32)
    angles = (counter[:, None] * counter[None, :] % length).astype(np.float32) * np.float32(
        2.0 * math.pi / length
    )
    wide = angles.astype(np.float64)
    cosine = np.cos(wide).astype(np.float32).astype(ml_dtypes.bfloat16)
    sine = np.sin(wide).astype(np.float32).astype(ml_dtypes.bfloat16)
    return cosine, sine


def band_table(length, box_edge):
    counter = np.arange(length, dtype=np.int32)
    offsets = (counter[None, :] - counter[:, None]) % length
    return jnp.asarray((offsets < box_edge).astype(np.float32))


def transform_tables(length, box_edge):
    cosine, sine = tables(length)
    across = np.concatenate([cosine, -sine], axis=1)
    mix = np.concatenate(
        [np.concatenate([cosine, sine], axis=1), np.concatenate([-sine, cosine], axis=1)], axis=0
    )
    box_across = np.concatenate([cosine[:box_edge], -sine[:box_edge]], axis=1)
    box_down = np.concatenate(
        [
            np.concatenate([cosine[:, :box_edge], sine[:, :box_edge]], axis=1),
            np.concatenate([-sine[:, :box_edge], cosine[:, :box_edge]], axis=1),
        ],
        axis=0,
    )
    return {
        name: jnp.asarray(value)
        for name, value in (
            ("across", across),
            ("mix", mix),
            ("box_across", box_across),
            ("box_down", box_down),
        )
    }


def pick_rows(chosen, source):
    counter = jnp.arange(source.shape[0], dtype=jnp.int32)
    selector = (chosen[:, None] == counter[None, :]).astype(source.dtype)
    flat = source.reshape(source.shape[0], -1)
    picked = jnp.dot(selector, flat, preferred_element_type=jnp.float32).astype(source.dtype)
    return picked.reshape((chosen.shape[0],) + source.shape[1:])


def pick_kernel(index_ref, table_ref, out_ref, picked_ref):
    columns = table_ref.shape[0]
    rows_in_table = table_ref.shape[1]
    lanes = index_ref.shape[1]
    shift = columns.bit_length() - 1

    def body(step, carry):
        index = index_ref[pl.ds(step, 1), :]
        high = jnp.right_shift(index, shift)
        low = jnp.bitwise_and(index, columns - 1)
        row_hot = (lax.broadcasted_iota(jnp.int32, (rows_in_table, lanes), 0) == high).astype(
            jnp.bfloat16
        )
        picked_rows = jnp.dot(table_ref[...], row_hot, preferred_element_type=jnp.float32)
        column_hot = lax.broadcasted_iota(jnp.int32, (columns, lanes), 0) == low
        chosen = jnp.where(column_hot, picked_rows, 0.0)
        picked_ref[pl.ds(step, 1), :] = jnp.sum(chosen, axis=0, keepdims=True)
        return carry

    lax.fori_loop(0, index_ref.shape[0], body, 0)
    picked = picked_ref[...].astype(out_ref.dtype)
    for copy in range(out_ref.shape[0]):
        out_ref[copy] = picked


def sample_template(template_volume, rotation_samples, copies):
    total = template_volume.size
    columns = 512
    table_t = template_volume.reshape(total // columns, columns).T.astype(jnp.bfloat16)
    return pl.pallas_call(
        pick_kernel,
        out_shape=jax.ShapeDtypeStruct((copies,) + rotation_samples.shape, jnp.bfloat16),
        in_specs=[pl.BlockSpec(memory_space=pltpu.VMEM)] * 2,
        out_specs=pl.BlockSpec(memory_space=pltpu.VMEM),
        scratch_shapes=[pltpu.VMEM(rotation_samples.shape, jnp.float32)],
    )(rotation_samples, table_t)


def share_samples(template_volume, rotation_samples):
    slab_count = lax.axis_size("slab")
    spread = sample_template(template_volume, rotation_samples, slab_count)
    return lax.all_to_all(spread, "slab", 0, 0, tiled=True)


def rows_to_blocks(values, rows):
    count = values.shape[0] // rows
    return jnp.concatenate([values[i * rows : (i + 1) * rows] for i in range(count)], axis=1)


def blocks_to_rows(values, width):
    count = values.shape[1] // width
    return jnp.concatenate(
        [values[:, i * width : (i + 1) * width] for i in range(count)], axis=0
    )


def forward_rows(values, across, down):
    width = across.shape[1] // 2
    height = down.shape[1] // 2
    first = jnp.dot(values, across, preferred_element_type=jnp.float32).astype(jnp.bfloat16)
    stacked = jnp.concatenate(
        [rows_to_blocks(first[:, :width], height), rows_to_blocks(first[:, width:], height)],
        axis=0,
    )
    second = jnp.dot(down, stacked, preferred_element_type=jnp.float32).astype(jnp.bfloat16)
    return second[:width], second[width:]


def inverse_blocks(real_part, imag_part, mix, back):
    length = real_part.shape[0]
    joined = jnp.concatenate(
        [blocks_to_rows(real_part, length), blocks_to_rows(imag_part, length)], axis=1
    )
    first = jnp.dot(joined, mix, preferred_element_type=jnp.float32).astype(jnp.bfloat16)
    stacked = jnp.concatenate(
        [rows_to_blocks(first[:, :length], length), rows_to_blocks(first[:, length:], length)],
        axis=0,
    )
    return jnp.dot(back, stacked, preferred_element_type=jnp.float32)


def template_kernel(values_ref, across_ref, down_ref, real_ref, imag_ref):
    real_part, imag_part = forward_rows(values_ref[...], across_ref[...], down_ref[...])
    real_ref[...] = real_part.astype(jnp.float32)
    imag_ref[...] = imag_part.astype(jnp.float32)


def split_three(values):
    high = values.astype(jnp.bfloat16)
    rest = values - high.astype(jnp.float32)
    middle = rest.astype(jnp.bfloat16)
    low = (rest - middle.astype(jnp.float32)).astype(jnp.bfloat16)
    return (high, middle, low)


def exact_dot(left, right, left_exact):
    total = None
    if left_exact:
        for part in split_three(right):
            term = jnp.dot(left, part, preferred_element_type=jnp.float32)
            total = term if total is None else total + term
    else:
        for part in split_three(left):
            term = jnp.dot(part, right, preferred_element_type=jnp.float32)
            total = term if total is None else total + term
    return total


def field_kernel(
    count_ref, own_ref, other_ref, wedge_ref, across_ref, mix_ref, back_ref, band_ref,
    band_t_ref, real_ref, imag_ref, rms_ref, *, box_edge
):
    home, planes, length, _ = own_ref.shape
    tiles = rms_ref.shape[0]
    maps = tiles * planes
    own_count = count_ref[0]
    picked = []
    for tile in range(tiles):
        source = jnp.clip(tiles + tile - own_count, 0, home - 1)
        chosen = jnp.where(tile < own_count, own_ref[tile], other_ref[source])
        picked.append(chosen.reshape(planes * length, length))
    values = jnp.concatenate(picked, axis=0)
    mix = mix_ref[...]
    real_part, imag_part = forward_rows(values, across_ref[...], mix)
    wedge = wedge_ref[...].astype(jnp.float32).astype(jnp.bfloat16)
    wedge = jnp.concatenate([wedge] * maps, axis=1)
    field = inverse_blocks(real_part * wedge, imag_part * wedge, mix, back_ref[...])
    field = (field * (1.0 / (length * length))).astype(jnp.bfloat16)
    square = jnp.square(field.astype(jnp.float32))
    energies = []
    for tile in range(tiles):
        energy = None
        for plane in range(planes):
            index = tile * planes + plane
            part = square[:, index * length : (index + 1) * length]
            energy = part if energy is None else energy + part
        energies.append(energy)
    energy = jnp.concatenate(energies, axis=1)
    summed = exact_dot(band_ref[...], energy, True)
    summed = exact_dot(blocks_to_rows(summed, length), band_t_ref[...], False)
    for tile in range(tiles):
        part = summed[tile * length : (tile + 1) * length]
        rms_ref[tile] = jnp.sqrt(part / (box_edge * box_edge * planes) + 1e-05)
    real_part, imag_part = forward_rows(blocks_to_rows(field, length), across_ref[...], mix)
    real_ref[...] = real_part.astype(jnp.float32)
    imag_ref[...] = imag_part.astype(jnp.float32)


def whole_call(kernel, out_shape, *args):
    return pl.pallas_call(
        kernel,
        out_shape=out_shape,
        in_specs=[pl.BlockSpec(memory_space=pltpu.VMEM)] * len(args),
        out_specs=tuple(pl.BlockSpec(memory_space=pltpu.VMEM) for _ in out_shape),
    )(*args)


def make_templates(sampled, box_edge, planes, table):
    count = sampled.shape[1]
    length = table["across"].shape[0]
    sampled = jnp.transpose(sampled, (1, 0, 2))
    sampled = sampled.reshape(count, planes, box_edge, box_edge)
    template_norm = jnp.sqrt(
        jnp.sum(jnp.square(sampled.astype(jnp.float32)), axis=(1, 2, 3)) + 1e-05
    )
    spec_shape = jax.ShapeDtypeStruct((length, count * planes * length), jnp.float32)
    spec_real, spec_imag = whole_call(
        template_kernel,
        (spec_shape, spec_shape),
        sampled.reshape(count * planes * box_edge, box_edge),
        table["box_across"],
        table["box_down"],
    )
    return (spec_real, spec_imag, template_norm)


def field_spectra(own_count, tiles_own, tiles_other, wedge_mask, table, band_sum, box_edge):
    home, planes, length, _ = tiles_own.shape
    tiles = home // 2
    spec_shape = jax.ShapeDtypeStruct((length, tiles * planes * length), jnp.float32)
    args = (
        own_count.reshape(1),
        tiles_own,
        tiles_other,
        wedge_mask,
        table["across"],
        table["mix"],
        table["across"],
        band_sum.astype(jnp.bfloat16),
        band_sum.T.astype(jnp.bfloat16),
    )
    out_shape = (
        spec_shape,
        spec_shape,
        jax.ShapeDtypeStruct((tiles, length, length), jnp.float32),
    )
    return pl.pallas_call(
        functools.partial(field_kernel, box_edge=box_edge),
        out_shape=out_shape,
        in_specs=[pl.BlockSpec(memory_space=pltpu.SMEM)]
        + [pl.BlockSpec(memory_space=pltpu.VMEM)] * (len(args) - 1),
        out_specs=tuple(pl.BlockSpec(memory_space=pltpu.VMEM) for _ in out_shape),
    )(*args)


def score_kernel(
    scale_ref, field_re_ref, field_im_ref, templ_re_ref, templ_im_ref, mix_ref, back_ref,
    rms_ref, out_ref
):
    length = field_re_ref.shape[0]
    per_step = rms_ref.shape[0]
    planes = field_re_ref.shape[1] // (per_step * length)
    count = templ_re_ref.shape[1] // (planes * length)
    group = 8 if count % 8 == 0 else 1

    def lanes(index):
        return slice(index * length, (index + 1) * length)

    for tile in range(per_step):
        best = None
        for step in range(count // group):
            joined = []
            for member in range(group):
                orient = step * group + member
                prod_re = None
                prod_im = None
                for plane in range(planes):
                    fr = field_re_ref[:, lanes(tile * planes + plane)]
                    fi = field_im_ref[:, lanes(tile * planes + plane)]
                    tr = templ_re_ref[:, lanes(orient * planes + plane)]
                    ti = templ_im_ref[:, lanes(orient * planes + plane)]
                    part_re = fr * tr + fi * ti
                    part_im = fi * tr - fr * ti
                    prod_re = part_re if prod_re is None else prod_re + part_re
                    prod_im = part_im if prod_im is None else prod_im + part_im
                joined.append(
                    jnp.concatenate(
                        [prod_re.astype(jnp.bfloat16), prod_im.astype(jnp.bfloat16)], axis=1
                    )
                )
            joined = jnp.concatenate(joined, axis=0)
            first = jnp.dot(joined, mix_ref[...], preferred_element_type=jnp.float32).astype(
                jnp.bfloat16
            )
            stacked = jnp.concatenate(
                [
                    rows_to_blocks(first[:, :length], length),
                    rows_to_blocks(first[:, length:], length),
                ],
                axis=0,
            )
            corr = jnp.dot(back_ref[...], stacked, preferred_element_type=jnp.float32)
            for member in range(group):
                orient = step * group + member
                value = corr[:, lanes(member)] * scale_ref[orient]
                best = value if best is None else jnp.maximum(best, value)
        result = (best / rms_ref[tile]).astype(out_ref.dtype)
        chunk = out_ref.shape[2]
        for part in range(out_ref.shape[0]):
            out_ref[part, tile] = result[part * chunk : (part + 1) * chunk]


def score_tiles(
    field_real, field_imag, local_rms, templ_real, templ_imag, template_norm, table
):
    length = field_real.shape[0]
    planes = field_real.shape[1] // (local_rms.shape[0] * length)
    scale = (1.0 / template_norm) * (1.0 / (length * length))
    mix = table["mix"]
    back = table["across"]
    tiles = local_rms.shape[0]
    groups = lax.axis_size("orient")
    per_step = 2 if tiles % 2 == 0 else 1
    tile_block = pl.BlockSpec((length, per_step * planes * length), lambda t: (0, t))
    templ_block = pl.BlockSpec(templ_real.shape, lambda t: (0, 0))
    return pl.pallas_call(
        score_kernel,
        grid=(tiles // per_step,),
        out_shape=jax.ShapeDtypeStruct((groups, tiles, length // groups, length), jnp.bfloat16),
        in_specs=[
            pl.BlockSpec(memory_space=pltpu.SMEM),
            tile_block,
            tile_block,
            templ_block,
            templ_block,
            pl.BlockSpec((2 * length, 2 * length), lambda t: (0, 0)),
            pl.BlockSpec((length, 2 * length), lambda t: (0, 0)),
            pl.BlockSpec((per_step, length, length), lambda t: (t, 0, 0)),
        ],
        out_specs=pl.BlockSpec(
            (groups, per_step, length // groups, length), lambda t: (0, t, 0, 0)
        ),
    )(
        scale,
        field_real,
        field_imag,
        templ_real,
        templ_imag,
        mix,
        back,
        local_rms,
    )


def orient_max(best):
    groups = lax.axis_size("orient")
    slot = lax.axis_index("orient")
    result = lax.dynamic_index_in_dim(best, slot, axis=0, keepdims=False)
    for shift in range(1, groups):
        target = lax.rem(slot + shift, groups)
        outgoing = lax.dynamic_index_in_dim(best, target, axis=0, keepdims=False)
        route = [(source, (source + shift) % groups) for source in range(groups)]
        result = jnp.maximum(result, lax.ppermute(outgoing, "orient", route))
    return result


def per_device(tiles, assigned_worker, wedge_mask, template_volume, rotation_samples):
    tile_len = tiles.shape[-1]
    planes = tiles.shape[1]
    home_slots = tiles.shape[0]
    work_slots = home_slots // 2
    box_edge = template_volume.shape[0]
    table = transform_tables(tile_len, box_edge)
    band_sum = band_table(tile_len, box_edge)
    sampled = share_samples(template_volume, rotation_samples)
    partner_tiles = partner(tiles, "slab", 0)
    occupied = assigned_worker >= 0
    own_count = jnp.sum(occupied.astype(jnp.int32))
    counter = jnp.arange(work_slots, dtype=jnp.int32)
    field_real, field_imag, local_rms = field_spectra(
        own_count, tiles, partner_tiles, wedge_mask, table, band_sum, box_edge
    )
    sampled, field_real = lax.optimization_barrier((sampled, field_real))
    templ_real, templ_imag, template_norm = make_templates(sampled, box_edge, planes, table)
    best = score_tiles(
        field_real,
        field_imag,
        local_rms,
        templ_real,
        templ_imag,
        template_norm,
        table,
    )
    best_rows = orient_max(best)
    outgoing = pick_rows(counter + own_count, best_rows)
    returned = partner(outgoing, "slab", 0)
    result = jnp.concatenate([best_rows, returned], axis=0)
    return jnp.where(occupied[:, None, None], result, jnp.zeros_like(result))


def solution(mesh):
    return jax.shard_map(
        per_device,
        mesh=mesh,
        in_specs=(P("slab", None, None, None), P("slab"), P(), P(), P("orient", "slab")),
        out_specs=P("slab", "orient", None),
        check_vma=False,
    )
```

```python
import functools
import math

import jax
import ml_dtypes
import numpy as np
import jax.numpy as jnp
from jax import lax
from jax.experimental import pallas as pl
from jax.experimental.pallas import tpu as pltpu
from jax.sharding import PartitionSpec as P


def partner(block, axis, bit):
    count = lax.axis_size(axis)
    route = []
    for low in range(count):
        high = low | 1 << bit
        if high != low and high < count:
            route += [(low, high), (high, low)]
    return lax.ppermute(block, axis, route)


def tables(length):
    counter = np.arange(length, dtype=np.int32)
    angles = (counter[:, None] * counter[None, :] % length).astype(np.float32) * np.float32(
        2.0 * math.pi / length
    )
    wide = angles.astype(np.float64)
    cosine = np.cos(wide).astype(np.float32).astype(ml_dtypes.bfloat16)
    sine = np.sin(wide).astype(np.float32).astype(ml_dtypes.bfloat16)
    return cosine, sine


def band_table(length, box_edge):
    counter = np.arange(length, dtype=np.int32)
    offsets = (counter[None, :] - counter[:, None]) % length
    return jnp.asarray((offsets < box_edge).astype(np.float32))


def transform_tables(length, box_edge):
    cosine, sine = tables(length)
    across = np.concatenate([cosine, -sine], axis=1)
    mix = np.concatenate(
        [np.concatenate([cosine, sine], axis=1), np.concatenate([-sine, cosine], axis=1)], axis=0
    )
    box_across = np.concatenate([cosine[:box_edge], -sine[:box_edge]], axis=1)
    box_down = np.concatenate(
        [
            np.concatenate([cosine[:, :box_edge], sine[:, :box_edge]], axis=1),
            np.concatenate([-sine[:, :box_edge], cosine[:, :box_edge]], axis=1),
        ],
        axis=0,
    )
    return {
        name: jnp.asarray(value)
        for name, value in (
            ("across", across),
            ("mix", mix),
            ("box_across", box_across),
            ("box_down", box_down),
        )
    }


def pick_rows(chosen, source):
    counter = jnp.arange(source.shape[0], dtype=jnp.int32)
    selector = (chosen[:, None] == counter[None, :]).astype(source.dtype)
    flat = source.reshape(source.shape[0], -1)
    picked = jnp.dot(selector, flat, preferred_element_type=jnp.float32).astype(source.dtype)
    return picked.reshape((chosen.shape[0],) + source.shape[1:])


def pick_kernel(index_ref, table_ref, out_ref, picked_ref):
    columns = table_ref.shape[0]
    rows_in_table = table_ref.shape[1]
    lanes = index_ref.shape[1]
    shift = columns.bit_length() - 1

    def body(step, carry):
        index = index_ref[pl.ds(step, 1), :]
        high = jnp.right_shift(index, shift)
        low = jnp.bitwise_and(index, columns - 1)
        row_hot = (lax.broadcasted_iota(jnp.int32, (rows_in_table, lanes), 0) == high).astype(
            jnp.bfloat16
        )
        picked_rows = jnp.dot(table_ref[...], row_hot, preferred_element_type=jnp.float32)
        column_hot = lax.broadcasted_iota(jnp.int32, (columns, lanes), 0) == low
        chosen = jnp.where(column_hot, picked_rows, 0.0)
        picked_ref[pl.ds(step, 1), :] = jnp.sum(chosen, axis=0, keepdims=True)
        return carry

    lax.fori_loop(0, index_ref.shape[0], body, 0, unroll=2)
    picked = picked_ref[...].astype(out_ref.dtype)
    for copy in range(out_ref.shape[0]):
        out_ref[copy] = picked


def sample_template(template_volume, rotation_samples, copies):
    total = template_volume.size
    columns = 512
    table_t = template_volume.reshape(total // columns, columns).T.astype(jnp.bfloat16)
    return pl.pallas_call(
        pick_kernel,
        out_shape=jax.ShapeDtypeStruct((copies,) + rotation_samples.shape, jnp.bfloat16),
        in_specs=[pl.BlockSpec(memory_space=pltpu.VMEM)] * 2,
        out_specs=pl.BlockSpec(memory_space=pltpu.VMEM),
        scratch_shapes=[pltpu.VMEM(rotation_samples.shape, jnp.float32)],
    )(rotation_samples, table_t)


def share_samples(template_volume, rotation_samples):
    slab_count = lax.axis_size("slab")
    spread = sample_template(template_volume, rotation_samples, slab_count)
    return lax.all_to_all(spread, "slab", 0, 0, tiled=True)


def rows_to_blocks(values, rows):
    count = values.shape[0] // rows
    return jnp.concatenate([values[i * rows : (i + 1) * rows] for i in range(count)], axis=1)


def blocks_to_rows(values, width):
    count = values.shape[1] // width
    return jnp.concatenate(
        [values[:, i * width : (i + 1) * width] for i in range(count)], axis=0
    )


def forward_rows(values, across, down):
    width = across.shape[1] // 2
    height = down.shape[1] // 2
    first = jnp.dot(values, across, preferred_element_type=jnp.float32).astype(jnp.bfloat16)
    stacked = jnp.concatenate(
        [rows_to_blocks(first[:, :width], height), rows_to_blocks(first[:, width:], height)],
        axis=0,
    )
    second = jnp.dot(down, stacked, preferred_element_type=jnp.float32).astype(jnp.bfloat16)
    return second[:width], second[width:]


def inverse_blocks(real_part, imag_part, mix, back):
    length = real_part.shape[0]
    joined = jnp.concatenate(
        [blocks_to_rows(real_part, length), blocks_to_rows(imag_part, length)], axis=1
    )
    first = jnp.dot(joined, mix, preferred_element_type=jnp.float32).astype(jnp.bfloat16)
    stacked = jnp.concatenate(
        [rows_to_blocks(first[:, :length], length), rows_to_blocks(first[:, length:], length)],
        axis=0,
    )
    return jnp.dot(back, stacked, preferred_element_type=jnp.float32)


def template_kernel(values_ref, across_ref, down_ref, real_ref, imag_ref):
    real_part, imag_part = forward_rows(values_ref[...], across_ref[...], down_ref[...])
    real_ref[...] = real_part.astype(jnp.float32)
    imag_ref[...] = imag_part.astype(jnp.float32)


def split_three(values):
    high = values.astype(jnp.bfloat16)
    rest = values - high.astype(jnp.float32)
    middle = rest.astype(jnp.bfloat16)
    low = (rest - middle.astype(jnp.float32)).astype(jnp.bfloat16)
    return (high, middle, low)


def exact_dot(left, right, left_exact):
    total = None
    if left_exact:
        for part in split_three(right):
            term = jnp.dot(left, part, preferred_element_type=jnp.float32)
            total = term if total is None else total + term
    else:
        for part in split_three(left):
            term = jnp.dot(part, right, preferred_element_type=jnp.float32)
            total = term if total is None else total + term
    return total


def field_kernel(
    count_ref, own_ref, other_ref, wedge_ref, across_ref, mix_ref, back_ref, band_ref,
    band_t_ref, real_ref, imag_ref, rms_ref, *, box_edge
):
    home, planes, length, _ = own_ref.shape
    tiles = rms_ref.shape[0]
    maps = tiles * planes
    own_count = count_ref[0]
    picked = []
    for tile in range(tiles):
        source = jnp.clip(tiles + tile - own_count, 0, home - 1)
        chosen = jnp.where(tile < own_count, own_ref[tile], other_ref[source])
        picked.append(chosen.reshape(planes * length, length))
    values = jnp.concatenate(picked, axis=0)
    mix = mix_ref[...]
    real_part, imag_part = forward_rows(values, across_ref[...], mix)
    wedge = wedge_ref[...].astype(jnp.float32).astype(jnp.bfloat16)
    wedge = jnp.concatenate([wedge] * maps, axis=1)
    field = inverse_blocks(real_part * wedge, imag_part * wedge, mix, back_ref[...])
    field = (field * (1.0 / (length * length))).astype(jnp.bfloat16)
    square = jnp.square(field.astype(jnp.float32))
    energies = []
    for tile in range(tiles):
        energy = None
        for plane in range(planes):
            index = tile * planes + plane
            part = square[:, index * length : (index + 1) * length]
            energy = part if energy is None else energy + part
        energies.append(energy)
    energy = jnp.concatenate(energies, axis=1)
    summed = exact_dot(band_ref[...], energy, True)
    summed = exact_dot(blocks_to_rows(summed, length), band_t_ref[...], False)
    for tile in range(tiles):
        part = summed[tile * length : (tile + 1) * length]
        rms_ref[tile] = jnp.sqrt(part / (box_edge * box_edge * planes) + 1e-05)
    real_part, imag_part = forward_rows(blocks_to_rows(field, length), across_ref[...], mix)
    real_ref[...] = real_part.astype(jnp.float32)
    imag_ref[...] = imag_part.astype(jnp.float32)


def whole_call(kernel, out_shape, *args):
    return pl.pallas_call(
        kernel,
        out_shape=out_shape,
        in_specs=[pl.BlockSpec(memory_space=pltpu.VMEM)] * len(args),
        out_specs=tuple(pl.BlockSpec(memory_space=pltpu.VMEM) for _ in out_shape),
    )(*args)


def make_templates(sampled, box_edge, planes, table):
    count = sampled.shape[1]
    length = table["across"].shape[0]
    sampled = jnp.transpose(sampled, (1, 0, 2))
    sampled = sampled.reshape(count, planes, box_edge, box_edge)
    template_norm = jnp.sqrt(
        jnp.sum(jnp.square(sampled.astype(jnp.float32)), axis=(1, 2, 3)) + 1e-05
    )
    spec_shape = jax.ShapeDtypeStruct((length, count * planes * length), jnp.float32)
    spec_real, spec_imag = whole_call(
        template_kernel,
        (spec_shape, spec_shape),
        sampled.reshape(count * planes * box_edge, box_edge),
        table["box_across"],
        table["box_down"],
    )
    return (spec_real, spec_imag, template_norm)


def field_spectra(own_count, tiles_own, tiles_other, wedge_mask, table, band_sum, box_edge):
    home, planes, length, _ = tiles_own.shape
    tiles = home // 2
    spec_shape = jax.ShapeDtypeStruct((length, tiles * planes * length), jnp.float32)
    args = (
        own_count.reshape(1),
        tiles_own,
        tiles_other,
        wedge_mask,
        table["across"],
        table["mix"],
        table["across"],
        band_sum.astype(jnp.bfloat16),
        band_sum.T.astype(jnp.bfloat16),
    )
    out_shape = (
        spec_shape,
        spec_shape,
        jax.ShapeDtypeStruct((tiles, length, length), jnp.float32),
    )
    return pl.pallas_call(
        functools.partial(field_kernel, box_edge=box_edge),
        out_shape=out_shape,
        in_specs=[pl.BlockSpec(memory_space=pltpu.SMEM)]
        + [pl.BlockSpec(memory_space=pltpu.VMEM)] * (len(args) - 1),
        out_specs=tuple(pl.BlockSpec(memory_space=pltpu.VMEM) for _ in out_shape),
    )(*args)


def score_kernel(
    scale_ref, field_re_ref, field_im_ref, templ_re_ref, templ_im_ref, mix_ref, back_ref,
    rms_ref, out_ref
):
    length = field_re_ref.shape[0]
    per_step = rms_ref.shape[0]
    planes = field_re_ref.shape[1] // (per_step * length)
    count = templ_re_ref.shape[1] // (planes * length)
    group = 8 if count % 8 == 0 else 1

    def lanes(index):
        return slice(index * length, (index + 1) * length)

    for tile in range(per_step):
        best = None
        for step in range(count // group):
            joined = []
            for member in range(group):
                orient = step * group + member
                prod_re = None
                prod_im = None
                for plane in range(planes):
                    fr = field_re_ref[:, lanes(tile * planes + plane)]
                    fi = field_im_ref[:, lanes(tile * planes + plane)]
                    tr = templ_re_ref[:, lanes(orient * planes + plane)]
                    ti = templ_im_ref[:, lanes(orient * planes + plane)]
                    part_re = fr * tr + fi * ti
                    part_im = fi * tr - fr * ti
                    prod_re = part_re if prod_re is None else prod_re + part_re
                    prod_im = part_im if prod_im is None else prod_im + part_im
                joined.append(
                    jnp.concatenate(
                        [prod_re.astype(jnp.bfloat16), prod_im.astype(jnp.bfloat16)], axis=1
                    )
                )
            joined = jnp.concatenate(joined, axis=0)
            first = jnp.dot(joined, mix_ref[...], preferred_element_type=jnp.float32).astype(
                jnp.bfloat16
            )
            stacked = jnp.concatenate(
                [
                    rows_to_blocks(first[:, :length], length),
                    rows_to_blocks(first[:, length:], length),
                ],
                axis=0,
            )
            corr = jnp.dot(back_ref[...], stacked, preferred_element_type=jnp.float32)
            for member in range(group):
                orient = step * group + member
                value = corr[:, lanes(member)] * scale_ref[orient]
                best = value if best is None else jnp.maximum(best, value)
        result = (best / rms_ref[tile]).astype(out_ref.dtype)
        chunk = out_ref.shape[2]
        for part in range(out_ref.shape[0]):
            out_ref[part, tile] = result[part * chunk : (part + 1) * chunk]


def score_tiles(
    field_real, field_imag, local_rms, templ_real, templ_imag, template_norm, table
):
    length = field_real.shape[0]
    planes = field_real.shape[1] // (local_rms.shape[0] * length)
    scale = (1.0 / template_norm) * (1.0 / (length * length))
    mix = table["mix"]
    back = table["across"]
    tiles = local_rms.shape[0]
    groups = lax.axis_size("orient")
    per_step = 2 if tiles % 2 == 0 else 1
    tile_block = pl.BlockSpec((length, per_step * planes * length), lambda t: (0, t))
    templ_block = pl.BlockSpec(templ_real.shape, lambda t: (0, 0))
    return pl.pallas_call(
        score_kernel,
        grid=(tiles // per_step,),
        out_shape=jax.ShapeDtypeStruct((groups, tiles, length // groups, length), jnp.bfloat16),
        in_specs=[
            pl.BlockSpec(memory_space=pltpu.SMEM),
            tile_block,
            tile_block,
            templ_block,
            templ_block,
            pl.BlockSpec((2 * length, 2 * length), lambda t: (0, 0)),
            pl.BlockSpec((length, 2 * length), lambda t: (0, 0)),
            pl.BlockSpec((per_step, length, length), lambda t: (t, 0, 0)),
        ],
        out_specs=pl.BlockSpec(
            (groups, per_step, length // groups, length), lambda t: (0, t, 0, 0)
        ),
    )(
        scale,
        field_real,
        field_imag,
        templ_real,
        templ_imag,
        mix,
        back,
        local_rms,
    )


def orient_max(best):
    groups = lax.axis_size("orient")
    slot = lax.axis_index("orient")
    result = lax.dynamic_index_in_dim(best, slot, axis=0, keepdims=False)
    for shift in range(1, groups):
        target = lax.rem(slot + shift, groups)
        outgoing = lax.dynamic_index_in_dim(best, target, axis=0, keepdims=False)
        route = [(source, (source + shift) % groups) for source in range(groups)]
        result = jnp.maximum(result, lax.ppermute(outgoing, "orient", route))
    return result


def per_device(tiles, assigned_worker, wedge_mask, template_volume, rotation_samples):
    tile_len = tiles.shape[-1]
    planes = tiles.shape[1]
    home_slots = tiles.shape[0]
    work_slots = home_slots // 2
    box_edge = template_volume.shape[0]
    table = transform_tables(tile_len, box_edge)
    band_sum = band_table(tile_len, box_edge)
    sampled = share_samples(template_volume, rotation_samples)
    partner_tiles = partner(tiles, "slab", 0)
    occupied = assigned_worker >= 0
    own_count = jnp.sum(occupied.astype(jnp.int32))
    counter = jnp.arange(work_slots, dtype=jnp.int32)
    field_real, field_imag, local_rms = field_spectra(
        own_count, tiles, partner_tiles, wedge_mask, table, band_sum, box_edge
    )
    sampled, field_real = lax.optimization_barrier((sampled, field_real))
    templ_real, templ_imag, template_norm = make_templates(sampled, box_edge, planes, table)
    best = score_tiles(
        field_real,
        field_imag,
        local_rms,
        templ_real,
        templ_imag,
        template_norm,
        table,
    )
    best_rows = orient_max(best)
    outgoing = pick_rows(counter + own_count, best_rows)
    returned = partner(outgoing, "slab", 0)
    result = jnp.concatenate([best_rows, returned], axis=0)
    return jnp.where(occupied[:, None, None], result, jnp.zeros_like(result))


def solution(mesh):
    return jax.shard_map(
        per_device,
        mesh=mesh,
        in_specs=(P("slab", None, None, None), P("slab"), P(), P(), P("orient", "slab")),
        out_specs=P("slab", "orient", None),
        check_vma=False,
    )
```

```python
import functools
import math

import jax
import ml_dtypes
import numpy as np
import jax.numpy as jnp
from jax import lax
from jax.experimental import pallas as pl
from jax.experimental.pallas import tpu as pltpu
from jax.sharding import PartitionSpec as P


def partner(block, axis, bit):
    count = lax.axis_size(axis)
    route = []
    for low in range(count):
        high = low | 1 << bit
        if high != low and high < count:
            route += [(low, high), (high, low)]
    return lax.ppermute(block, axis, route)


def tables(length):
    counter = np.arange(length, dtype=np.int32)
    angles = (counter[:, None] * counter[None, :] % length).astype(np.float32) * np.float32(
        2.0 * math.pi / length
    )
    wide = angles.astype(np.float64)
    cosine = np.cos(wide).astype(np.float32).astype(ml_dtypes.bfloat16)
    sine = np.sin(wide).astype(np.float32).astype(ml_dtypes.bfloat16)
    return cosine, sine


def band_table(length, box_edge):
    counter = np.arange(length, dtype=np.int32)
    offsets = (counter[None, :] - counter[:, None]) % length
    return jnp.asarray((offsets < box_edge).astype(np.float32))


def transform_tables(length, box_edge):
    cosine, sine = tables(length)
    across = np.concatenate([cosine, -sine], axis=1)
    mix = np.concatenate(
        [np.concatenate([cosine, sine], axis=1), np.concatenate([-sine, cosine], axis=1)], axis=0
    )
    box_across = np.concatenate([cosine[:box_edge], -sine[:box_edge]], axis=1)
    box_down = np.concatenate(
        [
            np.concatenate([cosine[:, :box_edge], sine[:, :box_edge]], axis=1),
            np.concatenate([-sine[:, :box_edge], cosine[:, :box_edge]], axis=1),
        ],
        axis=0,
    )
    return {
        name: jnp.asarray(value)
        for name, value in (
            ("across", across),
            ("mix", mix),
            ("box_across", box_across),
            ("box_down", box_down),
        )
    }


def pick_rows(chosen, source):
    counter = jnp.arange(source.shape[0], dtype=jnp.int32)
    selector = (chosen[:, None] == counter[None, :]).astype(source.dtype)
    flat = source.reshape(source.shape[0], -1)
    picked = jnp.dot(selector, flat, preferred_element_type=jnp.float32).astype(source.dtype)
    return picked.reshape((chosen.shape[0],) + source.shape[1:])


def pick_kernel(index_ref, table_ref, out_ref, picked_ref):
    columns = table_ref.shape[0]
    rows_in_table = table_ref.shape[1]
    lanes = index_ref.shape[1]
    shift = columns.bit_length() - 1

    def body(step, carry):
        index = index_ref[pl.ds(step, 1), :]
        high = jnp.right_shift(index, shift)
        low = jnp.bitwise_and(index, columns - 1)
        row_hot = (lax.broadcasted_iota(jnp.int32, (rows_in_table, lanes), 0) == high).astype(
            jnp.bfloat16
        )
        picked_rows = jnp.dot(table_ref[...], row_hot, preferred_element_type=jnp.float32)
        column_hot = lax.broadcasted_iota(jnp.int32, (columns, lanes), 0) == low
        chosen = jnp.where(column_hot, picked_rows, 0.0)
        picked_ref[pl.ds(step, 1), :] = jnp.sum(chosen, axis=0, keepdims=True)
        return carry

    lax.fori_loop(0, index_ref.shape[0], body, 0, unroll=2)
    picked = picked_ref[...].astype(out_ref.dtype)
    for copy in range(out_ref.shape[0]):
        out_ref[copy] = picked


def sample_template(template_volume, rotation_samples, copies):
    total = template_volume.size
    columns = 512
    table_t = template_volume.reshape(total // columns, columns).T.astype(jnp.bfloat16)
    return pl.pallas_call(
        pick_kernel,
        out_shape=jax.ShapeDtypeStruct((copies,) + rotation_samples.shape, jnp.bfloat16),
        in_specs=[pl.BlockSpec(memory_space=pltpu.VMEM)] * 2,
        out_specs=pl.BlockSpec(memory_space=pltpu.VMEM),
        scratch_shapes=[pltpu.VMEM(rotation_samples.shape, jnp.float32)],
    )(rotation_samples, table_t)


def share_samples(template_volume, rotation_samples):
    slab_count = lax.axis_size("slab")
    spread = sample_template(template_volume, rotation_samples, slab_count)
    return lax.all_to_all(spread, "slab", 0, 0, tiled=True)


def rows_to_blocks(values, rows):
    count = values.shape[0] // rows
    return jnp.concatenate([values[i * rows : (i + 1) * rows] for i in range(count)], axis=1)


def blocks_to_rows(values, width):
    count = values.shape[1] // width
    return jnp.concatenate(
        [values[:, i * width : (i + 1) * width] for i in range(count)], axis=0
    )


def forward_rows(values, across, down):
    width = across.shape[1] // 2
    height = down.shape[1] // 2
    first = jnp.dot(values, across, preferred_element_type=jnp.float32).astype(jnp.bfloat16)
    stacked = jnp.concatenate(
        [rows_to_blocks(first[:, :width], height), rows_to_blocks(first[:, width:], height)],
        axis=0,
    )
    second = jnp.dot(down, stacked, preferred_element_type=jnp.float32).astype(jnp.bfloat16)
    return second[:width], second[width:]


def inverse_blocks(real_part, imag_part, mix, back):
    length = real_part.shape[0]
    joined = jnp.concatenate(
        [blocks_to_rows(real_part, length), blocks_to_rows(imag_part, length)], axis=1
    )
    first = jnp.dot(joined, mix, preferred_element_type=jnp.float32).astype(jnp.bfloat16)
    stacked = jnp.concatenate(
        [rows_to_blocks(first[:, :length], length), rows_to_blocks(first[:, length:], length)],
        axis=0,
    )
    return jnp.dot(back, stacked, preferred_element_type=jnp.float32)


def template_kernel(values_ref, across_ref, down_ref, real_ref, imag_ref):
    real_part, imag_part = forward_rows(values_ref[...], across_ref[...], down_ref[...])
    real_ref[...] = real_part.astype(jnp.float32)
    imag_ref[...] = imag_part.astype(jnp.float32)


def split_three(values):
    high = values.astype(jnp.bfloat16)
    rest = values - high.astype(jnp.float32)
    middle = rest.astype(jnp.bfloat16)
    low = (rest - middle.astype(jnp.float32)).astype(jnp.bfloat16)
    return (high, middle, low)


def exact_dot(left, right, left_exact):
    total = None
    if left_exact:
        for part in split_three(right):
            term = jnp.dot(left, part, preferred_element_type=jnp.float32)
            total = term if total is None else total + term
    else:
        for part in split_three(left):
            term = jnp.dot(part, right, preferred_element_type=jnp.float32)
            total = term if total is None else total + term
    return total


def field_kernel(
    count_ref, own_ref, other_ref, wedge_ref, across_ref, mix_ref, back_ref, band_ref,
    band_t_ref, real_ref, imag_ref, rms_ref, *, box_edge
):
    home, planes, length, _ = own_ref.shape
    tiles = rms_ref.shape[0]
    maps = tiles * planes
    own_count = count_ref[0]
    picked = []
    for tile in range(tiles):
        source = jnp.clip(tiles + tile - own_count, 0, home - 1)
        chosen = jnp.where(tile < own_count, own_ref[tile], other_ref[source])
        picked.append(chosen.reshape(planes * length, length))
    values = jnp.concatenate(picked, axis=0)
    mix = mix_ref[...]
    real_part, imag_part = forward_rows(values, across_ref[...], mix)
    wedge = wedge_ref[...].astype(jnp.float32).astype(jnp.bfloat16)
    wedge = jnp.concatenate([wedge] * maps, axis=1)
    field = inverse_blocks(real_part * wedge, imag_part * wedge, mix, back_ref[...])
    field = (field * (1.0 / (length * length))).astype(jnp.bfloat16)
    square = jnp.square(field.astype(jnp.float32))
    energies = []
    for tile in range(tiles):
        energy = None
        for plane in range(planes):
            index = tile * planes + plane
            part = square[:, index * length : (index + 1) * length]
            energy = part if energy is None else energy + part
        energies.append(energy)
    energy = jnp.concatenate(energies, axis=1)
    summed = exact_dot(band_ref[...], energy, True)
    summed = exact_dot(blocks_to_rows(summed, length), band_t_ref[...], False)
    for tile in range(tiles):
        part = summed[tile * length : (tile + 1) * length]
        rms_ref[tile] = jnp.sqrt(part / (box_edge * box_edge * planes) + 1e-05)
    real_part, imag_part = forward_rows(blocks_to_rows(field, length), across_ref[...], mix)
    real_ref[...] = real_part.astype(jnp.float32)
    imag_ref[...] = imag_part.astype(jnp.float32)


def whole_call(kernel, out_shape, *args):
    return pl.pallas_call(
        kernel,
        out_shape=out_shape,
        in_specs=[pl.BlockSpec(memory_space=pltpu.VMEM)] * len(args),
        out_specs=tuple(pl.BlockSpec(memory_space=pltpu.VMEM) for _ in out_shape),
    )(*args)


def make_templates(sampled, box_edge, planes, table):
    count = sampled.shape[1]
    length = table["across"].shape[0]
    sampled = jnp.transpose(sampled, (1, 0, 2))
    sampled = sampled.reshape(count, planes, box_edge, box_edge)
    template_norm = jnp.sqrt(
        jnp.sum(jnp.square(sampled.astype(jnp.float32)), axis=(1, 2, 3)) + 1e-05
    )
    spec_shape = jax.ShapeDtypeStruct((length, count * planes * length), jnp.float32)
    spec_real, spec_imag = whole_call(
        template_kernel,
        (spec_shape, spec_shape),
        sampled.reshape(count * planes * box_edge, box_edge),
        table["box_across"],
        table["box_down"],
    )
    return (spec_real, spec_imag, template_norm)


def field_spectra(own_count, tiles_own, tiles_other, wedge_mask, table, band_sum, box_edge):
    home, planes, length, _ = tiles_own.shape
    tiles = home // 2
    spec_shape = jax.ShapeDtypeStruct((length, tiles * planes * length), jnp.float32)
    args = (
        own_count.reshape(1),
        tiles_own,
        tiles_other,
        wedge_mask,
        table["across"],
        table["mix"],
        table["across"],
        band_sum.astype(jnp.bfloat16),
        band_sum.T.astype(jnp.bfloat16),
    )
    out_shape = (
        spec_shape,
        spec_shape,
        jax.ShapeDtypeStruct((tiles, length, length), jnp.float32),
    )
    return pl.pallas_call(
        functools.partial(field_kernel, box_edge=box_edge),
        out_shape=out_shape,
        in_specs=[pl.BlockSpec(memory_space=pltpu.SMEM)]
        + [pl.BlockSpec(memory_space=pltpu.VMEM)] * (len(args) - 1),
        out_specs=tuple(pl.BlockSpec(memory_space=pltpu.VMEM) for _ in out_shape),
    )(*args)


def score_kernel(
    slot_ref, scale_ref, field_re_ref, field_im_ref, templ_re_ref, templ_im_ref, mix_ref,
    back_ref, rms_ref, out_ref, result_ref
):
    length = field_re_ref.shape[0]
    per_step = rms_ref.shape[0]
    planes = field_re_ref.shape[1] // (per_step * length)
    count = templ_re_ref.shape[1] // (planes * length)
    group = 8 if count % 8 == 0 else 1

    def lanes(index):
        return slice(index * length, (index + 1) * length)

    for tile in range(per_step):
        best = None
        for step in range(count // group):
            joined = []
            for member in range(group):
                orient = step * group + member
                prod_re = None
                prod_im = None
                for plane in range(planes):
                    fr = field_re_ref[:, lanes(tile * planes + plane)]
                    fi = field_im_ref[:, lanes(tile * planes + plane)]
                    tr = templ_re_ref[:, lanes(orient * planes + plane)]
                    ti = templ_im_ref[:, lanes(orient * planes + plane)]
                    part_re = fr * tr + fi * ti
                    part_im = fi * tr - fr * ti
                    prod_re = part_re if prod_re is None else prod_re + part_re
                    prod_im = part_im if prod_im is None else prod_im + part_im
                joined.append(
                    jnp.concatenate(
                        [prod_re.astype(jnp.bfloat16), prod_im.astype(jnp.bfloat16)], axis=1
                    )
                )
            joined = jnp.concatenate(joined, axis=0)
            first = jnp.dot(joined, mix_ref[...], preferred_element_type=jnp.float32).astype(
                jnp.bfloat16
            )
            stacked = jnp.concatenate(
                [
                    rows_to_blocks(first[:, :length], length),
                    rows_to_blocks(first[:, length:], length),
                ],
                axis=0,
            )
            corr = jnp.dot(back_ref[...], stacked, preferred_element_type=jnp.float32)
            for member in range(group):
                orient = step * group + member
                value = corr[:, lanes(member)] * scale_ref[orient]
                best = value if best is None else jnp.maximum(best, value)
        result_ref[...] = best / rms_ref[tile]
        groups = out_ref.shape[0]
        chunk = out_ref.shape[2]
        for part in range(groups):
            start = pl.multiple_of(lax.rem(slot_ref[0] + part, groups) * chunk, chunk)
            out_ref[part, tile] = result_ref[pl.ds(start, chunk), :].astype(out_ref.dtype)


def score_tiles(
    field_real, field_imag, local_rms, templ_real, templ_imag, template_norm, table
):
    length = field_real.shape[0]
    planes = field_real.shape[1] // (local_rms.shape[0] * length)
    scale = (1.0 / template_norm) * (1.0 / (length * length))
    mix = table["mix"]
    back = table["across"]
    tiles = local_rms.shape[0]
    groups = lax.axis_size("orient")
    per_step = 2 if tiles % 2 == 0 else 1
    tile_block = pl.BlockSpec((length, per_step * planes * length), lambda t: (0, t))
    templ_block = pl.BlockSpec(templ_real.shape, lambda t: (0, 0))
    return pl.pallas_call(
        score_kernel,
        grid=(tiles // per_step,),
        out_shape=jax.ShapeDtypeStruct((groups, tiles, length // groups, length), jnp.bfloat16),
        in_specs=[
            pl.BlockSpec(memory_space=pltpu.SMEM),
            pl.BlockSpec(memory_space=pltpu.SMEM),
            tile_block,
            tile_block,
            templ_block,
            templ_block,
            pl.BlockSpec((2 * length, 2 * length), lambda t: (0, 0)),
            pl.BlockSpec((length, 2 * length), lambda t: (0, 0)),
            pl.BlockSpec((per_step, length, length), lambda t: (t, 0, 0)),
        ],
        out_specs=pl.BlockSpec(
            (groups, per_step, length // groups, length), lambda t: (0, t, 0, 0)
        ),
        scratch_shapes=[pltpu.VMEM((length, length), jnp.float32)],
    )(
        lax.axis_index("orient").astype(jnp.int32).reshape(1),
        scale,
        field_real,
        field_imag,
        templ_real,
        templ_imag,
        mix,
        back,
        local_rms,
    )


def orient_max(best):
    groups = lax.axis_size("orient")
    result = best[0]
    for shift in range(1, groups):
        route = [(source, (source + shift) % groups) for source in range(groups)]
        result = jnp.maximum(result, lax.ppermute(best[shift], "orient", route))
    return result


def per_device(tiles, assigned_worker, wedge_mask, template_volume, rotation_samples):
    tile_len = tiles.shape[-1]
    planes = tiles.shape[1]
    home_slots = tiles.shape[0]
    work_slots = home_slots // 2
    box_edge = template_volume.shape[0]
    table = transform_tables(tile_len, box_edge)
    band_sum = band_table(tile_len, box_edge)
    sampled = share_samples(template_volume, rotation_samples)
    partner_tiles = partner(tiles, "slab", 0)
    occupied = assigned_worker >= 0
    own_count = jnp.sum(occupied.astype(jnp.int32))
    counter = jnp.arange(work_slots, dtype=jnp.int32)
    field_real, field_imag, local_rms = field_spectra(
        own_count, tiles, partner_tiles, wedge_mask, table, band_sum, box_edge
    )
    sampled, field_real = lax.optimization_barrier((sampled, field_real))
    templ_real, templ_imag, template_norm = make_templates(sampled, box_edge, planes, table)
    best = score_tiles(
        field_real,
        field_imag,
        local_rms,
        templ_real,
        templ_imag,
        template_norm,
        table,
    )
    best_rows = orient_max(best)
    outgoing = pick_rows(counter + own_count, best_rows)
    returned = partner(outgoing, "slab", 0)
    result = jnp.concatenate([best_rows, returned], axis=0)
    return jnp.where(occupied[:, None, None], result, jnp.zeros_like(result))


def solution(mesh):
    return jax.shard_map(
        per_device,
        mesh=mesh,
        in_specs=(P("slab", None, None, None), P("slab"), P(), P(), P("orient", "slab")),
        out_specs=P("slab", "orient", None),
        check_vma=False,
    )
```

```python
import functools
import math

import jax
import ml_dtypes
import numpy as np
import jax.numpy as jnp
from jax import lax
from jax.experimental import pallas as pl
from jax.experimental.pallas import tpu as pltpu
from jax.sharding import PartitionSpec as P


def partner(block, axis, bit):
    count = lax.axis_size(axis)
    route = []
    for low in range(count):
        high = low | 1 << bit
        if high != low and high < count:
            route += [(low, high), (high, low)]
    return lax.ppermute(block, axis, route)


def tables(length):
    counter = np.arange(length, dtype=np.int32)
    angles = (counter[:, None] * counter[None, :] % length).astype(np.float32) * np.float32(
        2.0 * math.pi / length
    )
    wide = angles.astype(np.float64)
    cosine = np.cos(wide).astype(np.float32).astype(ml_dtypes.bfloat16)
    sine = np.sin(wide).astype(np.float32).astype(ml_dtypes.bfloat16)
    return cosine, sine


def band_table(length, box_edge):
    counter = np.arange(length, dtype=np.int32)
    offsets = (counter[None, :] - counter[:, None]) % length
    return jnp.asarray((offsets < box_edge).astype(np.float32))


def transform_tables(length, box_edge):
    cosine, sine = tables(length)
    across = np.concatenate([cosine, -sine], axis=1)
    mix = np.concatenate(
        [np.concatenate([cosine, sine], axis=1), np.concatenate([-sine, cosine], axis=1)], axis=0
    )
    box_across = np.concatenate([cosine[:box_edge], -sine[:box_edge]], axis=1)
    box_down = np.concatenate(
        [
            np.concatenate([cosine[:, :box_edge], sine[:, :box_edge]], axis=1),
            np.concatenate([-sine[:, :box_edge], cosine[:, :box_edge]], axis=1),
        ],
        axis=0,
    )
    return {
        name: jnp.asarray(value)
        for name, value in (
            ("across", across),
            ("mix", mix),
            ("box_across", box_across),
            ("box_down", box_down),
        )
    }


def pick_rows(chosen, source):
    counter = jnp.arange(source.shape[0], dtype=jnp.int32)
    selector = (chosen[:, None] == counter[None, :]).astype(source.dtype)
    flat = source.reshape(source.shape[0], -1)
    picked = jnp.dot(selector, flat, preferred_element_type=jnp.float32).astype(source.dtype)
    return picked.reshape((chosen.shape[0],) + source.shape[1:])


def pick_kernel(index_ref, volume_ref, out_ref, picked_ref, table_ref):
    table_ref[...] = jnp.transpose(volume_ref[...]).astype(jnp.bfloat16)
    columns = table_ref.shape[0]
    rows_in_table = table_ref.shape[1]
    lanes = index_ref.shape[1]
    shift = columns.bit_length() - 1

    def body(step, carry):
        index = index_ref[pl.ds(step, 1), :]
        high = jnp.right_shift(index, shift)
        low = jnp.bitwise_and(index, columns - 1)
        row_hot = (lax.broadcasted_iota(jnp.int32, (rows_in_table, lanes), 0) == high).astype(
            jnp.bfloat16
        )
        picked_rows = jnp.dot(table_ref[...], row_hot, preferred_element_type=jnp.float32)
        column_hot = lax.broadcasted_iota(jnp.int32, (columns, lanes), 0) == low
        chosen = jnp.where(column_hot, picked_rows, 0.0)
        picked_ref[pl.ds(step, 1), :] = jnp.sum(chosen, axis=0, keepdims=True)
        return carry

    lax.fori_loop(0, index_ref.shape[0], body, 0, unroll=2)
    picked = picked_ref[...].astype(out_ref.dtype)
    for copy in range(out_ref.shape[0]):
        out_ref[copy] = picked


def sample_template(template_volume, rotation_samples, copies):
    total = template_volume.size
    columns = 512
    volume = template_volume.reshape(total // columns, columns)
    return pl.pallas_call(
        pick_kernel,
        out_shape=jax.ShapeDtypeStruct((copies,) + rotation_samples.shape, jnp.bfloat16),
        in_specs=[pl.BlockSpec(memory_space=pltpu.VMEM)] * 2,
        out_specs=pl.BlockSpec(memory_space=pltpu.VMEM),
        scratch_shapes=[
            pltpu.VMEM(rotation_samples.shape, jnp.float32),
            pltpu.VMEM((columns, total // columns), jnp.bfloat16),
        ],
    )(rotation_samples, volume)


def share_samples(template_volume, rotation_samples):
    slab_count = lax.axis_size("slab")
    spread = sample_template(template_volume, rotation_samples, slab_count)
    return lax.all_to_all(spread, "slab", 0, 0, tiled=True)


def rows_to_blocks(values, rows):
    count = values.shape[0] // rows
    return jnp.concatenate([values[i * rows : (i + 1) * rows] for i in range(count)], axis=1)


def blocks_to_rows(values, width):
    count = values.shape[1] // width
    return jnp.concatenate(
        [values[:, i * width : (i + 1) * width] for i in range(count)], axis=0
    )


def forward_rows(values, across, down):
    width = across.shape[1] // 2
    height = down.shape[1] // 2
    first = jnp.dot(values, across, preferred_element_type=jnp.float32).astype(jnp.bfloat16)
    stacked = jnp.concatenate(
        [rows_to_blocks(first[:, :width], height), rows_to_blocks(first[:, width:], height)],
        axis=0,
    )
    second = jnp.dot(down, stacked, preferred_element_type=jnp.float32).astype(jnp.bfloat16)
    return second[:width], second[width:]


def inverse_blocks(real_part, imag_part, mix, back):
    length = real_part.shape[0]
    joined = jnp.concatenate(
        [blocks_to_rows(real_part, length), blocks_to_rows(imag_part, length)], axis=1
    )
    first = jnp.dot(joined, mix, preferred_element_type=jnp.float32).astype(jnp.bfloat16)
    stacked = jnp.concatenate(
        [rows_to_blocks(first[:, :length], length), rows_to_blocks(first[:, length:], length)],
        axis=0,
    )
    return jnp.dot(back, stacked, preferred_element_type=jnp.float32)


def template_kernel(values_ref, across_ref, down_ref, real_ref, imag_ref):
    real_part, imag_part = forward_rows(values_ref[...], across_ref[...], down_ref[...])
    real_ref[...] = real_part.astype(jnp.float32)
    imag_ref[...] = imag_part.astype(jnp.float32)


def split_three(values):
    high = values.astype(jnp.bfloat16)
    rest = values - high.astype(jnp.float32)
    middle = rest.astype(jnp.bfloat16)
    low = (rest - middle.astype(jnp.float32)).astype(jnp.bfloat16)
    return (high, middle, low)


def exact_dot(left, right, left_exact):
    total = None
    if left_exact:
        for part in split_three(right):
            term = jnp.dot(left, part, preferred_element_type=jnp.float32)
            total = term if total is None else total + term
    else:
        for part in split_three(left):
            term = jnp.dot(part, right, preferred_element_type=jnp.float32)
            total = term if total is None else total + term
    return total


def field_kernel(
    count_ref, own_ref, other_ref, wedge_ref, across_ref, mix_ref, back_ref, band_ref,
    band_t_ref, real_ref, imag_ref, rms_ref, *, box_edge
):
    home, planes, length, _ = own_ref.shape
    tiles = rms_ref.shape[0]
    maps = tiles * planes
    own_count = count_ref[0]
    picked = []
    for tile in range(tiles):
        source = jnp.clip(tiles + tile - own_count, 0, home - 1)
        chosen = jnp.where(tile < own_count, own_ref[tile], other_ref[source])
        picked.append(chosen.reshape(planes * length, length))
    values = jnp.concatenate(picked, axis=0)
    mix = mix_ref[...]
    real_part, imag_part = forward_rows(values, across_ref[...], mix)
    wedge = wedge_ref[...].astype(jnp.float32).astype(jnp.bfloat16)
    wedge = jnp.concatenate([wedge] * maps, axis=1)
    field = inverse_blocks(real_part * wedge, imag_part * wedge, mix, back_ref[...])
    field = (field * (1.0 / (length * length))).astype(jnp.bfloat16)
    square = jnp.square(field.astype(jnp.float32))
    energies = []
    for tile in range(tiles):
        energy = None
        for plane in range(planes):
            index = tile * planes + plane
            part = square[:, index * length : (index + 1) * length]
            energy = part if energy is None else energy + part
        energies.append(energy)
    energy = jnp.concatenate(energies, axis=1)
    summed = exact_dot(band_ref[...], energy, True)
    summed = exact_dot(blocks_to_rows(summed, length), band_t_ref[...], False)
    for tile in range(tiles):
        part = summed[tile * length : (tile + 1) * length]
        rms_ref[tile] = jnp.sqrt(part / (box_edge * box_edge * planes) + 1e-05)
    real_part, imag_part = forward_rows(blocks_to_rows(field, length), across_ref[...], mix)
    real_ref[...] = real_part.astype(jnp.float32)
    imag_ref[...] = imag_part.astype(jnp.float32)


def whole_call(kernel, out_shape, *args):
    return pl.pallas_call(
        kernel,
        out_shape=out_shape,
        in_specs=[pl.BlockSpec(memory_space=pltpu.VMEM)] * len(args),
        out_specs=tuple(pl.BlockSpec(memory_space=pltpu.VMEM) for _ in out_shape),
    )(*args)


def make_templates(sampled, box_edge, planes, table):
    count = sampled.shape[1]
    length = table["across"].shape[0]
    sampled = jnp.transpose(sampled, (1, 0, 2))
    sampled = sampled.reshape(count, planes, box_edge, box_edge)
    template_norm = jnp.sqrt(
        jnp.sum(jnp.square(sampled.astype(jnp.float32)), axis=(1, 2, 3)) + 1e-05
    )
    spec_shape = jax.ShapeDtypeStruct((length, count * planes * length), jnp.float32)
    spec_real, spec_imag = whole_call(
        template_kernel,
        (spec_shape, spec_shape),
        sampled.reshape(count * planes * box_edge, box_edge),
        table["box_across"],
        table["box_down"],
    )
    return (spec_real, spec_imag, template_norm)


def field_spectra(own_count, tiles_own, tiles_other, wedge_mask, table, band_sum, box_edge):
    home, planes, length, _ = tiles_own.shape
    tiles = home // 2
    spec_shape = jax.ShapeDtypeStruct((length, tiles * planes * length), jnp.float32)
    args = (
        own_count.reshape(1),
        tiles_own,
        tiles_other,
        wedge_mask,
        table["across"],
        table["mix"],
        table["across"],
        band_sum.astype(jnp.bfloat16),
        band_sum.T.astype(jnp.bfloat16),
    )
    out_shape = (
        spec_shape,
        spec_shape,
        jax.ShapeDtypeStruct((tiles, length, length), jnp.float32),
    )
    return pl.pallas_call(
        functools.partial(field_kernel, box_edge=box_edge),
        out_shape=out_shape,
        in_specs=[pl.BlockSpec(memory_space=pltpu.SMEM)]
        + [pl.BlockSpec(memory_space=pltpu.VMEM)] * (len(args) - 1),
        out_specs=tuple(pl.BlockSpec(memory_space=pltpu.VMEM) for _ in out_shape),
    )(*args)


def score_kernel(
    slot_ref, scale_ref, field_re_ref, field_im_ref, templ_re_ref, templ_im_ref, mix_ref,
    back_ref, rms_ref, out_ref, result_ref
):
    length = field_re_ref.shape[0]
    per_step = rms_ref.shape[0]
    planes = field_re_ref.shape[1] // (per_step * length)
    count = templ_re_ref.shape[1] // (planes * length)
    group = 8 if count % 8 == 0 else 1

    def lanes(index):
        return slice(index * length, (index + 1) * length)

    for tile in range(per_step):
        best = None
        for step in range(count // group):
            joined = []
            for member in range(group):
                orient = step * group + member
                prod_re = None
                prod_im = None
                for plane in range(planes):
                    fr = field_re_ref[:, lanes(tile * planes + plane)]
                    fi = field_im_ref[:, lanes(tile * planes + plane)]
                    tr = templ_re_ref[:, lanes(orient * planes + plane)]
                    ti = templ_im_ref[:, lanes(orient * planes + plane)]
                    part_re = fr * tr + fi * ti
                    part_im = fi * tr - fr * ti
                    prod_re = part_re if prod_re is None else prod_re + part_re
                    prod_im = part_im if prod_im is None else prod_im + part_im
                joined.append(
                    jnp.concatenate(
                        [prod_re.astype(jnp.bfloat16), prod_im.astype(jnp.bfloat16)], axis=1
                    )
                )
            joined = jnp.concatenate(joined, axis=0)
            first = jnp.dot(joined, mix_ref[...], preferred_element_type=jnp.float32).astype(
                jnp.bfloat16
            )
            stacked = jnp.concatenate(
                [
                    rows_to_blocks(first[:, :length], length),
                    rows_to_blocks(first[:, length:], length),
                ],
                axis=0,
            )
            corr = jnp.dot(back_ref[...], stacked, preferred_element_type=jnp.float32)
            for member in range(group):
                orient = step * group + member
                value = corr[:, lanes(member)] * scale_ref[orient]
                best = value if best is None else jnp.maximum(best, value)
        result_ref[...] = best / rms_ref[tile]
        groups = out_ref.shape[0]
        chunk = out_ref.shape[2]
        for part in range(groups):
            start = pl.multiple_of(lax.rem(slot_ref[0] + part, groups) * chunk, chunk)
            out_ref[part, tile] = result_ref[pl.ds(start, chunk), :].astype(out_ref.dtype)


def score_tiles(
    field_real, field_imag, local_rms, templ_real, templ_imag, template_norm, table
):
    length = field_real.shape[0]
    planes = field_real.shape[1] // (local_rms.shape[0] * length)
    scale = (1.0 / template_norm) * (1.0 / (length * length))
    mix = table["mix"]
    back = table["across"]
    tiles = local_rms.shape[0]
    groups = lax.axis_size("orient")
    per_step = 2 if tiles % 2 == 0 else 1
    tile_block = pl.BlockSpec((length, per_step * planes * length), lambda t: (0, t))
    templ_block = pl.BlockSpec(templ_real.shape, lambda t: (0, 0))
    return pl.pallas_call(
        score_kernel,
        grid=(tiles // per_step,),
        out_shape=jax.ShapeDtypeStruct((groups, tiles, length // groups, length), jnp.bfloat16),
        in_specs=[
            pl.BlockSpec(memory_space=pltpu.SMEM),
            pl.BlockSpec(memory_space=pltpu.SMEM),
            tile_block,
            tile_block,
            templ_block,
            templ_block,
            pl.BlockSpec((2 * length, 2 * length), lambda t: (0, 0)),
            pl.BlockSpec((length, 2 * length), lambda t: (0, 0)),
            pl.BlockSpec((per_step, length, length), lambda t: (t, 0, 0)),
        ],
        out_specs=pl.BlockSpec(
            (groups, per_step, length // groups, length), lambda t: (0, t, 0, 0)
        ),
        scratch_shapes=[pltpu.VMEM((length, length), jnp.float32)],
    )(
        lax.axis_index("orient").astype(jnp.int32).reshape(1),
        scale,
        field_real,
        field_imag,
        templ_real,
        templ_imag,
        mix,
        back,
        local_rms,
    )


def orient_max(best):
    groups = lax.axis_size("orient")
    result = best[0]
    for shift in range(1, groups):
        route = [(source, (source + shift) % groups) for source in range(groups)]
        result = jnp.maximum(result, lax.ppermute(best[shift], "orient", route))
    return result


def per_device(tiles, assigned_worker, wedge_mask, template_volume, rotation_samples):
    tile_len = tiles.shape[-1]
    planes = tiles.shape[1]
    home_slots = tiles.shape[0]
    work_slots = home_slots // 2
    box_edge = template_volume.shape[0]
    table = transform_tables(tile_len, box_edge)
    band_sum = band_table(tile_len, box_edge)
    sampled = share_samples(template_volume, rotation_samples)
    partner_tiles = partner(tiles, "slab", 0)
    occupied = assigned_worker >= 0
    own_count = jnp.sum(occupied.astype(jnp.int32))
    counter = jnp.arange(work_slots, dtype=jnp.int32)
    field_real, field_imag, local_rms = field_spectra(
        own_count, tiles, partner_tiles, wedge_mask, table, band_sum, box_edge
    )
    sampled, field_real = lax.optimization_barrier((sampled, field_real))
    templ_real, templ_imag, template_norm = make_templates(sampled, box_edge, planes, table)
    best = score_tiles(
        field_real,
        field_imag,
        local_rms,
        templ_real,
        templ_imag,
        template_norm,
        table,
    )
    best_rows = orient_max(best)
    outgoing = pick_rows(counter + own_count, best_rows)
    returned = partner(outgoing, "slab", 0)
    result = jnp.concatenate([best_rows, returned], axis=0)
    return jnp.where(occupied[:, None, None], result, jnp.zeros_like(result))


def solution(mesh):
    return jax.shard_map(
        per_device,
        mesh=mesh,
        in_specs=(P("slab", None, None, None), P("slab"), P(), P(), P("orient", "slab")),
        out_specs=P("slab", "orient", None),
        check_vma=False,
    )
```

```python
import functools
import math

import jax
import ml_dtypes
import numpy as np
import jax.numpy as jnp
from jax import lax
from jax.experimental import pallas as pl
from jax.experimental.pallas import tpu as pltpu
from jax.sharding import PartitionSpec as P


def partner(block, axis, bit):
    count = lax.axis_size(axis)
    route = []
    for low in range(count):
        high = low | 1 << bit
        if high != low and high < count:
            route += [(low, high), (high, low)]
    return lax.ppermute(block, axis, route)


def tables(length):
    counter = np.arange(length, dtype=np.int32)
    angles = (counter[:, None] * counter[None, :] % length).astype(np.float32) * np.float32(
        2.0 * math.pi / length
    )
    wide = angles.astype(np.float64)
    cosine = np.cos(wide).astype(np.float32).astype(ml_dtypes.bfloat16)
    sine = np.sin(wide).astype(np.float32).astype(ml_dtypes.bfloat16)
    return cosine, sine


def band_table(length, box_edge):
    counter = np.arange(length, dtype=np.int32)
    offsets = (counter[None, :] - counter[:, None]) % length
    return jnp.asarray((offsets < box_edge).astype(np.float32))


def transform_tables(length, box_edge):
    cosine, sine = tables(length)
    across = np.concatenate([cosine, -sine], axis=1)
    mix = np.concatenate(
        [np.concatenate([cosine, sine], axis=1), np.concatenate([-sine, cosine], axis=1)], axis=0
    )
    box_across = np.concatenate([cosine[:box_edge], -sine[:box_edge]], axis=1)
    box_down = np.concatenate(
        [
            np.concatenate([cosine[:, :box_edge], sine[:, :box_edge]], axis=1),
            np.concatenate([-sine[:, :box_edge], cosine[:, :box_edge]], axis=1),
        ],
        axis=0,
    )
    return {
        name: jnp.asarray(value)
        for name, value in (
            ("across", across),
            ("mix", mix),
            ("box_across", box_across),
            ("box_down", box_down),
        )
    }


def pick_rows(chosen, source):
    counter = jnp.arange(source.shape[0], dtype=jnp.int32)
    selector = (chosen[:, None] == counter[None, :]).astype(source.dtype)
    flat = source.reshape(source.shape[0], -1)
    picked = jnp.dot(selector, flat, preferred_element_type=jnp.float32).astype(source.dtype)
    return picked.reshape((chosen.shape[0],) + source.shape[1:])


def pick_kernel(index_ref, volume_ref, out_ref, picked_ref, table_ref):
    width = volume_ref.shape[1]
    blocks = table_ref.shape[0] // width
    rows = table_ref.shape[1]
    for block in range(blocks):
        strided = volume_ref[pl.ds(block, rows, stride=blocks), :]
        table_ref[block * width : (block + 1) * width, :] = jnp.transpose(strided).astype(
            jnp.bfloat16
        )
    columns = table_ref.shape[0]
    rows_in_table = table_ref.shape[1]
    lanes = index_ref.shape[1]
    shift = columns.bit_length() - 1

    def body(step, carry):
        index = index_ref[pl.ds(step, 1), :]
        high = jnp.right_shift(index, shift)
        low = jnp.bitwise_and(index, columns - 1)
        row_hot = (lax.broadcasted_iota(jnp.int32, (rows_in_table, lanes), 0) == high).astype(
            jnp.bfloat16
        )
        picked_rows = jnp.dot(table_ref[...], row_hot, preferred_element_type=jnp.float32)
        column_hot = lax.broadcasted_iota(jnp.int32, (columns, lanes), 0) == low
        chosen = jnp.where(column_hot, picked_rows, 0.0)
        picked_ref[pl.ds(step, 1), :] = jnp.sum(chosen, axis=0, keepdims=True)
        return carry

    lax.fori_loop(0, index_ref.shape[0], body, 0, unroll=2)
    picked = picked_ref[...].astype(out_ref.dtype)
    for copy in range(out_ref.shape[0]):
        out_ref[copy] = picked


def sample_template(template_volume, rotation_samples, copies):
    total = template_volume.size
    columns = 512
    edge = template_volume.shape[-1]
    volume = template_volume.reshape(total // edge, edge)
    return pl.pallas_call(
        pick_kernel,
        out_shape=jax.ShapeDtypeStruct((copies,) + rotation_samples.shape, jnp.bfloat16),
        in_specs=[pl.BlockSpec(memory_space=pltpu.VMEM)] * 2,
        out_specs=pl.BlockSpec(memory_space=pltpu.VMEM),
        scratch_shapes=[
            pltpu.VMEM(rotation_samples.shape, jnp.float32),
            pltpu.VMEM((columns, total // columns), jnp.bfloat16),
        ],
    )(rotation_samples, volume)


def share_samples(template_volume, rotation_samples):
    slab_count = lax.axis_size("slab")
    spread = sample_template(template_volume, rotation_samples, slab_count)
    return lax.all_to_all(spread, "slab", 0, 0, tiled=True)


def rows_to_blocks(values, rows):
    count = values.shape[0] // rows
    return jnp.concatenate([values[i * rows : (i + 1) * rows] for i in range(count)], axis=1)


def blocks_to_rows(values, width):
    count = values.shape[1] // width
    return jnp.concatenate(
        [values[:, i * width : (i + 1) * width] for i in range(count)], axis=0
    )


def forward_rows(values, across, down):
    width = across.shape[1] // 2
    height = down.shape[1] // 2
    first = jnp.dot(values, across, preferred_element_type=jnp.float32).astype(jnp.bfloat16)
    stacked = jnp.concatenate(
        [rows_to_blocks(first[:, :width], height), rows_to_blocks(first[:, width:], height)],
        axis=0,
    )
    second = jnp.dot(down, stacked, preferred_element_type=jnp.float32).astype(jnp.bfloat16)
    return second[:width], second[width:]


def inverse_blocks(real_part, imag_part, mix, back):
    length = real_part.shape[0]
    joined = jnp.concatenate(
        [blocks_to_rows(real_part, length), blocks_to_rows(imag_part, length)], axis=1
    )
    first = jnp.dot(joined, mix, preferred_element_type=jnp.float32).astype(jnp.bfloat16)
    stacked = jnp.concatenate(
        [rows_to_blocks(first[:, :length], length), rows_to_blocks(first[:, length:], length)],
        axis=0,
    )
    return jnp.dot(back, stacked, preferred_element_type=jnp.float32)


def template_kernel(values_ref, across_ref, down_ref, real_ref, imag_ref):
    real_part, imag_part = forward_rows(values_ref[...], across_ref[...], down_ref[...])
    real_ref[...] = real_part.astype(jnp.float32)
    imag_ref[...] = imag_part.astype(jnp.float32)


def split_three(values):
    high = values.astype(jnp.bfloat16)
    rest = values - high.astype(jnp.float32)
    middle = rest.astype(jnp.bfloat16)
    low = (rest - middle.astype(jnp.float32)).astype(jnp.bfloat16)
    return (high, middle, low)


def exact_dot(left, right, left_exact):
    total = None
    if left_exact:
        for part in split_three(right):
            term = jnp.dot(left, part, preferred_element_type=jnp.float32)
            total = term if total is None else total + term
    else:
        for part in split_three(left):
            term = jnp.dot(part, right, preferred_element_type=jnp.float32)
            total = term if total is None else total + term
    return total


def field_kernel(
    count_ref, own_ref, other_ref, wedge_ref, across_ref, mix_ref, back_ref, band_ref,
    band_t_ref, real_ref, imag_ref, rms_ref, *, box_edge
):
    home, planes, length, _ = own_ref.shape
    tiles = rms_ref.shape[0]
    maps = tiles * planes
    own_count = count_ref[0]
    picked = []
    for tile in range(tiles):
        source = jnp.clip(tiles + tile - own_count, 0, home - 1)
        chosen = jnp.where(tile < own_count, own_ref[tile], other_ref[source])
        picked.append(chosen.reshape(planes * length, length))
    values = jnp.concatenate(picked, axis=0)
    mix = mix_ref[...]
    real_part, imag_part = forward_rows(values, across_ref[...], mix)
    wedge = wedge_ref[...].astype(jnp.float32).astype(jnp.bfloat16)
    wedge = jnp.concatenate([wedge] * maps, axis=1)
    field = inverse_blocks(real_part * wedge, imag_part * wedge, mix, back_ref[...])
    field = (field * (1.0 / (length * length))).astype(jnp.bfloat16)
    square = jnp.square(field.astype(jnp.float32))
    energies = []
    for tile in range(tiles):
        energy = None
        for plane in range(planes):
            index = tile * planes + plane
            part = square[:, index * length : (index + 1) * length]
            energy = part if energy is None else energy + part
        energies.append(energy)
    energy = jnp.concatenate(energies, axis=1)
    summed = exact_dot(band_ref[...], energy, True)
    summed = exact_dot(blocks_to_rows(summed, length), band_t_ref[...], False)
    for tile in range(tiles):
        part = summed[tile * length : (tile + 1) * length]
        rms_ref[tile] = jnp.sqrt(part / (box_edge * box_edge * planes) + 1e-05)
    real_part, imag_part = forward_rows(blocks_to_rows(field, length), across_ref[...], mix)
    real_ref[...] = real_part.astype(jnp.float32)
    imag_ref[...] = imag_part.astype(jnp.float32)


def whole_call(kernel, out_shape, *args):
    return pl.pallas_call(
        kernel,
        out_shape=out_shape,
        in_specs=[pl.BlockSpec(memory_space=pltpu.VMEM)] * len(args),
        out_specs=tuple(pl.BlockSpec(memory_space=pltpu.VMEM) for _ in out_shape),
    )(*args)


def make_templates(sampled, box_edge, planes, table):
    count = sampled.shape[1]
    length = table["across"].shape[0]
    sampled = jnp.transpose(sampled, (1, 0, 2))
    sampled = sampled.reshape(count, planes, box_edge, box_edge)
    template_norm = jnp.sqrt(
        jnp.sum(jnp.square(sampled.astype(jnp.float32)), axis=(1, 2, 3)) + 1e-05
    )
    spec_shape = jax.ShapeDtypeStruct((length, count * planes * length), jnp.float32)
    spec_real, spec_imag = whole_call(
        template_kernel,
        (spec_shape, spec_shape),
        sampled.reshape(count * planes * box_edge, box_edge),
        table["box_across"],
        table["box_down"],
    )
    return (spec_real, spec_imag, template_norm)


def field_spectra(own_count, tiles_own, tiles_other, wedge_mask, table, band_sum, box_edge):
    home, planes, length, _ = tiles_own.shape
    tiles = home // 2
    spec_shape = jax.ShapeDtypeStruct((length, tiles * planes * length), jnp.float32)
    args = (
        own_count.reshape(1),
        tiles_own,
        tiles_other,
        wedge_mask,
        table["across"],
        table["mix"],
        table["across"],
        band_sum.astype(jnp.bfloat16),
        band_sum.T.astype(jnp.bfloat16),
    )
    out_shape = (
        spec_shape,
        spec_shape,
        jax.ShapeDtypeStruct((tiles, length, length), jnp.float32),
    )
    return pl.pallas_call(
        functools.partial(field_kernel, box_edge=box_edge),
        out_shape=out_shape,
        in_specs=[pl.BlockSpec(memory_space=pltpu.SMEM)]
        + [pl.BlockSpec(memory_space=pltpu.VMEM)] * (len(args) - 1),
        out_specs=tuple(pl.BlockSpec(memory_space=pltpu.VMEM) for _ in out_shape),
    )(*args)


def score_kernel(
    slot_ref, scale_ref, field_re_ref, field_im_ref, templ_re_ref, templ_im_ref, mix_ref,
    back_ref, rms_ref, out_ref, result_ref
):
    length = field_re_ref.shape[0]
    per_step = rms_ref.shape[0]
    planes = field_re_ref.shape[1] // (per_step * length)
    count = templ_re_ref.shape[1] // (planes * length)
    group = 8 if count % 8 == 0 else 1

    def lanes(index):
        return slice(index * length, (index + 1) * length)

    for tile in range(per_step):
        best = None
        for step in range(count // group):
            joined = []
            for member in range(group):
                orient = step * group + member
                prod_re = None
                prod_im = None
                for plane in range(planes):
                    fr = field_re_ref[:, lanes(tile * planes + plane)]
                    fi = field_im_ref[:, lanes(tile * planes + plane)]
                    tr = templ_re_ref[:, lanes(orient * planes + plane)]
                    ti = templ_im_ref[:, lanes(orient * planes + plane)]
                    part_re = fr * tr + fi * ti
                    part_im = fi * tr - fr * ti
                    prod_re = part_re if prod_re is None else prod_re + part_re
                    prod_im = part_im if prod_im is None else prod_im + part_im
                joined.append(
                    jnp.concatenate(
                        [prod_re.astype(jnp.bfloat16), prod_im.astype(jnp.bfloat16)], axis=1
                    )
                )
            joined = jnp.concatenate(joined, axis=0)
            first = jnp.dot(joined, mix_ref[...], preferred_element_type=jnp.float32).astype(
                jnp.bfloat16
            )
            stacked = jnp.concatenate(
                [
                    rows_to_blocks(first[:, :length], length),
                    rows_to_blocks(first[:, length:], length),
                ],
                axis=0,
            )
            corr = jnp.dot(back_ref[...], stacked, preferred_element_type=jnp.float32)
            for member in range(group):
                orient = step * group + member
                value = corr[:, lanes(member)] * scale_ref[orient]
                best = value if best is None else jnp.maximum(best, value)
        result_ref[...] = best / rms_ref[tile]
        groups = out_ref.shape[0]
        chunk = out_ref.shape[2]
        for part in range(groups):
            start = pl.multiple_of(lax.rem(slot_ref[0] + part, groups) * chunk, chunk)
            out_ref[part, tile] = result_ref[pl.ds(start, chunk), :].astype(out_ref.dtype)


def score_tiles(
    field_real, field_imag, local_rms, templ_real, templ_imag, template_norm, table
):
    length = field_real.shape[0]
    planes = field_real.shape[1] // (local_rms.shape[0] * length)
    scale = (1.0 / template_norm) * (1.0 / (length * length))
    mix = table["mix"]
    back = table["across"]
    tiles = local_rms.shape[0]
    groups = lax.axis_size("orient")
    per_step = 2 if tiles % 2 == 0 else 1
    tile_block = pl.BlockSpec((length, per_step * planes * length), lambda t: (0, t))
    templ_block = pl.BlockSpec(templ_real.shape, lambda t: (0, 0))
    return pl.pallas_call(
        score_kernel,
        grid=(tiles // per_step,),
        out_shape=jax.ShapeDtypeStruct((groups, tiles, length // groups, length), jnp.bfloat16),
        in_specs=[
            pl.BlockSpec(memory_space=pltpu.SMEM),
            pl.BlockSpec(memory_space=pltpu.SMEM),
            tile_block,
            tile_block,
            templ_block,
            templ_block,
            pl.BlockSpec((2 * length, 2 * length), lambda t: (0, 0)),
            pl.BlockSpec((length, 2 * length), lambda t: (0, 0)),
            pl.BlockSpec((per_step, length, length), lambda t: (t, 0, 0)),
        ],
        out_specs=pl.BlockSpec(
            (groups, per_step, length // groups, length), lambda t: (0, t, 0, 0)
        ),
        scratch_shapes=[pltpu.VMEM((length, length), jnp.float32)],
    )(
        lax.axis_index("orient").astype(jnp.int32).reshape(1),
        scale,
        field_real,
        field_imag,
        templ_real,
        templ_imag,
        mix,
        back,
        local_rms,
    )


def orient_max(best):
    groups = lax.axis_size("orient")
    result = best[0]
    for shift in range(1, groups):
        route = [(source, (source + shift) % groups) for source in range(groups)]
        result = jnp.maximum(result, lax.ppermute(best[shift], "orient", route))
    return result


def per_device(tiles, assigned_worker, wedge_mask, template_volume, rotation_samples):
    tile_len = tiles.shape[-1]
    planes = tiles.shape[1]
    home_slots = tiles.shape[0]
    work_slots = home_slots // 2
    box_edge = template_volume.shape[0]
    table = transform_tables(tile_len, box_edge)
    band_sum = band_table(tile_len, box_edge)
    sampled = share_samples(template_volume, rotation_samples)
    partner_tiles = partner(tiles, "slab", 0)
    occupied = assigned_worker >= 0
    own_count = jnp.sum(occupied.astype(jnp.int32))
    counter = jnp.arange(work_slots, dtype=jnp.int32)
    field_real, field_imag, local_rms = field_spectra(
        own_count, tiles, partner_tiles, wedge_mask, table, band_sum, box_edge
    )
    sampled, field_real = lax.optimization_barrier((sampled, field_real))
    templ_real, templ_imag, template_norm = make_templates(sampled, box_edge, planes, table)
    best = score_tiles(
        field_real,
        field_imag,
        local_rms,
        templ_real,
        templ_imag,
        template_norm,
        table,
    )
    best_rows = orient_max(best)
    outgoing = pick_rows(counter + own_count, best_rows)
    returned = partner(outgoing, "slab", 0)
    result = jnp.concatenate([best_rows, returned], axis=0)
    return jnp.where(occupied[:, None, None], result, jnp.zeros_like(result))


def solution(mesh):
    return jax.shard_map(
        per_device,
        mesh=mesh,
        in_specs=(P("slab", None, None, None), P("slab"), P(), P(), P("orient", "slab")),
        out_specs=P("slab", "orient", None),
        check_vma=False,
    )
```

```python
import functools
import math

import jax
import ml_dtypes
import numpy as np
import jax.numpy as jnp
from jax import lax
from jax.experimental import pallas as pl
from jax.experimental.pallas import tpu as pltpu
from jax.sharding import PartitionSpec as P


def partner(block, axis, bit):
    count = lax.axis_size(axis)
    route = []
    for low in range(count):
        high = low | 1 << bit
        if high != low and high < count:
            route += [(low, high), (high, low)]
    return lax.ppermute(block, axis, route)


def tables(length):
    counter = np.arange(length, dtype=np.int32)
    angles = (counter[:, None] * counter[None, :] % length).astype(np.float32) * np.float32(
        2.0 * math.pi / length
    )
    wide = angles.astype(np.float64)
    cosine = np.cos(wide).astype(np.float32).astype(ml_dtypes.bfloat16)
    sine = np.sin(wide).astype(np.float32).astype(ml_dtypes.bfloat16)
    return cosine, sine


def band_table(length, box_edge):
    counter = np.arange(length, dtype=np.int32)
    offsets = (counter[None, :] - counter[:, None]) % length
    return jnp.asarray((offsets < box_edge).astype(np.float32))


def transform_tables(length, box_edge):
    cosine, sine = tables(length)
    across = np.concatenate([cosine, -sine], axis=1)
    mix = np.concatenate(
        [np.concatenate([cosine, sine], axis=1), np.concatenate([-sine, cosine], axis=1)], axis=0
    )
    box_across = np.concatenate([cosine[:box_edge], -sine[:box_edge]], axis=1)
    box_down = np.concatenate(
        [
            np.concatenate([cosine[:, :box_edge], sine[:, :box_edge]], axis=1),
            np.concatenate([-sine[:, :box_edge], cosine[:, :box_edge]], axis=1),
        ],
        axis=0,
    )
    return {
        name: jnp.asarray(value)
        for name, value in (
            ("across", across),
            ("mix", mix),
            ("box_across", box_across),
            ("box_down", box_down),
        )
    }


def pick_rows(chosen, source):
    counter = jnp.arange(source.shape[0], dtype=jnp.int32)
    selector = (chosen[:, None] == counter[None, :]).astype(source.dtype)
    flat = source.reshape(source.shape[0], -1)
    picked = jnp.dot(selector, flat, preferred_element_type=jnp.float32).astype(source.dtype)
    return picked.reshape((chosen.shape[0],) + source.shape[1:])


def pick_kernel(index_ref, volume_ref, out_ref, picked_ref, table_ref):
    width = volume_ref.shape[1]
    blocks = table_ref.shape[0] // width
    rows = table_ref.shape[1]
    for block in range(blocks):
        strided = volume_ref[pl.ds(block, rows, stride=blocks), :]
        table_ref[block * width : (block + 1) * width, :] = jnp.transpose(strided).astype(
            jnp.bfloat16
        )
    columns = table_ref.shape[0]
    rows_in_table = table_ref.shape[1]
    lanes = index_ref.shape[1]
    shift = columns.bit_length() - 1

    def body(step, carry):
        index = index_ref[pl.ds(step, 1), :]
        high = jnp.right_shift(index, shift)
        low = jnp.bitwise_and(index, columns - 1)
        row_hot = (lax.broadcasted_iota(jnp.int32, (rows_in_table, lanes), 0) == high).astype(
            jnp.bfloat16
        )
        picked_rows = jnp.dot(table_ref[...], row_hot, preferred_element_type=jnp.float32)
        column_hot = lax.broadcasted_iota(jnp.int32, (columns, lanes), 0) == low
        chosen = jnp.where(column_hot, picked_rows, 0.0)
        picked_ref[pl.ds(step, 1), :] = jnp.sum(chosen, axis=0, keepdims=True)
        return carry

    lax.fori_loop(0, index_ref.shape[0], body, 0, unroll=2)
    picked = picked_ref[...].astype(out_ref.dtype)
    for copy in range(out_ref.shape[0]):
        out_ref[copy] = picked


def sample_template(template_volume, rotation_samples, copies):
    total = template_volume.size
    columns = 512
    edge = template_volume.shape[-1]
    volume = template_volume.reshape(total // edge, edge)
    return pl.pallas_call(
        pick_kernel,
        out_shape=jax.ShapeDtypeStruct((copies,) + rotation_samples.shape, jnp.bfloat16),
        in_specs=[pl.BlockSpec(memory_space=pltpu.VMEM)] * 2,
        out_specs=pl.BlockSpec(memory_space=pltpu.VMEM),
        scratch_shapes=[
            pltpu.VMEM(rotation_samples.shape, jnp.float32),
            pltpu.VMEM((columns, total // columns), jnp.bfloat16),
        ],
    )(rotation_samples, volume)


def share_samples(template_volume, rotation_samples):
    slab_count = lax.axis_size("slab")
    spread = sample_template(template_volume, rotation_samples, slab_count)
    return lax.all_to_all(spread, "slab", 0, 0, tiled=True)


def rows_to_blocks(values, rows):
    count = values.shape[0] // rows
    return jnp.concatenate([values[i * rows : (i + 1) * rows] for i in range(count)], axis=1)


def blocks_to_rows(values, width):
    count = values.shape[1] // width
    return jnp.concatenate(
        [values[:, i * width : (i + 1) * width] for i in range(count)], axis=0
    )


def forward_rows(values, across, down):
    width = across.shape[1] // 2
    height = down.shape[1] // 2
    first = jnp.dot(values, across, preferred_element_type=jnp.float32).astype(jnp.bfloat16)
    stacked = jnp.concatenate(
        [rows_to_blocks(first[:, :width], height), rows_to_blocks(first[:, width:], height)],
        axis=0,
    )
    second = jnp.dot(down, stacked, preferred_element_type=jnp.float32).astype(jnp.bfloat16)
    return second[:width], second[width:]


def inverse_blocks(real_part, imag_part, mix, back):
    length = real_part.shape[0]
    joined = jnp.concatenate(
        [blocks_to_rows(real_part, length), blocks_to_rows(imag_part, length)], axis=1
    )
    first = jnp.dot(joined, mix, preferred_element_type=jnp.float32).astype(jnp.bfloat16)
    stacked = jnp.concatenate(
        [rows_to_blocks(first[:, :length], length), rows_to_blocks(first[:, length:], length)],
        axis=0,
    )
    return jnp.dot(back, stacked, preferred_element_type=jnp.float32)


def template_kernel(values_ref, across_ref, down_ref, real_ref, imag_ref):
    real_part, imag_part = forward_rows(values_ref[...], across_ref[...], down_ref[...])
    real_ref[...] = real_part.astype(jnp.float32)
    imag_ref[...] = imag_part.astype(jnp.float32)


def split_three(values):
    high = values.astype(jnp.bfloat16)
    rest = values - high.astype(jnp.float32)
    middle = rest.astype(jnp.bfloat16)
    low = (rest - middle.astype(jnp.float32)).astype(jnp.bfloat16)
    return (high, middle, low)


def exact_dot(left, right, left_exact):
    total = None
    if left_exact:
        for part in split_three(right):
            term = jnp.dot(left, part, preferred_element_type=jnp.float32)
            total = term if total is None else total + term
    else:
        for part in split_three(left):
            term = jnp.dot(part, right, preferred_element_type=jnp.float32)
            total = term if total is None else total + term
    return total


def field_kernel(
    count_ref, own_ref, other_ref, wedge_ref, across_ref, mix_ref, back_ref, band_ref,
    band_t_ref, real_ref, imag_ref, rms_ref, *, box_edge
):
    home, planes, length, _ = own_ref.shape
    tiles = rms_ref.shape[0]
    maps = tiles * planes
    own_count = count_ref[0]
    picked = []
    for tile in range(tiles):
        source = jnp.clip(tile - own_count, 0, other_ref.shape[0] - 1)
        chosen = jnp.where(tile < own_count, own_ref[tile], other_ref[source])
        picked.append(chosen.reshape(planes * length, length))
    values = jnp.concatenate(picked, axis=0)
    mix = mix_ref[...]
    real_part, imag_part = forward_rows(values, across_ref[...], mix)
    wedge = wedge_ref[...].astype(jnp.float32).astype(jnp.bfloat16)
    wedge = jnp.concatenate([wedge] * maps, axis=1)
    field = inverse_blocks(real_part * wedge, imag_part * wedge, mix, back_ref[...])
    field = (field * (1.0 / (length * length))).astype(jnp.bfloat16)
    square = jnp.square(field.astype(jnp.float32))
    energies = []
    for tile in range(tiles):
        energy = None
        for plane in range(planes):
            index = tile * planes + plane
            part = square[:, index * length : (index + 1) * length]
            energy = part if energy is None else energy + part
        energies.append(energy)
    energy = jnp.concatenate(energies, axis=1)
    summed = exact_dot(band_ref[...], energy, True)
    summed = exact_dot(blocks_to_rows(summed, length), band_t_ref[...], False)
    for tile in range(tiles):
        part = summed[tile * length : (tile + 1) * length]
        rms_ref[tile] = jnp.sqrt(part / (box_edge * box_edge * planes) + 1e-05)
    real_part, imag_part = forward_rows(blocks_to_rows(field, length), across_ref[...], mix)
    real_ref[...] = real_part.astype(jnp.float32)
    imag_ref[...] = imag_part.astype(jnp.float32)


def whole_call(kernel, out_shape, *args):
    return pl.pallas_call(
        kernel,
        out_shape=out_shape,
        in_specs=[pl.BlockSpec(memory_space=pltpu.VMEM)] * len(args),
        out_specs=tuple(pl.BlockSpec(memory_space=pltpu.VMEM) for _ in out_shape),
    )(*args)


def make_templates(sampled, box_edge, planes, table):
    count = sampled.shape[1]
    length = table["across"].shape[0]
    sampled = jnp.transpose(sampled, (1, 0, 2))
    sampled = sampled.reshape(count, planes, box_edge, box_edge)
    template_norm = jnp.sqrt(
        jnp.sum(jnp.square(sampled.astype(jnp.float32)), axis=(1, 2, 3)) + 1e-05
    )
    spec_shape = jax.ShapeDtypeStruct((length, count * planes * length), jnp.float32)
    spec_real, spec_imag = whole_call(
        template_kernel,
        (spec_shape, spec_shape),
        sampled.reshape(count * planes * box_edge, box_edge),
        table["box_across"],
        table["box_down"],
    )
    return (spec_real, spec_imag, template_norm)


def field_spectra(own_count, tiles_own, tiles_other, wedge_mask, table, band_sum, box_edge):
    home, planes, length, _ = tiles_own.shape
    tiles = home // 2
    spec_shape = jax.ShapeDtypeStruct((length, tiles * planes * length), jnp.float32)
    args = (
        own_count.reshape(1),
        tiles_own,
        tiles_other,
        wedge_mask,
        table["across"],
        table["mix"],
        table["across"],
        band_sum.astype(jnp.bfloat16),
        band_sum.T.astype(jnp.bfloat16),
    )
    out_shape = (
        spec_shape,
        spec_shape,
        jax.ShapeDtypeStruct((tiles, length, length), jnp.float32),
    )
    return pl.pallas_call(
        functools.partial(field_kernel, box_edge=box_edge),
        out_shape=out_shape,
        in_specs=[pl.BlockSpec(memory_space=pltpu.SMEM)]
        + [pl.BlockSpec(memory_space=pltpu.VMEM)] * (len(args) - 1),
        out_specs=tuple(pl.BlockSpec(memory_space=pltpu.VMEM) for _ in out_shape),
    )(*args)


def score_kernel(
    slot_ref, scale_ref, field_re_ref, field_im_ref, templ_re_ref, templ_im_ref, mix_ref,
    back_ref, rms_ref, out_ref, result_ref
):
    length = field_re_ref.shape[0]
    per_step = rms_ref.shape[0]
    planes = field_re_ref.shape[1] // (per_step * length)
    count = templ_re_ref.shape[1] // (planes * length)
    group = 8 if count % 8 == 0 else 1

    def lanes(index):
        return slice(index * length, (index + 1) * length)

    for tile in range(per_step):
        best = None
        for step in range(count // group):
            joined = []
            for member in range(group):
                orient = step * group + member
                prod_re = None
                prod_im = None
                for plane in range(planes):
                    fr = field_re_ref[:, lanes(tile * planes + plane)]
                    fi = field_im_ref[:, lanes(tile * planes + plane)]
                    tr = templ_re_ref[:, lanes(orient * planes + plane)]
                    ti = templ_im_ref[:, lanes(orient * planes + plane)]
                    part_re = fr * tr + fi * ti
                    part_im = fi * tr - fr * ti
                    prod_re = part_re if prod_re is None else prod_re + part_re
                    prod_im = part_im if prod_im is None else prod_im + part_im
                joined.append(
                    jnp.concatenate(
                        [prod_re.astype(jnp.bfloat16), prod_im.astype(jnp.bfloat16)], axis=1
                    )
                )
            joined = jnp.concatenate(joined, axis=0)
            first = jnp.dot(joined, mix_ref[...], preferred_element_type=jnp.float32).astype(
                jnp.bfloat16
            )
            stacked = jnp.concatenate(
                [
                    rows_to_blocks(first[:, :length], length),
                    rows_to_blocks(first[:, length:], length),
                ],
                axis=0,
            )
            corr = jnp.dot(back_ref[...], stacked, preferred_element_type=jnp.float32)
            for member in range(group):
                orient = step * group + member
                value = corr[:, lanes(member)] * scale_ref[orient]
                best = value if best is None else jnp.maximum(best, value)
        result_ref[...] = best / rms_ref[tile]
        groups = out_ref.shape[0]
        chunk = out_ref.shape[2]
        for part in range(groups):
            start = pl.multiple_of(lax.rem(slot_ref[0] + part, groups) * chunk, chunk)
            out_ref[part, tile] = result_ref[pl.ds(start, chunk), :].astype(out_ref.dtype)


def score_tiles(
    field_real, field_imag, local_rms, templ_real, templ_imag, template_norm, table
):
    length = field_real.shape[0]
    planes = field_real.shape[1] // (local_rms.shape[0] * length)
    scale = (1.0 / template_norm) * (1.0 / (length * length))
    mix = table["mix"]
    back = table["across"]
    tiles = local_rms.shape[0]
    groups = lax.axis_size("orient")
    per_step = 2 if tiles % 2 == 0 else 1
    tile_block = pl.BlockSpec((length, per_step * planes * length), lambda t: (0, t))
    templ_block = pl.BlockSpec(templ_real.shape, lambda t: (0, 0))
    return pl.pallas_call(
        score_kernel,
        grid=(tiles // per_step,),
        out_shape=jax.ShapeDtypeStruct((groups, tiles, length // groups, length), jnp.bfloat16),
        in_specs=[
            pl.BlockSpec(memory_space=pltpu.SMEM),
            pl.BlockSpec(memory_space=pltpu.SMEM),
            tile_block,
            tile_block,
            templ_block,
            templ_block,
            pl.BlockSpec((2 * length, 2 * length), lambda t: (0, 0)),
            pl.BlockSpec((length, 2 * length), lambda t: (0, 0)),
            pl.BlockSpec((per_step, length, length), lambda t: (t, 0, 0)),
        ],
        out_specs=pl.BlockSpec(
            (groups, per_step, length // groups, length), lambda t: (0, t, 0, 0)
        ),
        scratch_shapes=[pltpu.VMEM((length, length), jnp.float32)],
    )(
        lax.axis_index("orient").astype(jnp.int32).reshape(1),
        scale,
        field_real,
        field_imag,
        templ_real,
        templ_imag,
        mix,
        back,
        local_rms,
    )


def orient_max(best):
    groups = lax.axis_size("orient")
    result = best[0]
    for shift in range(1, groups):
        route = [(source, (source + shift) % groups) for source in range(groups)]
        result = jnp.maximum(result, lax.ppermute(best[shift], "orient", route))
    return result


def per_device(tiles, assigned_worker, wedge_mask, template_volume, rotation_samples):
    tile_len = tiles.shape[-1]
    planes = tiles.shape[1]
    home_slots = tiles.shape[0]
    work_slots = home_slots // 2
    box_edge = template_volume.shape[0]
    table = transform_tables(tile_len, box_edge)
    band_sum = band_table(tile_len, box_edge)
    sampled = share_samples(template_volume, rotation_samples)
    partner_tiles = partner(tiles[work_slots:], "slab", 0)
    occupied = assigned_worker >= 0
    own_count = jnp.sum(occupied.astype(jnp.int32))
    counter = jnp.arange(work_slots, dtype=jnp.int32)
    field_real, field_imag, local_rms = field_spectra(
        own_count, tiles, partner_tiles, wedge_mask, table, band_sum, box_edge
    )
    sampled, field_real = lax.optimization_barrier((sampled, field_real))
    templ_real, templ_imag, template_norm = make_templates(sampled, box_edge, planes, table)
    best = score_tiles(
        field_real,
        field_imag,
        local_rms,
        templ_real,
        templ_imag,
        template_norm,
        table,
    )
    best_rows = orient_max(best)
    outgoing = pick_rows(counter + own_count, best_rows)
    returned = partner(outgoing, "slab", 0)
    result = jnp.concatenate([best_rows, returned], axis=0)
    return jnp.where(occupied[:, None, None], result, jnp.zeros_like(result))


def solution(mesh):
    return jax.shard_map(
        per_device,
        mesh=mesh,
        in_specs=(P("slab", None, None, None), P("slab"), P(), P(), P("orient", "slab")),
        out_specs=P("slab", "orient", None),
        check_vma=False,
    )
```

```python
import functools
import math

import jax
import ml_dtypes
import numpy as np
import jax.numpy as jnp
from jax import lax
from jax.experimental import pallas as pl
from jax.experimental.pallas import tpu as pltpu
from jax.sharding import PartitionSpec as P


def partner(block, axis, bit):
    count = lax.axis_size(axis)
    route = []
    for low in range(count):
        high = low | 1 << bit
        if high != low and high < count:
            route += [(low, high), (high, low)]
    return lax.ppermute(block, axis, route)


def tables(length):
    counter = np.arange(length, dtype=np.int32)
    angles = (counter[:, None] * counter[None, :] % length).astype(np.float32) * np.float32(
        2.0 * math.pi / length
    )
    wide = angles.astype(np.float64)
    cosine = np.cos(wide).astype(np.float32).astype(ml_dtypes.bfloat16)
    sine = np.sin(wide).astype(np.float32).astype(ml_dtypes.bfloat16)
    return cosine, sine


def band_table(length, box_edge):
    counter = np.arange(length, dtype=np.int32)
    offsets = (counter[None, :] - counter[:, None]) % length
    return jnp.asarray((offsets < box_edge).astype(np.float32))


def transform_tables(length, box_edge):
    cosine, sine = tables(length)
    across = np.concatenate([cosine, -sine], axis=1)
    mix = np.concatenate(
        [np.concatenate([cosine, sine], axis=1), np.concatenate([-sine, cosine], axis=1)], axis=0
    )
    box_across = np.concatenate([cosine[:box_edge], -sine[:box_edge]], axis=1)
    box_down = np.concatenate(
        [
            np.concatenate([cosine[:, :box_edge], sine[:, :box_edge]], axis=1),
            np.concatenate([-sine[:, :box_edge], cosine[:, :box_edge]], axis=1),
        ],
        axis=0,
    )
    return {
        name: jnp.asarray(value)
        for name, value in (
            ("across", across),
            ("mix", mix),
            ("box_across", box_across),
            ("box_down", box_down),
        )
    }


def pick_rows(chosen, source):
    counter = jnp.arange(source.shape[0], dtype=jnp.int32)
    selector = (chosen[:, None] == counter[None, :]).astype(source.dtype)
    flat = source.reshape(source.shape[0], -1)
    picked = jnp.dot(selector, flat, preferred_element_type=jnp.float32).astype(source.dtype)
    return picked.reshape((chosen.shape[0],) + source.shape[1:])


def pick_kernel(index_ref, volume_ref, out_ref, picked_ref, table_ref):
    width = volume_ref.shape[1]
    blocks = table_ref.shape[0] // width
    rows = table_ref.shape[1]
    for block in range(blocks):
        strided = volume_ref[pl.ds(block, rows, stride=blocks), :]
        table_ref[block * width : (block + 1) * width, :] = jnp.transpose(strided).astype(
            jnp.bfloat16
        )
    columns = table_ref.shape[0]
    rows_in_table = table_ref.shape[1]
    lanes = index_ref.shape[1]
    shift = columns.bit_length() - 1

    def body(step, carry):
        index = index_ref[pl.ds(step, 1), :]
        high = jnp.right_shift(index, shift)
        low = jnp.bitwise_and(index, columns - 1)
        row_hot = (lax.broadcasted_iota(jnp.int32, (rows_in_table, lanes), 0) == high).astype(
            jnp.bfloat16
        )
        picked_rows = jnp.dot(table_ref[...], row_hot, preferred_element_type=jnp.float32)
        column_hot = lax.broadcasted_iota(jnp.int32, (columns, lanes), 0) == low
        chosen = jnp.where(column_hot, picked_rows, 0.0)
        picked_ref[pl.ds(step, 1), :] = jnp.sum(chosen, axis=0, keepdims=True)
        return carry

    lax.fori_loop(0, index_ref.shape[0], body, 0, unroll=2)
    picked = picked_ref[...].astype(out_ref.dtype)
    for copy in range(out_ref.shape[0]):
        out_ref[copy] = picked


def sample_template(template_volume, rotation_samples, copies):
    total = template_volume.size
    columns = 512
    edge = template_volume.shape[-1]
    volume = template_volume.reshape(total // edge, edge)
    return pl.pallas_call(
        pick_kernel,
        out_shape=jax.ShapeDtypeStruct((copies,) + rotation_samples.shape, jnp.bfloat16),
        in_specs=[pl.BlockSpec(memory_space=pltpu.VMEM)] * 2,
        out_specs=pl.BlockSpec(memory_space=pltpu.VMEM),
        scratch_shapes=[
            pltpu.VMEM(rotation_samples.shape, jnp.float32),
            pltpu.VMEM((columns, total // columns), jnp.bfloat16),
        ],
    )(rotation_samples, volume)


def share_samples(template_volume, rotation_samples):
    slab_count = lax.axis_size("slab")
    spread = sample_template(template_volume, rotation_samples, slab_count)
    return lax.all_to_all(spread, "slab", 0, 0, tiled=True)


def rows_to_blocks(values, rows):
    count = values.shape[0] // rows
    return jnp.concatenate([values[i * rows : (i + 1) * rows] for i in range(count)], axis=1)


def blocks_to_rows(values, width):
    count = values.shape[1] // width
    return jnp.concatenate(
        [values[:, i * width : (i + 1) * width] for i in range(count)], axis=0
    )


def forward_rows(values, across, down):
    width = across.shape[1] // 2
    height = down.shape[1] // 2
    first = jnp.dot(values, across, preferred_element_type=jnp.float32).astype(jnp.bfloat16)
    stacked = jnp.concatenate(
        [rows_to_blocks(first[:, :width], height), rows_to_blocks(first[:, width:], height)],
        axis=0,
    )
    second = jnp.dot(down, stacked, preferred_element_type=jnp.float32).astype(jnp.bfloat16)
    return second[:width], second[width:]


def inverse_blocks(real_part, imag_part, mix, back):
    length = real_part.shape[0]
    joined = jnp.concatenate(
        [blocks_to_rows(real_part, length), blocks_to_rows(imag_part, length)], axis=1
    )
    first = jnp.dot(joined, mix, preferred_element_type=jnp.float32).astype(jnp.bfloat16)
    stacked = jnp.concatenate(
        [rows_to_blocks(first[:, :length], length), rows_to_blocks(first[:, length:], length)],
        axis=0,
    )
    return jnp.dot(back, stacked, preferred_element_type=jnp.float32)


def template_kernel(values_ref, across_ref, down_ref, real_ref, imag_ref):
    real_part, imag_part = forward_rows(values_ref[...], across_ref[...], down_ref[...])
    real_ref[...] = real_part.astype(jnp.float32)
    imag_ref[...] = imag_part.astype(jnp.float32)


def split_three(values):
    high = values.astype(jnp.bfloat16)
    rest = values - high.astype(jnp.float32)
    middle = rest.astype(jnp.bfloat16)
    low = (rest - middle.astype(jnp.float32)).astype(jnp.bfloat16)
    return (high, middle, low)


def exact_dot(left, right, left_exact):
    total = None
    if left_exact:
        for part in split_three(right):
            term = jnp.dot(left, part, preferred_element_type=jnp.float32)
            total = term if total is None else total + term
    else:
        for part in split_three(left):
            term = jnp.dot(part, right, preferred_element_type=jnp.float32)
            total = term if total is None else total + term
    return total


def field_kernel(
    count_ref, own_ref, other_ref, wedge_ref, across_ref, mix_ref, back_ref, band_ref,
    band_t_ref, real_ref, imag_ref, rms_ref, *, box_edge
):
    home, planes, length, _ = own_ref.shape
    tiles = rms_ref.shape[0]
    maps = tiles * planes
    own_count = count_ref[0]
    picked = []
    for tile in range(tiles):
        source = jnp.clip(tile - own_count, 0, other_ref.shape[0] - 1)
        chosen = jnp.where(tile < own_count, own_ref[tile], other_ref[source])
        picked.append(chosen.reshape(planes * length, length))
    values = jnp.concatenate(picked, axis=0)
    mix = mix_ref[...]
    real_part, imag_part = forward_rows(values, across_ref[...], mix)
    wedge = wedge_ref[...].astype(jnp.float32).astype(jnp.bfloat16)
    wedge = jnp.concatenate([wedge] * maps, axis=1)
    field = inverse_blocks(real_part * wedge, imag_part * wedge, mix, back_ref[...])
    field = (field * (1.0 / (length * length))).astype(jnp.bfloat16)
    square = jnp.square(field.astype(jnp.float32))
    energies = []
    for tile in range(tiles):
        energy = None
        for plane in range(planes):
            index = tile * planes + plane
            part = square[:, index * length : (index + 1) * length]
            energy = part if energy is None else energy + part
        energies.append(energy)
    energy = jnp.concatenate(energies, axis=1)
    summed = exact_dot(band_ref[...], energy, True)
    summed = exact_dot(blocks_to_rows(summed, length), band_t_ref[...], False)
    for tile in range(tiles):
        part = summed[tile * length : (tile + 1) * length]
        rms_ref[tile] = jnp.sqrt(part / (box_edge * box_edge * planes) + 1e-05)
    real_part, imag_part = forward_rows(blocks_to_rows(field, length), across_ref[...], mix)
    real_ref[...] = real_part.astype(jnp.float32)
    imag_ref[...] = imag_part.astype(jnp.float32)


def whole_call(kernel, out_shape, *args):
    return pl.pallas_call(
        kernel,
        out_shape=out_shape,
        in_specs=[pl.BlockSpec(memory_space=pltpu.VMEM)] * len(args),
        out_specs=tuple(pl.BlockSpec(memory_space=pltpu.VMEM) for _ in out_shape),
    )(*args)


def make_templates(sampled, box_edge, planes, table):
    count = sampled.shape[1]
    length = table["across"].shape[0]
    sampled = jnp.transpose(sampled, (1, 0, 2))
    sampled = sampled.reshape(count, planes, box_edge, box_edge)
    template_norm = jnp.sqrt(
        jnp.sum(jnp.square(sampled.astype(jnp.float32)), axis=(1, 2, 3)) + 1e-05
    )
    spec_shape = jax.ShapeDtypeStruct((length, count * planes * length), jnp.float32)
    spec_real, spec_imag = whole_call(
        template_kernel,
        (spec_shape, spec_shape),
        sampled.reshape(count * planes * box_edge, box_edge),
        table["box_across"],
        table["box_down"],
    )
    return (spec_real, spec_imag, template_norm)


def field_spectra(own_count, tiles_own, tiles_other, wedge_mask, table, band_sum, box_edge):
    home, planes, length, _ = tiles_own.shape
    tiles = home // 2
    spec_shape = jax.ShapeDtypeStruct((length, tiles * planes * length), jnp.float32)
    args = (
        own_count.reshape(1),
        tiles_own,
        tiles_other,
        wedge_mask,
        table["across"],
        table["mix"],
        table["across"],
        band_sum.astype(jnp.bfloat16),
        band_sum.T.astype(jnp.bfloat16),
    )
    out_shape = (
        spec_shape,
        spec_shape,
        jax.ShapeDtypeStruct((tiles, length, length), jnp.float32),
    )
    return pl.pallas_call(
        functools.partial(field_kernel, box_edge=box_edge),
        out_shape=out_shape,
        in_specs=[pl.BlockSpec(memory_space=pltpu.SMEM)]
        + [pl.BlockSpec(memory_space=pltpu.VMEM)] * (len(args) - 1),
        out_specs=tuple(pl.BlockSpec(memory_space=pltpu.VMEM) for _ in out_shape),
    )(*args)


def score_kernel(
    slot_ref, scale_ref, field_re_ref, field_im_ref, templ_re_ref, templ_im_ref, mix_ref,
    back_ref, rms_ref, *refs
):
    out_refs = refs[:-1]
    result_ref = refs[-1]
    length = field_re_ref.shape[0]
    per_step = rms_ref.shape[0]
    planes = field_re_ref.shape[1] // (per_step * length)
    count = templ_re_ref.shape[1] // (planes * length)
    group = 8 if count % 8 == 0 else 1

    def lanes(index):
        return slice(index * length, (index + 1) * length)

    for tile in range(per_step):
        best = None
        for step in range(count // group):
            joined = []
            for member in range(group):
                orient = step * group + member
                prod_re = None
                prod_im = None
                for plane in range(planes):
                    fr = field_re_ref[:, lanes(tile * planes + plane)]
                    fi = field_im_ref[:, lanes(tile * planes + plane)]
                    tr = templ_re_ref[:, lanes(orient * planes + plane)]
                    ti = templ_im_ref[:, lanes(orient * planes + plane)]
                    part_re = fr * tr + fi * ti
                    part_im = fi * tr - fr * ti
                    prod_re = part_re if prod_re is None else prod_re + part_re
                    prod_im = part_im if prod_im is None else prod_im + part_im
                joined.append(
                    jnp.concatenate(
                        [prod_re.astype(jnp.bfloat16), prod_im.astype(jnp.bfloat16)], axis=1
                    )
                )
            joined = jnp.concatenate(joined, axis=0)
            first = jnp.dot(joined, mix_ref[...], preferred_element_type=jnp.float32).astype(
                jnp.bfloat16
            )
            stacked = jnp.concatenate(
                [
                    rows_to_blocks(first[:, :length], length),
                    rows_to_blocks(first[:, length:], length),
                ],
                axis=0,
            )
            corr = jnp.dot(back_ref[...], stacked, preferred_element_type=jnp.float32)
            for member in range(group):
                orient = step * group + member
                value = corr[:, lanes(member)] * scale_ref[orient]
                best = value if best is None else jnp.maximum(best, value)
        result_ref[...] = best / rms_ref[tile]
        groups = len(out_refs)
        chunk = out_refs[0].shape[1]
        for part in range(groups):
            start = pl.multiple_of(lax.rem(slot_ref[0] + part, groups) * chunk, chunk)
            out_refs[part][tile] = result_ref[pl.ds(start, chunk), :].astype(jnp.bfloat16)


def score_tiles(
    field_real, field_imag, local_rms, templ_real, templ_imag, template_norm, table
):
    length = field_real.shape[0]
    planes = field_real.shape[1] // (local_rms.shape[0] * length)
    scale = (1.0 / template_norm) * (1.0 / (length * length))
    mix = table["mix"]
    back = table["across"]
    tiles = local_rms.shape[0]
    groups = lax.axis_size("orient")
    per_step = 2 if tiles % 2 == 0 else 1
    tile_block = pl.BlockSpec((length, per_step * planes * length), lambda t: (0, t))
    templ_block = pl.BlockSpec(templ_real.shape, lambda t: (0, 0))
    return pl.pallas_call(
        score_kernel,
        grid=(tiles // per_step,),
        out_shape=tuple(
            jax.ShapeDtypeStruct((tiles, length // groups, length), jnp.bfloat16)
            for _ in range(groups)
        ),
        in_specs=[
            pl.BlockSpec(memory_space=pltpu.SMEM),
            pl.BlockSpec(memory_space=pltpu.SMEM),
            tile_block,
            tile_block,
            templ_block,
            templ_block,
            pl.BlockSpec((2 * length, 2 * length), lambda t: (0, 0)),
            pl.BlockSpec((length, 2 * length), lambda t: (0, 0)),
            pl.BlockSpec((per_step, length, length), lambda t: (t, 0, 0)),
        ],
        out_specs=tuple(
            pl.BlockSpec((per_step, length // groups, length), lambda t: (t, 0, 0))
            for _ in range(groups)
        ),
        scratch_shapes=[pltpu.VMEM((length, length), jnp.float32)],
    )(
        lax.axis_index("orient").astype(jnp.int32).reshape(1),
        scale,
        field_real,
        field_imag,
        templ_real,
        templ_imag,
        mix,
        back,
        local_rms,
    )


def orient_max(best):
    groups = lax.axis_size("orient")
    result = best[0]
    for shift in range(1, groups):
        route = [(source, (source + shift) % groups) for source in range(groups)]
        result = jnp.maximum(result, lax.ppermute(best[shift], "orient", route))
    return result


def per_device(tiles, assigned_worker, wedge_mask, template_volume, rotation_samples):
    tile_len = tiles.shape[-1]
    planes = tiles.shape[1]
    home_slots = tiles.shape[0]
    work_slots = home_slots // 2
    box_edge = template_volume.shape[0]
    table = transform_tables(tile_len, box_edge)
    band_sum = band_table(tile_len, box_edge)
    sampled = share_samples(template_volume, rotation_samples)
    partner_tiles = partner(tiles[work_slots:], "slab", 0)
    occupied = assigned_worker >= 0
    own_count = jnp.sum(occupied.astype(jnp.int32))
    field_real, field_imag, local_rms = field_spectra(
        own_count, tiles, partner_tiles, wedge_mask, table, band_sum, box_edge
    )
    sampled, field_real = lax.optimization_barrier((sampled, field_real))
    templ_real, templ_imag, template_norm = make_templates(sampled, box_edge, planes, table)
    best = score_tiles(
        field_real,
        field_imag,
        local_rms,
        templ_real,
        templ_imag,
        template_norm,
        table,
    )
    best_rows = orient_max(best)
    received = partner(best_rows, "slab", 0)
    padded = jnp.concatenate([received, jnp.zeros_like(received)], axis=0)
    returned = lax.dynamic_slice_in_dim(padded, home_slots - own_count, work_slots, axis=0)
    result = jnp.concatenate([best_rows, returned], axis=0)
    return jnp.where(occupied[:, None, None], result, jnp.zeros_like(result))


def solution(mesh):
    return jax.shard_map(
        per_device,
        mesh=mesh,
        in_specs=(P("slab", None, None, None), P("slab"), P(), P(), P("orient", "slab")),
        out_specs=P("slab", "orient", None),
        check_vma=False,
    )
```

```python
import functools
import math

import jax
import ml_dtypes
import numpy as np
import jax.numpy as jnp
from jax import lax
from jax.experimental import pallas as pl
from jax.experimental.pallas import tpu as pltpu
from jax.sharding import PartitionSpec as P


def partner(block, axis, bit):
    count = lax.axis_size(axis)
    route = []
    for low in range(count):
        high = low | 1 << bit
        if high != low and high < count:
            route += [(low, high), (high, low)]
    return lax.ppermute(block, axis, route)


def tables(length):
    counter = np.arange(length, dtype=np.int32)
    angles = (counter[:, None] * counter[None, :] % length).astype(np.float32) * np.float32(
        2.0 * math.pi / length
    )
    wide = angles.astype(np.float64)
    cosine = np.cos(wide).astype(np.float32).astype(ml_dtypes.bfloat16)
    sine = np.sin(wide).astype(np.float32).astype(ml_dtypes.bfloat16)
    return cosine, sine


def band_table(length, box_edge):
    counter = np.arange(length, dtype=np.int32)
    offsets = (counter[None, :] - counter[:, None]) % length
    return jnp.asarray((offsets < box_edge).astype(np.float32))


def transform_tables(length, box_edge):
    cosine, sine = tables(length)
    across = np.concatenate([cosine, -sine], axis=1)
    mix = np.concatenate(
        [np.concatenate([cosine, sine], axis=1), np.concatenate([-sine, cosine], axis=1)], axis=0
    )
    box_across = np.concatenate([cosine[:box_edge], -sine[:box_edge]], axis=1)
    box_down = np.concatenate(
        [
            np.concatenate([cosine[:, :box_edge], sine[:, :box_edge]], axis=1),
            np.concatenate([-sine[:, :box_edge], cosine[:, :box_edge]], axis=1),
        ],
        axis=0,
    )
    return {
        name: jnp.asarray(value)
        for name, value in (
            ("across", across),
            ("mix", mix),
            ("box_across", box_across),
            ("box_down", box_down),
        )
    }


def pick_rows(chosen, source):
    counter = jnp.arange(source.shape[0], dtype=jnp.int32)
    selector = (chosen[:, None] == counter[None, :]).astype(source.dtype)
    flat = source.reshape(source.shape[0], -1)
    picked = jnp.dot(selector, flat, preferred_element_type=jnp.float32).astype(source.dtype)
    return picked.reshape((chosen.shape[0],) + source.shape[1:])


def pick_kernel(index_ref, volume_ref, out_ref, picked_ref, table_ref):
    width = volume_ref.shape[1]
    blocks = table_ref.shape[0] // width
    rows = table_ref.shape[1]
    for block in range(blocks):
        strided = volume_ref[pl.ds(block, rows, stride=blocks), :]
        table_ref[block * width : (block + 1) * width, :] = jnp.transpose(strided).astype(
            jnp.bfloat16
        )
    columns = table_ref.shape[0]
    rows_in_table = table_ref.shape[1]
    lanes = index_ref.shape[1]
    shift = columns.bit_length() - 1

    def body(step, carry):
        index = index_ref[pl.ds(step, 1), :]
        high = jnp.right_shift(index, shift)
        low = jnp.bitwise_and(index, columns - 1)
        row_hot = (lax.broadcasted_iota(jnp.int32, (rows_in_table, lanes), 0) == high).astype(
            jnp.bfloat16
        )
        picked_rows = jnp.dot(table_ref[...], row_hot, preferred_element_type=jnp.float32)
        column_hot = lax.broadcasted_iota(jnp.int32, (columns, lanes), 0) == low
        chosen = jnp.where(column_hot, picked_rows, 0.0)
        picked_ref[pl.ds(step, 1), :] = jnp.sum(chosen, axis=0, keepdims=True)
        return carry

    lax.fori_loop(0, index_ref.shape[0], body, 0, unroll=2)
    picked = picked_ref[...].astype(out_ref.dtype)
    for copy in range(out_ref.shape[0]):
        out_ref[copy] = picked


def sample_template(template_volume, rotation_samples, copies):
    total = template_volume.size
    columns = 512
    edge = template_volume.shape[-1]
    volume = template_volume.reshape(total // edge, edge)
    return pl.pallas_call(
        pick_kernel,
        out_shape=jax.ShapeDtypeStruct((copies,) + rotation_samples.shape, jnp.bfloat16),
        in_specs=[pl.BlockSpec(memory_space=pltpu.VMEM)] * 2,
        out_specs=pl.BlockSpec(memory_space=pltpu.VMEM),
        scratch_shapes=[
            pltpu.VMEM(rotation_samples.shape, jnp.float32),
            pltpu.VMEM((columns, total // columns), jnp.bfloat16),
        ],
    )(rotation_samples, volume)


def share_samples(template_volume, rotation_samples):
    slab_count = lax.axis_size("slab")
    spread = sample_template(template_volume, rotation_samples, slab_count)
    return lax.all_to_all(spread, "slab", 0, 0, tiled=True)


def rows_to_blocks(values, rows):
    count = values.shape[0] // rows
    return jnp.concatenate([values[i * rows : (i + 1) * rows] for i in range(count)], axis=1)


def blocks_to_rows(values, width):
    count = values.shape[1] // width
    return jnp.concatenate(
        [values[:, i * width : (i + 1) * width] for i in range(count)], axis=0
    )


def forward_rows(values, across, down):
    width = across.shape[1] // 2
    height = down.shape[1] // 2
    first = jnp.dot(values, across, preferred_element_type=jnp.float32).astype(jnp.bfloat16)
    stacked = jnp.concatenate(
        [rows_to_blocks(first[:, :width], height), rows_to_blocks(first[:, width:], height)],
        axis=0,
    )
    second = jnp.dot(down, stacked, preferred_element_type=jnp.float32).astype(jnp.bfloat16)
    return second[:width], second[width:]


def inverse_blocks(real_part, imag_part, mix, back):
    length = real_part.shape[0]
    joined = jnp.concatenate(
        [blocks_to_rows(real_part, length), blocks_to_rows(imag_part, length)], axis=1
    )
    first = jnp.dot(joined, mix, preferred_element_type=jnp.float32).astype(jnp.bfloat16)
    stacked = jnp.concatenate(
        [rows_to_blocks(first[:, :length], length), rows_to_blocks(first[:, length:], length)],
        axis=0,
    )
    return jnp.dot(back, stacked, preferred_element_type=jnp.float32)


def template_kernel(values_ref, across_ref, down_ref, real_ref, imag_ref):
    real_part, imag_part = forward_rows(values_ref[...], across_ref[...], down_ref[...])
    real_ref[...] = real_part.astype(jnp.float32)
    imag_ref[...] = imag_part.astype(jnp.float32)


def split_three(values):
    high = values.astype(jnp.bfloat16)
    rest = values - high.astype(jnp.float32)
    middle = rest.astype(jnp.bfloat16)
    low = (rest - middle.astype(jnp.float32)).astype(jnp.bfloat16)
    return (high, middle, low)


def exact_dot(left, right, left_exact):
    total = None
    if left_exact:
        for part in split_three(right):
            term = jnp.dot(left, part, preferred_element_type=jnp.float32)
            total = term if total is None else total + term
    else:
        for part in split_three(left):
            term = jnp.dot(part, right, preferred_element_type=jnp.float32)
            total = term if total is None else total + term
    return total


def field_kernel(
    count_ref, own_ref, other_ref, wedge_ref, across_ref, mix_ref, back_ref, band_ref,
    band_t_ref, real_ref, imag_ref, rms_ref, *, box_edge
):
    home, planes, length, _ = own_ref.shape
    tiles = rms_ref.shape[0]
    maps = tiles * planes
    own_count = count_ref[0]
    picked = []
    for tile in range(tiles):
        source = jnp.clip(tile - own_count, 0, other_ref.shape[0] - 1)
        chosen = jnp.where(tile < own_count, own_ref[tile], other_ref[source])
        picked.append(chosen.reshape(planes * length, length))
    values = jnp.concatenate(picked, axis=0)
    mix = mix_ref[...]
    real_part, imag_part = forward_rows(values, across_ref[...], mix)
    wedge = wedge_ref[...].astype(jnp.float32).astype(jnp.bfloat16)
    wedge = jnp.concatenate([wedge] * maps, axis=1)
    field = inverse_blocks(real_part * wedge, imag_part * wedge, mix, back_ref[...])
    field = (field * (1.0 / (length * length))).astype(jnp.bfloat16)
    square = jnp.square(field.astype(jnp.float32))
    energies = []
    for tile in range(tiles):
        energy = None
        for plane in range(planes):
            index = tile * planes + plane
            part = square[:, index * length : (index + 1) * length]
            energy = part if energy is None else energy + part
        energies.append(energy)
    energy = jnp.concatenate(energies, axis=1)
    summed = exact_dot(band_ref[...], energy, True)
    summed = exact_dot(blocks_to_rows(summed, length), band_t_ref[...], False)
    for tile in range(tiles):
        part = summed[tile * length : (tile + 1) * length]
        rms_ref[tile] = jnp.sqrt(part / (box_edge * box_edge * planes) + 1e-05)
    real_part, imag_part = forward_rows(blocks_to_rows(field, length), across_ref[...], mix)
    real_ref[...] = real_part.astype(jnp.float32)
    imag_ref[...] = imag_part.astype(jnp.float32)


def whole_call(kernel, out_shape, *args):
    return pl.pallas_call(
        kernel,
        out_shape=out_shape,
        in_specs=[pl.BlockSpec(memory_space=pltpu.VMEM)] * len(args),
        out_specs=tuple(pl.BlockSpec(memory_space=pltpu.VMEM) for _ in out_shape),
    )(*args)


def make_templates(sampled, box_edge, planes, table):
    count = sampled.shape[1]
    length = table["across"].shape[0]
    sampled = jnp.transpose(sampled, (1, 0, 2))
    sampled = sampled.reshape(count, planes, box_edge, box_edge)
    template_norm = jnp.sqrt(
        jnp.sum(jnp.square(sampled.astype(jnp.float32)), axis=(1, 2, 3)) + 1e-05
    )
    spec_shape = jax.ShapeDtypeStruct((length, count * planes * length), jnp.float32)
    spec_real, spec_imag = whole_call(
        template_kernel,
        (spec_shape, spec_shape),
        sampled.reshape(count * planes * box_edge, box_edge),
        table["box_across"],
        table["box_down"],
    )
    return (spec_real, spec_imag, template_norm)


def field_spectra(own_count, tiles_own, tiles_other, wedge_mask, table, band_sum, box_edge):
    home, planes, length, _ = tiles_own.shape
    tiles = home // 2
    spec_shape = jax.ShapeDtypeStruct((length, tiles * planes * length), jnp.float32)
    args = (
        own_count.reshape(1),
        tiles_own,
        tiles_other,
        wedge_mask,
        table["across"],
        table["mix"],
        table["across"],
        band_sum.astype(jnp.bfloat16),
        band_sum.T.astype(jnp.bfloat16),
    )
    out_shape = (
        spec_shape,
        spec_shape,
        jax.ShapeDtypeStruct((tiles, length, length), jnp.float32),
    )
    return pl.pallas_call(
        functools.partial(field_kernel, box_edge=box_edge),
        out_shape=out_shape,
        in_specs=[pl.BlockSpec(memory_space=pltpu.SMEM)]
        + [pl.BlockSpec(memory_space=pltpu.VMEM)] * (len(args) - 1),
        out_specs=tuple(pl.BlockSpec(memory_space=pltpu.VMEM) for _ in out_shape),
    )(*args)


def score_kernel(
    slot_ref, scale_ref, field_re_ref, field_im_ref, templ_re_ref, templ_im_ref, mix_ref,
    back_ref, rms_ref, *refs
):
    out_refs = refs[:-1]
    result_ref = refs[-1]
    length = field_re_ref.shape[0]
    per_step = rms_ref.shape[0]
    planes = field_re_ref.shape[1] // (per_step * length)
    count = templ_re_ref.shape[1] // (planes * length)
    group = 8 if count % 8 == 0 else 1

    def lanes(index):
        return slice(index * length, (index + 1) * length)

    for tile in range(per_step):
        best = None
        for step in range(count // group):
            joined = []
            for member in range(group):
                orient = step * group + member
                prod_re = None
                prod_im = None
                for plane in range(planes):
                    fr = field_re_ref[:, lanes(tile * planes + plane)]
                    fi = field_im_ref[:, lanes(tile * planes + plane)]
                    tr = templ_re_ref[:, lanes(orient * planes + plane)]
                    ti = templ_im_ref[:, lanes(orient * planes + plane)]
                    part_re = fr * tr + fi * ti
                    part_im = fi * tr - fr * ti
                    prod_re = part_re if prod_re is None else prod_re + part_re
                    prod_im = part_im if prod_im is None else prod_im + part_im
                joined.append(
                    jnp.concatenate(
                        [prod_re.astype(jnp.bfloat16), prod_im.astype(jnp.bfloat16)], axis=1
                    )
                )
            joined = jnp.concatenate(joined, axis=0)
            first = jnp.dot(joined, mix_ref[...], preferred_element_type=jnp.float32).astype(
                jnp.bfloat16
            )
            stacked = jnp.concatenate(
                [
                    rows_to_blocks(first[:, :length], length),
                    rows_to_blocks(first[:, length:], length),
                ],
                axis=0,
            )
            corr = jnp.dot(back_ref[...], stacked, preferred_element_type=jnp.float32)
            for member in range(group):
                orient = step * group + member
                value = corr[:, lanes(member)] * scale_ref[orient]
                best = value if best is None else jnp.maximum(best, value)
        result_ref[...] = best / rms_ref[tile]
        groups = len(out_refs)
        chunk = out_refs[0].shape[1]
        for part in range(groups):
            start = pl.multiple_of(lax.rem(slot_ref[0] + part, groups) * chunk, chunk)
            out_refs[part][tile] = result_ref[pl.ds(start, chunk), :].astype(jnp.bfloat16)


def score_tiles(
    field_real, field_imag, local_rms, templ_real, templ_imag, template_norm, table
):
    length = field_real.shape[0]
    planes = field_real.shape[1] // (local_rms.shape[0] * length)
    scale = (1.0 / template_norm) * (1.0 / (length * length))
    mix = table["mix"]
    back = table["across"]
    tiles = local_rms.shape[0]
    groups = lax.axis_size("orient")
    per_step = 4 if tiles % 4 == 0 else 1
    tile_block = pl.BlockSpec((length, per_step * planes * length), lambda t: (0, t))
    templ_block = pl.BlockSpec(templ_real.shape, lambda t: (0, 0))
    return pl.pallas_call(
        score_kernel,
        grid=(tiles // per_step,),
        out_shape=tuple(
            jax.ShapeDtypeStruct((tiles, length // groups, length), jnp.bfloat16)
            for _ in range(groups)
        ),
        in_specs=[
            pl.BlockSpec(memory_space=pltpu.SMEM),
            pl.BlockSpec(memory_space=pltpu.SMEM),
            tile_block,
            tile_block,
            templ_block,
            templ_block,
            pl.BlockSpec((2 * length, 2 * length), lambda t: (0, 0)),
            pl.BlockSpec((length, 2 * length), lambda t: (0, 0)),
            pl.BlockSpec((per_step, length, length), lambda t: (t, 0, 0)),
        ],
        out_specs=tuple(
            pl.BlockSpec((per_step, length // groups, length), lambda t: (t, 0, 0))
            for _ in range(groups)
        ),
        scratch_shapes=[pltpu.VMEM((length, length), jnp.float32)],
    )(
        lax.axis_index("orient").astype(jnp.int32).reshape(1),
        scale,
        field_real,
        field_imag,
        templ_real,
        templ_imag,
        mix,
        back,
        local_rms,
    )


def orient_max(best):
    groups = lax.axis_size("orient")
    result = best[0]
    for shift in range(1, groups):
        route = [(source, (source + shift) % groups) for source in range(groups)]
        result = jnp.maximum(result, lax.ppermute(best[shift], "orient", route))
    return result


def per_device(tiles, assigned_worker, wedge_mask, template_volume, rotation_samples):
    tile_len = tiles.shape[-1]
    planes = tiles.shape[1]
    home_slots = tiles.shape[0]
    work_slots = home_slots // 2
    box_edge = template_volume.shape[0]
    table = transform_tables(tile_len, box_edge)
    band_sum = band_table(tile_len, box_edge)
    sampled = share_samples(template_volume, rotation_samples)
    partner_tiles = partner(tiles[work_slots:], "slab", 0)
    occupied = assigned_worker >= 0
    own_count = jnp.sum(occupied.astype(jnp.int32))
    field_real, field_imag, local_rms = field_spectra(
        own_count, tiles, partner_tiles, wedge_mask, table, band_sum, box_edge
    )
    sampled, field_real = lax.optimization_barrier((sampled, field_real))
    templ_real, templ_imag, template_norm = make_templates(sampled, box_edge, planes, table)
    best = score_tiles(
        field_real,
        field_imag,
        local_rms,
        templ_real,
        templ_imag,
        template_norm,
        table,
    )
    best_rows = orient_max(best)
    received = partner(best_rows, "slab", 0)
    padded = jnp.concatenate([received, jnp.zeros_like(received)], axis=0)
    returned = lax.dynamic_slice_in_dim(padded, home_slots - own_count, work_slots, axis=0)
    result = jnp.concatenate([best_rows, returned], axis=0)
    return jnp.where(occupied[:, None, None], result, jnp.zeros_like(result))


def solution(mesh):
    return jax.shard_map(
        per_device,
        mesh=mesh,
        in_specs=(P("slab", None, None, None), P("slab"), P(), P(), P("orient", "slab")),
        out_specs=P("slab", "orient", None),
        check_vma=False,
    )
```

```python
import functools
import math

import jax
import ml_dtypes
import numpy as np
import jax.numpy as jnp
from jax import lax
from jax.experimental import pallas as pl
from jax.experimental.pallas import tpu as pltpu
from jax.sharding import PartitionSpec as P


def partner(block, axis, bit):
    count = lax.axis_size(axis)
    route = []
    for low in range(count):
        high = low | 1 << bit
        if high != low and high < count:
            route += [(low, high), (high, low)]
    return lax.ppermute(block, axis, route)


def tables(length):
    counter = np.arange(length, dtype=np.int32)
    angles = (counter[:, None] * counter[None, :] % length).astype(np.float32) * np.float32(
        2.0 * math.pi / length
    )
    wide = angles.astype(np.float64)
    cosine = np.cos(wide).astype(np.float32).astype(ml_dtypes.bfloat16)
    sine = np.sin(wide).astype(np.float32).astype(ml_dtypes.bfloat16)
    return cosine, sine


def band_table(length, box_edge):
    counter = np.arange(length, dtype=np.int32)
    offsets = (counter[None, :] - counter[:, None]) % length
    return jnp.asarray((offsets < box_edge).astype(np.float32))


def transform_tables(length, box_edge):
    cosine, sine = tables(length)
    across = np.concatenate([cosine, -sine], axis=1)
    mix = np.concatenate(
        [np.concatenate([cosine, sine], axis=1), np.concatenate([-sine, cosine], axis=1)], axis=0
    )
    box_across = np.concatenate([cosine[:box_edge], -sine[:box_edge]], axis=1)
    box_down = np.concatenate(
        [
            np.concatenate([cosine[:, :box_edge], sine[:, :box_edge]], axis=1),
            np.concatenate([-sine[:, :box_edge], cosine[:, :box_edge]], axis=1),
        ],
        axis=0,
    )
    return {
        name: jnp.asarray(value)
        for name, value in (
            ("across", across),
            ("mix", mix),
            ("box_across", box_across),
            ("box_down", box_down),
        )
    }


def pick_rows(chosen, source):
    counter = jnp.arange(source.shape[0], dtype=jnp.int32)
    selector = (chosen[:, None] == counter[None, :]).astype(source.dtype)
    flat = source.reshape(source.shape[0], -1)
    picked = jnp.dot(selector, flat, preferred_element_type=jnp.float32).astype(source.dtype)
    return picked.reshape((chosen.shape[0],) + source.shape[1:])


def pick_kernel(index_ref, volume_ref, out_ref, picked_ref, table_ref):
    width = volume_ref.shape[1]
    blocks = table_ref.shape[0] // width
    rows = table_ref.shape[1]
    for block in range(blocks):
        strided = volume_ref[pl.ds(block, rows, stride=blocks), :]
        table_ref[block * width : (block + 1) * width, :] = jnp.transpose(strided).astype(
            jnp.bfloat16
        )
    columns = table_ref.shape[0]
    rows_in_table = table_ref.shape[1]
    lanes = index_ref.shape[1]
    shift = columns.bit_length() - 1

    def body(step, carry):
        index = index_ref[pl.ds(step, 1), :]
        high = jnp.right_shift(index, shift)
        low = jnp.bitwise_and(index, columns - 1)
        row_hot = (lax.broadcasted_iota(jnp.int32, (rows_in_table, lanes), 0) == high).astype(
            jnp.bfloat16
        )
        picked_rows = jnp.dot(table_ref[...], row_hot, preferred_element_type=jnp.float32)
        column_hot = lax.broadcasted_iota(jnp.int32, (columns, lanes), 0) == low
        chosen = jnp.where(column_hot, picked_rows, 0.0)
        picked_ref[pl.ds(step, 1), :] = jnp.sum(chosen, axis=0, keepdims=True)
        return carry

    lax.fori_loop(0, index_ref.shape[0], body, 0, unroll=4)
    picked = picked_ref[...].astype(out_ref.dtype)
    for copy in range(out_ref.shape[0]):
        out_ref[copy] = picked


def sample_template(template_volume, rotation_samples, copies):
    total = template_volume.size
    columns = 512
    edge = template_volume.shape[-1]
    volume = template_volume.reshape(total // edge, edge)
    return pl.pallas_call(
        pick_kernel,
        out_shape=jax.ShapeDtypeStruct((copies,) + rotation_samples.shape, jnp.bfloat16),
        in_specs=[pl.BlockSpec(memory_space=pltpu.VMEM)] * 2,
        out_specs=pl.BlockSpec(memory_space=pltpu.VMEM),
        scratch_shapes=[
            pltpu.VMEM(rotation_samples.shape, jnp.float32),
            pltpu.VMEM((columns, total // columns), jnp.bfloat16),
        ],
    )(rotation_samples, volume)


def share_samples(template_volume, rotation_samples):
    slab_count = lax.axis_size("slab")
    spread = sample_template(template_volume, rotation_samples, slab_count)
    return lax.all_to_all(spread, "slab", 0, 0, tiled=True)


def rows_to_blocks(values, rows):
    count = values.shape[0] // rows
    return jnp.concatenate([values[i * rows : (i + 1) * rows] for i in range(count)], axis=1)


def blocks_to_rows(values, width):
    count = values.shape[1] // width
    return jnp.concatenate(
        [values[:, i * width : (i + 1) * width] for i in range(count)], axis=0
    )


def forward_rows(values, across, down):
    width = across.shape[1] // 2
    height = down.shape[1] // 2
    first = jnp.dot(values, across, preferred_element_type=jnp.float32).astype(jnp.bfloat16)
    stacked = jnp.concatenate(
        [rows_to_blocks(first[:, :width], height), rows_to_blocks(first[:, width:], height)],
        axis=0,
    )
    second = jnp.dot(down, stacked, preferred_element_type=jnp.float32).astype(jnp.bfloat16)
    return second[:width], second[width:]


def inverse_blocks(real_part, imag_part, mix, back):
    length = real_part.shape[0]
    joined = jnp.concatenate(
        [blocks_to_rows(real_part, length), blocks_to_rows(imag_part, length)], axis=1
    )
    first = jnp.dot(joined, mix, preferred_element_type=jnp.float32).astype(jnp.bfloat16)
    stacked = jnp.concatenate(
        [rows_to_blocks(first[:, :length], length), rows_to_blocks(first[:, length:], length)],
        axis=0,
    )
    return jnp.dot(back, stacked, preferred_element_type=jnp.float32)


def template_kernel(values_ref, across_ref, down_ref, real_ref, imag_ref):
    real_part, imag_part = forward_rows(values_ref[...], across_ref[...], down_ref[...])
    real_ref[...] = real_part.astype(jnp.float32)
    imag_ref[...] = imag_part.astype(jnp.float32)


def split_three(values):
    high = values.astype(jnp.bfloat16)
    rest = values - high.astype(jnp.float32)
    middle = rest.astype(jnp.bfloat16)
    low = (rest - middle.astype(jnp.float32)).astype(jnp.bfloat16)
    return (high, middle, low)


def exact_dot(left, right, left_exact):
    total = None
    if left_exact:
        for part in split_three(right):
            term = jnp.dot(left, part, preferred_element_type=jnp.float32)
            total = term if total is None else total + term
    else:
        for part in split_three(left):
            term = jnp.dot(part, right, preferred_element_type=jnp.float32)
            total = term if total is None else total + term
    return total


def field_kernel(
    count_ref, own_ref, other_ref, wedge_ref, across_ref, mix_ref, back_ref, band_ref,
    band_t_ref, real_ref, imag_ref, rms_ref, *, box_edge
):
    home, planes, length, _ = own_ref.shape
    tiles = rms_ref.shape[0]
    maps = tiles * planes
    own_count = count_ref[0]
    picked = []
    for tile in range(tiles):
        source = jnp.clip(tile - own_count, 0, other_ref.shape[0] - 1)
        chosen = jnp.where(tile < own_count, own_ref[tile], other_ref[source])
        picked.append(chosen.reshape(planes * length, length))
    values = jnp.concatenate(picked, axis=0)
    mix = mix_ref[...]
    real_part, imag_part = forward_rows(values, across_ref[...], mix)
    wedge = wedge_ref[...].astype(jnp.float32).astype(jnp.bfloat16)
    wedge = jnp.concatenate([wedge] * maps, axis=1)
    field = inverse_blocks(real_part * wedge, imag_part * wedge, mix, back_ref[...])
    field = (field * (1.0 / (length * length))).astype(jnp.bfloat16)
    square = jnp.square(field.astype(jnp.float32))
    energies = []
    for tile in range(tiles):
        energy = None
        for plane in range(planes):
            index = tile * planes + plane
            part = square[:, index * length : (index + 1) * length]
            energy = part if energy is None else energy + part
        energies.append(energy)
    energy = jnp.concatenate(energies, axis=1)
    summed = exact_dot(band_ref[...], energy, True)
    summed = exact_dot(blocks_to_rows(summed, length), band_t_ref[...], False)
    for tile in range(tiles):
        part = summed[tile * length : (tile + 1) * length]
        rms_ref[tile] = jnp.sqrt(part / (box_edge * box_edge * planes) + 1e-05)
    real_part, imag_part = forward_rows(blocks_to_rows(field, length), across_ref[...], mix)
    real_ref[...] = real_part.astype(jnp.float32)
    imag_ref[...] = imag_part.astype(jnp.float32)


def whole_call(kernel, out_shape, *args):
    return pl.pallas_call(
        kernel,
        out_shape=out_shape,
        in_specs=[pl.BlockSpec(memory_space=pltpu.VMEM)] * len(args),
        out_specs=tuple(pl.BlockSpec(memory_space=pltpu.VMEM) for _ in out_shape),
    )(*args)


def make_templates(sampled, box_edge, planes, table):
    count = sampled.shape[1]
    length = table["across"].shape[0]
    sampled = jnp.transpose(sampled, (1, 0, 2))
    sampled = sampled.reshape(count, planes, box_edge, box_edge)
    template_norm = jnp.sqrt(
        jnp.sum(jnp.square(sampled.astype(jnp.float32)), axis=(1, 2, 3)) + 1e-05
    )
    spec_shape = jax.ShapeDtypeStruct((length, count * planes * length), jnp.float32)
    spec_real, spec_imag = whole_call(
        template_kernel,
        (spec_shape, spec_shape),
        sampled.reshape(count * planes * box_edge, box_edge),
        table["box_across"],
        table["box_down"],
    )
    return (spec_real, spec_imag, template_norm)


def field_spectra(own_count, tiles_own, tiles_other, wedge_mask, table, band_sum, box_edge):
    home, planes, length, _ = tiles_own.shape
    tiles = home // 2
    spec_shape = jax.ShapeDtypeStruct((length, tiles * planes * length), jnp.float32)
    args = (
        own_count.reshape(1),
        tiles_own,
        tiles_other,
        wedge_mask,
        table["across"],
        table["mix"],
        table["across"],
        band_sum.astype(jnp.bfloat16),
        band_sum.T.astype(jnp.bfloat16),
    )
    out_shape = (
        spec_shape,
        spec_shape,
        jax.ShapeDtypeStruct((tiles, length, length), jnp.float32),
    )
    return pl.pallas_call(
        functools.partial(field_kernel, box_edge=box_edge),
        out_shape=out_shape,
        in_specs=[pl.BlockSpec(memory_space=pltpu.SMEM)]
        + [pl.BlockSpec(memory_space=pltpu.VMEM)] * (len(args) - 1),
        out_specs=tuple(pl.BlockSpec(memory_space=pltpu.VMEM) for _ in out_shape),
    )(*args)


def score_kernel(
    slot_ref, scale_ref, field_re_ref, field_im_ref, templ_re_ref, templ_im_ref, mix_ref,
    back_ref, rms_ref, *refs
):
    out_refs = refs[:-1]
    result_ref = refs[-1]
    length = field_re_ref.shape[0]
    per_step = rms_ref.shape[0]
    planes = field_re_ref.shape[1] // (per_step * length)
    count = templ_re_ref.shape[1] // (planes * length)
    group = 8 if count % 8 == 0 else 1

    def lanes(index):
        return slice(index * length, (index + 1) * length)

    for tile in range(per_step):
        best = None
        for step in range(count // group):
            joined = []
            for member in range(group):
                orient = step * group + member
                prod_re = None
                prod_im = None
                for plane in range(planes):
                    fr = field_re_ref[:, lanes(tile * planes + plane)]
                    fi = field_im_ref[:, lanes(tile * planes + plane)]
                    tr = templ_re_ref[:, lanes(orient * planes + plane)]
                    ti = templ_im_ref[:, lanes(orient * planes + plane)]
                    part_re = fr * tr + fi * ti
                    part_im = fi * tr - fr * ti
                    prod_re = part_re if prod_re is None else prod_re + part_re
                    prod_im = part_im if prod_im is None else prod_im + part_im
                joined.append(
                    jnp.concatenate(
                        [prod_re.astype(jnp.bfloat16), prod_im.astype(jnp.bfloat16)], axis=1
                    )
                )
            joined = jnp.concatenate(joined, axis=0)
            first = jnp.dot(joined, mix_ref[...], preferred_element_type=jnp.float32).astype(
                jnp.bfloat16
            )
            stacked = jnp.concatenate(
                [
                    rows_to_blocks(first[:, :length], length),
                    rows_to_blocks(first[:, length:], length),
                ],
                axis=0,
            )
            corr = jnp.dot(back_ref[...], stacked, preferred_element_type=jnp.float32)
            for member in range(group):
                orient = step * group + member
                value = corr[:, lanes(member)] * scale_ref[orient]
                best = value if best is None else jnp.maximum(best, value)
        result_ref[...] = best / rms_ref[tile]
        groups = len(out_refs)
        chunk = out_refs[0].shape[1]
        for part in range(groups):
            start = pl.multiple_of(lax.rem(slot_ref[0] + part, groups) * chunk, chunk)
            out_refs[part][tile] = result_ref[pl.ds(start, chunk), :].astype(jnp.bfloat16)


def score_tiles(
    field_real, field_imag, local_rms, templ_real, templ_imag, template_norm, table
):
    length = field_real.shape[0]
    planes = field_real.shape[1] // (local_rms.shape[0] * length)
    scale = (1.0 / template_norm) * (1.0 / (length * length))
    mix = table["mix"]
    back = table["across"]
    tiles = local_rms.shape[0]
    groups = lax.axis_size("orient")
    per_step = tiles
    tile_block = pl.BlockSpec((length, per_step * planes * length), lambda t: (0, t))
    templ_block = pl.BlockSpec(templ_real.shape, lambda t: (0, 0))
    return pl.pallas_call(
        score_kernel,
        grid=(tiles // per_step,),
        out_shape=tuple(
            jax.ShapeDtypeStruct((tiles, length // groups, length), jnp.bfloat16)
            for _ in range(groups)
        ),
        in_specs=[
            pl.BlockSpec(memory_space=pltpu.SMEM),
            pl.BlockSpec(memory_space=pltpu.SMEM),
            tile_block,
            tile_block,
            templ_block,
            templ_block,
            pl.BlockSpec((2 * length, 2 * length), lambda t: (0, 0)),
            pl.BlockSpec((length, 2 * length), lambda t: (0, 0)),
            pl.BlockSpec((per_step, length, length), lambda t: (t, 0, 0)),
        ],
        out_specs=tuple(
            pl.BlockSpec((per_step, length // groups, length), lambda t: (t, 0, 0))
            for _ in range(groups)
        ),
        scratch_shapes=[pltpu.VMEM((length, length), jnp.float32)],
    )(
        lax.axis_index("orient").astype(jnp.int32).reshape(1),
        scale,
        field_real,
        field_imag,
        templ_real,
        templ_imag,
        mix,
        back,
        local_rms,
    )


def orient_max(best):
    groups = lax.axis_size("orient")
    result = best[0]
    for shift in range(1, groups):
        route = [(source, (source + shift) % groups) for source in range(groups)]
        result = jnp.maximum(result, lax.ppermute(best[shift], "orient", route))
    return result


def per_device(tiles, assigned_worker, wedge_mask, template_volume, rotation_samples):
    tile_len = tiles.shape[-1]
    planes = tiles.shape[1]
    home_slots = tiles.shape[0]
    work_slots = home_slots // 2
    box_edge = template_volume.shape[0]
    table = transform_tables(tile_len, box_edge)
    band_sum = band_table(tile_len, box_edge)
    sampled = share_samples(template_volume, rotation_samples)
    partner_tiles = partner(tiles[work_slots:], "slab", 0)
    occupied = assigned_worker >= 0
    own_count = jnp.sum(occupied.astype(jnp.int32))
    field_real, field_imag, local_rms = field_spectra(
        own_count, tiles, partner_tiles, wedge_mask, table, band_sum, box_edge
    )
    sampled, field_real = lax.optimization_barrier((sampled, field_real))
    templ_real, templ_imag, template_norm = make_templates(sampled, box_edge, planes, table)
    best = score_tiles(
        field_real,
        field_imag,
        local_rms,
        templ_real,
        templ_imag,
        template_norm,
        table,
    )
    best_rows = orient_max(best)
    received = partner(best_rows, "slab", 0)
    padded = jnp.concatenate([received, jnp.zeros_like(received)], axis=0)
    returned = lax.dynamic_slice_in_dim(padded, home_slots - own_count, work_slots, axis=0)
    result = jnp.concatenate([best_rows, returned], axis=0)
    return jnp.where(occupied[:, None, None], result, jnp.zeros_like(result))


def solution(mesh):
    return jax.shard_map(
        per_device,
        mesh=mesh,
        in_specs=(P("slab", None, None, None), P("slab"), P(), P(), P("orient", "slab")),
        out_specs=P("slab", "orient", None),
        check_vma=False,
    )
```

```python
import functools
import math

import jax
import ml_dtypes
import numpy as np
import jax.numpy as jnp
from jax import lax
from jax.experimental import pallas as pl
from jax.experimental.pallas import tpu as pltpu
from jax.sharding import PartitionSpec as P


def partner(block, axis, bit):
    count = lax.axis_size(axis)
    route = []
    for low in range(count):
        high = low | 1 << bit
        if high != low and high < count:
            route += [(low, high), (high, low)]
    return lax.ppermute(block, axis, route)


def tables(length):
    counter = np.arange(length, dtype=np.int32)
    angles = (counter[:, None] * counter[None, :] % length).astype(np.float32) * np.float32(
        2.0 * math.pi / length
    )
    wide = angles.astype(np.float64)
    cosine = np.cos(wide).astype(np.float32).astype(ml_dtypes.bfloat16)
    sine = np.sin(wide).astype(np.float32).astype(ml_dtypes.bfloat16)
    return cosine, sine


def band_table(length, box_edge):
    counter = np.arange(length, dtype=np.int32)
    offsets = (counter[None, :] - counter[:, None]) % length
    return jnp.asarray((offsets < box_edge).astype(np.float32))


def transform_tables(length, box_edge):
    cosine, sine = tables(length)
    across = np.concatenate([cosine, -sine], axis=1)
    mix = np.concatenate(
        [np.concatenate([cosine, sine], axis=1), np.concatenate([-sine, cosine], axis=1)], axis=0
    )
    box_across = np.concatenate([cosine[:box_edge], -sine[:box_edge]], axis=1)
    box_down = np.concatenate(
        [
            np.concatenate([cosine[:, :box_edge], sine[:, :box_edge]], axis=1),
            np.concatenate([-sine[:, :box_edge], cosine[:, :box_edge]], axis=1),
        ],
        axis=0,
    )
    return {
        name: jnp.asarray(value)
        for name, value in (
            ("across", across),
            ("mix", mix),
            ("box_across", box_across),
            ("box_down", box_down),
        )
    }


def pick_rows(chosen, source):
    counter = jnp.arange(source.shape[0], dtype=jnp.int32)
    selector = (chosen[:, None] == counter[None, :]).astype(source.dtype)
    flat = source.reshape(source.shape[0], -1)
    picked = jnp.dot(selector, flat, preferred_element_type=jnp.float32).astype(source.dtype)
    return picked.reshape((chosen.shape[0],) + source.shape[1:])


def pick_kernel(index_ref, volume_ref, out_ref, picked_ref, table_ref):
    width = volume_ref.shape[1]
    blocks = table_ref.shape[0] // width
    rows = table_ref.shape[1]
    for block in range(blocks):
        strided = volume_ref[pl.ds(block, rows, stride=blocks), :]
        table_ref[block * width : (block + 1) * width, :] = jnp.transpose(strided).astype(
            jnp.bfloat16
        )
    columns = table_ref.shape[0]
    rows_in_table = table_ref.shape[1]
    lanes = index_ref.shape[1]
    shift = columns.bit_length() - 1

    def body(step, carry):
        index = index_ref[pl.ds(step, 1), :]
        high = jnp.right_shift(index, shift)
        low = jnp.bitwise_and(index, columns - 1)
        row_hot = (lax.broadcasted_iota(jnp.int32, (rows_in_table, lanes), 0) == high).astype(
            jnp.bfloat16
        )
        picked_rows = jnp.dot(table_ref[...], row_hot, preferred_element_type=jnp.float32)
        column_hot = lax.broadcasted_iota(jnp.int32, (columns, lanes), 0) == low
        chosen = jnp.where(column_hot, picked_rows, 0.0)
        picked_ref[pl.ds(step, 1), :] = jnp.sum(chosen, axis=0, keepdims=True)
        return carry

    lax.fori_loop(0, index_ref.shape[0], body, 0, unroll=4)
    picked = picked_ref[...].astype(out_ref.dtype)
    for copy in range(out_ref.shape[0]):
        out_ref[copy] = picked


def sample_template(template_volume, rotation_samples, copies):
    total = template_volume.size
    columns = 512
    edge = template_volume.shape[-1]
    volume = template_volume.reshape(total // edge, edge)
    return pl.pallas_call(
        pick_kernel,
        out_shape=jax.ShapeDtypeStruct((copies,) + rotation_samples.shape, jnp.bfloat16),
        in_specs=[pl.BlockSpec(memory_space=pltpu.VMEM)] * 2,
        out_specs=pl.BlockSpec(memory_space=pltpu.VMEM),
        scratch_shapes=[
            pltpu.VMEM(rotation_samples.shape, jnp.float32),
            pltpu.VMEM((columns, total // columns), jnp.bfloat16),
        ],
    )(rotation_samples, volume)


def share_samples(template_volume, rotation_samples):
    slab_count = lax.axis_size("slab")
    spread = sample_template(template_volume, rotation_samples, slab_count)
    return lax.all_to_all(spread, "slab", 0, 0, tiled=True)


def rows_to_blocks(values, rows):
    count = values.shape[0] // rows
    return jnp.concatenate([values[i * rows : (i + 1) * rows] for i in range(count)], axis=1)


def blocks_to_rows(values, width):
    count = values.shape[1] // width
    return jnp.concatenate(
        [values[:, i * width : (i + 1) * width] for i in range(count)], axis=0
    )


def forward_rows(values, across, down):
    width = across.shape[1] // 2
    height = down.shape[1] // 2
    first = jnp.dot(values, across, preferred_element_type=jnp.float32).astype(jnp.bfloat16)
    stacked = jnp.concatenate(
        [rows_to_blocks(first[:, :width], height), rows_to_blocks(first[:, width:], height)],
        axis=0,
    )
    second = jnp.dot(down, stacked, preferred_element_type=jnp.float32).astype(jnp.bfloat16)
    return second[:width], second[width:]


def inverse_blocks(real_part, imag_part, mix, back):
    length = real_part.shape[0]
    joined = jnp.concatenate(
        [blocks_to_rows(real_part, length), blocks_to_rows(imag_part, length)], axis=1
    )
    first = jnp.dot(joined, mix, preferred_element_type=jnp.float32).astype(jnp.bfloat16)
    stacked = jnp.concatenate(
        [rows_to_blocks(first[:, :length], length), rows_to_blocks(first[:, length:], length)],
        axis=0,
    )
    return jnp.dot(back, stacked, preferred_element_type=jnp.float32)


def template_kernel(values_ref, across_ref, down_ref, real_ref, imag_ref):
    real_part, imag_part = forward_rows(values_ref[...], across_ref[...], down_ref[...])
    real_ref[...] = real_part.astype(jnp.float32)
    imag_ref[...] = imag_part.astype(jnp.float32)


def field_kernel(
    count_ref, own_ref, other_ref, wedge_ref, across_ref, mix_ref, back_ref, band_ref,
    band_t_ref, real_ref, imag_ref, rms_ref, *, box_edge
):
    home, planes, length, _ = own_ref.shape
    tiles = rms_ref.shape[0]
    maps = tiles * planes
    own_count = count_ref[0]
    picked = []
    for tile in range(tiles):
        source = jnp.clip(tile - own_count, 0, other_ref.shape[0] - 1)
        chosen = jnp.where(tile < own_count, own_ref[tile], other_ref[source])
        picked.append(chosen.reshape(planes * length, length))
    values = jnp.concatenate(picked, axis=0)
    mix = mix_ref[...]
    real_part, imag_part = forward_rows(values, across_ref[...], mix)
    wedge = wedge_ref[...].astype(jnp.float32).astype(jnp.bfloat16)
    wedge = jnp.concatenate([wedge] * maps, axis=1)
    field = inverse_blocks(real_part * wedge, imag_part * wedge, mix, back_ref[...])
    field = (field * (1.0 / (length * length))).astype(jnp.bfloat16)
    square = jnp.square(field.astype(jnp.float32))
    energies = []
    for tile in range(tiles):
        energy = None
        for plane in range(planes):
            index = tile * planes + plane
            part = square[:, index * length : (index + 1) * length]
            energy = part if energy is None else energy + part
        energies.append(energy)
    energy = jnp.concatenate(energies, axis=1)
    band = band_ref[...].astype(jnp.float32)
    band_t = band_t_ref[...].astype(jnp.float32)
    summed = jnp.dot(
        band, energy, preferred_element_type=jnp.float32, precision=lax.Precision.HIGHEST
    )
    summed = jnp.dot(
        blocks_to_rows(summed, length),
        band_t,
        preferred_element_type=jnp.float32,
        precision=lax.Precision.HIGHEST,
    )
    for tile in range(tiles):
        part = summed[tile * length : (tile + 1) * length]
        rms_ref[tile] = jnp.sqrt(part / (box_edge * box_edge * planes) + 1e-05)
    real_part, imag_part = forward_rows(blocks_to_rows(field, length), across_ref[...], mix)
    real_ref[...] = real_part.astype(jnp.float32)
    imag_ref[...] = imag_part.astype(jnp.float32)


def whole_call(kernel, out_shape, *args):
    return pl.pallas_call(
        kernel,
        out_shape=out_shape,
        in_specs=[pl.BlockSpec(memory_space=pltpu.VMEM)] * len(args),
        out_specs=tuple(pl.BlockSpec(memory_space=pltpu.VMEM) for _ in out_shape),
    )(*args)


def make_templates(sampled, box_edge, planes, table):
    count = sampled.shape[1]
    length = table["across"].shape[0]
    sampled = jnp.transpose(sampled, (1, 0, 2))
    sampled = sampled.reshape(count, planes, box_edge, box_edge)
    template_norm = jnp.sqrt(
        jnp.sum(jnp.square(sampled.astype(jnp.float32)), axis=(1, 2, 3)) + 1e-05
    )
    spec_shape = jax.ShapeDtypeStruct((length, count * planes * length), jnp.float32)
    spec_real, spec_imag = whole_call(
        template_kernel,
        (spec_shape, spec_shape),
        sampled.reshape(count * planes * box_edge, box_edge),
        table["box_across"],
        table["box_down"],
    )
    return (spec_real, spec_imag, template_norm)


def field_spectra(own_count, tiles_own, tiles_other, wedge_mask, table, band_sum, box_edge):
    home, planes, length, _ = tiles_own.shape
    tiles = home // 2
    spec_shape = jax.ShapeDtypeStruct((length, tiles * planes * length), jnp.float32)
    args = (
        own_count.reshape(1),
        tiles_own,
        tiles_other,
        wedge_mask,
        table["across"],
        table["mix"],
        table["across"],
        band_sum.astype(jnp.bfloat16),
        band_sum.T.astype(jnp.bfloat16),
    )
    out_shape = (
        spec_shape,
        spec_shape,
        jax.ShapeDtypeStruct((tiles, length, length), jnp.float32),
    )
    return pl.pallas_call(
        functools.partial(field_kernel, box_edge=box_edge),
        out_shape=out_shape,
        in_specs=[pl.BlockSpec(memory_space=pltpu.SMEM)]
        + [pl.BlockSpec(memory_space=pltpu.VMEM)] * (len(args) - 1),
        out_specs=tuple(pl.BlockSpec(memory_space=pltpu.VMEM) for _ in out_shape),
    )(*args)


def score_kernel(
    slot_ref, scale_ref, field_re_ref, field_im_ref, templ_re_ref, templ_im_ref, mix_ref,
    back_ref, rms_ref, *refs
):
    out_refs = refs[:-1]
    result_ref = refs[-1]
    length = field_re_ref.shape[0]
    per_step = rms_ref.shape[0]
    planes = field_re_ref.shape[1] // (per_step * length)
    count = templ_re_ref.shape[1] // (planes * length)
    group = 8 if count % 8 == 0 else 1

    def lanes(index):
        return slice(index * length, (index + 1) * length)

    for tile in range(per_step):
        best = None
        for step in range(count // group):
            joined = []
            for member in range(group):
                orient = step * group + member
                prod_re = None
                prod_im = None
                for plane in range(planes):
                    fr = field_re_ref[:, lanes(tile * planes + plane)]
                    fi = field_im_ref[:, lanes(tile * planes + plane)]
                    tr = templ_re_ref[:, lanes(orient * planes + plane)]
                    ti = templ_im_ref[:, lanes(orient * planes + plane)]
                    part_re = fr * tr + fi * ti
                    part_im = fi * tr - fr * ti
                    prod_re = part_re if prod_re is None else prod_re + part_re
                    prod_im = part_im if prod_im is None else prod_im + part_im
                joined.append(
                    jnp.concatenate(
                        [prod_re.astype(jnp.bfloat16), prod_im.astype(jnp.bfloat16)], axis=1
                    )
                )
            joined = jnp.concatenate(joined, axis=0)
            first = jnp.dot(joined, mix_ref[...], preferred_element_type=jnp.float32).astype(
                jnp.bfloat16
            )
            stacked = jnp.concatenate(
                [
                    rows_to_blocks(first[:, :length], length),
                    rows_to_blocks(first[:, length:], length),
                ],
                axis=0,
            )
            corr = jnp.dot(back_ref[...], stacked, preferred_element_type=jnp.float32)
            for member in range(group):
                orient = step * group + member
                value = corr[:, lanes(member)] * scale_ref[orient]
                best = value if best is None else jnp.maximum(best, value)
        result_ref[...] = best / rms_ref[tile]
        groups = len(out_refs)
        chunk = out_refs[0].shape[1]
        for part in range(groups):
            start = pl.multiple_of(lax.rem(slot_ref[0] + part, groups) * chunk, chunk)
            out_refs[part][tile] = result_ref[pl.ds(start, chunk), :].astype(jnp.bfloat16)


def score_tiles(
    field_real, field_imag, local_rms, templ_real, templ_imag, template_norm, table
):
    length = field_real.shape[0]
    planes = field_real.shape[1] // (local_rms.shape[0] * length)
    scale = (1.0 / template_norm) * (1.0 / (length * length))
    mix = table["mix"]
    back = table["across"]
    tiles = local_rms.shape[0]
    groups = lax.axis_size("orient")
    per_step = tiles
    tile_block = pl.BlockSpec((length, per_step * planes * length), lambda t: (0, t))
    templ_block = pl.BlockSpec(templ_real.shape, lambda t: (0, 0))
    return pl.pallas_call(
        score_kernel,
        grid=(tiles // per_step,),
        out_shape=tuple(
            jax.ShapeDtypeStruct((tiles, length // groups, length), jnp.bfloat16)
            for _ in range(groups)
        ),
        in_specs=[
            pl.BlockSpec(memory_space=pltpu.SMEM),
            pl.BlockSpec(memory_space=pltpu.SMEM),
            tile_block,
            tile_block,
            templ_block,
            templ_block,
            pl.BlockSpec((2 * length, 2 * length), lambda t: (0, 0)),
            pl.BlockSpec((length, 2 * length), lambda t: (0, 0)),
            pl.BlockSpec((per_step, length, length), lambda t: (t, 0, 0)),
        ],
        out_specs=tuple(
            pl.BlockSpec((per_step, length // groups, length), lambda t: (t, 0, 0))
            for _ in range(groups)
        ),
        scratch_shapes=[pltpu.VMEM((length, length), jnp.float32)],
    )(
        lax.axis_index("orient").astype(jnp.int32).reshape(1),
        scale,
        field_real,
        field_imag,
        templ_real,
        templ_imag,
        mix,
        back,
        local_rms,
    )


def orient_max(best):
    groups = lax.axis_size("orient")
    result = best[0]
    for shift in range(1, groups):
        route = [(source, (source + shift) % groups) for source in range(groups)]
        result = jnp.maximum(result, lax.ppermute(best[shift], "orient", route))
    return result


def per_device(tiles, assigned_worker, wedge_mask, template_volume, rotation_samples):
    tile_len = tiles.shape[-1]
    planes = tiles.shape[1]
    home_slots = tiles.shape[0]
    work_slots = home_slots // 2
    box_edge = template_volume.shape[0]
    table = transform_tables(tile_len, box_edge)
    band_sum = band_table(tile_len, box_edge)
    sampled = share_samples(template_volume, rotation_samples)
    partner_tiles = partner(tiles[work_slots:], "slab", 0)
    occupied = assigned_worker >= 0
    own_count = jnp.sum(occupied.astype(jnp.int32))
    field_real, field_imag, local_rms = field_spectra(
        own_count, tiles, partner_tiles, wedge_mask, table, band_sum, box_edge
    )
    sampled, field_real = lax.optimization_barrier((sampled, field_real))
    templ_real, templ_imag, template_norm = make_templates(sampled, box_edge, planes, table)
    best = score_tiles(
        field_real,
        field_imag,
        local_rms,
        templ_real,
        templ_imag,
        template_norm,
        table,
    )
    best_rows = orient_max(best)
    received = partner(best_rows, "slab", 0)
    padded = jnp.concatenate([received, jnp.zeros_like(received)], axis=0)
    returned = lax.dynamic_slice_in_dim(padded, home_slots - own_count, work_slots, axis=0)
    result = jnp.concatenate([best_rows, returned], axis=0)
    return jnp.where(occupied[:, None, None], result, jnp.zeros_like(result))


def solution(mesh):
    return jax.shard_map(
        per_device,
        mesh=mesh,
        in_specs=(P("slab", None, None, None), P("slab"), P(), P(), P("orient", "slab")),
        out_specs=P("slab", "orient", None),
        check_vma=False,
    )
```

```python
import functools
import math

import jax
import ml_dtypes
import numpy as np
import jax.numpy as jnp
from jax import lax
from jax.experimental import pallas as pl
from jax.experimental.pallas import tpu as pltpu
from jax.sharding import PartitionSpec as P


def partner(block, axis, bit):
    count = lax.axis_size(axis)
    route = []
    for low in range(count):
        high = low | 1 << bit
        if high != low and high < count:
            route += [(low, high), (high, low)]
    return lax.ppermute(block, axis, route)


def tables(length):
    counter = np.arange(length, dtype=np.int32)
    angles = (counter[:, None] * counter[None, :] % length).astype(np.float32) * np.float32(
        2.0 * math.pi / length
    )
    wide = angles.astype(np.float64)
    cosine = np.cos(wide).astype(np.float32).astype(ml_dtypes.bfloat16)
    sine = np.sin(wide).astype(np.float32).astype(ml_dtypes.bfloat16)
    return cosine, sine


def band_table(length, box_edge):
    counter = np.arange(length, dtype=np.int32)
    offsets = (counter[None, :] - counter[:, None]) % length
    return jnp.asarray((offsets < box_edge).astype(np.float32))


def transform_tables(length, box_edge):
    cosine, sine = tables(length)
    across = np.concatenate([cosine, -sine], axis=1)
    mix = np.concatenate(
        [np.concatenate([cosine, sine], axis=1), np.concatenate([-sine, cosine], axis=1)], axis=0
    )
    box_across = np.concatenate([cosine[:box_edge], -sine[:box_edge]], axis=1)
    box_down = np.concatenate(
        [
            np.concatenate([cosine[:, :box_edge], sine[:, :box_edge]], axis=1),
            np.concatenate([-sine[:, :box_edge], cosine[:, :box_edge]], axis=1),
        ],
        axis=0,
    )
    return {
        name: jnp.asarray(value)
        for name, value in (
            ("across", across),
            ("mix", mix),
            ("box_across", box_across),
            ("box_down", box_down),
        )
    }


def pick_rows(chosen, source):
    counter = jnp.arange(source.shape[0], dtype=jnp.int32)
    selector = (chosen[:, None] == counter[None, :]).astype(source.dtype)
    flat = source.reshape(source.shape[0], -1)
    picked = jnp.dot(selector, flat, preferred_element_type=jnp.float32).astype(source.dtype)
    return picked.reshape((chosen.shape[0],) + source.shape[1:])


def pick_kernel(index_ref, volume_ref, out_ref, picked_ref, table_ref):
    width = volume_ref.shape[1]
    blocks = table_ref.shape[0] // width
    rows = table_ref.shape[1]
    for block in range(blocks):
        strided = volume_ref[pl.ds(block, rows, stride=blocks), :]
        table_ref[block * width : (block + 1) * width, :] = jnp.transpose(strided).astype(
            jnp.bfloat16
        )
    columns = table_ref.shape[0]
    rows_in_table = table_ref.shape[1]
    lanes = index_ref.shape[1]
    shift = columns.bit_length() - 1

    def body(step, carry):
        index = index_ref[pl.ds(step, 1), :]
        high = jnp.right_shift(index, shift)
        low = jnp.bitwise_and(index, columns - 1)
        row_hot = (lax.broadcasted_iota(jnp.int32, (rows_in_table, lanes), 0) == high).astype(
            jnp.bfloat16
        )
        picked_rows = jnp.dot(table_ref[...], row_hot, preferred_element_type=jnp.float32)
        column_hot = lax.broadcasted_iota(jnp.int32, (columns, lanes), 0) == low
        chosen = jnp.where(column_hot, picked_rows, 0.0)
        picked_ref[pl.ds(step, 1), :] = jnp.sum(chosen, axis=0, keepdims=True)
        return carry

    lax.fori_loop(0, index_ref.shape[0], body, 0, unroll=4)
    picked = picked_ref[...].astype(out_ref.dtype)
    for copy in range(out_ref.shape[0]):
        out_ref[copy] = picked


def sample_template(template_volume, rotation_samples, copies):
    total = template_volume.size
    columns = 512
    edge = template_volume.shape[-1]
    volume = template_volume.reshape(total // edge, edge)
    return pl.pallas_call(
        pick_kernel,
        out_shape=jax.ShapeDtypeStruct((copies,) + rotation_samples.shape, jnp.bfloat16),
        in_specs=[pl.BlockSpec(memory_space=pltpu.VMEM)] * 2,
        out_specs=pl.BlockSpec(memory_space=pltpu.VMEM),
        scratch_shapes=[
            pltpu.VMEM(rotation_samples.shape, jnp.float32),
            pltpu.VMEM((columns, total // columns), jnp.bfloat16),
        ],
    )(rotation_samples, volume)


def share_samples(template_volume, rotation_samples):
    slab_count = lax.axis_size("slab")
    spread = sample_template(template_volume, rotation_samples, slab_count)
    return lax.all_to_all(spread, "slab", 0, 0, tiled=True)


def rows_to_blocks(values, rows):
    count = values.shape[0] // rows
    return jnp.concatenate([values[i * rows : (i + 1) * rows] for i in range(count)], axis=1)


def blocks_to_rows(values, width):
    count = values.shape[1] // width
    return jnp.concatenate(
        [values[:, i * width : (i + 1) * width] for i in range(count)], axis=0
    )


def forward_rows(values, across, down):
    width = across.shape[1] // 2
    height = down.shape[1] // 2
    first = jnp.dot(values, across, preferred_element_type=jnp.float32).astype(jnp.bfloat16)
    stacked = jnp.concatenate(
        [rows_to_blocks(first[:, :width], height), rows_to_blocks(first[:, width:], height)],
        axis=0,
    )
    second = jnp.dot(down, stacked, preferred_element_type=jnp.float32).astype(jnp.bfloat16)
    return second[:width], second[width:]


def inverse_blocks(real_part, imag_part, mix, back):
    length = real_part.shape[0]
    joined = jnp.concatenate(
        [blocks_to_rows(real_part, length), blocks_to_rows(imag_part, length)], axis=1
    )
    first = jnp.dot(joined, mix, preferred_element_type=jnp.float32).astype(jnp.bfloat16)
    stacked = jnp.concatenate(
        [rows_to_blocks(first[:, :length], length), rows_to_blocks(first[:, length:], length)],
        axis=0,
    )
    return jnp.dot(back, stacked, preferred_element_type=jnp.float32)


def template_kernel(values_ref, across_ref, down_ref, real_ref, imag_ref):
    real_part, imag_part = forward_rows(values_ref[...], across_ref[...], down_ref[...])
    real_ref[...] = real_part.astype(jnp.float32)
    imag_ref[...] = imag_part.astype(jnp.float32)


def split_three(values):
    high = values.astype(jnp.bfloat16)
    rest = values - high.astype(jnp.float32)
    middle = rest.astype(jnp.bfloat16)
    low = (rest - middle.astype(jnp.float32)).astype(jnp.bfloat16)
    return (high, middle, low)


def exact_dot(left, right, left_exact):
    total = None
    if left_exact:
        for part in split_three(right):
            term = jnp.dot(left, part, preferred_element_type=jnp.float32)
            total = term if total is None else total + term
    else:
        for part in split_three(left):
            term = jnp.dot(part, right, preferred_element_type=jnp.float32)
            total = term if total is None else total + term
    return total


def field_kernel(
    count_ref, own_ref, other_ref, wedge_ref, across_ref, mix_ref, back_ref, band_ref,
    band_t_ref, real_ref, imag_ref, rms_ref, *, box_edge
):
    home, planes, length, _ = own_ref.shape
    tiles = rms_ref.shape[0]
    maps = tiles * planes
    own_count = count_ref[0]
    picked = []
    for tile in range(tiles):
        source = jnp.clip(tile - own_count, 0, other_ref.shape[0] - 1)
        chosen = jnp.where(tile < own_count, own_ref[tile], other_ref[source])
        picked.append(chosen.reshape(planes * length, length))
    values = jnp.concatenate(picked, axis=0)
    mix = mix_ref[...]
    real_part, imag_part = forward_rows(values, across_ref[...], mix)
    wedge = wedge_ref[...].astype(jnp.float32).astype(jnp.bfloat16)
    wedge = jnp.concatenate([wedge] * maps, axis=1)
    field = inverse_blocks(real_part * wedge, imag_part * wedge, mix, back_ref[...])
    field = (field * (1.0 / (length * length))).astype(jnp.bfloat16)
    square = jnp.square(field.astype(jnp.float32))
    energies = []
    for tile in range(tiles):
        energy = None
        for plane in range(planes):
            index = tile * planes + plane
            part = square[:, index * length : (index + 1) * length]
            energy = part if energy is None else energy + part
        energies.append(energy)
    energy = jnp.concatenate(energies, axis=1)
    summed = exact_dot(band_ref[...], energy, True)
    summed = exact_dot(blocks_to_rows(summed, length), band_t_ref[...], False)
    for tile in range(tiles):
        part = summed[tile * length : (tile + 1) * length]
        rms_ref[tile] = jnp.sqrt(part / (box_edge * box_edge * planes) + 1e-05)
    real_part, imag_part = forward_rows(blocks_to_rows(field, length), across_ref[...], mix)
    real_ref[...] = real_part.astype(jnp.float32)
    imag_ref[...] = imag_part.astype(jnp.float32)


def whole_call(kernel, out_shape, *args):
    return pl.pallas_call(
        kernel,
        out_shape=out_shape,
        in_specs=[pl.BlockSpec(memory_space=pltpu.VMEM)] * len(args),
        out_specs=tuple(pl.BlockSpec(memory_space=pltpu.VMEM) for _ in out_shape),
    )(*args)


def make_templates(sampled, box_edge, planes, table):
    count = sampled.shape[1]
    length = table["across"].shape[0]
    sampled = jnp.transpose(sampled, (1, 0, 2))
    sampled = sampled.reshape(count, planes, box_edge, box_edge)
    template_norm = jnp.sqrt(
        jnp.sum(jnp.square(sampled.astype(jnp.float32)), axis=(1, 2, 3)) + 1e-05
    )
    spec_shape = jax.ShapeDtypeStruct((length, count * planes * length), jnp.float32)
    spec_real, spec_imag = whole_call(
        template_kernel,
        (spec_shape, spec_shape),
        sampled.reshape(count * planes * box_edge, box_edge),
        table["box_across"],
        table["box_down"],
    )
    return (spec_real, spec_imag, template_norm)


def field_spectra(own_count, tiles_own, tiles_other, wedge_mask, table, band_sum, box_edge):
    home, planes, length, _ = tiles_own.shape
    tiles = home // 2
    spec_shape = jax.ShapeDtypeStruct((length, tiles * planes * length), jnp.float32)
    args = (
        own_count.reshape(1),
        tiles_own,
        tiles_other,
        wedge_mask,
        table["across"],
        table["mix"],
        table["across"],
        band_sum.astype(jnp.bfloat16),
        band_sum.T.astype(jnp.bfloat16),
    )
    out_shape = (
        spec_shape,
        spec_shape,
        jax.ShapeDtypeStruct((tiles, length, length), jnp.float32),
    )
    return pl.pallas_call(
        functools.partial(field_kernel, box_edge=box_edge),
        out_shape=out_shape,
        in_specs=[pl.BlockSpec(memory_space=pltpu.SMEM)]
        + [pl.BlockSpec(memory_space=pltpu.VMEM)] * (len(args) - 1),
        out_specs=tuple(pl.BlockSpec(memory_space=pltpu.VMEM) for _ in out_shape),
    )(*args)


def score_kernel(
    slot_ref, scale_ref, field_re_ref, field_im_ref, templ_re_ref, templ_im_ref, mix_ref,
    back_ref, rms_ref, *refs
):
    out_refs = refs[:-1]
    result_ref = refs[-1]
    length = field_re_ref.shape[0]
    per_step = rms_ref.shape[0]
    planes = field_re_ref.shape[1] // (per_step * length)
    count = templ_re_ref.shape[1] // (planes * length)
    group = 16 if count % 16 == 0 else 1

    def lanes(index):
        return slice(index * length, (index + 1) * length)

    for tile in range(per_step):
        best = None
        for step in range(count // group):
            joined = []
            for member in range(group):
                orient = step * group + member
                prod_re = None
                prod_im = None
                for plane in range(planes):
                    fr = field_re_ref[:, lanes(tile * planes + plane)]
                    fi = field_im_ref[:, lanes(tile * planes + plane)]
                    tr = templ_re_ref[:, lanes(orient * planes + plane)]
                    ti = templ_im_ref[:, lanes(orient * planes + plane)]
                    part_re = fr * tr + fi * ti
                    part_im = fi * tr - fr * ti
                    prod_re = part_re if prod_re is None else prod_re + part_re
                    prod_im = part_im if prod_im is None else prod_im + part_im
                joined.append(
                    jnp.concatenate(
                        [prod_re.astype(jnp.bfloat16), prod_im.astype(jnp.bfloat16)], axis=1
                    )
                )
            joined = jnp.concatenate(joined, axis=0)
            first = jnp.dot(joined, mix_ref[...], preferred_element_type=jnp.float32).astype(
                jnp.bfloat16
            )
            stacked = jnp.concatenate(
                [
                    rows_to_blocks(first[:, :length], length),
                    rows_to_blocks(first[:, length:], length),
                ],
                axis=0,
            )
            corr = jnp.dot(back_ref[...], stacked, preferred_element_type=jnp.float32)
            for member in range(group):
                orient = step * group + member
                value = corr[:, lanes(member)] * scale_ref[orient]
                best = value if best is None else jnp.maximum(best, value)
        result_ref[...] = best / rms_ref[tile]
        groups = len(out_refs)
        chunk = out_refs[0].shape[1]
        for part in range(groups):
            start = pl.multiple_of(lax.rem(slot_ref[0] + part, groups) * chunk, chunk)
            out_refs[part][tile] = result_ref[pl.ds(start, chunk), :].astype(jnp.bfloat16)


def score_tiles(
    field_real, field_imag, local_rms, templ_real, templ_imag, template_norm, table
):
    length = field_real.shape[0]
    planes = field_real.shape[1] // (local_rms.shape[0] * length)
    scale = (1.0 / template_norm) * (1.0 / (length * length))
    mix = table["mix"]
    back = table["across"]
    tiles = local_rms.shape[0]
    groups = lax.axis_size("orient")
    per_step = tiles
    tile_block = pl.BlockSpec((length, per_step * planes * length), lambda t: (0, t))
    templ_block = pl.BlockSpec(templ_real.shape, lambda t: (0, 0))
    return pl.pallas_call(
        score_kernel,
        grid=(tiles // per_step,),
        out_shape=tuple(
            jax.ShapeDtypeStruct((tiles, length // groups, length), jnp.bfloat16)
            for _ in range(groups)
        ),
        in_specs=[
            pl.BlockSpec(memory_space=pltpu.SMEM),
            pl.BlockSpec(memory_space=pltpu.SMEM),
            tile_block,
            tile_block,
            templ_block,
            templ_block,
            pl.BlockSpec((2 * length, 2 * length), lambda t: (0, 0)),
            pl.BlockSpec((length, 2 * length), lambda t: (0, 0)),
            pl.BlockSpec((per_step, length, length), lambda t: (t, 0, 0)),
        ],
        out_specs=tuple(
            pl.BlockSpec((per_step, length // groups, length), lambda t: (t, 0, 0))
            for _ in range(groups)
        ),
        scratch_shapes=[pltpu.VMEM((length, length), jnp.float32)],
    )(
        lax.axis_index("orient").astype(jnp.int32).reshape(1),
        scale,
        field_real,
        field_imag,
        templ_real,
        templ_imag,
        mix,
        back,
        local_rms,
    )


def orient_max(best):
    groups = lax.axis_size("orient")
    result = best[0]
    for shift in range(1, groups):
        route = [(source, (source + shift) % groups) for source in range(groups)]
        result = jnp.maximum(result, lax.ppermute(best[shift], "orient", route))
    return result


def per_device(tiles, assigned_worker, wedge_mask, template_volume, rotation_samples):
    tile_len = tiles.shape[-1]
    planes = tiles.shape[1]
    home_slots = tiles.shape[0]
    work_slots = home_slots // 2
    box_edge = template_volume.shape[0]
    table = transform_tables(tile_len, box_edge)
    band_sum = band_table(tile_len, box_edge)
    sampled = share_samples(template_volume, rotation_samples)
    partner_tiles = partner(tiles[work_slots:], "slab", 0)
    occupied = assigned_worker >= 0
    own_count = jnp.sum(occupied.astype(jnp.int32))
    field_real, field_imag, local_rms = field_spectra(
        own_count, tiles, partner_tiles, wedge_mask, table, band_sum, box_edge
    )
    sampled, field_real = lax.optimization_barrier((sampled, field_real))
    templ_real, templ_imag, template_norm = make_templates(sampled, box_edge, planes, table)
    best = score_tiles(
        field_real,
        field_imag,
        local_rms,
        templ_real,
        templ_imag,
        template_norm,
        table,
    )
    best_rows = orient_max(best)
    received = partner(best_rows, "slab", 0)
    padded = jnp.concatenate([received, jnp.zeros_like(received)], axis=0)
    returned = lax.dynamic_slice_in_dim(padded, home_slots - own_count, work_slots, axis=0)
    result = jnp.concatenate([best_rows, returned], axis=0)
    return jnp.where(occupied[:, None, None], result, jnp.zeros_like(result))


def solution(mesh):
    return jax.shard_map(
        per_device,
        mesh=mesh,
        in_specs=(P("slab", None, None, None), P("slab"), P(), P(), P("orient", "slab")),
        out_specs=P("slab", "orient", None),
        check_vma=False,
    )
```

```python
import functools
import math

import jax
import ml_dtypes
import numpy as np
import jax.numpy as jnp
from jax import lax
from jax.experimental import pallas as pl
from jax.experimental.pallas import tpu as pltpu
from jax.sharding import PartitionSpec as P


def partner(block, axis, bit):
    count = lax.axis_size(axis)
    route = []
    for low in range(count):
        high = low | 1 << bit
        if high != low and high < count:
            route += [(low, high), (high, low)]
    return lax.ppermute(block, axis, route)


def tables(length):
    counter = np.arange(length, dtype=np.int32)
    angles = (counter[:, None] * counter[None, :] % length).astype(np.float32) * np.float32(
        2.0 * math.pi / length
    )
    wide = angles.astype(np.float64)
    cosine = np.cos(wide).astype(np.float32).astype(ml_dtypes.bfloat16)
    sine = np.sin(wide).astype(np.float32).astype(ml_dtypes.bfloat16)
    return cosine, sine


def band_table(length, box_edge):
    counter = np.arange(length, dtype=np.int32)
    offsets = (counter[None, :] - counter[:, None]) % length
    return jnp.asarray((offsets < box_edge).astype(np.float32))


def transform_tables(length, box_edge):
    cosine, sine = tables(length)
    across = np.concatenate([cosine, -sine], axis=1)
    mix = np.concatenate(
        [np.concatenate([cosine, sine], axis=1), np.concatenate([-sine, cosine], axis=1)], axis=0
    )
    box_across = np.concatenate([cosine[:box_edge], -sine[:box_edge]], axis=1)
    box_down = np.concatenate(
        [
            np.concatenate([cosine[:, :box_edge], sine[:, :box_edge]], axis=1),
            np.concatenate([-sine[:, :box_edge], cosine[:, :box_edge]], axis=1),
        ],
        axis=0,
    )
    return {
        name: jnp.asarray(value)
        for name, value in (
            ("across", across),
            ("mix", mix),
            ("box_across", box_across),
            ("box_down", box_down),
        )
    }


def pick_rows(chosen, source):
    counter = jnp.arange(source.shape[0], dtype=jnp.int32)
    selector = (chosen[:, None] == counter[None, :]).astype(source.dtype)
    flat = source.reshape(source.shape[0], -1)
    picked = jnp.dot(selector, flat, preferred_element_type=jnp.float32).astype(source.dtype)
    return picked.reshape((chosen.shape[0],) + source.shape[1:])


def pick_kernel(index_ref, volume_ref, out_ref, picked_ref, table_ref):
    width = volume_ref.shape[1]
    blocks = table_ref.shape[0] // width
    rows = table_ref.shape[1]
    for block in range(blocks):
        strided = volume_ref[pl.ds(block, rows, stride=blocks), :]
        table_ref[block * width : (block + 1) * width, :] = jnp.transpose(strided).astype(
            jnp.bfloat16
        )
    columns = table_ref.shape[0]
    rows_in_table = table_ref.shape[1]
    lanes = index_ref.shape[1]
    shift = columns.bit_length() - 1

    def body(step, carry):
        index = index_ref[pl.ds(step, 1), :]
        high = jnp.right_shift(index, shift)
        low = jnp.bitwise_and(index, columns - 1)
        row_hot = (lax.broadcasted_iota(jnp.int32, (rows_in_table, lanes), 0) == high).astype(
            jnp.bfloat16
        )
        picked_rows = jnp.dot(table_ref[...], row_hot, preferred_element_type=jnp.float32)
        column_hot = lax.broadcasted_iota(jnp.int32, (columns, lanes), 0) == low
        chosen = jnp.where(column_hot, picked_rows, 0.0)
        picked_ref[pl.ds(step, 1), :] = jnp.sum(chosen, axis=0, keepdims=True)
        return carry

    lax.fori_loop(0, index_ref.shape[0], body, 0, unroll=4)
    picked = picked_ref[...].astype(out_ref.dtype)
    for copy in range(out_ref.shape[0]):
        out_ref[copy] = picked


def sample_template(template_volume, rotation_samples, copies):
    total = template_volume.size
    columns = 512
    edge = template_volume.shape[-1]
    volume = template_volume.reshape(total // edge, edge)
    return pl.pallas_call(
        pick_kernel,
        out_shape=jax.ShapeDtypeStruct((copies,) + rotation_samples.shape, jnp.bfloat16),
        in_specs=[pl.BlockSpec(memory_space=pltpu.VMEM)] * 2,
        out_specs=pl.BlockSpec(memory_space=pltpu.VMEM),
        scratch_shapes=[
            pltpu.VMEM(rotation_samples.shape, jnp.float32),
            pltpu.VMEM((columns, total // columns), jnp.bfloat16),
        ],
    )(rotation_samples, volume)


def share_samples(template_volume, rotation_samples):
    slab_count = lax.axis_size("slab")
    spread = sample_template(template_volume, rotation_samples, slab_count)
    return lax.all_to_all(spread, "slab", 0, 0, tiled=True)


def rows_to_blocks(values, rows):
    count = values.shape[0] // rows
    return jnp.concatenate([values[i * rows : (i + 1) * rows] for i in range(count)], axis=1)


def blocks_to_rows(values, width):
    count = values.shape[1] // width
    return jnp.concatenate(
        [values[:, i * width : (i + 1) * width] for i in range(count)], axis=0
    )


def forward_rows(values, across, down):
    width = across.shape[1] // 2
    height = down.shape[1] // 2
    first = jnp.dot(values, across, preferred_element_type=jnp.float32).astype(jnp.bfloat16)
    stacked = jnp.concatenate(
        [rows_to_blocks(first[:, :width], height), rows_to_blocks(first[:, width:], height)],
        axis=0,
    )
    second = jnp.dot(down, stacked, preferred_element_type=jnp.float32).astype(jnp.bfloat16)
    return second[:width], second[width:]


def inverse_blocks(real_part, imag_part, mix, back):
    length = real_part.shape[0]
    joined = jnp.concatenate(
        [blocks_to_rows(real_part, length), blocks_to_rows(imag_part, length)], axis=1
    )
    first = jnp.dot(joined, mix, preferred_element_type=jnp.float32).astype(jnp.bfloat16)
    stacked = jnp.concatenate(
        [rows_to_blocks(first[:, :length], length), rows_to_blocks(first[:, length:], length)],
        axis=0,
    )
    return jnp.dot(back, stacked, preferred_element_type=jnp.float32)


def template_kernel(values_ref, across_ref, down_ref, real_ref, imag_ref):
    real_part, imag_part = forward_rows(values_ref[...], across_ref[...], down_ref[...])
    real_ref[...] = real_part.astype(jnp.float32)
    imag_ref[...] = imag_part.astype(jnp.float32)


def split_three(values):
    high = values.astype(jnp.bfloat16)
    rest = values - high.astype(jnp.float32)
    middle = rest.astype(jnp.bfloat16)
    low = (rest - middle.astype(jnp.float32)).astype(jnp.bfloat16)
    return (high, middle, low)


def exact_dot(left, right, left_exact):
    total = None
    if left_exact:
        for part in split_three(right):
            term = jnp.dot(left, part, preferred_element_type=jnp.float32)
            total = term if total is None else total + term
    else:
        for part in split_three(left):
            term = jnp.dot(part, right, preferred_element_type=jnp.float32)
            total = term if total is None else total + term
    return total


def field_kernel(
    count_ref, own_ref, other_ref, wedge_ref, across_ref, mix_ref, back_ref, band_ref,
    band_t_ref, real_ref, imag_ref, rms_ref, *, box_edge
):
    home, planes, length, _ = own_ref.shape
    tiles = rms_ref.shape[0]
    maps = tiles * planes
    own_count = count_ref[0]
    picked = []
    for tile in range(tiles):
        source = jnp.clip(tile - own_count, 0, other_ref.shape[0] - 1)
        chosen = jnp.where(tile < own_count, own_ref[tile], other_ref[source])
        picked.append(chosen.reshape(planes * length, length))
    values = jnp.concatenate(picked, axis=0)
    mix = mix_ref[...]
    real_part, imag_part = forward_rows(values, across_ref[...], mix)
    wedge = wedge_ref[...].astype(jnp.float32).astype(jnp.bfloat16)
    wedge = jnp.concatenate([wedge] * maps, axis=1)
    field = inverse_blocks(real_part * wedge, imag_part * wedge, mix, back_ref[...])
    field = (field * (1.0 / (length * length))).astype(jnp.bfloat16)
    square = jnp.square(field.astype(jnp.float32))
    energies = []
    for tile in range(tiles):
        energy = None
        for plane in range(planes):
            index = tile * planes + plane
            part = square[:, index * length : (index + 1) * length]
            energy = part if energy is None else energy + part
        energies.append(energy)
    energy = jnp.concatenate(energies, axis=1)
    summed = exact_dot(band_ref[...], energy, True)
    summed = exact_dot(blocks_to_rows(summed, length), band_t_ref[...], False)
    for tile in range(tiles):
        part = summed[tile * length : (tile + 1) * length]
        rms_ref[tile] = jnp.sqrt(part / (box_edge * box_edge * planes) + 1e-05)
    real_part, imag_part = forward_rows(blocks_to_rows(field, length), across_ref[...], mix)
    real_ref[...] = real_part.astype(jnp.float32)
    imag_ref[...] = imag_part.astype(jnp.float32)


def whole_call(kernel, out_shape, *args):
    return pl.pallas_call(
        kernel,
        out_shape=out_shape,
        in_specs=[pl.BlockSpec(memory_space=pltpu.VMEM)] * len(args),
        out_specs=tuple(pl.BlockSpec(memory_space=pltpu.VMEM) for _ in out_shape),
    )(*args)


def make_templates(sampled, box_edge, planes, table):
    count = sampled.shape[1]
    length = table["across"].shape[0]
    sampled = jnp.transpose(sampled, (1, 0, 2))
    sampled = sampled.reshape(count, planes, box_edge, box_edge)
    template_norm = jnp.sqrt(
        jnp.sum(jnp.square(sampled.astype(jnp.float32)), axis=(1, 2, 3)) + 1e-05
    )
    spec_shape = jax.ShapeDtypeStruct((length, count * planes * length), jnp.float32)
    spec_real, spec_imag = whole_call(
        template_kernel,
        (spec_shape, spec_shape),
        sampled.reshape(count * planes * box_edge, box_edge),
        table["box_across"],
        table["box_down"],
    )
    return (spec_real, spec_imag, template_norm)


def field_spectra(own_count, tiles_own, tiles_other, wedge_mask, table, band_sum, box_edge):
    home, planes, length, _ = tiles_own.shape
    tiles = home // 2
    spec_shape = jax.ShapeDtypeStruct((length, tiles * planes * length), jnp.float32)
    args = (
        own_count.reshape(1),
        tiles_own,
        tiles_other,
        wedge_mask,
        table["across"],
        table["mix"],
        table["across"],
        band_sum.astype(jnp.bfloat16),
        band_sum.T.astype(jnp.bfloat16),
    )
    out_shape = (
        spec_shape,
        spec_shape,
        jax.ShapeDtypeStruct((tiles, length, length), jnp.float32),
    )
    return pl.pallas_call(
        functools.partial(field_kernel, box_edge=box_edge),
        out_shape=out_shape,
        in_specs=[pl.BlockSpec(memory_space=pltpu.SMEM)]
        + [pl.BlockSpec(memory_space=pltpu.VMEM)] * (len(args) - 1),
        out_specs=tuple(pl.BlockSpec(memory_space=pltpu.VMEM) for _ in out_shape),
    )(*args)


def score_kernel(
    slot_ref, scale_ref, field_re_ref, field_im_ref, templ_re_ref, templ_im_ref, mix_ref,
    back_ref, rms_ref, *refs
):
    out_refs = refs[:-1]
    result_ref = refs[-1]
    length = field_re_ref.shape[0]
    per_step = rms_ref.shape[0]
    planes = field_re_ref.shape[1] // (per_step * length)
    count = templ_re_ref.shape[1] // (planes * length)
    group = 16 if count % 16 == 0 else 1

    def lanes(index):
        return slice(index * length, (index + 1) * length)

    pack = 2 if group == count and per_step % 2 == 0 else 1
    for lead in range(0, per_step, pack):
        bests = [None] * pack
        for step in range(count // group):
            joined = []
            for local in range(pack):
                tile = lead + local
                for member in range(group):
                    orient = step * group + member
                    prod_re = None
                    prod_im = None
                    for plane in range(planes):
                        fr = field_re_ref[:, lanes(tile * planes + plane)]
                        fi = field_im_ref[:, lanes(tile * planes + plane)]
                        tr = templ_re_ref[:, lanes(orient * planes + plane)]
                        ti = templ_im_ref[:, lanes(orient * planes + plane)]
                        part_re = fr * tr + fi * ti
                        part_im = fi * tr - fr * ti
                        prod_re = part_re if prod_re is None else prod_re + part_re
                        prod_im = part_im if prod_im is None else prod_im + part_im
                    joined.append(
                        jnp.concatenate(
                            [prod_re.astype(jnp.bfloat16), prod_im.astype(jnp.bfloat16)],
                            axis=1,
                        )
                    )
            joined = jnp.concatenate(joined, axis=0)
            first = jnp.dot(joined, mix_ref[...], preferred_element_type=jnp.float32).astype(
                jnp.bfloat16
            )
            stacked = jnp.concatenate(
                [
                    rows_to_blocks(first[:, :length], length),
                    rows_to_blocks(first[:, length:], length),
                ],
                axis=0,
            )
            corr = jnp.dot(back_ref[...], stacked, preferred_element_type=jnp.float32)
            for local in range(pack):
                for member in range(group):
                    orient = step * group + member
                    value = corr[:, lanes(local * group + member)] * scale_ref[orient]
                    best = bests[local]
                    bests[local] = value if best is None else jnp.maximum(best, value)
        for local in range(pack):
            tile = lead + local
            best = bests[local]
            result_ref[...] = best / rms_ref[tile]
            groups = len(out_refs)
            chunk = out_refs[0].shape[1]
            for part in range(groups):
                start = pl.multiple_of(lax.rem(slot_ref[0] + part, groups) * chunk, chunk)
                out_refs[part][tile] = result_ref[pl.ds(start, chunk), :].astype(jnp.bfloat16)


def score_tiles(
    field_real, field_imag, local_rms, templ_real, templ_imag, template_norm, table
):
    length = field_real.shape[0]
    planes = field_real.shape[1] // (local_rms.shape[0] * length)
    scale = (1.0 / template_norm) * (1.0 / (length * length))
    mix = table["mix"]
    back = table["across"]
    tiles = local_rms.shape[0]
    groups = lax.axis_size("orient")
    per_step = tiles
    tile_block = pl.BlockSpec((length, per_step * planes * length), lambda t: (0, t))
    templ_block = pl.BlockSpec(templ_real.shape, lambda t: (0, 0))
    return pl.pallas_call(
        score_kernel,
        grid=(tiles // per_step,),
        out_shape=tuple(
            jax.ShapeDtypeStruct((tiles, length // groups, length), jnp.bfloat16)
            for _ in range(groups)
        ),
        in_specs=[
            pl.BlockSpec(memory_space=pltpu.SMEM),
            pl.BlockSpec(memory_space=pltpu.SMEM),
            tile_block,
            tile_block,
            templ_block,
            templ_block,
            pl.BlockSpec((2 * length, 2 * length), lambda t: (0, 0)),
            pl.BlockSpec((length, 2 * length), lambda t: (0, 0)),
            pl.BlockSpec((per_step, length, length), lambda t: (t, 0, 0)),
        ],
        out_specs=tuple(
            pl.BlockSpec((per_step, length // groups, length), lambda t: (t, 0, 0))
            for _ in range(groups)
        ),
        scratch_shapes=[pltpu.VMEM((length, length), jnp.float32)],
    )(
        lax.axis_index("orient").astype(jnp.int32).reshape(1),
        scale,
        field_real,
        field_imag,
        templ_real,
        templ_imag,
        mix,
        back,
        local_rms,
    )


def orient_max(best):
    groups = lax.axis_size("orient")
    result = best[0]
    for shift in range(1, groups):
        route = [(source, (source + shift) % groups) for source in range(groups)]
        result = jnp.maximum(result, lax.ppermute(best[shift], "orient", route))
    return result


def per_device(tiles, assigned_worker, wedge_mask, template_volume, rotation_samples):
    tile_len = tiles.shape[-1]
    planes = tiles.shape[1]
    home_slots = tiles.shape[0]
    work_slots = home_slots // 2
    box_edge = template_volume.shape[0]
    table = transform_tables(tile_len, box_edge)
    band_sum = band_table(tile_len, box_edge)
    sampled = share_samples(template_volume, rotation_samples)
    partner_tiles = partner(tiles[work_slots:], "slab", 0)
    occupied = assigned_worker >= 0
    own_count = jnp.sum(occupied.astype(jnp.int32))
    field_real, field_imag, local_rms = field_spectra(
        own_count, tiles, partner_tiles, wedge_mask, table, band_sum, box_edge
    )
    sampled, field_real = lax.optimization_barrier((sampled, field_real))
    templ_real, templ_imag, template_norm = make_templates(sampled, box_edge, planes, table)
    best = score_tiles(
        field_real,
        field_imag,
        local_rms,
        templ_real,
        templ_imag,
        template_norm,
        table,
    )
    best_rows = orient_max(best)
    received = partner(best_rows, "slab", 0)
    padded = jnp.concatenate([received, jnp.zeros_like(received)], axis=0)
    returned = lax.dynamic_slice_in_dim(padded, home_slots - own_count, work_slots, axis=0)
    result = jnp.concatenate([best_rows, returned], axis=0)
    return jnp.where(occupied[:, None, None], result, jnp.zeros_like(result))


def solution(mesh):
    return jax.shard_map(
        per_device,
        mesh=mesh,
        in_specs=(P("slab", None, None, None), P("slab"), P(), P(), P("orient", "slab")),
        out_specs=P("slab", "orient", None),
        check_vma=False,
    )
```

```python
import functools
import math

import jax
import ml_dtypes
import numpy as np
import jax.numpy as jnp
from jax import lax
from jax.experimental import pallas as pl
from jax.experimental.pallas import tpu as pltpu
from jax.sharding import PartitionSpec as P


def partner(block, axis, bit):
    count = lax.axis_size(axis)
    route = []
    for low in range(count):
        high = low | 1 << bit
        if high != low and high < count:
            route += [(low, high), (high, low)]
    return lax.ppermute(block, axis, route)


def tables(length):
    counter = np.arange(length, dtype=np.int32)
    angles = (counter[:, None] * counter[None, :] % length).astype(np.float32) * np.float32(
        2.0 * math.pi / length
    )
    wide = angles.astype(np.float64)
    cosine = np.cos(wide).astype(np.float32).astype(ml_dtypes.bfloat16)
    sine = np.sin(wide).astype(np.float32).astype(ml_dtypes.bfloat16)
    return cosine, sine


def band_table(length, box_edge):
    counter = np.arange(length, dtype=np.int32)
    offsets = (counter[None, :] - counter[:, None]) % length
    return jnp.asarray((offsets < box_edge).astype(np.float32))


def transform_tables(length, box_edge):
    cosine, sine = tables(length)
    across = np.concatenate([cosine, -sine], axis=1)
    mix = np.concatenate(
        [np.concatenate([cosine, sine], axis=1), np.concatenate([-sine, cosine], axis=1)], axis=0
    )
    box_across = np.concatenate([cosine[:box_edge], -sine[:box_edge]], axis=1)
    box_down = np.concatenate(
        [
            np.concatenate([cosine[:, :box_edge], sine[:, :box_edge]], axis=1),
            np.concatenate([-sine[:, :box_edge], cosine[:, :box_edge]], axis=1),
        ],
        axis=0,
    )
    return {
        name: jnp.asarray(value)
        for name, value in (
            ("across", across),
            ("mix", mix),
            ("box_across", box_across),
            ("box_down", box_down),
        )
    }


def pick_rows(chosen, source):
    counter = jnp.arange(source.shape[0], dtype=jnp.int32)
    selector = (chosen[:, None] == counter[None, :]).astype(source.dtype)
    flat = source.reshape(source.shape[0], -1)
    picked = jnp.dot(selector, flat, preferred_element_type=jnp.float32).astype(source.dtype)
    return picked.reshape((chosen.shape[0],) + source.shape[1:])


def pick_kernel(index_ref, volume_ref, out_ref, picked_ref, table_ref):
    width = volume_ref.shape[1]
    blocks = table_ref.shape[0] // width
    rows = table_ref.shape[1]
    for block in range(blocks):
        strided = volume_ref[pl.ds(block, rows, stride=blocks), :]
        table_ref[block * width : (block + 1) * width, :] = jnp.transpose(strided).astype(
            jnp.bfloat16
        )
    columns = table_ref.shape[0]
    rows_in_table = table_ref.shape[1]
    lanes = index_ref.shape[1]
    shift = columns.bit_length() - 1

    def body(step, carry):
        index = index_ref[pl.ds(step, 1), :]
        high = jnp.right_shift(index, shift)
        low = jnp.bitwise_and(index, columns - 1)
        row_hot = (lax.broadcasted_iota(jnp.int32, (rows_in_table, lanes), 0) == high).astype(
            jnp.bfloat16
        )
        picked_rows = jnp.dot(table_ref[...], row_hot, preferred_element_type=jnp.float32)
        column_hot = lax.broadcasted_iota(jnp.int32, (columns, lanes), 0) == low
        chosen = jnp.where(column_hot, picked_rows, 0.0)
        picked_ref[pl.ds(step, 1), :] = jnp.sum(chosen, axis=0, keepdims=True)
        return carry

    lax.fori_loop(0, index_ref.shape[0], body, 0, unroll=4)
    picked = picked_ref[...].astype(out_ref.dtype)
    for copy in range(out_ref.shape[0]):
        out_ref[copy] = picked


def sample_template(template_volume, rotation_samples, copies):
    total = template_volume.size
    columns = 512
    edge = template_volume.shape[-1]
    volume = template_volume.reshape(total // edge, edge)
    return pl.pallas_call(
        pick_kernel,
        out_shape=jax.ShapeDtypeStruct((copies,) + rotation_samples.shape, jnp.bfloat16),
        in_specs=[pl.BlockSpec(memory_space=pltpu.VMEM)] * 2,
        out_specs=pl.BlockSpec(memory_space=pltpu.VMEM),
        scratch_shapes=[
            pltpu.VMEM(rotation_samples.shape, jnp.float32),
            pltpu.VMEM((columns, total // columns), jnp.bfloat16),
        ],
    )(rotation_samples, volume)


def share_samples(template_volume, rotation_samples):
    slab_count = lax.axis_size("slab")
    spread = sample_template(template_volume, rotation_samples, slab_count)
    return lax.all_to_all(spread, "slab", 0, 0, tiled=True)


def rows_to_blocks(values, rows):
    count = values.shape[0] // rows
    return jnp.concatenate([values[i * rows : (i + 1) * rows] for i in range(count)], axis=1)


def blocks_to_rows(values, width):
    count = values.shape[1] // width
    return jnp.concatenate(
        [values[:, i * width : (i + 1) * width] for i in range(count)], axis=0
    )


def forward_rows(values, across, down):
    width = across.shape[1] // 2
    height = down.shape[1] // 2
    first = jnp.dot(values, across, preferred_element_type=jnp.float32).astype(jnp.bfloat16)
    stacked = jnp.concatenate(
        [rows_to_blocks(first[:, :width], height), rows_to_blocks(first[:, width:], height)],
        axis=0,
    )
    second = jnp.dot(down, stacked, preferred_element_type=jnp.float32).astype(jnp.bfloat16)
    return second[:width], second[width:]


def inverse_blocks(real_part, imag_part, mix, back):
    length = real_part.shape[0]
    joined = jnp.concatenate(
        [blocks_to_rows(real_part, length), blocks_to_rows(imag_part, length)], axis=1
    )
    first = jnp.dot(joined, mix, preferred_element_type=jnp.float32).astype(jnp.bfloat16)
    stacked = jnp.concatenate(
        [rows_to_blocks(first[:, :length], length), rows_to_blocks(first[:, length:], length)],
        axis=0,
    )
    return jnp.dot(back, stacked, preferred_element_type=jnp.float32)


def template_kernel(values_ref, across_ref, down_ref, real_ref, imag_ref):
    real_part, imag_part = forward_rows(values_ref[...], across_ref[...], down_ref[...])
    real_ref[...] = real_part.astype(jnp.float32)
    imag_ref[...] = imag_part.astype(jnp.float32)


def split_three(values):
    high = values.astype(jnp.bfloat16)
    rest = values - high.astype(jnp.float32)
    middle = rest.astype(jnp.bfloat16)
    low = (rest - middle.astype(jnp.float32)).astype(jnp.bfloat16)
    return (high, middle, low)


def exact_dot(left, right, left_exact):
    total = None
    if left_exact:
        for part in split_three(right):
            term = jnp.dot(left, part, preferred_element_type=jnp.float32)
            total = term if total is None else total + term
    else:
        for part in split_three(left):
            term = jnp.dot(part, right, preferred_element_type=jnp.float32)
            total = term if total is None else total + term
    return total


def field_kernel(
    count_ref, own_ref, other_ref, wedge_ref, across_ref, mix_ref, back_ref, band_ref,
    band_t_ref, real_ref, imag_ref, rms_ref, *, box_edge
):
    home, planes, length, _ = own_ref.shape
    tiles = rms_ref.shape[0]
    maps = tiles * planes
    own_count = count_ref[0]
    picked = []
    for tile in range(tiles):
        source = jnp.clip(tile - own_count, 0, other_ref.shape[0] - 1)
        chosen = jnp.where(tile < own_count, own_ref[tile], other_ref[source])
        picked.append(chosen.reshape(planes * length, length))
    values = jnp.concatenate(picked, axis=0)
    mix = mix_ref[...]
    real_part, imag_part = forward_rows(values, across_ref[...], mix)
    wedge = wedge_ref[...].astype(jnp.float32).astype(jnp.bfloat16)
    wedge = jnp.concatenate([wedge] * maps, axis=1)
    field = inverse_blocks(real_part * wedge, imag_part * wedge, mix, back_ref[...])
    field = (field * (1.0 / (length * length))).astype(jnp.bfloat16)
    square = jnp.square(field.astype(jnp.float32))
    energies = []
    for tile in range(tiles):
        energy = None
        for plane in range(planes):
            index = tile * planes + plane
            part = square[:, index * length : (index + 1) * length]
            energy = part if energy is None else energy + part
        energies.append(energy)
    energy = jnp.concatenate(energies, axis=1)
    summed = exact_dot(band_ref[...], energy, True)
    summed = exact_dot(blocks_to_rows(summed, length), band_t_ref[...], False)
    for tile in range(tiles):
        part = summed[tile * length : (tile + 1) * length]
        rms_ref[tile] = jnp.sqrt(part / (box_edge * box_edge * planes) + 1e-05)
    real_part, imag_part = forward_rows(blocks_to_rows(field, length), across_ref[...], mix)
    real_ref[...] = real_part.astype(jnp.float32)
    imag_ref[...] = imag_part.astype(jnp.float32)


def whole_call(kernel, out_shape, *args):
    return pl.pallas_call(
        kernel,
        out_shape=out_shape,
        in_specs=[pl.BlockSpec(memory_space=pltpu.VMEM)] * len(args),
        out_specs=tuple(pl.BlockSpec(memory_space=pltpu.VMEM) for _ in out_shape),
    )(*args)


def make_templates(sampled, box_edge, planes, table):
    count = sampled.shape[1]
    length = table["across"].shape[0]
    sampled = jnp.transpose(sampled, (1, 0, 2))
    sampled = sampled.reshape(count, planes, box_edge, box_edge)
    template_norm = jnp.sqrt(
        jnp.sum(jnp.square(sampled.astype(jnp.float32)), axis=(1, 2, 3)) + 1e-05
    )
    spec_shape = jax.ShapeDtypeStruct((length, count * planes * length), jnp.float32)
    spec_real, spec_imag = whole_call(
        template_kernel,
        (spec_shape, spec_shape),
        sampled.reshape(count * planes * box_edge, box_edge),
        table["box_across"],
        table["box_down"],
    )
    return (spec_real, spec_imag, template_norm)


def field_spectra(own_count, tiles_own, tiles_other, wedge_mask, table, band_sum, box_edge):
    home, planes, length, _ = tiles_own.shape
    tiles = home // 2
    spec_shape = jax.ShapeDtypeStruct((length, tiles * planes * length), jnp.float32)
    args = (
        own_count.reshape(1),
        tiles_own,
        tiles_other,
        wedge_mask,
        table["across"],
        table["mix"],
        table["across"],
        band_sum.astype(jnp.bfloat16),
        band_sum.T.astype(jnp.bfloat16),
    )
    out_shape = (
        spec_shape,
        spec_shape,
        jax.ShapeDtypeStruct((tiles, length, length), jnp.float32),
    )
    return pl.pallas_call(
        functools.partial(field_kernel, box_edge=box_edge),
        out_shape=out_shape,
        in_specs=[pl.BlockSpec(memory_space=pltpu.SMEM)]
        + [pl.BlockSpec(memory_space=pltpu.VMEM)] * (len(args) - 1),
        out_specs=tuple(pl.BlockSpec(memory_space=pltpu.VMEM) for _ in out_shape),
    )(*args)


def score_kernel(
    slot_ref, scale_ref, field_re_ref, field_im_ref, templ_re_ref, templ_im_ref, mix_ref,
    back_ref, rms_ref, *refs
):
    out_refs = refs[:-1]
    result_ref = refs[-1]
    length = field_re_ref.shape[0]
    per_step = rms_ref.shape[0]
    planes = field_re_ref.shape[1] // (per_step * length)
    count = templ_re_ref.shape[1] // (planes * length)
    group = 16 if count % 16 == 0 else 1

    def lanes(index):
        return slice(index * length, (index + 1) * length)

    pack = 4 if group == count and per_step % 4 == 0 else 1
    for lead in range(0, per_step, pack):
        bests = [None] * pack
        for step in range(count // group):
            joined = []
            for local in range(pack):
                tile = lead + local
                for member in range(group):
                    orient = step * group + member
                    prod_re = None
                    prod_im = None
                    for plane in range(planes):
                        fr = field_re_ref[:, lanes(tile * planes + plane)]
                        fi = field_im_ref[:, lanes(tile * planes + plane)]
                        tr = templ_re_ref[:, lanes(orient * planes + plane)]
                        ti = templ_im_ref[:, lanes(orient * planes + plane)]
                        part_re = fr * tr + fi * ti
                        part_im = fi * tr - fr * ti
                        prod_re = part_re if prod_re is None else prod_re + part_re
                        prod_im = part_im if prod_im is None else prod_im + part_im
                    joined.append(
                        jnp.concatenate(
                            [prod_re.astype(jnp.bfloat16), prod_im.astype(jnp.bfloat16)],
                            axis=1,
                        )
                    )
            joined = jnp.concatenate(joined, axis=0)
            first = jnp.dot(joined, mix_ref[...], preferred_element_type=jnp.float32).astype(
                jnp.bfloat16
            )
            stacked = jnp.concatenate(
                [
                    rows_to_blocks(first[:, :length], length),
                    rows_to_blocks(first[:, length:], length),
                ],
                axis=0,
            )
            corr = jnp.dot(back_ref[...], stacked, preferred_element_type=jnp.float32)
            for local in range(pack):
                for member in range(group):
                    orient = step * group + member
                    value = corr[:, lanes(local * group + member)] * scale_ref[orient]
                    best = bests[local]
                    bests[local] = value if best is None else jnp.maximum(best, value)
        for local in range(pack):
            tile = lead + local
            best = bests[local]
            result_ref[...] = best / rms_ref[tile]
            groups = len(out_refs)
            chunk = out_refs[0].shape[1]
            for part in range(groups):
                start = pl.multiple_of(lax.rem(slot_ref[0] + part, groups) * chunk, chunk)
                out_refs[part][tile] = result_ref[pl.ds(start, chunk), :].astype(jnp.bfloat16)


def score_tiles(
    field_real, field_imag, local_rms, templ_real, templ_imag, template_norm, table
):
    length = field_real.shape[0]
    planes = field_real.shape[1] // (local_rms.shape[0] * length)
    scale = (1.0 / template_norm) * (1.0 / (length * length))
    mix = table["mix"]
    back = table["across"]
    tiles = local_rms.shape[0]
    groups = lax.axis_size("orient")
    per_step = tiles
    tile_block = pl.BlockSpec((length, per_step * planes * length), lambda t: (0, t))
    templ_block = pl.BlockSpec(templ_real.shape, lambda t: (0, 0))
    return pl.pallas_call(
        score_kernel,
        grid=(tiles // per_step,),
        out_shape=tuple(
            jax.ShapeDtypeStruct((tiles, length // groups, length), jnp.bfloat16)
            for _ in range(groups)
        ),
        in_specs=[
            pl.BlockSpec(memory_space=pltpu.SMEM),
            pl.BlockSpec(memory_space=pltpu.SMEM),
            tile_block,
            tile_block,
            templ_block,
            templ_block,
            pl.BlockSpec((2 * length, 2 * length), lambda t: (0, 0)),
            pl.BlockSpec((length, 2 * length), lambda t: (0, 0)),
            pl.BlockSpec((per_step, length, length), lambda t: (t, 0, 0)),
        ],
        out_specs=tuple(
            pl.BlockSpec((per_step, length // groups, length), lambda t: (t, 0, 0))
            for _ in range(groups)
        ),
        scratch_shapes=[pltpu.VMEM((length, length), jnp.float32)],
    )(
        lax.axis_index("orient").astype(jnp.int32).reshape(1),
        scale,
        field_real,
        field_imag,
        templ_real,
        templ_imag,
        mix,
        back,
        local_rms,
    )


def orient_max(best):
    groups = lax.axis_size("orient")
    result = best[0]
    for shift in range(1, groups):
        route = [(source, (source + shift) % groups) for source in range(groups)]
        result = jnp.maximum(result, lax.ppermute(best[shift], "orient", route))
    return result


def per_device(tiles, assigned_worker, wedge_mask, template_volume, rotation_samples):
    tile_len = tiles.shape[-1]
    planes = tiles.shape[1]
    home_slots = tiles.shape[0]
    work_slots = home_slots // 2
    box_edge = template_volume.shape[0]
    table = transform_tables(tile_len, box_edge)
    band_sum = band_table(tile_len, box_edge)
    sampled = share_samples(template_volume, rotation_samples)
    partner_tiles = partner(tiles[work_slots:], "slab", 0)
    occupied = assigned_worker >= 0
    own_count = jnp.sum(occupied.astype(jnp.int32))
    field_real, field_imag, local_rms = field_spectra(
        own_count, tiles, partner_tiles, wedge_mask, table, band_sum, box_edge
    )
    sampled, field_real = lax.optimization_barrier((sampled, field_real))
    templ_real, templ_imag, template_norm = make_templates(sampled, box_edge, planes, table)
    best = score_tiles(
        field_real,
        field_imag,
        local_rms,
        templ_real,
        templ_imag,
        template_norm,
        table,
    )
    best_rows = orient_max(best)
    received = partner(best_rows, "slab", 0)
    padded = jnp.concatenate([received, jnp.zeros_like(received)], axis=0)
    returned = lax.dynamic_slice_in_dim(padded, home_slots - own_count, work_slots, axis=0)
    result = jnp.concatenate([best_rows, returned], axis=0)
    return jnp.where(occupied[:, None, None], result, jnp.zeros_like(result))


def solution(mesh):
    return jax.shard_map(
        per_device,
        mesh=mesh,
        in_specs=(P("slab", None, None, None), P("slab"), P(), P(), P("orient", "slab")),
        out_specs=P("slab", "orient", None),
        check_vma=False,
    )
```

```python
import functools
import math

import jax
import ml_dtypes
import numpy as np
import jax.numpy as jnp
from jax import lax
from jax.experimental import pallas as pl
from jax.experimental.pallas import tpu as pltpu
from jax.sharding import PartitionSpec as P


def partner(block, axis, bit):
    count = lax.axis_size(axis)
    route = []
    for low in range(count):
        high = low | 1 << bit
        if high != low and high < count:
            route += [(low, high), (high, low)]
    return lax.ppermute(block, axis, route)


def tables(length):
    counter = np.arange(length, dtype=np.int32)
    angles = (counter[:, None] * counter[None, :] % length).astype(np.float32) * np.float32(
        2.0 * math.pi / length
    )
    wide = angles.astype(np.float64)
    cosine = np.cos(wide).astype(np.float32).astype(ml_dtypes.bfloat16)
    sine = np.sin(wide).astype(np.float32).astype(ml_dtypes.bfloat16)
    return cosine, sine


def band_table(length, box_edge):
    counter = np.arange(length, dtype=np.int32)
    offsets = (counter[None, :] - counter[:, None]) % length
    return jnp.asarray((offsets < box_edge).astype(np.float32))


def transform_tables(length, box_edge):
    cosine, sine = tables(length)
    across = np.concatenate([cosine, -sine], axis=1)
    mix = np.concatenate(
        [np.concatenate([cosine, sine], axis=1), np.concatenate([-sine, cosine], axis=1)], axis=0
    )
    box_across = np.concatenate([cosine[:box_edge], -sine[:box_edge]], axis=1)
    box_down = np.concatenate(
        [
            np.concatenate([cosine[:, :box_edge], sine[:, :box_edge]], axis=1),
            np.concatenate([-sine[:, :box_edge], cosine[:, :box_edge]], axis=1),
        ],
        axis=0,
    )
    return {
        name: jnp.asarray(value)
        for name, value in (
            ("across", across),
            ("mix", mix),
            ("box_across", box_across),
            ("box_down", box_down),
        )
    }


def pick_rows(chosen, source):
    counter = jnp.arange(source.shape[0], dtype=jnp.int32)
    selector = (chosen[:, None] == counter[None, :]).astype(source.dtype)
    flat = source.reshape(source.shape[0], -1)
    picked = jnp.dot(selector, flat, preferred_element_type=jnp.float32).astype(source.dtype)
    return picked.reshape((chosen.shape[0],) + source.shape[1:])


def pick_kernel(index_ref, volume_ref, out_ref, picked_ref, table_ref):
    width = volume_ref.shape[1]
    blocks = table_ref.shape[0] // width
    rows = table_ref.shape[1]
    for block in range(blocks):
        strided = volume_ref[pl.ds(block, rows, stride=blocks), :]
        table_ref[block * width : (block + 1) * width, :] = jnp.transpose(strided).astype(
            jnp.bfloat16
        )
    columns = table_ref.shape[0]
    rows_in_table = table_ref.shape[1]
    lanes = index_ref.shape[1]
    shift = columns.bit_length() - 1

    def body(step, carry):
        index = index_ref[pl.ds(step, 1), :]
        high = jnp.right_shift(index, shift)
        low = jnp.bitwise_and(index, columns - 1)
        row_hot = (lax.broadcasted_iota(jnp.int32, (rows_in_table, lanes), 0) == high).astype(
            jnp.bfloat16
        )
        picked_rows = jnp.dot(table_ref[...], row_hot, preferred_element_type=jnp.float32)
        column_hot = lax.broadcasted_iota(jnp.int32, (columns, lanes), 0) == low
        chosen = jnp.where(column_hot, picked_rows, 0.0)
        picked_ref[pl.ds(step, 1), :] = jnp.sum(chosen, axis=0, keepdims=True)
        return carry

    lax.fori_loop(0, index_ref.shape[0], body, 0, unroll=4)
    picked = picked_ref[...].astype(out_ref.dtype)
    for copy in range(out_ref.shape[0]):
        out_ref[copy] = picked


def sample_template(template_volume, rotation_samples, copies):
    total = template_volume.size
    columns = 512
    edge = template_volume.shape[-1]
    volume = template_volume.reshape(total // edge, edge)
    return pl.pallas_call(
        pick_kernel,
        out_shape=jax.ShapeDtypeStruct((copies,) + rotation_samples.shape, jnp.bfloat16),
        in_specs=[pl.BlockSpec(memory_space=pltpu.VMEM)] * 2,
        out_specs=pl.BlockSpec(memory_space=pltpu.VMEM),
        scratch_shapes=[
            pltpu.VMEM(rotation_samples.shape, jnp.float32),
            pltpu.VMEM((columns, total // columns), jnp.bfloat16),
        ],
    )(rotation_samples, volume)


def share_samples(template_volume, rotation_samples):
    slab_count = lax.axis_size("slab")
    spread = sample_template(template_volume, rotation_samples, slab_count)
    return lax.all_to_all(spread, "slab", 0, 0, tiled=True)


def rows_to_blocks(values, rows):
    count = values.shape[0] // rows
    return jnp.concatenate([values[i * rows : (i + 1) * rows] for i in range(count)], axis=1)


def blocks_to_rows(values, width):
    count = values.shape[1] // width
    return jnp.concatenate(
        [values[:, i * width : (i + 1) * width] for i in range(count)], axis=0
    )


def forward_rows(values, across, down):
    width = across.shape[1] // 2
    height = down.shape[1] // 2
    first = jnp.dot(values, across, preferred_element_type=jnp.float32).astype(jnp.bfloat16)
    stacked = jnp.concatenate(
        [rows_to_blocks(first[:, :width], height), rows_to_blocks(first[:, width:], height)],
        axis=0,
    )
    second = jnp.dot(down, stacked, preferred_element_type=jnp.float32).astype(jnp.bfloat16)
    return second[:width], second[width:]


def inverse_blocks(real_part, imag_part, mix, back):
    length = real_part.shape[0]
    joined = jnp.concatenate(
        [blocks_to_rows(real_part, length), blocks_to_rows(imag_part, length)], axis=1
    )
    first = jnp.dot(joined, mix, preferred_element_type=jnp.float32).astype(jnp.bfloat16)
    stacked = jnp.concatenate(
        [rows_to_blocks(first[:, :length], length), rows_to_blocks(first[:, length:], length)],
        axis=0,
    )
    return jnp.dot(back, stacked, preferred_element_type=jnp.float32)


def template_kernel(values_ref, across_ref, down_ref, real_ref, imag_ref):
    real_part, imag_part = forward_rows(values_ref[...], across_ref[...], down_ref[...])
    real_ref[...] = real_part.astype(jnp.float32)
    imag_ref[...] = imag_part.astype(jnp.float32)


def split_three(values):
    high = values.astype(jnp.bfloat16)
    rest = values - high.astype(jnp.float32)
    middle = rest.astype(jnp.bfloat16)
    low = (rest - middle.astype(jnp.float32)).astype(jnp.bfloat16)
    return (high, middle, low)


def exact_dot(left, right, left_exact):
    total = None
    if left_exact:
        for part in split_three(right):
            term = jnp.dot(left, part, preferred_element_type=jnp.float32)
            total = term if total is None else total + term
    else:
        for part in split_three(left):
            term = jnp.dot(part, right, preferred_element_type=jnp.float32)
            total = term if total is None else total + term
    return total


def field_kernel(
    count_ref, own_ref, other_ref, wedge_ref, across_ref, mix_ref, back_ref, band_ref,
    band_t_ref, real_ref, imag_ref, rms_ref, *, box_edge
):
    home, planes, length, _ = own_ref.shape
    tiles = rms_ref.shape[0]
    maps = tiles * planes
    own_count = count_ref[0]
    picked = []
    for tile in range(tiles):
        source = jnp.clip(tile - own_count, 0, other_ref.shape[0] - 1)
        chosen = jnp.where(tile < own_count, own_ref[tile], other_ref[source])
        picked.append(chosen.reshape(planes * length, length))
    values = jnp.concatenate(picked, axis=0)
    mix = mix_ref[...]
    real_part, imag_part = forward_rows(values, across_ref[...], mix)
    wedge = wedge_ref[...].astype(jnp.float32).astype(jnp.bfloat16)
    wedge = jnp.concatenate([wedge] * maps, axis=1)
    field = inverse_blocks(real_part * wedge, imag_part * wedge, mix, back_ref[...])
    field = (field * (1.0 / (length * length))).astype(jnp.bfloat16)
    square = jnp.square(field.astype(jnp.float32))
    energies = []
    for tile in range(tiles):
        energy = None
        for plane in range(planes):
            index = tile * planes + plane
            part = square[:, index * length : (index + 1) * length]
            energy = part if energy is None else energy + part
        energies.append(energy)
    energy = jnp.concatenate(energies, axis=1)
    summed = exact_dot(band_ref[...], energy, True)
    summed = exact_dot(blocks_to_rows(summed, length), band_t_ref[...], False)
    for tile in range(tiles):
        part = summed[tile * length : (tile + 1) * length]
        rms_ref[tile] = jnp.sqrt(part / (box_edge * box_edge * planes) + 1e-05)
    real_part, imag_part = forward_rows(blocks_to_rows(field, length), across_ref[...], mix)
    real_ref[...] = real_part.astype(jnp.float32)
    imag_ref[...] = imag_part.astype(jnp.float32)


def whole_call(kernel, out_shape, *args):
    return pl.pallas_call(
        kernel,
        out_shape=out_shape,
        in_specs=[pl.BlockSpec(memory_space=pltpu.VMEM)] * len(args),
        out_specs=tuple(pl.BlockSpec(memory_space=pltpu.VMEM) for _ in out_shape),
    )(*args)


def make_templates(sampled, box_edge, planes, table):
    count = sampled.shape[1]
    length = table["across"].shape[0]
    sampled = jnp.transpose(sampled, (1, 0, 2))
    sampled = sampled.reshape(count, planes, box_edge, box_edge)
    template_norm = jnp.sqrt(
        jnp.sum(jnp.square(sampled.astype(jnp.float32)), axis=(1, 2, 3)) + 1e-05
    )
    spec_shape = jax.ShapeDtypeStruct((length, count * planes * length), jnp.float32)
    spec_real, spec_imag = whole_call(
        template_kernel,
        (spec_shape, spec_shape),
        sampled.reshape(count * planes * box_edge, box_edge),
        table["box_across"],
        table["box_down"],
    )
    return (spec_real, spec_imag, template_norm)


def field_spectra(own_count, tiles_own, tiles_other, wedge_mask, table, band_sum, box_edge):
    home, planes, length, _ = tiles_own.shape
    tiles = home // 2
    spec_shape = jax.ShapeDtypeStruct((length, tiles * planes * length), jnp.float32)
    args = (
        own_count.reshape(1),
        tiles_own,
        tiles_other,
        wedge_mask,
        table["across"],
        table["mix"],
        table["across"],
        band_sum.astype(jnp.bfloat16),
        band_sum.T.astype(jnp.bfloat16),
    )
    out_shape = (
        spec_shape,
        spec_shape,
        jax.ShapeDtypeStruct((tiles, length, length), jnp.float32),
    )
    return pl.pallas_call(
        functools.partial(field_kernel, box_edge=box_edge),
        out_shape=out_shape,
        in_specs=[pl.BlockSpec(memory_space=pltpu.SMEM)]
        + [pl.BlockSpec(memory_space=pltpu.VMEM)] * (len(args) - 1),
        out_specs=tuple(pl.BlockSpec(memory_space=pltpu.VMEM) for _ in out_shape),
    )(*args)


def score_kernel(
    slot_ref, scale_ref, field_re_ref, field_im_ref, templ_re_ref, templ_im_ref, mix_ref,
    back_ref, rms_ref, *refs
):
    out_refs = refs[:-1]
    result_ref = refs[-1]
    length = field_re_ref.shape[0]
    per_step = rms_ref.shape[0]
    planes = field_re_ref.shape[1] // (per_step * length)
    count = templ_re_ref.shape[1] // (planes * length)
    group = 16 if count % 16 == 0 else 1

    def lanes(index):
        return slice(index * length, (index + 1) * length)

    pack = 6 if group == count and per_step % 6 == 0 else 1
    for lead in range(0, per_step, pack):
        bests = [None] * pack
        for step in range(count // group):
            joined = []
            for local in range(pack):
                tile = lead + local
                for member in range(group):
                    orient = step * group + member
                    prod_re = None
                    prod_im = None
                    for plane in range(planes):
                        fr = field_re_ref[:, lanes(tile * planes + plane)]
                        fi = field_im_ref[:, lanes(tile * planes + plane)]
                        tr = templ_re_ref[:, lanes(orient * planes + plane)]
                        ti = templ_im_ref[:, lanes(orient * planes + plane)]
                        part_re = fr * tr + fi * ti
                        part_im = fi * tr - fr * ti
                        prod_re = part_re if prod_re is None else prod_re + part_re
                        prod_im = part_im if prod_im is None else prod_im + part_im
                    joined.append(
                        jnp.concatenate(
                            [prod_re.astype(jnp.bfloat16), prod_im.astype(jnp.bfloat16)],
                            axis=1,
                        )
                    )
            joined = jnp.concatenate(joined, axis=0)
            first = jnp.dot(joined, mix_ref[...], preferred_element_type=jnp.float32).astype(
                jnp.bfloat16
            )
            stacked = jnp.concatenate(
                [
                    rows_to_blocks(first[:, :length], length),
                    rows_to_blocks(first[:, length:], length),
                ],
                axis=0,
            )
            corr = jnp.dot(back_ref[...], stacked, preferred_element_type=jnp.float32)
            for local in range(pack):
                for member in range(group):
                    orient = step * group + member
                    value = corr[:, lanes(local * group + member)] * scale_ref[orient]
                    best = bests[local]
                    bests[local] = value if best is None else jnp.maximum(best, value)
        for local in range(pack):
            tile = lead + local
            best = bests[local]
            result_ref[...] = best / rms_ref[tile]
            groups = len(out_refs)
            chunk = out_refs[0].shape[1]
            for part in range(groups):
                start = pl.multiple_of(lax.rem(slot_ref[0] + part, groups) * chunk, chunk)
                out_refs[part][tile] = result_ref[pl.ds(start, chunk), :].astype(jnp.bfloat16)


def score_tiles(
    field_real, field_imag, local_rms, templ_real, templ_imag, template_norm, table
):
    length = field_real.shape[0]
    planes = field_real.shape[1] // (local_rms.shape[0] * length)
    scale = (1.0 / template_norm) * (1.0 / (length * length))
    mix = table["mix"]
    back = table["across"]
    tiles = local_rms.shape[0]
    groups = lax.axis_size("orient")
    per_step = tiles
    tile_block = pl.BlockSpec((length, per_step * planes * length), lambda t: (0, t))
    templ_block = pl.BlockSpec(templ_real.shape, lambda t: (0, 0))
    return pl.pallas_call(
        score_kernel,
        grid=(tiles // per_step,),
        out_shape=tuple(
            jax.ShapeDtypeStruct((tiles, length // groups, length), jnp.bfloat16)
            for _ in range(groups)
        ),
        in_specs=[
            pl.BlockSpec(memory_space=pltpu.SMEM),
            pl.BlockSpec(memory_space=pltpu.SMEM),
            tile_block,
            tile_block,
            templ_block,
            templ_block,
            pl.BlockSpec((2 * length, 2 * length), lambda t: (0, 0)),
            pl.BlockSpec((length, 2 * length), lambda t: (0, 0)),
            pl.BlockSpec((per_step, length, length), lambda t: (t, 0, 0)),
        ],
        out_specs=tuple(
            pl.BlockSpec((per_step, length // groups, length), lambda t: (t, 0, 0))
            for _ in range(groups)
        ),
        scratch_shapes=[pltpu.VMEM((length, length), jnp.float32)],
    )(
        lax.axis_index("orient").astype(jnp.int32).reshape(1),
        scale,
        field_real,
        field_imag,
        templ_real,
        templ_imag,
        mix,
        back,
        local_rms,
    )


def orient_max(best):
    groups = lax.axis_size("orient")
    result = best[0]
    for shift in range(1, groups):
        route = [(source, (source + shift) % groups) for source in range(groups)]
        result = jnp.maximum(result, lax.ppermute(best[shift], "orient", route))
    return result


def per_device(tiles, assigned_worker, wedge_mask, template_volume, rotation_samples):
    tile_len = tiles.shape[-1]
    planes = tiles.shape[1]
    home_slots = tiles.shape[0]
    work_slots = home_slots // 2
    box_edge = template_volume.shape[0]
    table = transform_tables(tile_len, box_edge)
    band_sum = band_table(tile_len, box_edge)
    sampled = share_samples(template_volume, rotation_samples)
    partner_tiles = partner(tiles[work_slots:], "slab", 0)
    occupied = assigned_worker >= 0
    own_count = jnp.sum(occupied.astype(jnp.int32))
    field_real, field_imag, local_rms = field_spectra(
        own_count, tiles, partner_tiles, wedge_mask, table, band_sum, box_edge
    )
    sampled, field_real = lax.optimization_barrier((sampled, field_real))
    templ_real, templ_imag, template_norm = make_templates(sampled, box_edge, planes, table)
    best = score_tiles(
        field_real,
        field_imag,
        local_rms,
        templ_real,
        templ_imag,
        template_norm,
        table,
    )
    best_rows = orient_max(best)
    received = partner(best_rows, "slab", 0)
    padded = jnp.concatenate([received, jnp.zeros_like(received)], axis=0)
    returned = lax.dynamic_slice_in_dim(padded, home_slots - own_count, work_slots, axis=0)
    result = jnp.concatenate([best_rows, returned], axis=0)
    return jnp.where(occupied[:, None, None], result, jnp.zeros_like(result))


def solution(mesh):
    return jax.shard_map(
        per_device,
        mesh=mesh,
        in_specs=(P("slab", None, None, None), P("slab"), P(), P(), P("orient", "slab")),
        out_specs=P("slab", "orient", None),
        check_vma=False,
    )
```

```python
import functools
import math

import jax
import ml_dtypes
import numpy as np
import jax.numpy as jnp
from jax import lax
from jax.experimental import pallas as pl
from jax.experimental.pallas import tpu as pltpu
from jax.sharding import PartitionSpec as P


def partner(block, axis, bit):
    count = lax.axis_size(axis)
    route = []
    for low in range(count):
        high = low | 1 << bit
        if high != low and high < count:
            route += [(low, high), (high, low)]
    return lax.ppermute(block, axis, route)


def tables(length):
    counter = np.arange(length, dtype=np.int32)
    angles = (counter[:, None] * counter[None, :] % length).astype(np.float32) * np.float32(
        2.0 * math.pi / length
    )
    wide = angles.astype(np.float64)
    cosine = np.cos(wide).astype(np.float32).astype(ml_dtypes.bfloat16)
    sine = np.sin(wide).astype(np.float32).astype(ml_dtypes.bfloat16)
    return cosine, sine


def band_table(length, box_edge):
    counter = np.arange(length, dtype=np.int32)
    offsets = (counter[None, :] - counter[:, None]) % length
    return jnp.asarray((offsets < box_edge).astype(np.float32))


def transform_tables(length, box_edge):
    cosine, sine = tables(length)
    across = np.concatenate([cosine, -sine], axis=1)
    mix = np.concatenate(
        [np.concatenate([cosine, sine], axis=1), np.concatenate([-sine, cosine], axis=1)], axis=0
    )
    box_across = np.concatenate([cosine[:box_edge], -sine[:box_edge]], axis=1)
    box_down = np.concatenate(
        [
            np.concatenate([cosine[:, :box_edge], sine[:, :box_edge]], axis=1),
            np.concatenate([-sine[:, :box_edge], cosine[:, :box_edge]], axis=1),
        ],
        axis=0,
    )
    return {
        name: jnp.asarray(value)
        for name, value in (
            ("across", across),
            ("mix", mix),
            ("box_across", box_across),
            ("box_down", box_down),
        )
    }


def pick_rows(chosen, source):
    counter = jnp.arange(source.shape[0], dtype=jnp.int32)
    selector = (chosen[:, None] == counter[None, :]).astype(source.dtype)
    flat = source.reshape(source.shape[0], -1)
    picked = jnp.dot(selector, flat, preferred_element_type=jnp.float32).astype(source.dtype)
    return picked.reshape((chosen.shape[0],) + source.shape[1:])


def pick_kernel(index_ref, volume_ref, out_ref, picked_ref, table_ref):
    width = volume_ref.shape[1]
    blocks = table_ref.shape[0] // width
    rows = table_ref.shape[1]
    for block in range(blocks):
        strided = volume_ref[pl.ds(block, rows, stride=blocks), :]
        table_ref[block * width : (block + 1) * width, :] = jnp.transpose(strided).astype(
            jnp.bfloat16
        )
    columns = table_ref.shape[0]
    rows_in_table = table_ref.shape[1]
    lanes = index_ref.shape[1]
    shift = columns.bit_length() - 1

    def body(step, carry):
        index = index_ref[pl.ds(step, 1), :]
        high = jnp.right_shift(index, shift)
        low = jnp.bitwise_and(index, columns - 1)
        row_hot = (lax.broadcasted_iota(jnp.int32, (rows_in_table, lanes), 0) == high).astype(
            jnp.bfloat16
        )
        picked_rows = jnp.dot(table_ref[...], row_hot, preferred_element_type=jnp.float32)
        column_hot = lax.broadcasted_iota(jnp.int32, (columns, lanes), 0) == low
        chosen = jnp.where(column_hot, picked_rows, 0.0)
        picked_ref[pl.ds(step, 1), :] = jnp.sum(chosen, axis=0, keepdims=True)
        return carry

    lax.fori_loop(0, index_ref.shape[0], body, 0, unroll=True)
    picked = picked_ref[...].astype(out_ref.dtype)
    for copy in range(out_ref.shape[0]):
        out_ref[copy] = picked


def sample_template(template_volume, rotation_samples, copies):
    total = template_volume.size
    columns = 512
    edge = template_volume.shape[-1]
    volume = template_volume.reshape(total // edge, edge)
    return pl.pallas_call(
        pick_kernel,
        out_shape=jax.ShapeDtypeStruct((copies,) + rotation_samples.shape, jnp.bfloat16),
        in_specs=[pl.BlockSpec(memory_space=pltpu.VMEM)] * 2,
        out_specs=pl.BlockSpec(memory_space=pltpu.VMEM),
        scratch_shapes=[
            pltpu.VMEM(rotation_samples.shape, jnp.float32),
            pltpu.VMEM((columns, total // columns), jnp.bfloat16),
        ],
    )(rotation_samples, volume)


def share_samples(template_volume, rotation_samples):
    slab_count = lax.axis_size("slab")
    spread = sample_template(template_volume, rotation_samples, slab_count)
    return lax.all_to_all(spread, "slab", 0, 0, tiled=True)


def rows_to_blocks(values, rows):
    count = values.shape[0] // rows
    return jnp.concatenate([values[i * rows : (i + 1) * rows] for i in range(count)], axis=1)


def blocks_to_rows(values, width):
    count = values.shape[1] // width
    return jnp.concatenate(
        [values[:, i * width : (i + 1) * width] for i in range(count)], axis=0
    )


def forward_rows(values, across, down):
    width = across.shape[1] // 2
    height = down.shape[1] // 2
    first = jnp.dot(values, across, preferred_element_type=jnp.float32).astype(jnp.bfloat16)
    stacked = jnp.concatenate(
        [rows_to_blocks(first[:, :width], height), rows_to_blocks(first[:, width:], height)],
        axis=0,
    )
    second = jnp.dot(down, stacked, preferred_element_type=jnp.float32).astype(jnp.bfloat16)
    return second[:width], second[width:]


def inverse_blocks(real_part, imag_part, mix, back):
    length = real_part.shape[0]
    joined = jnp.concatenate(
        [blocks_to_rows(real_part, length), blocks_to_rows(imag_part, length)], axis=1
    )
    first = jnp.dot(joined, mix, preferred_element_type=jnp.float32).astype(jnp.bfloat16)
    stacked = jnp.concatenate(
        [rows_to_blocks(first[:, :length], length), rows_to_blocks(first[:, length:], length)],
        axis=0,
    )
    return jnp.dot(back, stacked, preferred_element_type=jnp.float32)


def template_kernel(values_ref, across_ref, down_ref, real_ref, imag_ref):
    real_part, imag_part = forward_rows(values_ref[...], across_ref[...], down_ref[...])
    real_ref[...] = real_part.astype(jnp.float32)
    imag_ref[...] = imag_part.astype(jnp.float32)


def split_three(values):
    high = values.astype(jnp.bfloat16)
    rest = values - high.astype(jnp.float32)
    middle = rest.astype(jnp.bfloat16)
    low = (rest - middle.astype(jnp.float32)).astype(jnp.bfloat16)
    return (high, middle, low)


def exact_dot(left, right, left_exact):
    total = None
    if left_exact:
        for part in split_three(right):
            term = jnp.dot(left, part, preferred_element_type=jnp.float32)
            total = term if total is None else total + term
    else:
        for part in split_three(left):
            term = jnp.dot(part, right, preferred_element_type=jnp.float32)
            total = term if total is None else total + term
    return total


def field_kernel(
    count_ref, own_ref, other_ref, wedge_ref, across_ref, mix_ref, back_ref, band_ref,
    band_t_ref, real_ref, imag_ref, rms_ref, *, box_edge
):
    home, planes, length, _ = own_ref.shape
    tiles = rms_ref.shape[0]
    maps = tiles * planes
    own_count = count_ref[0]
    picked = []
    for tile in range(tiles):
        source = jnp.clip(tile - own_count, 0, other_ref.shape[0] - 1)
        chosen = jnp.where(tile < own_count, own_ref[tile], other_ref[source])
        picked.append(chosen.reshape(planes * length, length))
    values = jnp.concatenate(picked, axis=0)
    mix = mix_ref[...]
    real_part, imag_part = forward_rows(values, across_ref[...], mix)
    wedge = wedge_ref[...].astype(jnp.float32).astype(jnp.bfloat16)
    wedge = jnp.concatenate([wedge] * maps, axis=1)
    field = inverse_blocks(real_part * wedge, imag_part * wedge, mix, back_ref[...])
    field = (field * (1.0 / (length * length))).astype(jnp.bfloat16)
    square = jnp.square(field.astype(jnp.float32))
    energies = []
    for tile in range(tiles):
        energy = None
        for plane in range(planes):
            index = tile * planes + plane
            part = square[:, index * length : (index + 1) * length]
            energy = part if energy is None else energy + part
        energies.append(energy)
    energy = jnp.concatenate(energies, axis=1)
    summed = exact_dot(band_ref[...], energy, True)
    summed = exact_dot(blocks_to_rows(summed, length), band_t_ref[...], False)
    for tile in range(tiles):
        part = summed[tile * length : (tile + 1) * length]
        rms_ref[tile] = jnp.sqrt(part / (box_edge * box_edge * planes) + 1e-05)
    real_part, imag_part = forward_rows(blocks_to_rows(field, length), across_ref[...], mix)
    real_ref[...] = real_part.astype(jnp.float32)
    imag_ref[...] = imag_part.astype(jnp.float32)


def whole_call(kernel, out_shape, *args):
    return pl.pallas_call(
        kernel,
        out_shape=out_shape,
        in_specs=[pl.BlockSpec(memory_space=pltpu.VMEM)] * len(args),
        out_specs=tuple(pl.BlockSpec(memory_space=pltpu.VMEM) for _ in out_shape),
    )(*args)


def make_templates(sampled, box_edge, planes, table):
    count = sampled.shape[1]
    length = table["across"].shape[0]
    sampled = jnp.transpose(sampled, (1, 0, 2))
    sampled = sampled.reshape(count, planes, box_edge, box_edge)
    template_norm = jnp.sqrt(
        jnp.sum(jnp.square(sampled.astype(jnp.float32)), axis=(1, 2, 3)) + 1e-05
    )
    spec_shape = jax.ShapeDtypeStruct((length, count * planes * length), jnp.float32)
    spec_real, spec_imag = whole_call(
        template_kernel,
        (spec_shape, spec_shape),
        sampled.reshape(count * planes * box_edge, box_edge),
        table["box_across"],
        table["box_down"],
    )
    return (spec_real, spec_imag, template_norm)


def field_spectra(own_count, tiles_own, tiles_other, wedge_mask, table, band_sum, box_edge):
    home, planes, length, _ = tiles_own.shape
    tiles = home // 2
    spec_shape = jax.ShapeDtypeStruct((length, tiles * planes * length), jnp.float32)
    args = (
        own_count.reshape(1),
        tiles_own,
        tiles_other,
        wedge_mask,
        table["across"],
        table["mix"],
        table["across"],
        band_sum.astype(jnp.bfloat16),
        band_sum.T.astype(jnp.bfloat16),
    )
    out_shape = (
        spec_shape,
        spec_shape,
        jax.ShapeDtypeStruct((tiles, length, length), jnp.float32),
    )
    return pl.pallas_call(
        functools.partial(field_kernel, box_edge=box_edge),
        out_shape=out_shape,
        in_specs=[pl.BlockSpec(memory_space=pltpu.SMEM)]
        + [pl.BlockSpec(memory_space=pltpu.VMEM)] * (len(args) - 1),
        out_specs=tuple(pl.BlockSpec(memory_space=pltpu.VMEM) for _ in out_shape),
    )(*args)


def score_kernel(
    slot_ref, scale_ref, field_re_ref, field_im_ref, templ_re_ref, templ_im_ref, mix_ref,
    back_ref, rms_ref, *refs
):
    out_refs = refs[:-1]
    result_ref = refs[-1]
    length = field_re_ref.shape[0]
    per_step = rms_ref.shape[0]
    planes = field_re_ref.shape[1] // (per_step * length)
    count = templ_re_ref.shape[1] // (planes * length)
    group = 16 if count % 16 == 0 else 1

    def lanes(index):
        return slice(index * length, (index + 1) * length)

    pack = 4 if group == count and per_step % 4 == 0 else 1
    for lead in range(0, per_step, pack):
        bests = [None] * pack
        for step in range(count // group):
            joined = []
            for local in range(pack):
                tile = lead + local
                for member in range(group):
                    orient = step * group + member
                    prod_re = None
                    prod_im = None
                    for plane in range(planes):
                        fr = field_re_ref[:, lanes(tile * planes + plane)]
                        fi = field_im_ref[:, lanes(tile * planes + plane)]
                        tr = templ_re_ref[:, lanes(orient * planes + plane)]
                        ti = templ_im_ref[:, lanes(orient * planes + plane)]
                        part_re = fr * tr + fi * ti
                        part_im = fi * tr - fr * ti
                        prod_re = part_re if prod_re is None else prod_re + part_re
                        prod_im = part_im if prod_im is None else prod_im + part_im
                    joined.append(
                        jnp.concatenate(
                            [prod_re.astype(jnp.bfloat16), prod_im.astype(jnp.bfloat16)],
                            axis=1,
                        )
                    )
            joined = jnp.concatenate(joined, axis=0)
            first = jnp.dot(joined, mix_ref[...], preferred_element_type=jnp.float32).astype(
                jnp.bfloat16
            )
            stacked = jnp.concatenate(
                [
                    rows_to_blocks(first[:, :length], length),
                    rows_to_blocks(first[:, length:], length),
                ],
                axis=0,
            )
            corr = jnp.dot(back_ref[...], stacked, preferred_element_type=jnp.float32)
            for local in range(pack):
                for member in range(group):
                    orient = step * group + member
                    value = corr[:, lanes(local * group + member)] * scale_ref[orient]
                    best = bests[local]
                    bests[local] = value if best is None else jnp.maximum(best, value)
        for local in range(pack):
            tile = lead + local
            best = bests[local]
            result_ref[...] = best / rms_ref[tile]
            groups = len(out_refs)
            chunk = out_refs[0].shape[1]
            for part in range(groups):
                start = pl.multiple_of(lax.rem(slot_ref[0] + part, groups) * chunk, chunk)
                out_refs[part][tile] = result_ref[pl.ds(start, chunk), :].astype(jnp.bfloat16)


def score_tiles(
    field_real, field_imag, local_rms, templ_real, templ_imag, template_norm, table
):
    length = field_real.shape[0]
    planes = field_real.shape[1] // (local_rms.shape[0] * length)
    scale = (1.0 / template_norm) * (1.0 / (length * length))
    mix = table["mix"]
    back = table["across"]
    tiles = local_rms.shape[0]
    groups = lax.axis_size("orient")
    per_step = tiles
    tile_block = pl.BlockSpec((length, per_step * planes * length), lambda t: (0, t))
    templ_block = pl.BlockSpec(templ_real.shape, lambda t: (0, 0))
    return pl.pallas_call(
        score_kernel,
        grid=(tiles // per_step,),
        out_shape=tuple(
            jax.ShapeDtypeStruct((tiles, length // groups, length), jnp.bfloat16)
            for _ in range(groups)
        ),
        in_specs=[
            pl.BlockSpec(memory_space=pltpu.SMEM),
            pl.BlockSpec(memory_space=pltpu.SMEM),
            tile_block,
            tile_block,
            templ_block,
            templ_block,
            pl.BlockSpec((2 * length, 2 * length), lambda t: (0, 0)),
            pl.BlockSpec((length, 2 * length), lambda t: (0, 0)),
            pl.BlockSpec((per_step, length, length), lambda t: (t, 0, 0)),
        ],
        out_specs=tuple(
            pl.BlockSpec((per_step, length // groups, length), lambda t: (t, 0, 0))
            for _ in range(groups)
        ),
        scratch_shapes=[pltpu.VMEM((length, length), jnp.float32)],
    )(
        lax.axis_index("orient").astype(jnp.int32).reshape(1),
        scale,
        field_real,
        field_imag,
        templ_real,
        templ_imag,
        mix,
        back,
        local_rms,
    )


def orient_max(best):
    groups = lax.axis_size("orient")
    result = best[0]
    for shift in range(1, groups):
        route = [(source, (source + shift) % groups) for source in range(groups)]
        result = jnp.maximum(result, lax.ppermute(best[shift], "orient", route))
    return result


def per_device(tiles, assigned_worker, wedge_mask, template_volume, rotation_samples):
    tile_len = tiles.shape[-1]
    planes = tiles.shape[1]
    home_slots = tiles.shape[0]
    work_slots = home_slots // 2
    box_edge = template_volume.shape[0]
    table = transform_tables(tile_len, box_edge)
    band_sum = band_table(tile_len, box_edge)
    sampled = share_samples(template_volume, rotation_samples)
    partner_tiles = partner(tiles[work_slots:], "slab", 0)
    occupied = assigned_worker >= 0
    own_count = jnp.sum(occupied.astype(jnp.int32))
    field_real, field_imag, local_rms = field_spectra(
        own_count, tiles, partner_tiles, wedge_mask, table, band_sum, box_edge
    )
    sampled, field_real = lax.optimization_barrier((sampled, field_real))
    templ_real, templ_imag, template_norm = make_templates(sampled, box_edge, planes, table)
    best = score_tiles(
        field_real,
        field_imag,
        local_rms,
        templ_real,
        templ_imag,
        template_norm,
        table,
    )
    best_rows = orient_max(best)
    received = partner(best_rows, "slab", 0)
    padded = jnp.concatenate([received, jnp.zeros_like(received)], axis=0)
    returned = lax.dynamic_slice_in_dim(padded, home_slots - own_count, work_slots, axis=0)
    result = jnp.concatenate([best_rows, returned], axis=0)
    return jnp.where(occupied[:, None, None], result, jnp.zeros_like(result))


def solution(mesh):
    return jax.shard_map(
        per_device,
        mesh=mesh,
        in_specs=(P("slab", None, None, None), P("slab"), P(), P(), P("orient", "slab")),
        out_specs=P("slab", "orient", None),
        check_vma=False,
    )
```

```python
import functools
import math

import jax
import ml_dtypes
import numpy as np
import jax.numpy as jnp
from jax import lax
from jax.experimental import pallas as pl
from jax.experimental.pallas import tpu as pltpu
from jax.sharding import PartitionSpec as P


def partner(block, axis, bit):
    count = lax.axis_size(axis)
    route = []
    for low in range(count):
        high = low | 1 << bit
        if high != low and high < count:
            route += [(low, high), (high, low)]
    return lax.ppermute(block, axis, route)


def tables(length):
    counter = np.arange(length, dtype=np.int32)
    angles = (counter[:, None] * counter[None, :] % length).astype(np.float32) * np.float32(
        2.0 * math.pi / length
    )
    wide = angles.astype(np.float64)
    cosine = np.cos(wide).astype(np.float32).astype(ml_dtypes.bfloat16)
    sine = np.sin(wide).astype(np.float32).astype(ml_dtypes.bfloat16)
    return cosine, sine


def band_table(length, box_edge):
    counter = np.arange(length, dtype=np.int32)
    offsets = (counter[None, :] - counter[:, None]) % length
    return jnp.asarray((offsets < box_edge).astype(np.float32))


def transform_tables(length, box_edge):
    cosine, sine = tables(length)
    across = np.concatenate([cosine, -sine], axis=1)
    mix = np.concatenate(
        [np.concatenate([cosine, sine], axis=1), np.concatenate([-sine, cosine], axis=1)], axis=0
    )
    box_across = np.concatenate([cosine[:box_edge], -sine[:box_edge]], axis=1)
    box_down = np.concatenate(
        [
            np.concatenate([cosine[:, :box_edge], sine[:, :box_edge]], axis=1),
            np.concatenate([-sine[:, :box_edge], cosine[:, :box_edge]], axis=1),
        ],
        axis=0,
    )
    return {
        name: jnp.asarray(value)
        for name, value in (
            ("across", across),
            ("mix", mix),
            ("box_across", box_across),
            ("box_down", box_down),
        )
    }


def pick_rows(chosen, source):
    counter = jnp.arange(source.shape[0], dtype=jnp.int32)
    selector = (chosen[:, None] == counter[None, :]).astype(source.dtype)
    flat = source.reshape(source.shape[0], -1)
    picked = jnp.dot(selector, flat, preferred_element_type=jnp.float32).astype(source.dtype)
    return picked.reshape((chosen.shape[0],) + source.shape[1:])


def pick_kernel(index_ref, volume_ref, out_ref, picked_ref, table_ref):
    width = volume_ref.shape[1]
    blocks = table_ref.shape[0] // width
    rows = table_ref.shape[1]
    for block in range(blocks):
        strided = volume_ref[pl.ds(block, rows, stride=blocks), :]
        table_ref[block * width : (block + 1) * width, :] = jnp.transpose(strided).astype(
            jnp.bfloat16
        )
    columns = table_ref.shape[0]
    rows_in_table = table_ref.shape[1]
    lanes = index_ref.shape[1]
    shift = columns.bit_length() - 1

    def body(step, carry):
        index = index_ref[pl.ds(step, 1), :]
        high = jnp.right_shift(index, shift)
        low = jnp.bitwise_and(index, columns - 1)
        row_hot = (lax.broadcasted_iota(jnp.int32, (rows_in_table, lanes), 0) == high).astype(
            jnp.bfloat16
        )
        picked_rows = jnp.dot(table_ref[...], row_hot, preferred_element_type=jnp.float32)
        column_hot = lax.broadcasted_iota(jnp.int32, (columns, lanes), 0) == low
        chosen = jnp.where(column_hot, picked_rows, 0.0)
        picked_ref[pl.ds(step, 1), :] = jnp.sum(chosen, axis=0, keepdims=True)
        return carry

    lax.fori_loop(0, index_ref.shape[0], body, 0, unroll=True)
    picked = picked_ref[...].astype(out_ref.dtype)
    for copy in range(out_ref.shape[0]):
        out_ref[copy] = picked


def sample_template(template_volume, rotation_samples, copies):
    total = template_volume.size
    columns = 512
    edge = template_volume.shape[-1]
    volume = template_volume.reshape(total // edge, edge)
    return pl.pallas_call(
        pick_kernel,
        out_shape=jax.ShapeDtypeStruct((copies,) + rotation_samples.shape, jnp.bfloat16),
        in_specs=[pl.BlockSpec(memory_space=pltpu.VMEM)] * 2,
        out_specs=pl.BlockSpec(memory_space=pltpu.VMEM),
        scratch_shapes=[
            pltpu.VMEM(rotation_samples.shape, jnp.float32),
            pltpu.VMEM((columns, total // columns), jnp.bfloat16),
        ],
    )(rotation_samples, volume)


def share_samples(template_volume, rotation_samples):
    slab_count = lax.axis_size("slab")
    spread = sample_template(template_volume, rotation_samples, slab_count)
    return lax.all_to_all(spread, "slab", 0, 0, tiled=True)


def rows_to_blocks(values, rows):
    count = values.shape[0] // rows
    return jnp.concatenate([values[i * rows : (i + 1) * rows] for i in range(count)], axis=1)


def blocks_to_rows(values, width):
    count = values.shape[1] // width
    return jnp.concatenate(
        [values[:, i * width : (i + 1) * width] for i in range(count)], axis=0
    )


def forward_rows(values, across, down):
    width = across.shape[1] // 2
    height = down.shape[1] // 2
    first = jnp.dot(values, across, preferred_element_type=jnp.float32).astype(jnp.bfloat16)
    stacked = jnp.concatenate(
        [rows_to_blocks(first[:, :width], height), rows_to_blocks(first[:, width:], height)],
        axis=0,
    )
    second = jnp.dot(down, stacked, preferred_element_type=jnp.float32).astype(jnp.bfloat16)
    return second[:width], second[width:]


def inverse_blocks(real_part, imag_part, mix, back):
    length = real_part.shape[0]
    joined = jnp.concatenate(
        [blocks_to_rows(real_part, length), blocks_to_rows(imag_part, length)], axis=1
    )
    first = jnp.dot(joined, mix, preferred_element_type=jnp.float32).astype(jnp.bfloat16)
    stacked = jnp.concatenate(
        [rows_to_blocks(first[:, :length], length), rows_to_blocks(first[:, length:], length)],
        axis=0,
    )
    return jnp.dot(back, stacked, preferred_element_type=jnp.float32)


def template_kernel(values_ref, across_ref, down_ref, real_ref, imag_ref):
    real_part, imag_part = forward_rows(values_ref[...], across_ref[...], down_ref[...])
    real_ref[...] = real_part.astype(jnp.float32)
    imag_ref[...] = imag_part.astype(jnp.float32)


def split_three(values):
    high = values.astype(jnp.bfloat16)
    rest = values - high.astype(jnp.float32)
    middle = rest.astype(jnp.bfloat16)
    low = (rest - middle.astype(jnp.float32)).astype(jnp.bfloat16)
    return (high, middle, low)


def exact_dot(left, right, left_exact):
    total = None
    if left_exact:
        for part in split_three(right):
            term = jnp.dot(left, part, preferred_element_type=jnp.float32)
            total = term if total is None else total + term
    else:
        for part in split_three(left):
            term = jnp.dot(part, right, preferred_element_type=jnp.float32)
            total = term if total is None else total + term
    return total


def field_kernel(
    count_ref, own_ref, other_ref, wedge_ref, across_ref, mix_ref, back_ref, band_ref,
    band_t_ref, real_ref, imag_ref, rms_ref, *, box_edge
):
    home, planes, length, _ = own_ref.shape
    tiles = rms_ref.shape[0]
    maps = tiles * planes
    own_count = count_ref[0]
    picked = []
    for tile in range(tiles):
        source = jnp.clip(tile - own_count, 0, other_ref.shape[0] - 1)
        chosen = jnp.where(tile < own_count, own_ref[tile], other_ref[source])
        picked.append(chosen.reshape(planes * length, length))
    values = jnp.concatenate(picked, axis=0)
    mix = mix_ref[...]
    real_part, imag_part = forward_rows(values, across_ref[...], mix)
    wedge = wedge_ref[...].astype(jnp.float32).astype(jnp.bfloat16)
    wedge = jnp.concatenate([wedge] * maps, axis=1)
    field = inverse_blocks(real_part * wedge, imag_part * wedge, mix, back_ref[...])
    field = (field * (1.0 / (length * length))).astype(jnp.bfloat16)
    square = jnp.square(field.astype(jnp.float32))
    energies = []
    for tile in range(tiles):
        energy = None
        for plane in range(planes):
            index = tile * planes + plane
            part = square[:, index * length : (index + 1) * length]
            energy = part if energy is None else energy + part
        energies.append(energy)
    energy = jnp.concatenate(energies, axis=1)
    summed = exact_dot(band_ref[...], energy, True)
    summed = exact_dot(blocks_to_rows(summed, length), band_t_ref[...], False)
    for tile in range(tiles):
        part = summed[tile * length : (tile + 1) * length]
        rms_ref[tile] = 1.0 / jnp.sqrt(part / (box_edge * box_edge * planes) + 1e-05)
    real_part, imag_part = forward_rows(blocks_to_rows(field, length), across_ref[...], mix)
    real_ref[...] = real_part.astype(jnp.float32)
    imag_ref[...] = imag_part.astype(jnp.float32)


def whole_call(kernel, out_shape, *args):
    return pl.pallas_call(
        kernel,
        out_shape=out_shape,
        in_specs=[pl.BlockSpec(memory_space=pltpu.VMEM)] * len(args),
        out_specs=tuple(pl.BlockSpec(memory_space=pltpu.VMEM) for _ in out_shape),
    )(*args)


def make_templates(sampled, box_edge, planes, table):
    count = sampled.shape[1]
    length = table["across"].shape[0]
    sampled = jnp.transpose(sampled, (1, 0, 2))
    sampled = sampled.reshape(count, planes, box_edge, box_edge)
    template_norm = jnp.sqrt(
        jnp.sum(jnp.square(sampled.astype(jnp.float32)), axis=(1, 2, 3)) + 1e-05
    )
    spec_shape = jax.ShapeDtypeStruct((length, count * planes * length), jnp.float32)
    spec_real, spec_imag = whole_call(
        template_kernel,
        (spec_shape, spec_shape),
        sampled.reshape(count * planes * box_edge, box_edge),
        table["box_across"],
        table["box_down"],
    )
    return (spec_real, spec_imag, template_norm)


def field_spectra(own_count, tiles_own, tiles_other, wedge_mask, table, band_sum, box_edge):
    home, planes, length, _ = tiles_own.shape
    tiles = home // 2
    spec_shape = jax.ShapeDtypeStruct((length, tiles * planes * length), jnp.float32)
    args = (
        own_count.reshape(1),
        tiles_own,
        tiles_other,
        wedge_mask,
        table["across"],
        table["mix"],
        table["across"],
        band_sum.astype(jnp.bfloat16),
        band_sum.T.astype(jnp.bfloat16),
    )
    out_shape = (
        spec_shape,
        spec_shape,
        jax.ShapeDtypeStruct((tiles, length, length), jnp.float32),
    )
    return pl.pallas_call(
        functools.partial(field_kernel, box_edge=box_edge),
        out_shape=out_shape,
        in_specs=[pl.BlockSpec(memory_space=pltpu.SMEM)]
        + [pl.BlockSpec(memory_space=pltpu.VMEM)] * (len(args) - 1),
        out_specs=tuple(pl.BlockSpec(memory_space=pltpu.VMEM) for _ in out_shape),
    )(*args)


def score_kernel(
    slot_ref, scale_ref, field_re_ref, field_im_ref, templ_re_ref, templ_im_ref, mix_ref,
    back_ref, rms_ref, *refs
):
    out_refs = refs[:-1]
    result_ref = refs[-1]
    length = field_re_ref.shape[0]
    per_step = rms_ref.shape[0]
    planes = field_re_ref.shape[1] // (per_step * length)
    count = templ_re_ref.shape[1] // (planes * length)
    group = 16 if count % 16 == 0 else 1

    def lanes(index):
        return slice(index * length, (index + 1) * length)

    pack = 4 if group == count and per_step % 4 == 0 else 1
    for lead in range(0, per_step, pack):
        bests = [None] * pack
        for step in range(count // group):
            joined = []
            for local in range(pack):
                tile = lead + local
                for member in range(group):
                    orient = step * group + member
                    prod_re = None
                    prod_im = None
                    for plane in range(planes):
                        fr = field_re_ref[:, lanes(tile * planes + plane)]
                        fi = field_im_ref[:, lanes(tile * planes + plane)]
                        tr = templ_re_ref[:, lanes(orient * planes + plane)]
                        ti = templ_im_ref[:, lanes(orient * planes + plane)]
                        part_re = fr * tr + fi * ti
                        part_im = fi * tr - fr * ti
                        prod_re = part_re if prod_re is None else prod_re + part_re
                        prod_im = part_im if prod_im is None else prod_im + part_im
                    joined.append(
                        jnp.concatenate(
                            [prod_re.astype(jnp.bfloat16), prod_im.astype(jnp.bfloat16)],
                            axis=1,
                        )
                    )
            joined = jnp.concatenate(joined, axis=0)
            first = jnp.dot(joined, mix_ref[...], preferred_element_type=jnp.float32).astype(
                jnp.bfloat16
            )
            stacked = jnp.concatenate(
                [
                    rows_to_blocks(first[:, :length], length),
                    rows_to_blocks(first[:, length:], length),
                ],
                axis=0,
            )
            corr = jnp.dot(back_ref[...], stacked, preferred_element_type=jnp.float32)
            for local in range(pack):
                for member in range(group):
                    orient = step * group + member
                    value = corr[:, lanes(local * group + member)] * scale_ref[orient]
                    best = bests[local]
                    bests[local] = value if best is None else jnp.maximum(best, value)
        for local in range(pack):
            tile = lead + local
            best = bests[local]
            result_ref[...] = best * rms_ref[tile]
            groups = len(out_refs)
            chunk = out_refs[0].shape[1]
            for part in range(groups):
                start = pl.multiple_of(lax.rem(slot_ref[0] + part, groups) * chunk, chunk)
                out_refs[part][tile] = result_ref[pl.ds(start, chunk), :].astype(jnp.bfloat16)


def score_tiles(
    field_real, field_imag, local_rms, templ_real, templ_imag, template_norm, table
):
    length = field_real.shape[0]
    planes = field_real.shape[1] // (local_rms.shape[0] * length)
    scale = (1.0 / template_norm) * (1.0 / (length * length))
    mix = table["mix"]
    back = table["across"]
    tiles = local_rms.shape[0]
    groups = lax.axis_size("orient")
    per_step = tiles
    tile_block = pl.BlockSpec((length, per_step * planes * length), lambda t: (0, t))
    templ_block = pl.BlockSpec(templ_real.shape, lambda t: (0, 0))
    return pl.pallas_call(
        score_kernel,
        grid=(tiles // per_step,),
        out_shape=tuple(
            jax.ShapeDtypeStruct((tiles, length // groups, length), jnp.bfloat16)
            for _ in range(groups)
        ),
        in_specs=[
            pl.BlockSpec(memory_space=pltpu.SMEM),
            pl.BlockSpec(memory_space=pltpu.SMEM),
            tile_block,
            tile_block,
            templ_block,
            templ_block,
            pl.BlockSpec((2 * length, 2 * length), lambda t: (0, 0)),
            pl.BlockSpec((length, 2 * length), lambda t: (0, 0)),
            pl.BlockSpec((per_step, length, length), lambda t: (t, 0, 0)),
        ],
        out_specs=tuple(
            pl.BlockSpec((per_step, length // groups, length), lambda t: (t, 0, 0))
            for _ in range(groups)
        ),
        scratch_shapes=[pltpu.VMEM((length, length), jnp.float32)],
    )(
        lax.axis_index("orient").astype(jnp.int32).reshape(1),
        scale,
        field_real,
        field_imag,
        templ_real,
        templ_imag,
        mix,
        back,
        local_rms,
    )


def orient_max(best):
    groups = lax.axis_size("orient")
    result = best[0]
    for shift in range(1, groups):
        route = [(source, (source + shift) % groups) for source in range(groups)]
        result = jnp.maximum(result, lax.ppermute(best[shift], "orient", route))
    return result


def per_device(tiles, assigned_worker, wedge_mask, template_volume, rotation_samples):
    tile_len = tiles.shape[-1]
    planes = tiles.shape[1]
    home_slots = tiles.shape[0]
    work_slots = home_slots // 2
    box_edge = template_volume.shape[0]
    table = transform_tables(tile_len, box_edge)
    band_sum = band_table(tile_len, box_edge)
    sampled = share_samples(template_volume, rotation_samples)
    partner_tiles = partner(tiles[work_slots:], "slab", 0)
    occupied = assigned_worker >= 0
    own_count = jnp.sum(occupied.astype(jnp.int32))
    field_real, field_imag, local_rms = field_spectra(
        own_count, tiles, partner_tiles, wedge_mask, table, band_sum, box_edge
    )
    sampled, field_real = lax.optimization_barrier((sampled, field_real))
    templ_real, templ_imag, template_norm = make_templates(sampled, box_edge, planes, table)
    best = score_tiles(
        field_real,
        field_imag,
        local_rms,
        templ_real,
        templ_imag,
        template_norm,
        table,
    )
    best_rows = orient_max(best)
    received = partner(best_rows, "slab", 0)
    padded = jnp.concatenate([received, jnp.zeros_like(received)], axis=0)
    returned = lax.dynamic_slice_in_dim(padded, home_slots - own_count, work_slots, axis=0)
    result = jnp.concatenate([best_rows, returned], axis=0)
    return jnp.where(occupied[:, None, None], result, jnp.zeros_like(result))


def solution(mesh):
    return jax.shard_map(
        per_device,
        mesh=mesh,
        in_specs=(P("slab", None, None, None), P("slab"), P(), P(), P("orient", "slab")),
        out_specs=P("slab", "orient", None),
        check_vma=False,
    )
```
